32 devices in a mesh: rep: 8 (over z, core), shard: 4 (over y, x).
Axes of the slice: x: 2, y: 2, z: 4, core: 2. Of those that a mesh axis runs over, the one named last changes fastest.
Arguments:
- tokens: bfloat16 [32, 768, 768], P('rep', 'shard'), may hold values from -6 to 6
- lengths: int32 [32, 4], P('rep'), may hold values from 1 to 192, 752 in all within a row
- cotangent: float32 [32, 768, 768], P('rep', 'shard'), may hold values from -6 to 6
- attention_weight: bfloat16 [768, 2304], P('shard'), may hold values from -0.21875 to 0.21875
- output_weight: bfloat16 [768, 768], P('shard'), may hold values from -5 to 5
- expand_weight: bfloat16 [768, 3072], P('shard'), may hold values from -0.21875 to 0.21875
- contract_weight: bfloat16 [3072, 768], P('shard'), may hold values from -0.21875 to 0.21875
- first_gain: bfloat16 [768], P('shard'), may hold values from 0.25 to 1.75
- first_shift: bfloat16 [768], P('shard'), may hold values from -3 to 3
- query_bias: bfloat16 [768], P('shard'), may hold values from -3 to 3
- value_bias: bfloat16 [768], P('shard'), may hold values from -3 to 3
- output_bias: bfloat16 [768], P('shard'), may hold values from -3 to 3
- second_gain: bfloat16 [768], P('shard'), may hold values from 0.25 to 1.75
- second_shift: bfloat16 [768], P('shard'), may hold values from -3 to 3
- expand_bias: bfloat16 [3072], P('shard'), may hold values from -3 to 3
- contract_bias: bfloat16 [768], P('shard'), may hold values from -3 to 3
Outputs:
- block_output: float32 [32, 768, 768], P('rep', 'shard')
- input_grad: float32 [32, 768, 768], P('rep', 'shard')
- attention_grad: float32 [768, 2304], P('shard')
- output_grad: float32 [768, 768], P('shard')
- expand_grad: float32 [768, 3072], P('shard')
- contract_grad: float32 [3072, 768], P('shard')
- first_gain_grad: float32 [768], P('shard')
- first_shift_grad: float32 [768], P('shard')
- query_bias_grad: float32 [768], P('shard')
- value_bias_grad: float32 [768], P('shard')
- output_bias_grad: float32 [768], P('shard')
- second_gain_grad: float32 [768], P('shard')
- second_shift_grad: float32 [768], P('shard')
- expand_bias_grad: float32 [3072], P('shard')
- contract_bias_grad: float32 [768], P('shard')
The draws below stay inside these ranges and needn't reach their ends.
Inputs may be any that keep to these rules, and one draw needn't show every extreme that they name: `lengths`: each row sums to 752; every block has at least one live frame and some block of each row has exactly 192.
All inputs are finite; a program needn't handle non-finite values.
Results may differ from the reference program's by a relative error of at most 0.012.
The reference program's roundings to bfloat16 on the way count: a program that leaves them out, or rounds other values in their place, can miss the bound.
Values may be sent and summed in bfloat16 or wider, within the bound.
No kernel may reach another device: no remote copies, remote signals or barrier semaphores. Data moves between devices by JAX's collectives and lax.ppermute only.
A program may use at most 256 MiB of HBM per device.

```python
import math
import jax
import jax.numpy as jnp
import numpy as np
from jax import lax

D = 768
HEADS = 12
HEAD = 64
FF = 3072
SLOT = 192
FRAMES = 768
CLIP = 752
CLIPS = 32
N_SHARD = 4


def shard_levels(own_key, dims, split, smallest, high):
    loudness = 1.0
    for axis_at, shards_of in split:
        draws = jax.random.uniform(jax.random.fold_in(jax.random.fold_in(own_key, 6), axis_at), (shards_of,), jnp.float32, smallest / len(split), high / len(split))
        loudness = loudness * jnp.repeat(jnp.exp(draws), dims[axis_at] // shards_of).reshape((-1,) + (1,) * (len(dims) - 1 - axis_at))
    return loudness


def profile(count, total, limit, skew):
    portions = [(1 << 20) // math.isqrt(standing ** skew) + 1 for standing in range(2, count + 1)]
    spare, counts = total - limit - (count - 1), [1] * (count - 1)
    while spare > 0:
        candidates = [i for i in range(count - 1) if counts[i] < limit]
        mass, remaining = sum([portions[i] for i in candidates]), spare
        for i in candidates:
            addition = min(limit - counts[i], max(1, remaining * portions[i] // mass), spare)
            counts[i] = counts[i] + addition
            spare = spare - addition
    return np.array([limit] + counts)


def ragged(key, count, total, most, slope):
    if count == 2:
        one = jax.random.randint(key, (), max(1, total - most), min(most, total - 1) + 1)
        return jnp.stack([one, total - one])
    tallies = jnp.asarray(profile(count, total, most, slope), jnp.int32)
    twos = (count - 1) // 2
    giver, taker = tallies[1:1 + 2 * twos:2], tallies[2:2 + 2 * twos:2]
    slack = jnp.minimum(giver - 1, most - taker)
    passed = jax.random.randint(jax.random.fold_in(key, 1), (twos,), 0, 1 << 20) % (slack + 1)
    tallies = tallies.at[1:1 + 2 * twos:2].set(giver - passed).at[2:2 + 2 * twos:2].set(taker + passed)
    return tallies[jax.random.permutation(jax.random.fold_in(key, 2), count)]


def noise(own_key, extent, deviation, most, cuts=(), kind=jnp.bfloat16):
    level = shard_levels(own_key, extent, cuts, -0.22, 0.18) if cuts else 1.0
    drawn = jax.random.normal(own_key, extent, jnp.float32) * deviation * level
    return jnp.minimum(jnp.maximum(drawn, -most), most).astype(kind)


def setup_inputs(seed: int = 0) -> dict:
    splits = jax.random.split(jax.random.key(seed), 17)
    return {
        "tokens": noise(splits[0], (CLIPS, FRAMES, D), 1.0, 6.0, ((0, 8), (1, 4))),
        "lengths": jax.vmap(lambda own: ragged(own, N_SHARD, CLIP, SLOT, 1))(jax.random.split(splits[1], CLIPS)).reshape((CLIPS, N_SHARD)).astype(jnp.int32),
        "cotangent": noise(splits[2], (CLIPS, FRAMES, D), 1.0, 6.0, ((0, 8), (1, 4)), jnp.float32),
        "attention_weight": noise(splits[3], (D, 3 * D), D ** -0.5, 0.21875, ((0, 4),)),
        "output_weight": noise(splits[4], (D, D), (FRAMES ** 0.5 * D ** -0.5), 5.0, ((0, 4),)),
        "expand_weight": noise(splits[5], (D, FF), D ** -0.5, 0.21875, ((0, 4),)),
        "contract_weight": noise(splits[6], (FF, D), (FF // 4) ** -0.5, 0.21875, ((0, 4),)),
        "first_gain": jnp.clip(1.0 + 0.15 * jax.random.normal(splits[7], (D,), jnp.float32), 0.25, 1.75).astype(jnp.bfloat16),
        "first_shift": noise(splits[8], (D,), 0.5, 3.0, ((0, 4),)),
        "query_bias": noise(splits[9], (D,), 0.5, 3.0, ((0, 4),)),
        "value_bias": noise(splits[10], (D,), 0.5, 3.0, ((0, 4),)),
        "output_bias": noise(splits[11], (D,), 0.5, 3.0, ((0, 4),)),
        "second_gain": jnp.clip(1.0 + 0.15 * jax.random.normal(splits[12], (D,), jnp.float32), 0.25, 1.75).astype(jnp.bfloat16),
        "second_shift": noise(splits[13], (D,), 0.5, 3.0, ((0, 4),)),
        "expand_bias": noise(splits[14], (FF,), 0.5, 3.0, ((0, 4),)),
        "contract_bias": noise(splits[15], (D,), 0.5, 3.0, ((0, 4),)),
    }


EPSILON = 1e-05
NEGATIVE = -1e+30

def norm_forward(values, gain, shift):
    centred = values - lax.optimization_barrier(jnp.mean(values, axis=-1, keepdims=True))
    inverse = lax.rsqrt(lax.optimization_barrier(jnp.mean(centred * centred, axis=-1, keepdims=True)) + EPSILON)
    normed = centred * inverse
    return (normed, inverse, (normed * gain + shift).astype(jnp.bfloat16))

def norm_backward(upstream, normed, inverse, gain):
    scaled = upstream * gain
    return inverse * (scaled - lax.optimization_barrier(jnp.mean(scaled, axis=-1, keepdims=True)) - normed * lax.optimization_barrier(jnp.mean(scaled * normed, axis=-1, keepdims=True)))

def gelu_slope(values):
    return 0.5 * (1.0 + jax.scipy.special.erf(values * 0.7071067811865476)) + values * jnp.exp(-0.5 * values * values) * 0.3989422804014327

def clip_pass(tokens_clip, lengths_clip, cotangent_clip, weights):
    attention_weight, output_weight, expand_weight, contract_weight, first_gain, first_shift, query_bias, value_bias, output_bias, second_gain, second_shift, expand_bias, contract_bias = weights
    frame_count, width = tokens_clip.shape
    slot_count = frame_count // lengths_clip.shape[0]
    live = (jnp.arange(slot_count)[None, :] < lengths_clip[:, None]).reshape(frame_count)
    scale = HEAD ** (-0.5)
    inputs = tokens_clip.astype(jnp.float32)
    first_normed, first_inverse, first_act = norm_forward(inputs, first_gain, first_shift)
    mixed = jnp.dot(first_act, attention_weight, preferred_element_type=jnp.float32)
    mixed = mixed + jnp.concatenate([query_bias, jnp.zeros_like(query_bias), value_bias])
    mixed_low = mixed.astype(jnp.bfloat16)
    queries = mixed_low[:, :width].astype(jnp.float32).reshape(frame_count, HEADS, HEAD)
    keys = mixed_low[:, width:2 * width].astype(jnp.float32).reshape(frame_count, HEADS, HEAD)
    values = mixed_low[:, 2 * width:].astype(jnp.float32).reshape(frame_count, HEADS, HEAD)
    scores = jnp.einsum('qhd,khd->hqk', queries, keys) * scale
    scores = jnp.where(live[None, None, :], scores, NEGATIVE)
    highest = lax.optimization_barrier(jnp.max(scores, axis=-1, keepdims=True))
    logsum = highest + jnp.log(lax.optimization_barrier(jnp.sum(jnp.exp(scores - highest), axis=-1, keepdims=True)))
    probs = jnp.exp(scores - logsum)
    probs_low = probs.astype(jnp.bfloat16)
    attended = jnp.einsum('hqk,khd->qhd', probs_low.astype(jnp.float32), values).reshape(frame_count, width).astype(jnp.bfloat16)
    residual = inputs + jnp.dot(attended, output_weight, preferred_element_type=jnp.float32) + output_bias
    second_normed, second_inverse, second_act = norm_forward(residual, second_gain, second_shift)
    pre = jnp.dot(second_act, expand_weight, preferred_element_type=jnp.float32) + expand_bias
    hidden_act = jax.nn.gelu(pre, approximate=False).astype(jnp.bfloat16)
    block_output = residual + jnp.dot(hidden_act, contract_weight, preferred_element_type=jnp.float32) + contract_bias
    error = cotangent_clip * live[:, None].astype(jnp.float32)
    error_low = error.astype(jnp.bfloat16)
    contract_bias_grad = lax.optimization_barrier(jnp.sum(error, axis=0))
    contract_grad = jnp.dot(hidden_act.T, error_low, preferred_element_type=jnp.float32)
    dpre = jnp.dot(error_low, contract_weight.T, preferred_element_type=jnp.float32) * gelu_slope(pre)
    expand_bias_grad = lax.optimization_barrier(jnp.sum(dpre, axis=0))
    dpre_low = dpre.astype(jnp.bfloat16)
    expand_grad = jnp.dot(second_act.T, dpre_low, preferred_element_type=jnp.float32)
    dsecond = jnp.dot(dpre_low, expand_weight.T, preferred_element_type=jnp.float32)
    second_gain_grad = lax.optimization_barrier(jnp.sum(dsecond * second_normed, axis=0))
    second_shift_grad = lax.optimization_barrier(jnp.sum(dsecond, axis=0))
    dresidual = error + norm_backward(dsecond, second_normed, second_inverse, second_gain)
    output_bias_grad = lax.optimization_barrier(jnp.sum(dresidual, axis=0))
    dresidual_low = dresidual.astype(jnp.bfloat16)
    output_grad = jnp.dot(attended.T, dresidual_low, preferred_element_type=jnp.float32)
    dattended = jnp.dot(dresidual_low, output_weight.T, preferred_element_type=jnp.float32).astype(jnp.bfloat16)
    dattended_heads = dattended.astype(jnp.float32).reshape(frame_count, HEADS, HEAD)
    attended_heads = attended.astype(jnp.float32).reshape(frame_count, HEADS, HEAD)
    delta = lax.optimization_barrier(jnp.sum(dattended_heads * attended_heads, axis=-1))
    dprob = jnp.einsum('qhd,khd->hqk', dattended_heads, values)
    dscore = (probs * (dprob - delta.T[:, :, None]) * scale).astype(jnp.bfloat16).astype(jnp.float32)
    dqueries = jnp.einsum('hqk,khd->qhd', dscore, keys).reshape(frame_count, width)
    dkeys = jnp.einsum('hqk,qhd->khd', dscore, queries).reshape(frame_count, width)
    dvalues = jnp.einsum('hqk,qhd->khd', probs_low.astype(jnp.float32), dattended_heads).reshape(frame_count, width)
    dmixed = jnp.concatenate([dqueries, dkeys, dvalues], axis=1)
    query_bias_grad = lax.optimization_barrier(jnp.sum(dqueries, axis=0))
    value_bias_grad = lax.optimization_barrier(jnp.sum(dvalues, axis=0))
    dmixed_low = dmixed.astype(jnp.bfloat16)
    attention_grad = jnp.dot(first_act.T, dmixed_low, preferred_element_type=jnp.float32)
    dfirst = jnp.dot(dmixed_low, attention_weight.T, preferred_element_type=jnp.float32)
    first_gain_grad = lax.optimization_barrier(jnp.sum(dfirst * first_normed, axis=0))
    first_shift_grad = lax.optimization_barrier(jnp.sum(dfirst, axis=0))
    input_grad = dresidual + norm_backward(dfirst, first_normed, first_inverse, first_gain)
    grads = (attention_grad, output_grad, expand_grad, contract_grad, first_gain_grad, first_shift_grad, query_bias_grad, value_bias_grad, output_bias_grad, second_gain_grad, second_shift_grad, expand_bias_grad, contract_bias_grad)
    return (block_output, input_grad, grads)

def reference(tokens, lengths, cotangent, attention_weight, output_weight, expand_weight, contract_weight, first_gain, first_shift, query_bias, value_bias, output_bias, second_gain, second_shift, expand_bias, contract_bias):
    vectors = (first_gain, first_shift, query_bias, value_bias, output_bias, second_gain, second_shift, expand_bias, contract_bias)
    weights = (attention_weight, output_weight, expand_weight, contract_weight) + tuple((entry.astype(jnp.float32) for entry in vectors))
    initial = tuple((jnp.zeros(entry.shape, jnp.float32) for entry in weights))

    def advance(carry, items):
        tokens_clip, lengths_clip, cotangent_clip = items
        block_output, input_grad, grads = clip_pass(tokens_clip, lengths_clip, cotangent_clip, weights)
        return (tuple((total + grad for total, grad in zip(carry, grads))), (block_output, input_grad))
    totals, (outputs, input_grads) = lax.scan(advance, initial, (tokens, lengths, cotangent))
    return (outputs, input_grads, totals[0], totals[1], totals[2], totals[3], totals[4], totals[5], totals[6], totals[7], totals[8], totals[9], totals[10], totals[11], totals[12])
```

```python
import jax
import jax.numpy as jnp
from jax import lax
from jax.sharding import PartitionSpec as P

HEADS = 12
HEAD = 64


EPSILON = 1e-05
NEGATIVE = -1e30


def norm_forward(values, gain, shift):
    centred = values - jnp.mean(values, axis=-1, keepdims=True)
    inverse = lax.rsqrt(jnp.mean(centred * centred, axis=-1, keepdims=True) + EPSILON)
    normed = centred * inverse
    return (normed, inverse, (normed * gain + shift).astype(jnp.bfloat16))


def norm_backward(upstream, normed, inverse, gain):
    scaled = upstream * gain
    return inverse * (
        scaled
        - jnp.mean(scaled, axis=-1, keepdims=True)
        - normed * jnp.mean(scaled * normed, axis=-1, keepdims=True)
    )


def gelu_slope(values):
    return (
        0.5 * (1.0 + jax.scipy.special.erf(values * 0.7071067811865476))
        + values * jnp.exp(-0.5 * values * values) * 0.3989422804014327
    )


def inner_rows(left, right):
    return lax.dot_general(
        left, right, (((0,), (0,)), ((), ())), preferred_element_type=jnp.float32
    )


def heads_view(matrix):
    return matrix.reshape(matrix.shape[0], HEADS, HEAD)


def score_block(query_rows, key_rows, key_live):
    scores = jnp.einsum(
        "qhd,khd->hqk",
        heads_view(query_rows),
        heads_view(key_rows),
        preferred_element_type=jnp.float32,
    ) * HEAD ** (-0.5)
    return jnp.where(key_live[None, None, :], scores, NEGATIVE)


def attend_clip(items):
    query_rows, pair_rows, key_live = items
    width = query_rows.shape[1]
    scores = score_block(query_rows, pair_rows[:, :width], key_live)
    highest = jnp.max(scores, axis=-1, keepdims=True)
    logsum = highest + jnp.log(jnp.sum(jnp.exp(scores - highest), axis=-1, keepdims=True))
    probs_low = jnp.exp(scores - logsum).astype(jnp.bfloat16)
    attended = jnp.einsum(
        "hqk,khd->qhd",
        probs_low,
        heads_view(pair_rows[:, width:]),
        preferred_element_type=jnp.float32,
    )
    return (attended.reshape(query_rows.shape[0], width).astype(jnp.bfloat16), logsum[:, :, 0].T)


def score_grads(query_rows, dattended, logsum, delta, pair_rows, key_live):
    width = query_rows.shape[1]
    scores = score_block(query_rows, pair_rows[:, :width], key_live)
    probs = jnp.exp(scores - logsum.T[:, :, None])
    dprob = jnp.einsum(
        "qhd,khd->hqk",
        heads_view(dattended),
        heads_view(pair_rows[:, width:]),
        preferred_element_type=jnp.float32,
    )
    dscore = (probs * (dprob - delta.T[:, :, None]) * HEAD ** (-0.5)).astype(jnp.bfloat16)
    return (probs.astype(jnp.bfloat16), dscore)


def both_grads(items):
    query_rows, dattended, logsum, delta, pair_rows, key_live = items
    width = query_rows.shape[1]
    probs_low, dscore = score_grads(query_rows, dattended, logsum, delta, pair_rows, key_live)
    dqueries = jnp.einsum(
        "hqk,khd->qhd", dscore, heads_view(pair_rows[:, :width]), preferred_element_type=jnp.float32
    ).reshape(query_rows.shape[0], width)
    dkeys = jnp.einsum(
        "hqk,qhd->khd", dscore, heads_view(query_rows), preferred_element_type=jnp.float32
    )
    dvalues = jnp.einsum(
        "hqk,qhd->khd", probs_low, heads_view(dattended), preferred_element_type=jnp.float32
    )
    key_count = pair_rows.shape[0]
    return (
        dqueries,
        jnp.concatenate(
            [dkeys.reshape(key_count, width), dvalues.reshape(key_count, width)], axis=1
        ),
    )


def local(
    tokens,
    lengths,
    cotangent,
    attention_weight,
    output_weight,
    expand_weight,
    contract_weight,
    first_gain,
    first_shift,
    query_bias,
    value_bias,
    output_bias,
    second_gain,
    second_shift,
    expand_bias,
    contract_bias,
):
    clip_count, slot_count, width = tokens.shape
    parts = lax.axis_size("shard")
    frame_count = slot_count * parts
    place = lax.axis_index("shard")
    row_total = clip_count * slot_count
    gathered = (
        lax.all_gather(attention_weight, "shard", axis=0, tiled=True),
        lax.all_gather(output_weight, "shard", axis=0, tiled=True),
        lax.all_gather(expand_weight, "shard", axis=0, tiled=True),
        lax.all_gather(contract_weight, "shard", axis=0, tiled=True),
        lax.all_gather(first_gain, "shard", axis=0, tiled=True),
        lax.all_gather(first_shift, "shard", axis=0, tiled=True),
        lax.all_gather(query_bias, "shard", axis=0, tiled=True),
        lax.all_gather(value_bias, "shard", axis=0, tiled=True),
        lax.all_gather(output_bias, "shard", axis=0, tiled=True),
        lax.all_gather(second_gain, "shard", axis=0, tiled=True),
        lax.all_gather(second_shift, "shard", axis=0, tiled=True),
        lax.all_gather(expand_bias, "shard", axis=0, tiled=True),
        lax.all_gather(contract_bias, "shard", axis=0, tiled=True),
    )
    vectors = [entry.astype(jnp.float32) for entry in gathered[4:]]
    own_length = jnp.sum(jnp.where(jnp.arange(parts)[None, :] == place, lengths, 0), axis=1)
    row_live = jnp.arange(slot_count)[None, :] < own_length[:, None]
    key_live = (jnp.arange(slot_count)[None, None, :] < lengths[:, :, None]).reshape(
        clip_count, frame_count
    )
    inputs = tokens.reshape(row_total, width).astype(jnp.float32)
    first_normed, first_inverse, first_act = norm_forward(inputs, vectors[0], vectors[1])
    mixed = jnp.dot(first_act, gathered[0], preferred_element_type=jnp.float32)
    mixed = mixed + jnp.concatenate([vectors[2], jnp.zeros_like(vectors[2]), vectors[3]])
    mixed_low = mixed.astype(jnp.bfloat16)
    query_rows = mixed_low[:, :width].reshape(clip_count, slot_count, width)
    pair_own = mixed_low[:, width:].reshape(clip_count, slot_count, 2 * width)
    pair_all = lax.all_gather(pair_own, "shard", axis=1, tiled=True)
    attended, logsum = lax.map(attend_clip, (query_rows, pair_all, key_live))
    attended_flat = attended.reshape(row_total, width)
    residual = (
        inputs
        + jnp.dot(attended_flat, gathered[1], preferred_element_type=jnp.float32)
        + vectors[4]
    )
    second_normed, second_inverse, second_act = norm_forward(residual, vectors[5], vectors[6])
    pre = jnp.dot(second_act, gathered[2], preferred_element_type=jnp.float32) + vectors[7]
    hidden_act = jax.nn.gelu(pre, approximate=False).astype(jnp.bfloat16)
    block_output = (
        residual + jnp.dot(hidden_act, gathered[3], preferred_element_type=jnp.float32) + vectors[8]
    )
    backward = (
        lax.all_gather(attention_weight, "shard", axis=0, tiled=True),
        lax.all_gather(output_weight, "shard", axis=0, tiled=True),
        lax.all_gather(expand_weight, "shard", axis=0, tiled=True),
        lax.all_gather(contract_weight, "shard", axis=0, tiled=True),
        lax.all_gather(first_gain, "shard", axis=0, tiled=True),
        lax.all_gather(first_shift, "shard", axis=0, tiled=True),
        lax.all_gather(query_bias, "shard", axis=0, tiled=True),
        lax.all_gather(value_bias, "shard", axis=0, tiled=True),
        lax.all_gather(output_bias, "shard", axis=0, tiled=True),
        lax.all_gather(second_gain, "shard", axis=0, tiled=True),
        lax.all_gather(second_shift, "shard", axis=0, tiled=True),
        lax.all_gather(expand_bias, "shard", axis=0, tiled=True),
        lax.all_gather(contract_bias, "shard", axis=0, tiled=True),
    )
    back_vectors = [entry.astype(jnp.float32) for entry in backward[4:]]
    error = cotangent.reshape(row_total, width) * row_live.reshape(row_total, 1).astype(jnp.float32)
    error_low = error.astype(jnp.bfloat16)
    contract_bias_grad = jnp.sum(error, axis=0)
    contract_grad = inner_rows(hidden_act, error_low)
    dpre = lax.dot_general(
        error_low, backward[3], (((1,), (1,)), ((), ())), preferred_element_type=jnp.float32
    ) * gelu_slope(pre)
    expand_bias_grad = jnp.sum(dpre, axis=0)
    dpre_low = dpre.astype(jnp.bfloat16)
    expand_grad = inner_rows(second_act, dpre_low)
    dsecond = lax.dot_general(
        dpre_low, backward[2], (((1,), (1,)), ((), ())), preferred_element_type=jnp.float32
    )
    second_gain_grad = jnp.sum(dsecond * second_normed, axis=0)
    second_shift_grad = jnp.sum(dsecond, axis=0)
    dresidual = error + norm_backward(dsecond, second_normed, second_inverse, back_vectors[5])
    output_bias_grad = jnp.sum(dresidual, axis=0)
    dresidual_low = dresidual.astype(jnp.bfloat16)
    output_grad = inner_rows(attended_flat, dresidual_low)
    dattended = lax.dot_general(
        dresidual_low, backward[1], (((1,), (1,)), ((), ())), preferred_element_type=jnp.float32
    ).astype(jnp.bfloat16)
    delta = jnp.sum(
        heads_view(dattended.astype(jnp.float32)) * heads_view(attended_flat.astype(jnp.float32)),
        axis=-1,
    )
    delta = delta.reshape(clip_count, slot_count, HEADS)
    dattended_clips = dattended.reshape(clip_count, slot_count, width)
    dqueries, pair_terms = lax.map(
        both_grads, (query_rows, dattended_clips, logsum, delta, pair_all, key_live)
    )
    pair_grads = lax.psum_scatter(pair_terms, "shard", scatter_dimension=1, tiled=True)
    dqueries_flat = dqueries.reshape(row_total, width)
    pair_flat = pair_grads.reshape(row_total, 2 * width)
    dmixed = jnp.concatenate([dqueries_flat, pair_flat], axis=1)
    query_bias_grad = jnp.sum(dqueries_flat, axis=0)
    value_bias_grad = jnp.sum(pair_flat[:, width:], axis=0)
    dmixed_low = dmixed.astype(jnp.bfloat16)
    attention_grad = inner_rows(first_act, dmixed_low)
    dfirst = lax.dot_general(
        dmixed_low, backward[0], (((1,), (1,)), ((), ())), preferred_element_type=jnp.float32
    )
    first_gain_grad = jnp.sum(dfirst * first_normed, axis=0)
    first_shift_grad = jnp.sum(dfirst, axis=0)
    input_grad = dresidual + norm_backward(dfirst, first_normed, first_inverse, back_vectors[0])
    shares = (
        lax.psum_scatter(attention_grad, "shard", scatter_dimension=0, tiled=True),
        lax.psum_scatter(output_grad, "shard", scatter_dimension=0, tiled=True),
        lax.psum_scatter(expand_grad, "shard", scatter_dimension=0, tiled=True),
        lax.psum_scatter(contract_grad, "shard", scatter_dimension=0, tiled=True),
        lax.psum_scatter(first_gain_grad, "shard", scatter_dimension=0, tiled=True),
        lax.psum_scatter(first_shift_grad, "shard", scatter_dimension=0, tiled=True),
        lax.psum_scatter(query_bias_grad, "shard", scatter_dimension=0, tiled=True),
        lax.psum_scatter(value_bias_grad, "shard", scatter_dimension=0, tiled=True),
        lax.psum_scatter(output_bias_grad, "shard", scatter_dimension=0, tiled=True),
        lax.psum_scatter(second_gain_grad, "shard", scatter_dimension=0, tiled=True),
        lax.psum_scatter(second_shift_grad, "shard", scatter_dimension=0, tiled=True),
        lax.psum_scatter(expand_bias_grad, "shard", scatter_dimension=0, tiled=True),
        lax.psum_scatter(contract_bias_grad, "shard", scatter_dimension=0, tiled=True),
    )
    totals = lax.psum(
        (
            shares[0],
            shares[1],
            shares[2],
            shares[3],
            shares[4],
            shares[5],
            shares[6],
            shares[7],
            shares[8],
            shares[9],
            shares[10],
            shares[11],
            shares[12],
        ),
        "rep",
    )
    return (
        block_output.reshape(clip_count, slot_count, width),
        input_grad.reshape(clip_count, slot_count, width),
        totals[0],
        totals[1],
        totals[2],
        totals[3],
        totals[4],
        totals[5],
        totals[6],
        totals[7],
        totals[8],
        totals[9],
        totals[10],
        totals[11],
        totals[12],
    )


def clip_layer(tokens, lengths, cotangent, weights, vectors):
    attention_weight, output_weight, expand_weight, contract_weight = weights
    (first_gain, first_shift, query_bias, value_bias, output_bias, second_gain, second_shift,
     expand_bias, contract_bias) = vectors
    clip_count, frame_count, width = tokens.shape
    block_count = lengths.shape[1]
    slot_count = frame_count // block_count
    rows = clip_count * frame_count
    live = (jnp.arange(slot_count)[None, None, :] < lengths[:, :, None]).reshape(clip_count, frame_count)
    scale = HEAD ** (-0.5)
    inputs = tokens.reshape(rows, width).astype(jnp.float32)
    first_normed, first_inverse, first_act = norm_forward(inputs, first_gain, first_shift)
    mixed = jnp.dot(first_act, attention_weight, preferred_element_type=jnp.float32)
    mixed = mixed + jnp.concatenate([query_bias, jnp.zeros_like(query_bias), value_bias])
    mixed_low = mixed.astype(jnp.bfloat16).reshape(clip_count, frame_count, 3, HEADS, HEAD)
    queries = mixed_low[:, :, 0]
    keys = mixed_low[:, :, 1]
    values = mixed_low[:, :, 2]
    scores = jnp.einsum("cqhd,ckhd->chqk", queries, keys, preferred_element_type=jnp.float32) * scale
    scores = jnp.where(live[:, None, None, :], scores, NEGATIVE)
    highest = jnp.max(scores, axis=-1, keepdims=True)
    logsum = highest + jnp.log(jnp.sum(jnp.exp(scores - highest), axis=-1, keepdims=True))
    probs = jnp.exp(scores - logsum)
    probs_low = probs.astype(jnp.bfloat16)
    attended = jnp.einsum("chqk,ckhd->cqhd", probs_low, values, preferred_element_type=jnp.float32)
    attended_flat = attended.reshape(rows, width).astype(jnp.bfloat16)
    residual = inputs + jnp.dot(attended_flat, output_weight, preferred_element_type=jnp.float32) + output_bias
    second_normed, second_inverse, second_act = norm_forward(residual, second_gain, second_shift)
    pre = jnp.dot(second_act, expand_weight, preferred_element_type=jnp.float32) + expand_bias
    hidden_act = jax.nn.gelu(pre, approximate=False).astype(jnp.bfloat16)
    block_output = residual + jnp.dot(hidden_act, contract_weight, preferred_element_type=jnp.float32) + contract_bias
    error = cotangent.reshape(rows, width) * live.reshape(rows, 1).astype(jnp.float32)
    error_low = error.astype(jnp.bfloat16)
    contract_bias_grad = jnp.sum(error, axis=0)
    contract_grad = inner_rows(hidden_act, error_low)
    dpre = lax.dot_general(
        error_low, contract_weight, (((1,), (1,)), ((), ())), preferred_element_type=jnp.float32
    ) * gelu_slope(pre)
    expand_bias_grad = jnp.sum(dpre, axis=0)
    dpre_low = dpre.astype(jnp.bfloat16)
    expand_grad = inner_rows(second_act, dpre_low)
    dsecond = lax.dot_general(
        dpre_low, expand_weight, (((1,), (1,)), ((), ())), preferred_element_type=jnp.float32
    )
    second_gain_grad = jnp.sum(dsecond * second_normed, axis=0)
    second_shift_grad = jnp.sum(dsecond, axis=0)
    dresidual = error + norm_backward(dsecond, second_normed, second_inverse, second_gain)
    output_bias_grad = jnp.sum(dresidual, axis=0)
    dresidual_low = dresidual.astype(jnp.bfloat16)
    output_grad = inner_rows(attended_flat, dresidual_low)
    dattended = lax.dot_general(
        dresidual_low, output_weight, (((1,), (1,)), ((), ())), preferred_element_type=jnp.float32
    ).astype(jnp.bfloat16)
    dattended_heads = dattended.reshape(clip_count, frame_count, HEADS, HEAD)
    attended_heads = attended_flat.reshape(clip_count, frame_count, HEADS, HEAD)
    delta = jnp.sum(
        dattended_heads.astype(jnp.float32) * attended_heads.astype(jnp.float32), axis=-1
    )
    dprob = jnp.einsum("cqhd,ckhd->chqk", dattended_heads, values, preferred_element_type=jnp.float32)
    dscore = (probs * (dprob - jnp.transpose(delta, (0, 2, 1))[:, :, :, None]) * scale).astype(jnp.bfloat16)
    dqueries = jnp.einsum("chqk,ckhd->cqhd", dscore, keys, preferred_element_type=jnp.float32)
    dkeys = jnp.einsum("chqk,cqhd->ckhd", dscore, queries, preferred_element_type=jnp.float32)
    dvalues = jnp.einsum("chqk,cqhd->ckhd", probs_low, dattended_heads, preferred_element_type=jnp.float32)
    dmixed = jnp.concatenate(
        [dqueries.reshape(rows, width), dkeys.reshape(rows, width), dvalues.reshape(rows, width)], axis=1
    )
    query_bias_grad = jnp.sum(dmixed[:, :width], axis=0)
    value_bias_grad = jnp.sum(dmixed[:, 2 * width:], axis=0)
    dmixed_low = dmixed.astype(jnp.bfloat16)
    attention_grad = inner_rows(first_act, dmixed_low)
    dfirst = lax.dot_general(
        dmixed_low, attention_weight, (((1,), (1,)), ((), ())), preferred_element_type=jnp.float32
    )
    first_gain_grad = jnp.sum(dfirst * first_normed, axis=0)
    first_shift_grad = jnp.sum(dfirst, axis=0)
    input_grad = dresidual + norm_backward(dfirst, first_normed, first_inverse, first_gain)
    weight_grads = (attention_grad, output_grad, expand_grad, contract_grad)
    vector_grads = (first_gain_grad, first_shift_grad, query_bias_grad, value_bias_grad, output_bias_grad,
                    second_gain_grad, second_shift_grad, expand_bias_grad, contract_bias_grad)
    return (
        block_output.reshape(clip_count, frame_count, width),
        input_grad.reshape(clip_count, frame_count, width),
        weight_grads,
        vector_grads,
    )


def clip_local(tokens, lengths, cotangent, *params):
    clip_count, slot_count, width = tokens.shape
    parts = lax.axis_size("shard")
    place = lax.axis_index("shard")
    own = clip_count // parts
    weight_shards = params[:4]
    vector_shards = params[4:]
    vector_row = jnp.concatenate([entry.reshape(-1) for entry in vector_shards])
    row_width = weight_shards[0].shape[1]
    pad = (-vector_row.shape[0]) % row_width
    vector_rows = jnp.pad(vector_row, (0, pad)).reshape(-1, row_width)
    extra = vector_rows.shape[0]
    attention_block = jnp.concatenate([weight_shards[0], vector_rows], axis=0)
    attention_all = lax.all_gather(attention_block, "shard", axis=0, tiled=False)
    shard_rows = weight_shards[0].shape[0]
    attention_weight = attention_all[:, :shard_rows].reshape(parts * shard_rows, row_width)
    vector_all = attention_all[:, shard_rows:].reshape(parts, extra * row_width)[:, : vector_row.shape[0]]
    vectors = []
    offset = 0
    for entry in vector_shards:
        size = entry.shape[0]
        vectors.append(vector_all[:, offset:offset + size].reshape(parts * size).astype(jnp.float32))
        offset += size
    weights = (
        attention_weight,
        lax.all_gather(weight_shards[1], "shard", axis=0, tiled=True),
        lax.all_gather(weight_shards[2], "shard", axis=0, tiled=True),
        lax.all_gather(weight_shards[3], "shard", axis=0, tiled=True),
    )
    tokens_clip = lax.all_to_all(tokens, "shard", 0, 1, tiled=True)
    cotangent_clip = lax.all_to_all(cotangent, "shard", 0, 1, tiled=True)
    lengths_clip = lax.dynamic_slice_in_dim(lengths, place * own, own, axis=0)
    block_output, input_grad, weight_grads, vector_grads = clip_layer(
        tokens_clip, lengths_clip, cotangent_clip, weights, vectors
    )
    block_output = lax.all_to_all(block_output, "shard", 1, 0, tiled=True)
    input_grad = lax.all_to_all(input_grad, "shard", 1, 0, tiled=True)
    contract_grad = weight_grads[3]
    contract_width = contract_grad.shape[1]
    vector_parts = jnp.concatenate(
        [entry.reshape(parts, -1) for entry in vector_grads], axis=1
    )
    vector_size = vector_parts.shape[1]
    vpad = (-vector_size) % contract_width
    vector_parts = jnp.pad(vector_parts, ((0, 0), (0, vpad))).reshape(parts, -1, contract_width)
    contract_rows = contract_grad.shape[0] // parts
    contract_block = jnp.concatenate(
        [contract_grad.reshape(parts, contract_rows, contract_width), vector_parts], axis=1
    )
    shares = (
        lax.psum_scatter(weight_grads[0], "shard", scatter_dimension=0, tiled=True),
        lax.psum_scatter(weight_grads[1], "shard", scatter_dimension=0, tiled=True),
        lax.psum_scatter(weight_grads[2], "shard", scatter_dimension=0, tiled=True),
        lax.psum_scatter(contract_block, "shard", scatter_dimension=0, tiled=False),
    )
    totals = lax.psum(shares, "rep")
    contract_total = totals[3][:contract_rows]
    vector_total = totals[3][contract_rows:].reshape(-1)[:vector_size]
    vector_outs = []
    offset = 0
    for entry in vector_shards:
        size = entry.shape[0]
        vector_outs.append(vector_total[offset:offset + size])
        offset += size
    return (block_output, input_grad, totals[0], totals[1], totals[2], contract_total) + tuple(vector_outs)


def dispatch(tokens, lengths, cotangent, *params):
    parts = lax.axis_size("shard")
    if tokens.shape[0] % parts == 0:
        return clip_local(tokens, lengths, cotangent, *params)
    return local(tokens, lengths, cotangent, *params)


def solution(mesh):
    in_specs = (
        P("rep", "shard", None),
        P("rep", None),
        P("rep", "shard", None),
        P("shard", None),
        P("shard", None),
        P("shard", None),
        P("shard", None),
        P("shard"),
        P("shard"),
        P("shard"),
        P("shard"),
        P("shard"),
        P("shard"),
        P("shard"),
        P("shard"),
        P("shard"),
    )
    out_specs = (
        P("rep", "shard", None),
        P("rep", "shard", None),
        P("shard", None),
        P("shard", None),
        P("shard", None),
        P("shard", None),
        P("shard"),
        P("shard"),
        P("shard"),
        P("shard"),
        P("shard"),
        P("shard"),
        P("shard"),
        P("shard"),
        P("shard"),
    )
    return jax.shard_map(dispatch, mesh=mesh, in_specs=in_specs, out_specs=out_specs, check_vma=False)
```

```python
import jax
import jax.numpy as jnp
from jax import lax
from jax.sharding import Mesh, PartitionSpec as P
import numpy as np

HEADS = 12
HEAD = 64


EPSILON = 1e-05
NEGATIVE = -1e30


def norm_forward(values, gain, shift):
    centred = values - jnp.mean(values, axis=-1, keepdims=True)
    inverse = lax.rsqrt(jnp.mean(centred * centred, axis=-1, keepdims=True) + EPSILON)
    normed = centred * inverse
    return (normed, inverse, (normed * gain + shift).astype(jnp.bfloat16))


def norm_backward(upstream, normed, inverse, gain):
    scaled = upstream * gain
    return inverse * (
        scaled
        - jnp.mean(scaled, axis=-1, keepdims=True)
        - normed * jnp.mean(scaled * normed, axis=-1, keepdims=True)
    )


def gelu_slope(values):
    return (
        0.5 * (1.0 + jax.scipy.special.erf(values * 0.7071067811865476))
        + values * jnp.exp(-0.5 * values * values) * 0.3989422804014327
    )


def inner_rows(left, right):
    return lax.dot_general(
        left, right, (((0,), (0,)), ((), ())), preferred_element_type=jnp.float32
    )


def heads_view(matrix):
    return matrix.reshape(matrix.shape[0], HEADS, HEAD)


def score_block(query_rows, key_rows, key_live):
    scores = jnp.einsum(
        "qhd,khd->hqk",
        heads_view(query_rows),
        heads_view(key_rows),
        preferred_element_type=jnp.float32,
    ) * HEAD ** (-0.5)
    return jnp.where(key_live[None, None, :], scores, NEGATIVE)


def attend_clip(items):
    query_rows, pair_rows, key_live = items
    width = query_rows.shape[1]
    scores = score_block(query_rows, pair_rows[:, :width], key_live)
    highest = jnp.max(scores, axis=-1, keepdims=True)
    logsum = highest + jnp.log(jnp.sum(jnp.exp(scores - highest), axis=-1, keepdims=True))
    probs_low = jnp.exp(scores - logsum).astype(jnp.bfloat16)
    attended = jnp.einsum(
        "hqk,khd->qhd",
        probs_low,
        heads_view(pair_rows[:, width:]),
        preferred_element_type=jnp.float32,
    )
    return (attended.reshape(query_rows.shape[0], width).astype(jnp.bfloat16), logsum[:, :, 0].T)


def score_grads(query_rows, dattended, logsum, delta, pair_rows, key_live):
    width = query_rows.shape[1]
    scores = score_block(query_rows, pair_rows[:, :width], key_live)
    probs = jnp.exp(scores - logsum.T[:, :, None])
    dprob = jnp.einsum(
        "qhd,khd->hqk",
        heads_view(dattended),
        heads_view(pair_rows[:, width:]),
        preferred_element_type=jnp.float32,
    )
    dscore = (probs * (dprob - delta.T[:, :, None]) * HEAD ** (-0.5)).astype(jnp.bfloat16)
    return (probs.astype(jnp.bfloat16), dscore)


def both_grads(items):
    query_rows, dattended, logsum, delta, pair_rows, key_live = items
    width = query_rows.shape[1]
    probs_low, dscore = score_grads(query_rows, dattended, logsum, delta, pair_rows, key_live)
    dqueries = jnp.einsum(
        "hqk,khd->qhd", dscore, heads_view(pair_rows[:, :width]), preferred_element_type=jnp.float32
    ).reshape(query_rows.shape[0], width)
    dkeys = jnp.einsum(
        "hqk,qhd->khd", dscore, heads_view(query_rows), preferred_element_type=jnp.float32
    )
    dvalues = jnp.einsum(
        "hqk,qhd->khd", probs_low, heads_view(dattended), preferred_element_type=jnp.float32
    )
    key_count = pair_rows.shape[0]
    return (
        dqueries,
        jnp.concatenate(
            [dkeys.reshape(key_count, width), dvalues.reshape(key_count, width)], axis=1
        ),
    )


def local(
    tokens,
    lengths,
    cotangent,
    attention_weight,
    output_weight,
    expand_weight,
    contract_weight,
    first_gain,
    first_shift,
    query_bias,
    value_bias,
    output_bias,
    second_gain,
    second_shift,
    expand_bias,
    contract_bias,
):
    clip_count, slot_count, width = tokens.shape
    parts = lax.axis_size("shard")
    frame_count = slot_count * parts
    place = lax.axis_index("shard")
    row_total = clip_count * slot_count
    gathered = (
        lax.all_gather(attention_weight, "shard", axis=0, tiled=True),
        lax.all_gather(output_weight, "shard", axis=0, tiled=True),
        lax.all_gather(expand_weight, "shard", axis=0, tiled=True),
        lax.all_gather(contract_weight, "shard", axis=0, tiled=True),
        lax.all_gather(first_gain, "shard", axis=0, tiled=True),
        lax.all_gather(first_shift, "shard", axis=0, tiled=True),
        lax.all_gather(query_bias, "shard", axis=0, tiled=True),
        lax.all_gather(value_bias, "shard", axis=0, tiled=True),
        lax.all_gather(output_bias, "shard", axis=0, tiled=True),
        lax.all_gather(second_gain, "shard", axis=0, tiled=True),
        lax.all_gather(second_shift, "shard", axis=0, tiled=True),
        lax.all_gather(expand_bias, "shard", axis=0, tiled=True),
        lax.all_gather(contract_bias, "shard", axis=0, tiled=True),
    )
    vectors = [entry.astype(jnp.float32) for entry in gathered[4:]]
    own_length = jnp.sum(jnp.where(jnp.arange(parts)[None, :] == place, lengths, 0), axis=1)
    row_live = jnp.arange(slot_count)[None, :] < own_length[:, None]
    key_live = (jnp.arange(slot_count)[None, None, :] < lengths[:, :, None]).reshape(
        clip_count, frame_count
    )
    inputs = tokens.reshape(row_total, width).astype(jnp.float32)
    first_normed, first_inverse, first_act = norm_forward(inputs, vectors[0], vectors[1])
    mixed = jnp.dot(first_act, gathered[0], preferred_element_type=jnp.float32)
    mixed = mixed + jnp.concatenate([vectors[2], jnp.zeros_like(vectors[2]), vectors[3]])
    mixed_low = mixed.astype(jnp.bfloat16)
    query_rows = mixed_low[:, :width].reshape(clip_count, slot_count, width)
    pair_own = mixed_low[:, width:].reshape(clip_count, slot_count, 2 * width)
    pair_all = lax.all_gather(pair_own, "shard", axis=1, tiled=True)
    attended, logsum = lax.map(attend_clip, (query_rows, pair_all, key_live))
    attended_flat = attended.reshape(row_total, width)
    residual = (
        inputs
        + jnp.dot(attended_flat, gathered[1], preferred_element_type=jnp.float32)
        + vectors[4]
    )
    second_normed, second_inverse, second_act = norm_forward(residual, vectors[5], vectors[6])
    pre = jnp.dot(second_act, gathered[2], preferred_element_type=jnp.float32) + vectors[7]
    hidden_act = jax.nn.gelu(pre, approximate=False).astype(jnp.bfloat16)
    block_output = (
        residual + jnp.dot(hidden_act, gathered[3], preferred_element_type=jnp.float32) + vectors[8]
    )
    backward = (
        lax.all_gather(attention_weight, "shard", axis=0, tiled=True),
        lax.all_gather(output_weight, "shard", axis=0, tiled=True),
        lax.all_gather(expand_weight, "shard", axis=0, tiled=True),
        lax.all_gather(contract_weight, "shard", axis=0, tiled=True),
        lax.all_gather(first_gain, "shard", axis=0, tiled=True),
        lax.all_gather(first_shift, "shard", axis=0, tiled=True),
        lax.all_gather(query_bias, "shard", axis=0, tiled=True),
        lax.all_gather(value_bias, "shard", axis=0, tiled=True),
        lax.all_gather(output_bias, "shard", axis=0, tiled=True),
        lax.all_gather(second_gain, "shard", axis=0, tiled=True),
        lax.all_gather(second_shift, "shard", axis=0, tiled=True),
        lax.all_gather(expand_bias, "shard", axis=0, tiled=True),
        lax.all_gather(contract_bias, "shard", axis=0, tiled=True),
    )
    back_vectors = [entry.astype(jnp.float32) for entry in backward[4:]]
    error = cotangent.reshape(row_total, width) * row_live.reshape(row_total, 1).astype(jnp.float32)
    error_low = error.astype(jnp.bfloat16)
    contract_bias_grad = jnp.sum(error, axis=0)
    contract_grad = inner_rows(hidden_act, error_low)
    dpre = lax.dot_general(
        error_low, backward[3], (((1,), (1,)), ((), ())), preferred_element_type=jnp.float32
    ) * gelu_slope(pre)
    expand_bias_grad = jnp.sum(dpre, axis=0)
    dpre_low = dpre.astype(jnp.bfloat16)
    expand_grad = inner_rows(second_act, dpre_low)
    dsecond = lax.dot_general(
        dpre_low, backward[2], (((1,), (1,)), ((), ())), preferred_element_type=jnp.float32
    )
    second_gain_grad = jnp.sum(dsecond * second_normed, axis=0)
    second_shift_grad = jnp.sum(dsecond, axis=0)
    dresidual = error + norm_backward(dsecond, second_normed, second_inverse, back_vectors[5])
    output_bias_grad = jnp.sum(dresidual, axis=0)
    dresidual_low = dresidual.astype(jnp.bfloat16)
    output_grad = inner_rows(attended_flat, dresidual_low)
    dattended = lax.dot_general(
        dresidual_low, backward[1], (((1,), (1,)), ((), ())), preferred_element_type=jnp.float32
    ).astype(jnp.bfloat16)
    delta = jnp.sum(
        heads_view(dattended.astype(jnp.float32)) * heads_view(attended_flat.astype(jnp.float32)),
        axis=-1,
    )
    delta = delta.reshape(clip_count, slot_count, HEADS)
    dattended_clips = dattended.reshape(clip_count, slot_count, width)
    dqueries, pair_terms = lax.map(
        both_grads, (query_rows, dattended_clips, logsum, delta, pair_all, key_live)
    )
    pair_grads = lax.psum_scatter(pair_terms, "shard", scatter_dimension=1, tiled=True)
    dqueries_flat = dqueries.reshape(row_total, width)
    pair_flat = pair_grads.reshape(row_total, 2 * width)
    dmixed = jnp.concatenate([dqueries_flat, pair_flat], axis=1)
    query_bias_grad = jnp.sum(dqueries_flat, axis=0)
    value_bias_grad = jnp.sum(pair_flat[:, width:], axis=0)
    dmixed_low = dmixed.astype(jnp.bfloat16)
    attention_grad = inner_rows(first_act, dmixed_low)
    dfirst = lax.dot_general(
        dmixed_low, backward[0], (((1,), (1,)), ((), ())), preferred_element_type=jnp.float32
    )
    first_gain_grad = jnp.sum(dfirst * first_normed, axis=0)
    first_shift_grad = jnp.sum(dfirst, axis=0)
    input_grad = dresidual + norm_backward(dfirst, first_normed, first_inverse, back_vectors[0])
    shares = (
        lax.psum_scatter(attention_grad, "shard", scatter_dimension=0, tiled=True),
        lax.psum_scatter(output_grad, "shard", scatter_dimension=0, tiled=True),
        lax.psum_scatter(expand_grad, "shard", scatter_dimension=0, tiled=True),
        lax.psum_scatter(contract_grad, "shard", scatter_dimension=0, tiled=True),
        lax.psum_scatter(first_gain_grad, "shard", scatter_dimension=0, tiled=True),
        lax.psum_scatter(first_shift_grad, "shard", scatter_dimension=0, tiled=True),
        lax.psum_scatter(query_bias_grad, "shard", scatter_dimension=0, tiled=True),
        lax.psum_scatter(value_bias_grad, "shard", scatter_dimension=0, tiled=True),
        lax.psum_scatter(output_bias_grad, "shard", scatter_dimension=0, tiled=True),
        lax.psum_scatter(second_gain_grad, "shard", scatter_dimension=0, tiled=True),
        lax.psum_scatter(second_shift_grad, "shard", scatter_dimension=0, tiled=True),
        lax.psum_scatter(expand_bias_grad, "shard", scatter_dimension=0, tiled=True),
        lax.psum_scatter(contract_bias_grad, "shard", scatter_dimension=0, tiled=True),
    )
    totals = lax.psum(
        (
            shares[0],
            shares[1],
            shares[2],
            shares[3],
            shares[4],
            shares[5],
            shares[6],
            shares[7],
            shares[8],
            shares[9],
            shares[10],
            shares[11],
            shares[12],
        ),
        "rep",
    )
    return (
        block_output.reshape(clip_count, slot_count, width),
        input_grad.reshape(clip_count, slot_count, width),
        totals[0],
        totals[1],
        totals[2],
        totals[3],
        totals[4],
        totals[5],
        totals[6],
        totals[7],
        totals[8],
        totals[9],
        totals[10],
        totals[11],
        totals[12],
    )


def clip_layer(tokens, lengths, cotangent, weights, vectors):
    attention_weight, output_weight, expand_weight, contract_weight = weights
    (first_gain, first_shift, query_bias, value_bias, output_bias, second_gain, second_shift,
     expand_bias, contract_bias) = vectors
    clip_count, frame_count, width = tokens.shape
    block_count = lengths.shape[1]
    slot_count = frame_count // block_count
    rows = clip_count * frame_count
    live = (jnp.arange(slot_count)[None, None, :] < lengths[:, :, None]).reshape(clip_count, frame_count)
    scale = HEAD ** (-0.5)
    inputs = tokens.reshape(rows, width).astype(jnp.float32)
    first_normed, first_inverse, first_act = norm_forward(inputs, first_gain, first_shift)
    mixed = jnp.dot(first_act, attention_weight, preferred_element_type=jnp.float32)
    mixed = mixed + jnp.concatenate([query_bias, jnp.zeros_like(query_bias), value_bias])
    mixed_low = mixed.astype(jnp.bfloat16).reshape(clip_count, frame_count, 3, HEADS, HEAD)
    queries = mixed_low[:, :, 0]
    keys = mixed_low[:, :, 1]
    values = mixed_low[:, :, 2]
    scores = jnp.einsum("cqhd,ckhd->chqk", queries, keys, preferred_element_type=jnp.float32) * scale
    scores = jnp.where(live[:, None, None, :], scores, NEGATIVE)
    highest = jnp.max(scores, axis=-1, keepdims=True)
    logsum = highest + jnp.log(jnp.sum(jnp.exp(scores - highest), axis=-1, keepdims=True))
    probs = jnp.exp(scores - logsum)
    probs_low = probs.astype(jnp.bfloat16)
    attended = jnp.einsum("chqk,ckhd->cqhd", probs_low, values, preferred_element_type=jnp.float32)
    attended_flat = attended.reshape(rows, width).astype(jnp.bfloat16)
    residual = inputs + jnp.dot(attended_flat, output_weight, preferred_element_type=jnp.float32) + output_bias
    second_normed, second_inverse, second_act = norm_forward(residual, second_gain, second_shift)
    pre = jnp.dot(second_act, expand_weight, preferred_element_type=jnp.float32) + expand_bias
    hidden_act = jax.nn.gelu(pre, approximate=False).astype(jnp.bfloat16)
    block_output = residual + jnp.dot(hidden_act, contract_weight, preferred_element_type=jnp.float32) + contract_bias
    error = cotangent.reshape(rows, width) * live.reshape(rows, 1).astype(jnp.float32)
    error_low = error.astype(jnp.bfloat16)
    contract_bias_grad = jnp.sum(error, axis=0)
    contract_grad = inner_rows(hidden_act, error_low)
    dpre = lax.dot_general(
        error_low, contract_weight, (((1,), (1,)), ((), ())), preferred_element_type=jnp.float32
    ) * gelu_slope(pre)
    expand_bias_grad = jnp.sum(dpre, axis=0)
    dpre_low = dpre.astype(jnp.bfloat16)
    expand_grad = inner_rows(second_act, dpre_low)
    dsecond = lax.dot_general(
        dpre_low, expand_weight, (((1,), (1,)), ((), ())), preferred_element_type=jnp.float32
    )
    second_gain_grad = jnp.sum(dsecond * second_normed, axis=0)
    second_shift_grad = jnp.sum(dsecond, axis=0)
    dresidual = error + norm_backward(dsecond, second_normed, second_inverse, second_gain)
    output_bias_grad = jnp.sum(dresidual, axis=0)
    dresidual_low = dresidual.astype(jnp.bfloat16)
    output_grad = inner_rows(attended_flat, dresidual_low)
    dattended = lax.dot_general(
        dresidual_low, output_weight, (((1,), (1,)), ((), ())), preferred_element_type=jnp.float32
    ).astype(jnp.bfloat16)
    dattended_heads = dattended.reshape(clip_count, frame_count, HEADS, HEAD)
    attended_heads = attended_flat.reshape(clip_count, frame_count, HEADS, HEAD)
    delta = jnp.sum(
        dattended_heads.astype(jnp.float32) * attended_heads.astype(jnp.float32), axis=-1
    )
    dprob = jnp.einsum("cqhd,ckhd->chqk", dattended_heads, values, preferred_element_type=jnp.float32)
    dscore = (probs * (dprob - jnp.transpose(delta, (0, 2, 1))[:, :, :, None]) * scale).astype(jnp.bfloat16)
    dqueries = jnp.einsum("chqk,ckhd->cqhd", dscore, keys, preferred_element_type=jnp.float32)
    dkeys = jnp.einsum("chqk,cqhd->ckhd", dscore, queries, preferred_element_type=jnp.float32)
    dvalues = jnp.einsum("chqk,cqhd->ckhd", probs_low, dattended_heads, preferred_element_type=jnp.float32)
    dmixed = jnp.concatenate(
        [dqueries.reshape(rows, width), dkeys.reshape(rows, width), dvalues.reshape(rows, width)], axis=1
    )
    query_bias_grad = jnp.sum(dmixed[:, :width], axis=0)
    value_bias_grad = jnp.sum(dmixed[:, 2 * width:], axis=0)
    dmixed_low = dmixed.astype(jnp.bfloat16)
    attention_grad = inner_rows(first_act, dmixed_low)
    dfirst = lax.dot_general(
        dmixed_low, attention_weight, (((1,), (1,)), ((), ())), preferred_element_type=jnp.float32
    )
    first_gain_grad = jnp.sum(dfirst * first_normed, axis=0)
    first_shift_grad = jnp.sum(dfirst, axis=0)
    input_grad = dresidual + norm_backward(dfirst, first_normed, first_inverse, first_gain)
    weight_grads = (attention_grad, output_grad, expand_grad, contract_grad)
    vector_grads = (first_gain_grad, first_shift_grad, query_bias_grad, value_bias_grad, output_bias_grad,
                    second_gain_grad, second_shift_grad, expand_bias_grad, contract_bias_grad)
    return (
        block_output.reshape(clip_count, frame_count, width),
        input_grad.reshape(clip_count, frame_count, width),
        weight_grads,
        vector_grads,
    )


PAIR = [(0, 1), (1, 0)]
OUTER = ("outer", "inner")


def core_pick(core, first, second):
    return jnp.where(core == 0, first, second)


def gather_weight(shard_rows, extra=None):
    parts = lax.axis_size("shard")
    core = lax.axis_index("core")
    rows, width = shard_rows.shape
    half = rows // 2
    mine = lax.dynamic_slice_in_dim(shard_rows, core * half, half, axis=0)
    if extra is not None:
        mine = jnp.concatenate([mine, extra], axis=0)
    mine = lax.all_gather(mine, "shard", axis=0, tiled=False)
    other = lax.ppermute(mine, "core", PAIR)
    first = core_pick(core, mine, other)
    second = core_pick(core, other, mine)
    full = jnp.stack([first[:, :half], second[:, :half]], axis=1).reshape(parts * rows, width)
    if extra is None:
        return full, None
    return full, first[:, half:]


def reduce_weight(grad, extra=None):
    parts = lax.axis_size("shard")
    core = lax.axis_index("core")
    width = grad.shape[1]
    rows = grad.shape[0] // parts
    half = rows // 2
    quarters = grad.reshape(parts, 2, half, width)
    keep = lax.dynamic_index_in_dim(quarters, core, axis=1, keepdims=False)
    send = lax.dynamic_index_in_dim(quarters, 1 - core, axis=1, keepdims=False)
    if extra is not None:
        on_first = (core == 0).astype(extra.dtype)
        keep = jnp.concatenate([keep, extra * on_first], axis=1)
        send = jnp.concatenate([send, extra * (1 - on_first)], axis=1)
    chip = keep + lax.ppermute(send, "core", PAIR)
    part = lax.psum_scatter(chip, "shard", scatter_dimension=0, tiled=False)
    total = lax.psum(part, OUTER)
    other = lax.ppermute(total, "core", PAIR)
    first = core_pick(core, total, other)
    second = core_pick(core, other, total)
    out = jnp.concatenate([first[:half], second[:half]], axis=0)
    if extra is None:
        return out, None
    return out, first[half:]


def clip_local(tokens, lengths, cotangent, *params):
    clip_count, slot_count, width = tokens.shape
    parts = lax.axis_size("shard")
    place = lax.axis_index("shard")
    own = clip_count // parts
    weight_shards = params[:4]
    vector_shards = params[4:]
    vector_row = jnp.concatenate([entry.reshape(-1) for entry in vector_shards])
    row_width = weight_shards[0].shape[1]
    pad = (-vector_row.shape[0]) % row_width
    vector_rows = jnp.pad(vector_row, (0, pad)).reshape(-1, row_width)
    attention_weight, vector_all = gather_weight(weight_shards[0], vector_rows)
    vector_all = vector_all.reshape(parts, -1)[:, : vector_row.shape[0]]
    vectors = []
    offset = 0
    for entry in vector_shards:
        size = entry.shape[0]
        vectors.append(vector_all[:, offset:offset + size].reshape(parts * size).astype(jnp.float32))
        offset += size
    weights = (
        attention_weight,
        gather_weight(weight_shards[1])[0],
        gather_weight(weight_shards[2])[0],
        gather_weight(weight_shards[3])[0],
    )
    tokens_clip = lax.all_to_all(tokens, "shard", 0, 1, tiled=True)
    cotangent_clip = lax.all_to_all(cotangent, "shard", 0, 1, tiled=True)
    lengths_clip = lax.dynamic_slice_in_dim(lengths, place * own, own, axis=0)
    block_output, input_grad, weight_grads, vector_grads = clip_layer(
        tokens_clip, lengths_clip, cotangent_clip, weights, vectors
    )
    block_output = lax.all_to_all(block_output, "shard", 1, 0, tiled=True)
    input_grad = lax.all_to_all(input_grad, "shard", 1, 0, tiled=True)
    contract_grad = weight_grads[3]
    contract_width = contract_grad.shape[1]
    vector_parts = jnp.concatenate([entry.reshape(parts, -1) for entry in vector_grads], axis=1)
    vector_size = vector_parts.shape[1]
    vpad = (-vector_size) % contract_width
    vector_parts = jnp.pad(vector_parts, ((0, 0), (0, vpad))).reshape(parts, -1, contract_width)
    contract_total, vector_total = reduce_weight(contract_grad, vector_parts)
    totals = (
        reduce_weight(weight_grads[0])[0],
        reduce_weight(weight_grads[1])[0],
        reduce_weight(weight_grads[2])[0],
        contract_total,
    )
    vector_total = vector_total.reshape(-1)[:vector_size]
    vector_outs = []
    offset = 0
    for entry in vector_shards:
        size = entry.shape[0]
        vector_outs.append(vector_total[offset:offset + size])
        offset += size
    return (block_output, input_grad) + totals + tuple(vector_outs)


def split_rep(mesh):
    devices = mesh.devices
    rep, parts = devices.shape
    first = devices[0, 0]
    stride = None
    for index in range(1, rep):
        other = devices[index, 0]
        if tuple(other.coords) == tuple(first.coords) and other.core_on_chip != first.core_on_chip:
            stride = index
            break
    if stride is None or rep % (2 * stride):
        return None
    grid = devices.reshape(rep // (2 * stride), 2, stride, parts)
    for spot in np.ndindex(grid.shape[0], grid.shape[2], grid.shape[3]):
        low = grid[spot[0], 0, spot[1], spot[2]]
        high = grid[spot[0], 1, spot[1], spot[2]]
        if tuple(low.coords) != tuple(high.coords) or low.core_on_chip == high.core_on_chip:
            return None
    return Mesh(grid, ("outer", "core", "inner", "shard"))


def solution(mesh):
    def specs(rep):
        ins = (P(rep, "shard", None), P(rep, None), P(rep, "shard", None)) + (P("shard", None),) * 4 + (
            P("shard"),
        ) * 9
        outs = (P(rep, "shard", None), P(rep, "shard", None)) + (P("shard", None),) * 4 + (P("shard"),) * 9
        return ins, outs

    ins, outs = specs("rep")
    plain = jax.shard_map(local, mesh=mesh, in_specs=ins, out_specs=outs, check_vma=False)
    split = split_rep(mesh)
    if split is None:
        return plain
    ins, outs = specs(("outer", "core", "inner"))
    fast = jax.shard_map(clip_local, mesh=split, in_specs=ins, out_specs=outs, check_vma=False)
    rep, parts = mesh.devices.shape

    def run(*args):
        if (args[0].shape[0] // rep) % parts == 0:
            return fast(*args)
        return plain(*args)

    return run
```

```python
import jax
import jax.numpy as jnp
from jax import lax
from jax.sharding import Mesh, PartitionSpec as P
import numpy as np

HEADS = 12
HEAD = 64


EPSILON = 1e-05
NEGATIVE = -1e30


def norm_forward(values, gain, shift):
    centred = values - jnp.mean(values, axis=-1, keepdims=True)
    inverse = lax.rsqrt(jnp.mean(centred * centred, axis=-1, keepdims=True) + EPSILON)
    normed = centred * inverse
    return (normed, inverse, (normed * gain + shift).astype(jnp.bfloat16))


def norm_backward(upstream, normed, inverse, gain):
    scaled = upstream * gain
    return inverse * (
        scaled
        - jnp.mean(scaled, axis=-1, keepdims=True)
        - normed * jnp.mean(scaled * normed, axis=-1, keepdims=True)
    )


def gelu_slope(values):
    return (
        0.5 * (1.0 + jax.scipy.special.erf(values * 0.7071067811865476))
        + values * jnp.exp(-0.5 * values * values) * 0.3989422804014327
    )


def inner_rows(left, right):
    return lax.dot_general(
        left, right, (((0,), (0,)), ((), ())), preferred_element_type=jnp.float32
    )


def heads_view(matrix):
    return matrix.reshape(matrix.shape[0], HEADS, HEAD)


def score_block(query_rows, key_rows, key_live):
    scores = jnp.einsum(
        "qhd,khd->hqk",
        heads_view(query_rows),
        heads_view(key_rows),
        preferred_element_type=jnp.float32,
    ) * HEAD ** (-0.5)
    return jnp.where(key_live[None, None, :], scores, NEGATIVE)


def attend_clip(items):
    query_rows, pair_rows, key_live = items
    width = query_rows.shape[1]
    scores = score_block(query_rows, pair_rows[:, :width], key_live)
    highest = jnp.max(scores, axis=-1, keepdims=True)
    logsum = highest + jnp.log(jnp.sum(jnp.exp(scores - highest), axis=-1, keepdims=True))
    probs_low = jnp.exp(scores - logsum).astype(jnp.bfloat16)
    attended = jnp.einsum(
        "hqk,khd->qhd",
        probs_low,
        heads_view(pair_rows[:, width:]),
        preferred_element_type=jnp.float32,
    )
    return (attended.reshape(query_rows.shape[0], width).astype(jnp.bfloat16), logsum[:, :, 0].T)


def score_grads(query_rows, dattended, logsum, delta, pair_rows, key_live):
    width = query_rows.shape[1]
    scores = score_block(query_rows, pair_rows[:, :width], key_live)
    probs = jnp.exp(scores - logsum.T[:, :, None])
    dprob = jnp.einsum(
        "qhd,khd->hqk",
        heads_view(dattended),
        heads_view(pair_rows[:, width:]),
        preferred_element_type=jnp.float32,
    )
    dscore = (probs * (dprob - delta.T[:, :, None]) * HEAD ** (-0.5)).astype(jnp.bfloat16)
    return (probs.astype(jnp.bfloat16), dscore)


def both_grads(items):
    query_rows, dattended, logsum, delta, pair_rows, key_live = items
    width = query_rows.shape[1]
    probs_low, dscore = score_grads(query_rows, dattended, logsum, delta, pair_rows, key_live)
    dqueries = jnp.einsum(
        "hqk,khd->qhd", dscore, heads_view(pair_rows[:, :width]), preferred_element_type=jnp.float32
    ).reshape(query_rows.shape[0], width)
    dkeys = jnp.einsum(
        "hqk,qhd->khd", dscore, heads_view(query_rows), preferred_element_type=jnp.float32
    )
    dvalues = jnp.einsum(
        "hqk,qhd->khd", probs_low, heads_view(dattended), preferred_element_type=jnp.float32
    )
    key_count = pair_rows.shape[0]
    return (
        dqueries,
        jnp.concatenate(
            [dkeys.reshape(key_count, width), dvalues.reshape(key_count, width)], axis=1
        ),
    )


def local(
    tokens,
    lengths,
    cotangent,
    attention_weight,
    output_weight,
    expand_weight,
    contract_weight,
    first_gain,
    first_shift,
    query_bias,
    value_bias,
    output_bias,
    second_gain,
    second_shift,
    expand_bias,
    contract_bias,
):
    clip_count, slot_count, width = tokens.shape
    parts = lax.axis_size("shard")
    frame_count = slot_count * parts
    place = lax.axis_index("shard")
    row_total = clip_count * slot_count
    gathered = (
        lax.all_gather(attention_weight, "shard", axis=0, tiled=True),
        lax.all_gather(output_weight, "shard", axis=0, tiled=True),
        lax.all_gather(expand_weight, "shard", axis=0, tiled=True),
        lax.all_gather(contract_weight, "shard", axis=0, tiled=True),
        lax.all_gather(first_gain, "shard", axis=0, tiled=True),
        lax.all_gather(first_shift, "shard", axis=0, tiled=True),
        lax.all_gather(query_bias, "shard", axis=0, tiled=True),
        lax.all_gather(value_bias, "shard", axis=0, tiled=True),
        lax.all_gather(output_bias, "shard", axis=0, tiled=True),
        lax.all_gather(second_gain, "shard", axis=0, tiled=True),
        lax.all_gather(second_shift, "shard", axis=0, tiled=True),
        lax.all_gather(expand_bias, "shard", axis=0, tiled=True),
        lax.all_gather(contract_bias, "shard", axis=0, tiled=True),
    )
    vectors = [entry.astype(jnp.float32) for entry in gathered[4:]]
    own_length = jnp.sum(jnp.where(jnp.arange(parts)[None, :] == place, lengths, 0), axis=1)
    row_live = jnp.arange(slot_count)[None, :] < own_length[:, None]
    key_live = (jnp.arange(slot_count)[None, None, :] < lengths[:, :, None]).reshape(
        clip_count, frame_count
    )
    inputs = tokens.reshape(row_total, width).astype(jnp.float32)
    first_normed, first_inverse, first_act = norm_forward(inputs, vectors[0], vectors[1])
    mixed = jnp.dot(first_act, gathered[0], preferred_element_type=jnp.float32)
    mixed = mixed + jnp.concatenate([vectors[2], jnp.zeros_like(vectors[2]), vectors[3]])
    mixed_low = mixed.astype(jnp.bfloat16)
    query_rows = mixed_low[:, :width].reshape(clip_count, slot_count, width)
    pair_own = mixed_low[:, width:].reshape(clip_count, slot_count, 2 * width)
    pair_all = lax.all_gather(pair_own, "shard", axis=1, tiled=True)
    attended, logsum = lax.map(attend_clip, (query_rows, pair_all, key_live))
    attended_flat = attended.reshape(row_total, width)
    residual = (
        inputs
        + jnp.dot(attended_flat, gathered[1], preferred_element_type=jnp.float32)
        + vectors[4]
    )
    second_normed, second_inverse, second_act = norm_forward(residual, vectors[5], vectors[6])
    pre = jnp.dot(second_act, gathered[2], preferred_element_type=jnp.float32) + vectors[7]
    hidden_act = jax.nn.gelu(pre, approximate=False).astype(jnp.bfloat16)
    block_output = (
        residual + jnp.dot(hidden_act, gathered[3], preferred_element_type=jnp.float32) + vectors[8]
    )
    backward = (
        lax.all_gather(attention_weight, "shard", axis=0, tiled=True),
        lax.all_gather(output_weight, "shard", axis=0, tiled=True),
        lax.all_gather(expand_weight, "shard", axis=0, tiled=True),
        lax.all_gather(contract_weight, "shard", axis=0, tiled=True),
        lax.all_gather(first_gain, "shard", axis=0, tiled=True),
        lax.all_gather(first_shift, "shard", axis=0, tiled=True),
        lax.all_gather(query_bias, "shard", axis=0, tiled=True),
        lax.all_gather(value_bias, "shard", axis=0, tiled=True),
        lax.all_gather(output_bias, "shard", axis=0, tiled=True),
        lax.all_gather(second_gain, "shard", axis=0, tiled=True),
        lax.all_gather(second_shift, "shard", axis=0, tiled=True),
        lax.all_gather(expand_bias, "shard", axis=0, tiled=True),
        lax.all_gather(contract_bias, "shard", axis=0, tiled=True),
    )
    back_vectors = [entry.astype(jnp.float32) for entry in backward[4:]]
    error = cotangent.reshape(row_total, width) * row_live.reshape(row_total, 1).astype(jnp.float32)
    error_low = error.astype(jnp.bfloat16)
    contract_bias_grad = jnp.sum(error, axis=0)
    contract_grad = inner_rows(hidden_act, error_low)
    dpre = lax.dot_general(
        error_low, backward[3], (((1,), (1,)), ((), ())), preferred_element_type=jnp.float32
    ) * gelu_slope(pre)
    expand_bias_grad = jnp.sum(dpre, axis=0)
    dpre_low = dpre.astype(jnp.bfloat16)
    expand_grad = inner_rows(second_act, dpre_low)
    dsecond = lax.dot_general(
        dpre_low, backward[2], (((1,), (1,)), ((), ())), preferred_element_type=jnp.float32
    )
    second_gain_grad = jnp.sum(dsecond * second_normed, axis=0)
    second_shift_grad = jnp.sum(dsecond, axis=0)
    dresidual = error + norm_backward(dsecond, second_normed, second_inverse, back_vectors[5])
    output_bias_grad = jnp.sum(dresidual, axis=0)
    dresidual_low = dresidual.astype(jnp.bfloat16)
    output_grad = inner_rows(attended_flat, dresidual_low)
    dattended = lax.dot_general(
        dresidual_low, backward[1], (((1,), (1,)), ((), ())), preferred_element_type=jnp.float32
    ).astype(jnp.bfloat16)
    delta = jnp.sum(
        heads_view(dattended.astype(jnp.float32)) * heads_view(attended_flat.astype(jnp.float32)),
        axis=-1,
    )
    delta = delta.reshape(clip_count, slot_count, HEADS)
    dattended_clips = dattended.reshape(clip_count, slot_count, width)
    dqueries, pair_terms = lax.map(
        both_grads, (query_rows, dattended_clips, logsum, delta, pair_all, key_live)
    )
    pair_grads = lax.psum_scatter(pair_terms, "shard", scatter_dimension=1, tiled=True)
    dqueries_flat = dqueries.reshape(row_total, width)
    pair_flat = pair_grads.reshape(row_total, 2 * width)
    dmixed = jnp.concatenate([dqueries_flat, pair_flat], axis=1)
    query_bias_grad = jnp.sum(dqueries_flat, axis=0)
    value_bias_grad = jnp.sum(pair_flat[:, width:], axis=0)
    dmixed_low = dmixed.astype(jnp.bfloat16)
    attention_grad = inner_rows(first_act, dmixed_low)
    dfirst = lax.dot_general(
        dmixed_low, backward[0], (((1,), (1,)), ((), ())), preferred_element_type=jnp.float32
    )
    first_gain_grad = jnp.sum(dfirst * first_normed, axis=0)
    first_shift_grad = jnp.sum(dfirst, axis=0)
    input_grad = dresidual + norm_backward(dfirst, first_normed, first_inverse, back_vectors[0])
    shares = (
        lax.psum_scatter(attention_grad, "shard", scatter_dimension=0, tiled=True),
        lax.psum_scatter(output_grad, "shard", scatter_dimension=0, tiled=True),
        lax.psum_scatter(expand_grad, "shard", scatter_dimension=0, tiled=True),
        lax.psum_scatter(contract_grad, "shard", scatter_dimension=0, tiled=True),
        lax.psum_scatter(first_gain_grad, "shard", scatter_dimension=0, tiled=True),
        lax.psum_scatter(first_shift_grad, "shard", scatter_dimension=0, tiled=True),
        lax.psum_scatter(query_bias_grad, "shard", scatter_dimension=0, tiled=True),
        lax.psum_scatter(value_bias_grad, "shard", scatter_dimension=0, tiled=True),
        lax.psum_scatter(output_bias_grad, "shard", scatter_dimension=0, tiled=True),
        lax.psum_scatter(second_gain_grad, "shard", scatter_dimension=0, tiled=True),
        lax.psum_scatter(second_shift_grad, "shard", scatter_dimension=0, tiled=True),
        lax.psum_scatter(expand_bias_grad, "shard", scatter_dimension=0, tiled=True),
        lax.psum_scatter(contract_bias_grad, "shard", scatter_dimension=0, tiled=True),
    )
    totals = lax.psum(
        (
            shares[0],
            shares[1],
            shares[2],
            shares[3],
            shares[4],
            shares[5],
            shares[6],
            shares[7],
            shares[8],
            shares[9],
            shares[10],
            shares[11],
            shares[12],
        ),
        "rep",
    )
    return (
        block_output.reshape(clip_count, slot_count, width),
        input_grad.reshape(clip_count, slot_count, width),
        totals[0],
        totals[1],
        totals[2],
        totals[3],
        totals[4],
        totals[5],
        totals[6],
        totals[7],
        totals[8],
        totals[9],
        totals[10],
        totals[11],
        totals[12],
    )


def clip_layer(tokens, lengths, cotangent, weights, vectors):
    attention_weight, output_weight, expand_weight, contract_weight = weights
    (first_gain, first_shift, query_bias, value_bias, output_bias, second_gain, second_shift,
     expand_bias, contract_bias) = vectors
    clip_count, frame_count, width = tokens.shape
    block_count = lengths.shape[1]
    slot_count = frame_count // block_count
    rows = clip_count * frame_count
    live = (jnp.arange(slot_count)[None, None, :] < lengths[:, :, None]).reshape(clip_count, frame_count)
    scale = HEAD ** (-0.5)
    inputs = tokens.reshape(rows, width).astype(jnp.float32)
    first_normed, first_inverse, first_act = norm_forward(inputs, first_gain, first_shift)
    mixed = jnp.dot(first_act, attention_weight, preferred_element_type=jnp.float32)
    mixed = mixed + jnp.concatenate([query_bias, jnp.zeros_like(query_bias), value_bias])
    mixed_low = mixed.astype(jnp.bfloat16).reshape(clip_count, frame_count, 3, HEADS, HEAD)
    queries = mixed_low[:, :, 0]
    keys = mixed_low[:, :, 1]
    values = mixed_low[:, :, 2]
    scores = jnp.einsum("cqhd,ckhd->chqk", queries, keys, preferred_element_type=jnp.float32) * scale
    scores = jnp.where(live[:, None, None, :], scores, NEGATIVE)
    highest = jnp.max(scores, axis=-1, keepdims=True)
    logsum = highest + jnp.log(jnp.sum(jnp.exp(scores - highest), axis=-1, keepdims=True))
    probs = jnp.exp(scores - logsum)
    probs_low = probs.astype(jnp.bfloat16)
    attended = jnp.einsum("chqk,ckhd->cqhd", probs_low, values, preferred_element_type=jnp.float32)
    attended_flat = attended.reshape(rows, width).astype(jnp.bfloat16)
    residual = inputs + jnp.dot(attended_flat, output_weight, preferred_element_type=jnp.float32) + output_bias
    second_normed, second_inverse, second_act = norm_forward(residual, second_gain, second_shift)
    pre = jnp.dot(second_act, expand_weight, preferred_element_type=jnp.float32) + expand_bias
    hidden_act = jax.nn.gelu(pre, approximate=False).astype(jnp.bfloat16)
    block_output = residual + jnp.dot(hidden_act, contract_weight, preferred_element_type=jnp.float32) + contract_bias
    error = cotangent.reshape(rows, width) * live.reshape(rows, 1).astype(jnp.float32)
    error_low = error.astype(jnp.bfloat16)
    contract_bias_grad = jnp.sum(error, axis=0)
    contract_grad = inner_rows(hidden_act, error_low)
    dpre = lax.dot_general(
        error_low, contract_weight, (((1,), (1,)), ((), ())), preferred_element_type=jnp.float32
    ) * gelu_slope(pre)
    expand_bias_grad = jnp.sum(dpre, axis=0)
    dpre_low = dpre.astype(jnp.bfloat16)
    expand_grad = inner_rows(second_act, dpre_low)
    dsecond = lax.dot_general(
        dpre_low, expand_weight, (((1,), (1,)), ((), ())), preferred_element_type=jnp.float32
    )
    second_gain_grad = jnp.sum(dsecond * second_normed, axis=0)
    second_shift_grad = jnp.sum(dsecond, axis=0)
    dresidual = error + norm_backward(dsecond, second_normed, second_inverse, second_gain)
    output_bias_grad = jnp.sum(dresidual, axis=0)
    dresidual_low = dresidual.astype(jnp.bfloat16)
    output_grad = inner_rows(attended_flat, dresidual_low)
    dattended = lax.dot_general(
        dresidual_low, output_weight, (((1,), (1,)), ((), ())), preferred_element_type=jnp.float32
    ).astype(jnp.bfloat16)
    dattended_heads = dattended.reshape(clip_count, frame_count, HEADS, HEAD)
    attended_heads = attended_flat.reshape(clip_count, frame_count, HEADS, HEAD)
    delta = jnp.sum(
        dattended_heads.astype(jnp.float32) * attended_heads.astype(jnp.float32), axis=-1
    )
    dprob = jnp.einsum("cqhd,ckhd->chqk", dattended_heads, values, preferred_element_type=jnp.float32)
    dscore = (probs * (dprob - jnp.transpose(delta, (0, 2, 1))[:, :, :, None]) * scale).astype(jnp.bfloat16)
    dqueries = jnp.einsum("chqk,ckhd->cqhd", dscore, keys, preferred_element_type=jnp.float32)
    dkeys = jnp.einsum("chqk,cqhd->ckhd", dscore, queries, preferred_element_type=jnp.float32)
    dvalues = jnp.einsum("chqk,cqhd->ckhd", probs_low, dattended_heads, preferred_element_type=jnp.float32)
    dmixed = jnp.concatenate(
        [dqueries.reshape(rows, width), dkeys.reshape(rows, width), dvalues.reshape(rows, width)], axis=1
    )
    query_bias_grad = jnp.sum(dmixed[:, :width], axis=0)
    value_bias_grad = jnp.sum(dmixed[:, 2 * width:], axis=0)
    dmixed_low = dmixed.astype(jnp.bfloat16)
    attention_grad = inner_rows(first_act, dmixed_low)
    dfirst = lax.dot_general(
        dmixed_low, attention_weight, (((1,), (1,)), ((), ())), preferred_element_type=jnp.float32
    )
    first_gain_grad = jnp.sum(dfirst * first_normed, axis=0)
    first_shift_grad = jnp.sum(dfirst, axis=0)
    input_grad = dresidual + norm_backward(dfirst, first_normed, first_inverse, first_gain)
    weight_grads = (attention_grad, output_grad, expand_grad, contract_grad)
    vector_grads = (first_gain_grad, first_shift_grad, query_bias_grad, value_bias_grad, output_bias_grad,
                    second_gain_grad, second_shift_grad, expand_bias_grad, contract_bias_grad)
    return (
        block_output.reshape(clip_count, frame_count, width),
        input_grad.reshape(clip_count, frame_count, width),
        weight_grads,
        vector_grads,
    )


PAIR = [(0, 1), (1, 0)]
OUTER = ("outer", "inner")


def core_pick(core, first, second):
    return jnp.where(core == 0, first, second)


def gather_weight(shard_rows, extra=None):
    parts = lax.axis_size("shard")
    core = lax.axis_index("core")
    rows, width = shard_rows.shape
    half = rows // 2
    mine = lax.dynamic_slice_in_dim(shard_rows, core * half, half, axis=0)
    if extra is not None:
        mine = jnp.concatenate([mine, extra], axis=0)
    mine = lax.all_gather(mine, "shard", axis=0, tiled=False)
    other = lax.ppermute(mine, "core", PAIR)
    first = core_pick(core, mine, other)
    second = core_pick(core, other, mine)
    full = jnp.stack([first[:, :half], second[:, :half]], axis=1).reshape(parts * rows, width)
    if extra is None:
        return full, None
    return full, first[:, half:]


def reduce_weight(grad, extra=None):
    parts = lax.axis_size("shard")
    core = lax.axis_index("core")
    width = grad.shape[1]
    rows = grad.shape[0] // parts
    half = rows // 2
    quarters = grad.reshape(parts, 2, half, width)
    keep = lax.dynamic_index_in_dim(quarters, core, axis=1, keepdims=False)
    send = lax.dynamic_index_in_dim(quarters, 1 - core, axis=1, keepdims=False)
    if extra is not None:
        on_first = (core == 0).astype(extra.dtype)
        keep = jnp.concatenate([keep, extra * on_first], axis=1)
        send = jnp.concatenate([send, extra * (1 - on_first)], axis=1)
    chip = keep + lax.ppermute(send, "core", PAIR)
    groups = lax.axis_size(OUTER)
    length = chip.shape[1]
    padded = -(-length // groups) * groups
    chip = jnp.pad(chip, ((0, 0), (0, padded - length), (0, 0)))
    chip = chip.reshape(parts * groups, padded // groups, width)
    piece = lax.psum_scatter(chip, ("shard",) + OUTER, scatter_dimension=0, tiled=False)
    total = lax.all_gather(piece, OUTER, axis=0, tiled=True)[:length]
    other = lax.ppermute(total, "core", PAIR)
    first = core_pick(core, total, other)
    second = core_pick(core, other, total)
    out = jnp.concatenate([first[:half], second[:half]], axis=0)
    if extra is None:
        return out, None
    return out, first[half:]


def clip_local(tokens, lengths, cotangent, *params):
    clip_count, slot_count, width = tokens.shape
    parts = lax.axis_size("shard")
    place = lax.axis_index("shard")
    own = clip_count // parts
    weight_shards = params[:4]
    vector_shards = params[4:]
    vector_row = jnp.concatenate([entry.reshape(-1) for entry in vector_shards])
    row_width = weight_shards[0].shape[1]
    pad = (-vector_row.shape[0]) % row_width
    vector_rows = jnp.pad(vector_row, (0, pad)).reshape(-1, row_width)
    attention_weight, vector_all = gather_weight(weight_shards[0], vector_rows)
    vector_all = vector_all.reshape(parts, -1)[:, : vector_row.shape[0]]
    vectors = []
    offset = 0
    for entry in vector_shards:
        size = entry.shape[0]
        vectors.append(vector_all[:, offset:offset + size].reshape(parts * size).astype(jnp.float32))
        offset += size
    weights = (
        attention_weight,
        gather_weight(weight_shards[1])[0],
        gather_weight(weight_shards[2])[0],
        gather_weight(weight_shards[3])[0],
    )
    tokens_clip = lax.all_to_all(tokens, "shard", 0, 1, tiled=True)
    cotangent_clip = lax.all_to_all(cotangent, "shard", 0, 1, tiled=True)
    lengths_clip = lax.dynamic_slice_in_dim(lengths, place * own, own, axis=0)
    block_output, input_grad, weight_grads, vector_grads = clip_layer(
        tokens_clip, lengths_clip, cotangent_clip, weights, vectors
    )
    block_output = lax.all_to_all(block_output, "shard", 1, 0, tiled=True)
    input_grad = lax.all_to_all(input_grad, "shard", 1, 0, tiled=True)
    contract_grad = weight_grads[3]
    contract_width = contract_grad.shape[1]
    vector_parts = jnp.concatenate([entry.reshape(parts, -1) for entry in vector_grads], axis=1)
    vector_size = vector_parts.shape[1]
    vpad = (-vector_size) % contract_width
    vector_parts = jnp.pad(vector_parts, ((0, 0), (0, vpad))).reshape(parts, -1, contract_width)
    contract_total, vector_total = reduce_weight(contract_grad, vector_parts)
    totals = (
        reduce_weight(weight_grads[0])[0],
        reduce_weight(weight_grads[1])[0],
        reduce_weight(weight_grads[2])[0],
        contract_total,
    )
    vector_total = vector_total.reshape(-1)[:vector_size]
    vector_outs = []
    offset = 0
    for entry in vector_shards:
        size = entry.shape[0]
        vector_outs.append(vector_total[offset:offset + size])
        offset += size
    return (block_output, input_grad) + totals + tuple(vector_outs)


def split_rep(mesh):
    devices = mesh.devices
    rep, parts = devices.shape
    first = devices[0, 0]
    stride = None
    for index in range(1, rep):
        other = devices[index, 0]
        if tuple(other.coords) == tuple(first.coords) and other.core_on_chip != first.core_on_chip:
            stride = index
            break
    if stride is None or rep % (2 * stride):
        return None
    grid = devices.reshape(rep // (2 * stride), 2, stride, parts)
    for spot in np.ndindex(grid.shape[0], grid.shape[2], grid.shape[3]):
        low = grid[spot[0], 0, spot[1], spot[2]]
        high = grid[spot[0], 1, spot[1], spot[2]]
        if tuple(low.coords) != tuple(high.coords) or low.core_on_chip == high.core_on_chip:
            return None
    return Mesh(grid, ("outer", "core", "inner", "shard"))


def solution(mesh):
    def specs(rep):
        ins = (P(rep, "shard", None), P(rep, None), P(rep, "shard", None)) + (P("shard", None),) * 4 + (
            P("shard"),
        ) * 9
        outs = (P(rep, "shard", None), P(rep, "shard", None)) + (P("shard", None),) * 4 + (P("shard"),) * 9
        return ins, outs

    ins, outs = specs("rep")
    plain = jax.shard_map(local, mesh=mesh, in_specs=ins, out_specs=outs, check_vma=False)
    split = split_rep(mesh)
    if split is None:
        return plain
    ins, outs = specs(("outer", "core", "inner"))
    fast = jax.shard_map(clip_local, mesh=split, in_specs=ins, out_specs=outs, check_vma=False)
    rep, parts = mesh.devices.shape

    def run(*args):
        if (args[0].shape[0] // rep) % parts == 0:
            return fast(*args)
        return plain(*args)

    return run
```

```python
import jax
import jax.numpy as jnp
from jax import lax
from jax.sharding import Mesh, PartitionSpec as P
import numpy as np

HEADS = 12
HEAD = 64


EPSILON = 1e-05
NEGATIVE = -1e30


def norm_forward(values, gain, shift):
    centred = values - jnp.mean(values, axis=-1, keepdims=True)
    inverse = lax.rsqrt(jnp.mean(centred * centred, axis=-1, keepdims=True) + EPSILON)
    normed = centred * inverse
    return (normed, inverse, (normed * gain + shift).astype(jnp.bfloat16))


def norm_backward(upstream, normed, inverse, gain):
    scaled = upstream * gain
    return inverse * (
        scaled
        - jnp.mean(scaled, axis=-1, keepdims=True)
        - normed * jnp.mean(scaled * normed, axis=-1, keepdims=True)
    )


def gelu_slope(values):
    return (
        0.5 * (1.0 + jax.scipy.special.erf(values * 0.7071067811865476))
        + values * jnp.exp(-0.5 * values * values) * 0.3989422804014327
    )


def inner_rows(left, right):
    return lax.dot_general(
        left, right, (((0,), (0,)), ((), ())), preferred_element_type=jnp.float32
    )


def heads_view(matrix):
    return matrix.reshape(matrix.shape[0], HEADS, HEAD)


def score_block(query_rows, key_rows, key_live):
    scores = jnp.einsum(
        "qhd,khd->hqk",
        heads_view(query_rows),
        heads_view(key_rows),
        preferred_element_type=jnp.float32,
    ) * HEAD ** (-0.5)
    return jnp.where(key_live[None, None, :], scores, NEGATIVE)


def attend_clip(items):
    query_rows, pair_rows, key_live = items
    width = query_rows.shape[1]
    scores = score_block(query_rows, pair_rows[:, :width], key_live)
    highest = jnp.max(scores, axis=-1, keepdims=True)
    logsum = highest + jnp.log(jnp.sum(jnp.exp(scores - highest), axis=-1, keepdims=True))
    probs_low = jnp.exp(scores - logsum).astype(jnp.bfloat16)
    attended = jnp.einsum(
        "hqk,khd->qhd",
        probs_low,
        heads_view(pair_rows[:, width:]),
        preferred_element_type=jnp.float32,
    )
    return (attended.reshape(query_rows.shape[0], width).astype(jnp.bfloat16), logsum[:, :, 0].T)


def score_grads(query_rows, dattended, logsum, delta, pair_rows, key_live):
    width = query_rows.shape[1]
    scores = score_block(query_rows, pair_rows[:, :width], key_live)
    probs = jnp.exp(scores - logsum.T[:, :, None])
    dprob = jnp.einsum(
        "qhd,khd->hqk",
        heads_view(dattended),
        heads_view(pair_rows[:, width:]),
        preferred_element_type=jnp.float32,
    )
    dscore = (probs * (dprob - delta.T[:, :, None]) * HEAD ** (-0.5)).astype(jnp.bfloat16)
    return (probs.astype(jnp.bfloat16), dscore)


def both_grads(items):
    query_rows, dattended, logsum, delta, pair_rows, key_live = items
    width = query_rows.shape[1]
    probs_low, dscore = score_grads(query_rows, dattended, logsum, delta, pair_rows, key_live)
    dqueries = jnp.einsum(
        "hqk,khd->qhd", dscore, heads_view(pair_rows[:, :width]), preferred_element_type=jnp.float32
    ).reshape(query_rows.shape[0], width)
    dkeys = jnp.einsum(
        "hqk,qhd->khd", dscore, heads_view(query_rows), preferred_element_type=jnp.float32
    )
    dvalues = jnp.einsum(
        "hqk,qhd->khd", probs_low, heads_view(dattended), preferred_element_type=jnp.float32
    )
    key_count = pair_rows.shape[0]
    return (
        dqueries,
        jnp.concatenate(
            [dkeys.reshape(key_count, width), dvalues.reshape(key_count, width)], axis=1
        ),
    )


def local(
    tokens,
    lengths,
    cotangent,
    attention_weight,
    output_weight,
    expand_weight,
    contract_weight,
    first_gain,
    first_shift,
    query_bias,
    value_bias,
    output_bias,
    second_gain,
    second_shift,
    expand_bias,
    contract_bias,
):
    clip_count, slot_count, width = tokens.shape
    parts = lax.axis_size("shard")
    frame_count = slot_count * parts
    place = lax.axis_index("shard")
    row_total = clip_count * slot_count
    gathered = (
        lax.all_gather(attention_weight, "shard", axis=0, tiled=True),
        lax.all_gather(output_weight, "shard", axis=0, tiled=True),
        lax.all_gather(expand_weight, "shard", axis=0, tiled=True),
        lax.all_gather(contract_weight, "shard", axis=0, tiled=True),
        lax.all_gather(first_gain, "shard", axis=0, tiled=True),
        lax.all_gather(first_shift, "shard", axis=0, tiled=True),
        lax.all_gather(query_bias, "shard", axis=0, tiled=True),
        lax.all_gather(value_bias, "shard", axis=0, tiled=True),
        lax.all_gather(output_bias, "shard", axis=0, tiled=True),
        lax.all_gather(second_gain, "shard", axis=0, tiled=True),
        lax.all_gather(second_shift, "shard", axis=0, tiled=True),
        lax.all_gather(expand_bias, "shard", axis=0, tiled=True),
        lax.all_gather(contract_bias, "shard", axis=0, tiled=True),
    )
    vectors = [entry.astype(jnp.float32) for entry in gathered[4:]]
    own_length = jnp.sum(jnp.where(jnp.arange(parts)[None, :] == place, lengths, 0), axis=1)
    row_live = jnp.arange(slot_count)[None, :] < own_length[:, None]
    key_live = (jnp.arange(slot_count)[None, None, :] < lengths[:, :, None]).reshape(
        clip_count, frame_count
    )
    inputs = tokens.reshape(row_total, width).astype(jnp.float32)
    first_normed, first_inverse, first_act = norm_forward(inputs, vectors[0], vectors[1])
    mixed = jnp.dot(first_act, gathered[0], preferred_element_type=jnp.float32)
    mixed = mixed + jnp.concatenate([vectors[2], jnp.zeros_like(vectors[2]), vectors[3]])
    mixed_low = mixed.astype(jnp.bfloat16)
    query_rows = mixed_low[:, :width].reshape(clip_count, slot_count, width)
    pair_own = mixed_low[:, width:].reshape(clip_count, slot_count, 2 * width)
    pair_all = lax.all_gather(pair_own, "shard", axis=1, tiled=True)
    attended, logsum = lax.map(attend_clip, (query_rows, pair_all, key_live))
    attended_flat = attended.reshape(row_total, width)
    residual = (
        inputs
        + jnp.dot(attended_flat, gathered[1], preferred_element_type=jnp.float32)
        + vectors[4]
    )
    second_normed, second_inverse, second_act = norm_forward(residual, vectors[5], vectors[6])
    pre = jnp.dot(second_act, gathered[2], preferred_element_type=jnp.float32) + vectors[7]
    hidden_act = jax.nn.gelu(pre, approximate=False).astype(jnp.bfloat16)
    block_output = (
        residual + jnp.dot(hidden_act, gathered[3], preferred_element_type=jnp.float32) + vectors[8]
    )
    backward = (
        lax.all_gather(attention_weight, "shard", axis=0, tiled=True),
        lax.all_gather(output_weight, "shard", axis=0, tiled=True),
        lax.all_gather(expand_weight, "shard", axis=0, tiled=True),
        lax.all_gather(contract_weight, "shard", axis=0, tiled=True),
        lax.all_gather(first_gain, "shard", axis=0, tiled=True),
        lax.all_gather(first_shift, "shard", axis=0, tiled=True),
        lax.all_gather(query_bias, "shard", axis=0, tiled=True),
        lax.all_gather(value_bias, "shard", axis=0, tiled=True),
        lax.all_gather(output_bias, "shard", axis=0, tiled=True),
        lax.all_gather(second_gain, "shard", axis=0, tiled=True),
        lax.all_gather(second_shift, "shard", axis=0, tiled=True),
        lax.all_gather(expand_bias, "shard", axis=0, tiled=True),
        lax.all_gather(contract_bias, "shard", axis=0, tiled=True),
    )
    back_vectors = [entry.astype(jnp.float32) for entry in backward[4:]]
    error = cotangent.reshape(row_total, width) * row_live.reshape(row_total, 1).astype(jnp.float32)
    error_low = error.astype(jnp.bfloat16)
    contract_bias_grad = jnp.sum(error, axis=0)
    contract_grad = inner_rows(hidden_act, error_low)
    dpre = lax.dot_general(
        error_low, backward[3], (((1,), (1,)), ((), ())), preferred_element_type=jnp.float32
    ) * gelu_slope(pre)
    expand_bias_grad = jnp.sum(dpre, axis=0)
    dpre_low = dpre.astype(jnp.bfloat16)
    expand_grad = inner_rows(second_act, dpre_low)
    dsecond = lax.dot_general(
        dpre_low, backward[2], (((1,), (1,)), ((), ())), preferred_element_type=jnp.float32
    )
    second_gain_grad = jnp.sum(dsecond * second_normed, axis=0)
    second_shift_grad = jnp.sum(dsecond, axis=0)
    dresidual = error + norm_backward(dsecond, second_normed, second_inverse, back_vectors[5])
    output_bias_grad = jnp.sum(dresidual, axis=0)
    dresidual_low = dresidual.astype(jnp.bfloat16)
    output_grad = inner_rows(attended_flat, dresidual_low)
    dattended = lax.dot_general(
        dresidual_low, backward[1], (((1,), (1,)), ((), ())), preferred_element_type=jnp.float32
    ).astype(jnp.bfloat16)
    delta = jnp.sum(
        heads_view(dattended.astype(jnp.float32)) * heads_view(attended_flat.astype(jnp.float32)),
        axis=-1,
    )
    delta = delta.reshape(clip_count, slot_count, HEADS)
    dattended_clips = dattended.reshape(clip_count, slot_count, width)
    dqueries, pair_terms = lax.map(
        both_grads, (query_rows, dattended_clips, logsum, delta, pair_all, key_live)
    )
    pair_grads = lax.psum_scatter(pair_terms, "shard", scatter_dimension=1, tiled=True)
    dqueries_flat = dqueries.reshape(row_total, width)
    pair_flat = pair_grads.reshape(row_total, 2 * width)
    dmixed = jnp.concatenate([dqueries_flat, pair_flat], axis=1)
    query_bias_grad = jnp.sum(dqueries_flat, axis=0)
    value_bias_grad = jnp.sum(pair_flat[:, width:], axis=0)
    dmixed_low = dmixed.astype(jnp.bfloat16)
    attention_grad = inner_rows(first_act, dmixed_low)
    dfirst = lax.dot_general(
        dmixed_low, backward[0], (((1,), (1,)), ((), ())), preferred_element_type=jnp.float32
    )
    first_gain_grad = jnp.sum(dfirst * first_normed, axis=0)
    first_shift_grad = jnp.sum(dfirst, axis=0)
    input_grad = dresidual + norm_backward(dfirst, first_normed, first_inverse, back_vectors[0])
    shares = (
        lax.psum_scatter(attention_grad, "shard", scatter_dimension=0, tiled=True),
        lax.psum_scatter(output_grad, "shard", scatter_dimension=0, tiled=True),
        lax.psum_scatter(expand_grad, "shard", scatter_dimension=0, tiled=True),
        lax.psum_scatter(contract_grad, "shard", scatter_dimension=0, tiled=True),
        lax.psum_scatter(first_gain_grad, "shard", scatter_dimension=0, tiled=True),
        lax.psum_scatter(first_shift_grad, "shard", scatter_dimension=0, tiled=True),
        lax.psum_scatter(query_bias_grad, "shard", scatter_dimension=0, tiled=True),
        lax.psum_scatter(value_bias_grad, "shard", scatter_dimension=0, tiled=True),
        lax.psum_scatter(output_bias_grad, "shard", scatter_dimension=0, tiled=True),
        lax.psum_scatter(second_gain_grad, "shard", scatter_dimension=0, tiled=True),
        lax.psum_scatter(second_shift_grad, "shard", scatter_dimension=0, tiled=True),
        lax.psum_scatter(expand_bias_grad, "shard", scatter_dimension=0, tiled=True),
        lax.psum_scatter(contract_bias_grad, "shard", scatter_dimension=0, tiled=True),
    )
    totals = lax.psum(
        (
            shares[0],
            shares[1],
            shares[2],
            shares[3],
            shares[4],
            shares[5],
            shares[6],
            shares[7],
            shares[8],
            shares[9],
            shares[10],
            shares[11],
            shares[12],
        ),
        "rep",
    )
    return (
        block_output.reshape(clip_count, slot_count, width),
        input_grad.reshape(clip_count, slot_count, width),
        totals[0],
        totals[1],
        totals[2],
        totals[3],
        totals[4],
        totals[5],
        totals[6],
        totals[7],
        totals[8],
        totals[9],
        totals[10],
        totals[11],
        totals[12],
    )


def clip_layer(tokens, lengths, cotangent, weights, vectors):
    attention_weight, output_weight, expand_weight, contract_weight = weights
    (first_gain, first_shift, query_bias, value_bias, output_bias, second_gain, second_shift,
     expand_bias, contract_bias) = vectors
    clip_count, frame_count, width = tokens.shape
    block_count = lengths.shape[1]
    slot_count = frame_count // block_count
    rows = clip_count * frame_count
    live = (jnp.arange(slot_count)[None, None, :] < lengths[:, :, None]).reshape(clip_count, frame_count)
    scale = HEAD ** (-0.5)
    inputs = tokens.reshape(rows, width).astype(jnp.float32)
    first_normed, first_inverse, first_act = norm_forward(inputs, first_gain, first_shift)
    mixed = jnp.dot(first_act, attention_weight, preferred_element_type=jnp.float32)
    mixed = mixed + jnp.concatenate([query_bias, jnp.zeros_like(query_bias), value_bias])
    mixed_low = mixed.astype(jnp.bfloat16).reshape(clip_count, frame_count, 3, HEADS, HEAD)
    queries = mixed_low[:, :, 0]
    keys = mixed_low[:, :, 1]
    values = mixed_low[:, :, 2]
    scores = jnp.einsum("cqhd,ckhd->chqk", queries, keys, preferred_element_type=jnp.float32) * scale
    scores = jnp.where(live[:, None, None, :], scores, NEGATIVE)
    highest = jnp.max(scores, axis=-1, keepdims=True)
    logsum = highest + jnp.log(jnp.sum(jnp.exp(scores - highest), axis=-1, keepdims=True))
    probs = jnp.exp(scores - logsum)
    probs_low = probs.astype(jnp.bfloat16)
    attended = jnp.einsum("chqk,ckhd->cqhd", probs_low, values, preferred_element_type=jnp.float32)
    attended_flat = attended.reshape(rows, width).astype(jnp.bfloat16)
    residual = inputs + jnp.dot(attended_flat, output_weight, preferred_element_type=jnp.float32) + output_bias
    second_normed, second_inverse, second_act = norm_forward(residual, second_gain, second_shift)
    pre = jnp.dot(second_act, expand_weight, preferred_element_type=jnp.float32) + expand_bias
    hidden_act = jax.nn.gelu(pre, approximate=False).astype(jnp.bfloat16)
    block_output = residual + jnp.dot(hidden_act, contract_weight, preferred_element_type=jnp.float32) + contract_bias
    error = cotangent.reshape(rows, width) * live.reshape(rows, 1).astype(jnp.float32)
    error_low = error.astype(jnp.bfloat16)
    contract_bias_grad = jnp.sum(error, axis=0)
    contract_grad = inner_rows(hidden_act, error_low)
    dpre = lax.dot_general(
        error_low, contract_weight, (((1,), (1,)), ((), ())), preferred_element_type=jnp.float32
    ) * gelu_slope(pre)
    expand_bias_grad = jnp.sum(dpre, axis=0)
    dpre_low = dpre.astype(jnp.bfloat16)
    expand_grad = inner_rows(second_act, dpre_low)
    dsecond = lax.dot_general(
        dpre_low, expand_weight, (((1,), (1,)), ((), ())), preferred_element_type=jnp.float32
    )
    second_gain_grad = jnp.sum(dsecond * second_normed, axis=0)
    second_shift_grad = jnp.sum(dsecond, axis=0)
    dresidual = error + norm_backward(dsecond, second_normed, second_inverse, second_gain)
    output_bias_grad = jnp.sum(dresidual, axis=0)
    dresidual_low = dresidual.astype(jnp.bfloat16)
    output_grad = inner_rows(attended_flat, dresidual_low)
    dattended = lax.dot_general(
        dresidual_low, output_weight, (((1,), (1,)), ((), ())), preferred_element_type=jnp.float32
    ).astype(jnp.bfloat16)
    dattended_heads = dattended.reshape(clip_count, frame_count, HEADS, HEAD)
    attended_heads = attended_flat.reshape(clip_count, frame_count, HEADS, HEAD)
    delta = jnp.sum(
        dattended_heads.astype(jnp.float32) * attended_heads.astype(jnp.float32), axis=-1
    )
    dprob = jnp.einsum("cqhd,ckhd->chqk", dattended_heads, values, preferred_element_type=jnp.float32)
    dscore = (probs * (dprob - jnp.transpose(delta, (0, 2, 1))[:, :, :, None]) * scale).astype(jnp.bfloat16)
    dqueries = jnp.einsum("chqk,ckhd->cqhd", dscore, keys, preferred_element_type=jnp.float32)
    dkeys = jnp.einsum("chqk,cqhd->ckhd", dscore, queries, preferred_element_type=jnp.float32)
    dvalues = jnp.einsum("chqk,cqhd->ckhd", probs_low, dattended_heads, preferred_element_type=jnp.float32)
    dmixed = jnp.concatenate(
        [dqueries.reshape(rows, width), dkeys.reshape(rows, width), dvalues.reshape(rows, width)], axis=1
    )
    query_bias_grad = jnp.sum(dmixed[:, :width], axis=0)
    value_bias_grad = jnp.sum(dmixed[:, 2 * width:], axis=0)
    dmixed_low = dmixed.astype(jnp.bfloat16)
    attention_grad = inner_rows(first_act, dmixed_low)
    dfirst = lax.dot_general(
        dmixed_low, attention_weight, (((1,), (1,)), ((), ())), preferred_element_type=jnp.float32
    )
    first_gain_grad = jnp.sum(dfirst * first_normed, axis=0)
    first_shift_grad = jnp.sum(dfirst, axis=0)
    input_grad = dresidual + norm_backward(dfirst, first_normed, first_inverse, first_gain)
    weight_grads = (attention_grad, output_grad, expand_grad, contract_grad)
    vector_grads = (first_gain_grad, first_shift_grad, query_bias_grad, value_bias_grad, output_bias_grad,
                    second_gain_grad, second_shift_grad, expand_bias_grad, contract_bias_grad)
    return (
        block_output.reshape(clip_count, frame_count, width),
        input_grad.reshape(clip_count, frame_count, width),
        weight_grads,
        vector_grads,
    )


PAIR = [(0, 1), (1, 0)]
OUTER = ("outer", "inner")


def core_pick(core, first, second):
    return jnp.where(core == 0, first, second)


def gather_weight(shard_rows, extra=None):
    parts = lax.axis_size("shard")
    core = lax.axis_index("core")
    rows, width = shard_rows.shape
    half = rows // 2
    mine = lax.dynamic_slice_in_dim(shard_rows, core * half, half, axis=0)
    if extra is not None:
        mine = jnp.concatenate([mine, extra], axis=0)
    mine = lax.all_gather(mine, "shard", axis=0, tiled=False)
    other = lax.ppermute(mine, "core", PAIR)
    first = core_pick(core, mine, other)
    second = core_pick(core, other, mine)
    full = jnp.stack([first[:, :half], second[:, :half]], axis=1).reshape(parts * rows, width)
    if extra is None:
        return full, None
    return full, first[:, half:]


def reduce_weight(grad, extra=None):
    parts = lax.axis_size("shard")
    core = lax.axis_index("core")
    width = grad.shape[1]
    rows = grad.shape[0] // parts
    half = rows // 2
    quarters = grad.reshape(parts, 2, half, width)
    keep = lax.dynamic_index_in_dim(quarters, core, axis=1, keepdims=False)
    send = lax.dynamic_index_in_dim(quarters, 1 - core, axis=1, keepdims=False)
    if extra is not None:
        on_first = (core == 0).astype(extra.dtype)
        keep = jnp.concatenate([keep, extra * on_first], axis=1)
        send = jnp.concatenate([send, extra * (1 - on_first)], axis=1)
    chip = keep + lax.ppermute(send, "core", PAIR)
    part = lax.psum_scatter(chip, "shard", scatter_dimension=0, tiled=False)
    if lax.axis_size("inner") > 1:
        part = lax.psum(part, "inner")
    total = line_sum(part)
    other = lax.ppermute(total, "core", PAIR)
    first = core_pick(core, total, other)
    second = core_pick(core, other, total)
    out = jnp.concatenate([first[:half], second[:half]], axis=0)
    if extra is None:
        return out, None
    return out, first[half:]


def line_sum(values):
    groups = lax.axis_size("outer")
    if groups == 1:
        return values
    if groups & (groups - 1):
        return lax.psum(values, "outer")
    here = lax.axis_index("outer")
    length = values.shape[0]
    padded = -(-length // groups) * groups
    held = jnp.pad(values, ((0, padded - length),) + ((0, 0),) * (values.ndim - 1))
    held = held.reshape((groups, padded // groups) + values.shape[1:])
    step = 1
    while step < groups:
        held = held.reshape((held.shape[0] // 2, 2) + held.shape[1:])
        bit = (here // step) % 2
        keep = lax.dynamic_index_in_dim(held, bit, axis=1, keepdims=False)
        send = lax.dynamic_index_in_dim(held, 1 - bit, axis=1, keepdims=False)
        held = keep + lax.ppermute(send, "outer", [(j, j ^ step) for j in range(groups)])
        step *= 2
    step = groups // 2
    while step >= 1:
        bit = (here // step) % 2
        other = lax.ppermute(held, "outer", [(j, j ^ step) for j in range(groups)])
        low = jnp.where(bit == 0, held, other)
        high = jnp.where(bit == 0, other, held)
        held = jnp.stack([low, high], axis=1)
        held = held.reshape((held.shape[0] * 2,) + held.shape[2:])
        step //= 2
    return held.reshape((padded,) + values.shape[1:])[:length]


def clip_local(tokens, lengths, cotangent, *params):
    clip_count, slot_count, width = tokens.shape
    parts = lax.axis_size("shard")
    place = lax.axis_index("shard")
    own = clip_count // parts
    weight_shards = params[:4]
    vector_shards = params[4:]
    vector_row = jnp.concatenate([entry.reshape(-1) for entry in vector_shards])
    row_width = weight_shards[0].shape[1]
    pad = (-vector_row.shape[0]) % row_width
    vector_rows = jnp.pad(vector_row, (0, pad)).reshape(-1, row_width)
    attention_weight, vector_all = gather_weight(weight_shards[0], vector_rows)
    vector_all = vector_all.reshape(parts, -1)[:, : vector_row.shape[0]]
    vectors = []
    offset = 0
    for entry in vector_shards:
        size = entry.shape[0]
        vectors.append(vector_all[:, offset:offset + size].reshape(parts * size).astype(jnp.float32))
        offset += size
    weights = (
        attention_weight,
        gather_weight(weight_shards[1])[0],
        gather_weight(weight_shards[2])[0],
        gather_weight(weight_shards[3])[0],
    )
    tokens_clip = lax.all_to_all(tokens, "shard", 0, 1, tiled=True)
    cotangent_clip = lax.all_to_all(cotangent, "shard", 0, 1, tiled=True)
    lengths_clip = lax.dynamic_slice_in_dim(lengths, place * own, own, axis=0)
    block_output, input_grad, weight_grads, vector_grads = clip_layer(
        tokens_clip, lengths_clip, cotangent_clip, weights, vectors
    )
    block_output = lax.all_to_all(block_output, "shard", 1, 0, tiled=True)
    input_grad = lax.all_to_all(input_grad, "shard", 1, 0, tiled=True)
    attention_grad = weight_grads[0]
    attention_width = attention_grad.shape[1]
    vector_parts = jnp.concatenate([entry.reshape(parts, -1) for entry in vector_grads], axis=1)
    vector_size = vector_parts.shape[1]
    vpad = (-vector_size) % attention_width
    vector_parts = jnp.pad(vector_parts, ((0, 0), (0, vpad))).reshape(parts, -1, attention_width)
    attention_total, vector_total = reduce_weight(attention_grad, vector_parts)
    totals = (
        attention_total,
        reduce_weight(weight_grads[1])[0],
        reduce_weight(weight_grads[2])[0],
        reduce_weight(weight_grads[3])[0],
    )
    vector_total = vector_total.reshape(-1)[:vector_size]
    vector_outs = []
    offset = 0
    for entry in vector_shards:
        size = entry.shape[0]
        vector_outs.append(vector_total[offset:offset + size])
        offset += size
    return (block_output, input_grad) + totals + tuple(vector_outs)


def split_rep(mesh):
    devices = mesh.devices
    rep, parts = devices.shape
    first = devices[0, 0]
    stride = None
    for index in range(1, rep):
        other = devices[index, 0]
        if tuple(other.coords) == tuple(first.coords) and other.core_on_chip != first.core_on_chip:
            stride = index
            break
    if stride is None or rep % (2 * stride):
        return None
    grid = devices.reshape(rep // (2 * stride), 2, stride, parts)
    for spot in np.ndindex(grid.shape[0], grid.shape[2], grid.shape[3]):
        low = grid[spot[0], 0, spot[1], spot[2]]
        high = grid[spot[0], 1, spot[1], spot[2]]
        if tuple(low.coords) != tuple(high.coords) or low.core_on_chip == high.core_on_chip:
            return None
    return Mesh(grid, ("outer", "core", "inner", "shard"))


def solution(mesh):
    def specs(rep):
        ins = (P(rep, "shard", None), P(rep, None), P(rep, "shard", None)) + (P("shard", None),) * 4 + (
            P("shard"),
        ) * 9
        outs = (P(rep, "shard", None), P(rep, "shard", None)) + (P("shard", None),) * 4 + (P("shard"),) * 9
        return ins, outs

    ins, outs = specs("rep")
    plain = jax.shard_map(local, mesh=mesh, in_specs=ins, out_specs=outs, check_vma=False)
    split = split_rep(mesh)
    if split is None:
        return plain
    ins, outs = specs(("outer", "core", "inner"))
    fast = jax.shard_map(clip_local, mesh=split, in_specs=ins, out_specs=outs, check_vma=False)
    rep, parts = mesh.devices.shape

    def run(*args):
        if (args[0].shape[0] // rep) % parts == 0:
            return fast(*args)
        return plain(*args)

    return run
```

```python
import jax
import jax.numpy as jnp
from jax import lax
from jax.sharding import Mesh, PartitionSpec as P
import numpy as np

HEADS = 12
HEAD = 64


EPSILON = 1e-05
NEGATIVE = -1e30


def norm_forward(values, gain, shift):
    centred = values - jnp.mean(values, axis=-1, keepdims=True)
    inverse = lax.rsqrt(jnp.mean(centred * centred, axis=-1, keepdims=True) + EPSILON)
    normed = centred * inverse
    return (normed, inverse, (normed * gain + shift).astype(jnp.bfloat16))


def norm_backward(upstream, normed, inverse, gain):
    scaled = upstream * gain
    return inverse * (
        scaled
        - jnp.mean(scaled, axis=-1, keepdims=True)
        - normed * jnp.mean(scaled * normed, axis=-1, keepdims=True)
    )


def gelu_slope(values):
    return (
        0.5 * (1.0 + jax.scipy.special.erf(values * 0.7071067811865476))
        + values * jnp.exp(-0.5 * values * values) * 0.3989422804014327
    )


def inner_rows(left, right):
    return lax.dot_general(
        left, right, (((0,), (0,)), ((), ())), preferred_element_type=jnp.float32
    )


def heads_view(matrix):
    return matrix.reshape(matrix.shape[0], HEADS, HEAD)


def score_block(query_rows, key_rows, key_live):
    scores = jnp.einsum(
        "qhd,khd->hqk",
        heads_view(query_rows),
        heads_view(key_rows),
        preferred_element_type=jnp.float32,
    ) * HEAD ** (-0.5)
    return jnp.where(key_live[None, None, :], scores, NEGATIVE)


def attend_clip(items):
    query_rows, pair_rows, key_live = items
    width = query_rows.shape[1]
    scores = score_block(query_rows, pair_rows[:, :width], key_live)
    highest = jnp.max(scores, axis=-1, keepdims=True)
    logsum = highest + jnp.log(jnp.sum(jnp.exp(scores - highest), axis=-1, keepdims=True))
    probs_low = jnp.exp(scores - logsum).astype(jnp.bfloat16)
    attended = jnp.einsum(
        "hqk,khd->qhd",
        probs_low,
        heads_view(pair_rows[:, width:]),
        preferred_element_type=jnp.float32,
    )
    return (attended.reshape(query_rows.shape[0], width).astype(jnp.bfloat16), logsum[:, :, 0].T)


def score_grads(query_rows, dattended, logsum, delta, pair_rows, key_live):
    width = query_rows.shape[1]
    scores = score_block(query_rows, pair_rows[:, :width], key_live)
    probs = jnp.exp(scores - logsum.T[:, :, None])
    dprob = jnp.einsum(
        "qhd,khd->hqk",
        heads_view(dattended),
        heads_view(pair_rows[:, width:]),
        preferred_element_type=jnp.float32,
    )
    dscore = (probs * (dprob - delta.T[:, :, None]) * HEAD ** (-0.5)).astype(jnp.bfloat16)
    return (probs.astype(jnp.bfloat16), dscore)


def both_grads(items):
    query_rows, dattended, logsum, delta, pair_rows, key_live = items
    width = query_rows.shape[1]
    probs_low, dscore = score_grads(query_rows, dattended, logsum, delta, pair_rows, key_live)
    dqueries = jnp.einsum(
        "hqk,khd->qhd", dscore, heads_view(pair_rows[:, :width]), preferred_element_type=jnp.float32
    ).reshape(query_rows.shape[0], width)
    dkeys = jnp.einsum(
        "hqk,qhd->khd", dscore, heads_view(query_rows), preferred_element_type=jnp.float32
    )
    dvalues = jnp.einsum(
        "hqk,qhd->khd", probs_low, heads_view(dattended), preferred_element_type=jnp.float32
    )
    key_count = pair_rows.shape[0]
    return (
        dqueries,
        jnp.concatenate(
            [dkeys.reshape(key_count, width), dvalues.reshape(key_count, width)], axis=1
        ),
    )


def local(
    tokens,
    lengths,
    cotangent,
    attention_weight,
    output_weight,
    expand_weight,
    contract_weight,
    first_gain,
    first_shift,
    query_bias,
    value_bias,
    output_bias,
    second_gain,
    second_shift,
    expand_bias,
    contract_bias,
):
    clip_count, slot_count, width = tokens.shape
    parts = lax.axis_size("shard")
    frame_count = slot_count * parts
    place = lax.axis_index("shard")
    row_total = clip_count * slot_count
    gathered = (
        lax.all_gather(attention_weight, "shard", axis=0, tiled=True),
        lax.all_gather(output_weight, "shard", axis=0, tiled=True),
        lax.all_gather(expand_weight, "shard", axis=0, tiled=True),
        lax.all_gather(contract_weight, "shard", axis=0, tiled=True),
        lax.all_gather(first_gain, "shard", axis=0, tiled=True),
        lax.all_gather(first_shift, "shard", axis=0, tiled=True),
        lax.all_gather(query_bias, "shard", axis=0, tiled=True),
        lax.all_gather(value_bias, "shard", axis=0, tiled=True),
        lax.all_gather(output_bias, "shard", axis=0, tiled=True),
        lax.all_gather(second_gain, "shard", axis=0, tiled=True),
        lax.all_gather(second_shift, "shard", axis=0, tiled=True),
        lax.all_gather(expand_bias, "shard", axis=0, tiled=True),
        lax.all_gather(contract_bias, "shard", axis=0, tiled=True),
    )
    vectors = [entry.astype(jnp.float32) for entry in gathered[4:]]
    own_length = jnp.sum(jnp.where(jnp.arange(parts)[None, :] == place, lengths, 0), axis=1)
    row_live = jnp.arange(slot_count)[None, :] < own_length[:, None]
    key_live = (jnp.arange(slot_count)[None, None, :] < lengths[:, :, None]).reshape(
        clip_count, frame_count
    )
    inputs = tokens.reshape(row_total, width).astype(jnp.float32)
    first_normed, first_inverse, first_act = norm_forward(inputs, vectors[0], vectors[1])
    mixed = jnp.dot(first_act, gathered[0], preferred_element_type=jnp.float32)
    mixed = mixed + jnp.concatenate([vectors[2], jnp.zeros_like(vectors[2]), vectors[3]])
    mixed_low = mixed.astype(jnp.bfloat16)
    query_rows = mixed_low[:, :width].reshape(clip_count, slot_count, width)
    pair_own = mixed_low[:, width:].reshape(clip_count, slot_count, 2 * width)
    pair_all = lax.all_gather(pair_own, "shard", axis=1, tiled=True)
    attended, logsum = lax.map(attend_clip, (query_rows, pair_all, key_live))
    attended_flat = attended.reshape(row_total, width)
    residual = (
        inputs
        + jnp.dot(attended_flat, gathered[1], preferred_element_type=jnp.float32)
        + vectors[4]
    )
    second_normed, second_inverse, second_act = norm_forward(residual, vectors[5], vectors[6])
    pre = jnp.dot(second_act, gathered[2], preferred_element_type=jnp.float32) + vectors[7]
    hidden_act = jax.nn.gelu(pre, approximate=False).astype(jnp.bfloat16)
    block_output = (
        residual + jnp.dot(hidden_act, gathered[3], preferred_element_type=jnp.float32) + vectors[8]
    )
    backward = (
        lax.all_gather(attention_weight, "shard", axis=0, tiled=True),
        lax.all_gather(output_weight, "shard", axis=0, tiled=True),
        lax.all_gather(expand_weight, "shard", axis=0, tiled=True),
        lax.all_gather(contract_weight, "shard", axis=0, tiled=True),
        lax.all_gather(first_gain, "shard", axis=0, tiled=True),
        lax.all_gather(first_shift, "shard", axis=0, tiled=True),
        lax.all_gather(query_bias, "shard", axis=0, tiled=True),
        lax.all_gather(value_bias, "shard", axis=0, tiled=True),
        lax.all_gather(output_bias, "shard", axis=0, tiled=True),
        lax.all_gather(second_gain, "shard", axis=0, tiled=True),
        lax.all_gather(second_shift, "shard", axis=0, tiled=True),
        lax.all_gather(expand_bias, "shard", axis=0, tiled=True),
        lax.all_gather(contract_bias, "shard", axis=0, tiled=True),
    )
    back_vectors = [entry.astype(jnp.float32) for entry in backward[4:]]
    error = cotangent.reshape(row_total, width) * row_live.reshape(row_total, 1).astype(jnp.float32)
    error_low = error.astype(jnp.bfloat16)
    contract_bias_grad = jnp.sum(error, axis=0)
    contract_grad = inner_rows(hidden_act, error_low)
    dpre = lax.dot_general(
        error_low, backward[3], (((1,), (1,)), ((), ())), preferred_element_type=jnp.float32
    ) * gelu_slope(pre)
    expand_bias_grad = jnp.sum(dpre, axis=0)
    dpre_low = dpre.astype(jnp.bfloat16)
    expand_grad = inner_rows(second_act, dpre_low)
    dsecond = lax.dot_general(
        dpre_low, backward[2], (((1,), (1,)), ((), ())), preferred_element_type=jnp.float32
    )
    second_gain_grad = jnp.sum(dsecond * second_normed, axis=0)
    second_shift_grad = jnp.sum(dsecond, axis=0)
    dresidual = error + norm_backward(dsecond, second_normed, second_inverse, back_vectors[5])
    output_bias_grad = jnp.sum(dresidual, axis=0)
    dresidual_low = dresidual.astype(jnp.bfloat16)
    output_grad = inner_rows(attended_flat, dresidual_low)
    dattended = lax.dot_general(
        dresidual_low, backward[1], (((1,), (1,)), ((), ())), preferred_element_type=jnp.float32
    ).astype(jnp.bfloat16)
    delta = jnp.sum(
        heads_view(dattended.astype(jnp.float32)) * heads_view(attended_flat.astype(jnp.float32)),
        axis=-1,
    )
    delta = delta.reshape(clip_count, slot_count, HEADS)
    dattended_clips = dattended.reshape(clip_count, slot_count, width)
    dqueries, pair_terms = lax.map(
        both_grads, (query_rows, dattended_clips, logsum, delta, pair_all, key_live)
    )
    pair_grads = lax.psum_scatter(pair_terms, "shard", scatter_dimension=1, tiled=True)
    dqueries_flat = dqueries.reshape(row_total, width)
    pair_flat = pair_grads.reshape(row_total, 2 * width)
    dmixed = jnp.concatenate([dqueries_flat, pair_flat], axis=1)
    query_bias_grad = jnp.sum(dqueries_flat, axis=0)
    value_bias_grad = jnp.sum(pair_flat[:, width:], axis=0)
    dmixed_low = dmixed.astype(jnp.bfloat16)
    attention_grad = inner_rows(first_act, dmixed_low)
    dfirst = lax.dot_general(
        dmixed_low, backward[0], (((1,), (1,)), ((), ())), preferred_element_type=jnp.float32
    )
    first_gain_grad = jnp.sum(dfirst * first_normed, axis=0)
    first_shift_grad = jnp.sum(dfirst, axis=0)
    input_grad = dresidual + norm_backward(dfirst, first_normed, first_inverse, back_vectors[0])
    shares = (
        lax.psum_scatter(attention_grad, "shard", scatter_dimension=0, tiled=True),
        lax.psum_scatter(output_grad, "shard", scatter_dimension=0, tiled=True),
        lax.psum_scatter(expand_grad, "shard", scatter_dimension=0, tiled=True),
        lax.psum_scatter(contract_grad, "shard", scatter_dimension=0, tiled=True),
        lax.psum_scatter(first_gain_grad, "shard", scatter_dimension=0, tiled=True),
        lax.psum_scatter(first_shift_grad, "shard", scatter_dimension=0, tiled=True),
        lax.psum_scatter(query_bias_grad, "shard", scatter_dimension=0, tiled=True),
        lax.psum_scatter(value_bias_grad, "shard", scatter_dimension=0, tiled=True),
        lax.psum_scatter(output_bias_grad, "shard", scatter_dimension=0, tiled=True),
        lax.psum_scatter(second_gain_grad, "shard", scatter_dimension=0, tiled=True),
        lax.psum_scatter(second_shift_grad, "shard", scatter_dimension=0, tiled=True),
        lax.psum_scatter(expand_bias_grad, "shard", scatter_dimension=0, tiled=True),
        lax.psum_scatter(contract_bias_grad, "shard", scatter_dimension=0, tiled=True),
    )
    totals = lax.psum(
        (
            shares[0],
            shares[1],
            shares[2],
            shares[3],
            shares[4],
            shares[5],
            shares[6],
            shares[7],
            shares[8],
            shares[9],
            shares[10],
            shares[11],
            shares[12],
        ),
        "rep",
    )
    return (
        block_output.reshape(clip_count, slot_count, width),
        input_grad.reshape(clip_count, slot_count, width),
        totals[0],
        totals[1],
        totals[2],
        totals[3],
        totals[4],
        totals[5],
        totals[6],
        totals[7],
        totals[8],
        totals[9],
        totals[10],
        totals[11],
        totals[12],
    )


def clip_layer(tokens, lengths, cotangent, weights, vectors):
    attention_weight, output_weight, later_weights = weights
    (first_gain, first_shift, query_bias, value_bias, output_bias, second_gain, second_shift,
     expand_bias, contract_bias) = vectors
    clip_count, frame_count, width = tokens.shape
    block_count = lengths.shape[1]
    slot_count = frame_count // block_count
    rows = clip_count * frame_count
    live = (jnp.arange(slot_count)[None, None, :] < lengths[:, :, None]).reshape(clip_count, frame_count)
    scale = HEAD ** (-0.5)
    inputs = tokens.reshape(rows, width).astype(jnp.float32)
    first_normed, first_inverse, first_act = norm_forward(inputs, first_gain, first_shift)
    mixed = jnp.dot(first_act, attention_weight, preferred_element_type=jnp.float32)
    mixed = mixed + jnp.concatenate([query_bias, jnp.zeros_like(query_bias), value_bias])
    mixed_low = mixed.astype(jnp.bfloat16).reshape(clip_count, frame_count, 3, HEADS, HEAD)
    expand_weight, contract_weight = later_weights(mixed_low[0, 0, 0, 0, :1])
    queries = mixed_low[:, :, 0]
    keys = mixed_low[:, :, 1]
    values = mixed_low[:, :, 2]
    scores = jnp.einsum("cqhd,ckhd->chqk", queries, keys, preferred_element_type=jnp.float32) * scale
    scores = jnp.where(live[:, None, None, :], scores, NEGATIVE)
    highest = jnp.max(scores, axis=-1, keepdims=True)
    logsum = highest + jnp.log(jnp.sum(jnp.exp(scores - highest), axis=-1, keepdims=True))
    probs = jnp.exp(scores - logsum)
    probs_low = probs.astype(jnp.bfloat16)
    attended = jnp.einsum("chqk,ckhd->cqhd", probs_low, values, preferred_element_type=jnp.float32)
    attended_flat = attended.reshape(rows, width).astype(jnp.bfloat16)
    residual = inputs + jnp.dot(attended_flat, output_weight, preferred_element_type=jnp.float32) + output_bias
    second_normed, second_inverse, second_act = norm_forward(residual, second_gain, second_shift)
    pre = jnp.dot(second_act, expand_weight, preferred_element_type=jnp.float32) + expand_bias
    hidden_act = jax.nn.gelu(pre, approximate=False).astype(jnp.bfloat16)
    block_output = residual + jnp.dot(hidden_act, contract_weight, preferred_element_type=jnp.float32) + contract_bias
    error = cotangent.reshape(rows, width) * live.reshape(rows, 1).astype(jnp.float32)
    error_low = error.astype(jnp.bfloat16)
    contract_bias_grad = jnp.sum(error, axis=0)
    contract_grad = inner_rows(hidden_act, error_low)
    contract_grad, error_low = lax.optimization_barrier((contract_grad, error_low))
    dpre = lax.dot_general(
        error_low, contract_weight, (((1,), (1,)), ((), ())), preferred_element_type=jnp.float32
    ) * gelu_slope(pre)
    expand_bias_grad = jnp.sum(dpre, axis=0)
    dpre_low = dpre.astype(jnp.bfloat16)
    expand_grad = inner_rows(second_act, dpre_low)
    expand_grad, dpre_low = lax.optimization_barrier((expand_grad, dpre_low))
    dsecond = lax.dot_general(
        dpre_low, expand_weight, (((1,), (1,)), ((), ())), preferred_element_type=jnp.float32
    )
    second_gain_grad = jnp.sum(dsecond * second_normed, axis=0)
    second_shift_grad = jnp.sum(dsecond, axis=0)
    dresidual = error + norm_backward(dsecond, second_normed, second_inverse, second_gain)
    output_bias_grad = jnp.sum(dresidual, axis=0)
    dresidual_low = dresidual.astype(jnp.bfloat16)
    output_grad = inner_rows(attended_flat, dresidual_low)
    output_grad, dresidual_low = lax.optimization_barrier((output_grad, dresidual_low))
    dattended = lax.dot_general(
        dresidual_low, output_weight, (((1,), (1,)), ((), ())), preferred_element_type=jnp.float32
    ).astype(jnp.bfloat16)
    dattended_heads = dattended.reshape(clip_count, frame_count, HEADS, HEAD)
    attended_heads = attended_flat.reshape(clip_count, frame_count, HEADS, HEAD)
    delta = jnp.sum(
        dattended_heads.astype(jnp.float32) * attended_heads.astype(jnp.float32), axis=-1
    )
    dprob = jnp.einsum("cqhd,ckhd->chqk", dattended_heads, values, preferred_element_type=jnp.float32)
    dscore = (probs * (dprob - jnp.transpose(delta, (0, 2, 1))[:, :, :, None]) * scale).astype(jnp.bfloat16)
    dqueries = jnp.einsum("chqk,ckhd->cqhd", dscore, keys, preferred_element_type=jnp.float32)
    dkeys = jnp.einsum("chqk,cqhd->ckhd", dscore, queries, preferred_element_type=jnp.float32)
    dvalues = jnp.einsum("chqk,cqhd->ckhd", probs_low, dattended_heads, preferred_element_type=jnp.float32)
    dmixed = jnp.concatenate(
        [dqueries.reshape(rows, width), dkeys.reshape(rows, width), dvalues.reshape(rows, width)], axis=1
    )
    query_bias_grad = jnp.sum(dmixed[:, :width], axis=0)
    value_bias_grad = jnp.sum(dmixed[:, 2 * width:], axis=0)
    dmixed_low = dmixed.astype(jnp.bfloat16)
    attention_grad = inner_rows(first_act, dmixed_low)
    dfirst = lax.dot_general(
        dmixed_low, attention_weight, (((1,), (1,)), ((), ())), preferred_element_type=jnp.float32
    )
    first_gain_grad = jnp.sum(dfirst * first_normed, axis=0)
    first_shift_grad = jnp.sum(dfirst, axis=0)
    input_grad = dresidual + norm_backward(dfirst, first_normed, first_inverse, first_gain)
    weight_grads = (attention_grad, output_grad, expand_grad, contract_grad)
    vector_grads = (first_gain_grad, first_shift_grad, query_bias_grad, value_bias_grad, output_bias_grad,
                    second_gain_grad, second_shift_grad, expand_bias_grad, contract_bias_grad)
    return (
        block_output.reshape(clip_count, frame_count, width),
        input_grad.reshape(clip_count, frame_count, width),
        weight_grads,
        vector_grads,
    )


PAIR = [(0, 1), (1, 0)]
OUTER = ("outer", "inner")


def core_pick(core, first, second):
    return jnp.where(core == 0, first, second)


def gather_weight(shard_rows, extra=None):
    parts = lax.axis_size("shard")
    core = lax.axis_index("core")
    rows, width = shard_rows.shape
    half = rows // 2
    mine = lax.dynamic_slice_in_dim(shard_rows, core * half, half, axis=0)
    if extra is not None:
        mine = jnp.concatenate([mine, extra], axis=0)
    mine = lax.all_gather(mine, "shard", axis=0, tiled=False)
    other = lax.ppermute(mine, "core", PAIR)
    first = core_pick(core, mine, other)
    second = core_pick(core, other, mine)
    full = jnp.stack([first[:, :half], second[:, :half]], axis=1).reshape(parts * rows, width)
    if extra is None:
        return full, None
    return full, first[:, half:]


def reduce_weight(grad, extra=None):
    parts = lax.axis_size("shard")
    core = lax.axis_index("core")
    width = grad.shape[1]
    rows = grad.shape[0] // parts
    half = rows // 2
    quarters = grad.reshape(parts, 2, half, width)
    keep = lax.dynamic_index_in_dim(quarters, core, axis=1, keepdims=False)
    send = lax.dynamic_index_in_dim(quarters, 1 - core, axis=1, keepdims=False)
    if extra is not None:
        on_first = (core == 0).astype(extra.dtype)
        keep = jnp.concatenate([keep, extra * on_first], axis=1)
        send = jnp.concatenate([send, extra * (1 - on_first)], axis=1)
    chip = keep + lax.ppermute(send, "core", PAIR)
    part = lax.psum_scatter(chip, "shard", scatter_dimension=0, tiled=False)
    if lax.axis_size("inner") > 1:
        part = lax.psum(part, "inner")
    total = line_sum(part)
    other = lax.ppermute(total, "core", PAIR)
    first = core_pick(core, total, other)
    second = core_pick(core, other, total)
    out = jnp.concatenate([first[:half], second[:half]], axis=0)
    if extra is None:
        return out, None
    return out, first[half:]


def line_sum(values):
    groups = lax.axis_size("outer")
    if groups == 1:
        return values
    if groups & (groups - 1):
        return lax.psum(values, "outer")
    here = lax.axis_index("outer")
    length = values.shape[0]
    padded = -(-length // groups) * groups
    held = jnp.pad(values, ((0, padded - length),) + ((0, 0),) * (values.ndim - 1))
    held = held.reshape((groups, padded // groups) + values.shape[1:])
    step = 1
    while step < groups:
        held = held.reshape((held.shape[0] // 2, 2) + held.shape[1:])
        bit = (here // step) % 2
        keep = lax.dynamic_index_in_dim(held, bit, axis=1, keepdims=False)
        send = lax.dynamic_index_in_dim(held, 1 - bit, axis=1, keepdims=False)
        held = keep + lax.ppermute(send, "outer", [(j, j ^ step) for j in range(groups)])
        step *= 2
    step = groups // 2
    while step >= 1:
        bit = (here // step) % 2
        other = lax.ppermute(held, "outer", [(j, j ^ step) for j in range(groups)])
        low = jnp.where(bit == 0, held, other)
        high = jnp.where(bit == 0, other, held)
        held = jnp.stack([low, high], axis=1)
        held = held.reshape((held.shape[0] * 2,) + held.shape[2:])
        step //= 2
    return held.reshape((padded,) + values.shape[1:])[:length]


def gather_packed(blocks, after=None):
    core = lax.axis_index("core")
    mine = lax.all_gather(jnp.concatenate(blocks, axis=0), "shard", axis=0, tiled=False)
    if after is not None:
        mine = mine + (after * 0).astype(mine.dtype)
    other = lax.ppermute(mine, "core", PAIR)
    return core_pick(core, mine, other), core_pick(core, other, mine)


def unpack_rows(first, second, begin, count, shape):
    parts = first.shape[0]
    rows, width = shape
    low = first[:, begin:begin + count].reshape(parts, -1, width)
    high = second[:, begin:begin + count].reshape(parts, -1, width)
    return jnp.stack([low, high], axis=1).reshape(rows, width)


def core_half(shard_rows):
    core = lax.axis_index("core")
    half = shard_rows.shape[0] // 2
    return lax.dynamic_slice_in_dim(shard_rows, core * half, half, axis=0)


def clip_local(tokens, lengths, cotangent, *params):
    clip_count, slot_count, width = tokens.shape
    parts = lax.axis_size("shard")
    place = lax.axis_index("shard")
    own = clip_count // parts
    weight_shards = params[:4]
    vector_shards = params[4:]
    wide = weight_shards[0].shape[1]
    vector_row = jnp.concatenate([entry.reshape(-1) for entry in vector_shards])
    pad = (-vector_row.shape[0]) % wide
    vector_rows = jnp.pad(vector_row, (0, pad)).reshape(-1, wide)
    attention_half = core_half(weight_shards[0])
    output_half = core_half(weight_shards[1]).reshape(-1, wide)
    first, second = gather_packed([attention_half, output_half, vector_rows])
    a_rows = attention_half.shape[0]
    o_rows = output_half.shape[0]
    attention_weight = unpack_rows(first, second, 0, a_rows, (parts * weight_shards[0].shape[0], wide))
    output_weight = unpack_rows(
        first, second, a_rows, o_rows, (parts * weight_shards[1].shape[0], weight_shards[1].shape[1])
    )
    vector_all = first[:, a_rows + o_rows:].reshape(parts, -1)[:, : vector_row.shape[0]]
    vectors = []
    offset = 0
    for entry in vector_shards:
        size = entry.shape[0]
        vectors.append(vector_all[:, offset:offset + size].reshape(parts * size).astype(jnp.float32))
        offset += size
    late = weight_shards[2].shape[1]
    expand_half = core_half(weight_shards[2])
    contract_half = core_half(weight_shards[3]).reshape(-1, late)

    def later_weights(after):
        first_b, second_b = gather_packed([expand_half, contract_half], after)
        e_rows = expand_half.shape[0]
        expand_weight = unpack_rows(first_b, second_b, 0, e_rows, (parts * weight_shards[2].shape[0], late))
        contract_weight = unpack_rows(
            first_b, second_b, e_rows, contract_half.shape[0],
            (parts * weight_shards[3].shape[0], weight_shards[3].shape[1]),
        )
        return expand_weight, contract_weight

    weights = (attention_weight, output_weight, later_weights)
    tokens_clip = lax.all_to_all(tokens, "shard", 0, 1, tiled=True)
    cotangent_clip = lax.all_to_all(cotangent, "shard", 0, 1, tiled=True)
    lengths_clip = lax.dynamic_slice_in_dim(lengths, place * own, own, axis=0)
    block_output, input_grad, weight_grads, vector_grads = clip_layer(
        tokens_clip, lengths_clip, cotangent_clip, weights, vectors
    )
    block_output = lax.all_to_all(block_output, "shard", 1, 0, tiled=True)
    input_grad = lax.all_to_all(input_grad, "shard", 1, 0, tiled=True)
    attention_grad = weight_grads[0]
    attention_width = attention_grad.shape[1]
    vector_parts = jnp.concatenate([entry.reshape(parts, -1) for entry in vector_grads], axis=1)
    vector_size = vector_parts.shape[1]
    vpad = (-vector_size) % attention_width
    vector_parts = jnp.pad(vector_parts, ((0, 0), (0, vpad))).reshape(parts, -1, attention_width)
    attention_total, vector_total = reduce_weight(attention_grad, vector_parts)
    totals = (
        attention_total,
        reduce_weight(weight_grads[1])[0],
        reduce_weight(weight_grads[2])[0],
        reduce_weight(weight_grads[3])[0],
    )
    vector_total = vector_total.reshape(-1)[:vector_size]
    vector_outs = []
    offset = 0
    for entry in vector_shards:
        size = entry.shape[0]
        vector_outs.append(vector_total[offset:offset + size])
        offset += size
    return (block_output, input_grad) + totals + tuple(vector_outs)


def split_rep(mesh):
    devices = mesh.devices
    rep, parts = devices.shape
    first = devices[0, 0]
    stride = None
    for index in range(1, rep):
        other = devices[index, 0]
        if tuple(other.coords) == tuple(first.coords) and other.core_on_chip != first.core_on_chip:
            stride = index
            break
    if stride is None or rep % (2 * stride):
        return None
    grid = devices.reshape(rep // (2 * stride), 2, stride, parts)
    for spot in np.ndindex(grid.shape[0], grid.shape[2], grid.shape[3]):
        low = grid[spot[0], 0, spot[1], spot[2]]
        high = grid[spot[0], 1, spot[1], spot[2]]
        if tuple(low.coords) != tuple(high.coords) or low.core_on_chip == high.core_on_chip:
            return None
    return Mesh(grid, ("outer", "core", "inner", "shard"))


def solution(mesh):
    def specs(rep):
        ins = (P(rep, "shard", None), P(rep, None), P(rep, "shard", None)) + (P("shard", None),) * 4 + (
            P("shard"),
        ) * 9
        outs = (P(rep, "shard", None), P(rep, "shard", None)) + (P("shard", None),) * 4 + (P("shard"),) * 9
        return ins, outs

    ins, outs = specs("rep")
    plain = jax.shard_map(local, mesh=mesh, in_specs=ins, out_specs=outs, check_vma=False)
    split = split_rep(mesh)
    if split is None:
        return plain
    ins, outs = specs(("outer", "core", "inner"))
    fast = jax.shard_map(clip_local, mesh=split, in_specs=ins, out_specs=outs, check_vma=False)
    rep, parts = mesh.devices.shape

    def run(*args):
        if (args[0].shape[0] // rep) % parts == 0:
            return fast(*args)
        return plain(*args)

    return run
```

```python
import jax
import jax.numpy as jnp
from jax import lax
from jax.sharding import Mesh, PartitionSpec as P
import numpy as np

HEADS = 12
HEAD = 64


EPSILON = 1e-05
NEGATIVE = -1e30


def norm_forward(values, gain, shift):
    centred = values - jnp.mean(values, axis=-1, keepdims=True)
    inverse = lax.rsqrt(jnp.mean(centred * centred, axis=-1, keepdims=True) + EPSILON)
    normed = centred * inverse
    return (normed, inverse, (normed * gain + shift).astype(jnp.bfloat16))


def norm_backward(upstream, normed, inverse, gain):
    scaled = upstream * gain
    return inverse * (
        scaled
        - jnp.mean(scaled, axis=-1, keepdims=True)
        - normed * jnp.mean(scaled * normed, axis=-1, keepdims=True)
    )


def gelu_slope(values):
    return (
        0.5 * (1.0 + jax.scipy.special.erf(values * 0.7071067811865476))
        + values * jnp.exp(-0.5 * values * values) * 0.3989422804014327
    )


def inner_rows(left, right):
    return lax.dot_general(
        left, right, (((0,), (0,)), ((), ())), preferred_element_type=jnp.float32
    )


def heads_view(matrix):
    return matrix.reshape(matrix.shape[0], HEADS, HEAD)


def score_block(query_rows, key_rows, key_live):
    scores = jnp.einsum(
        "qhd,khd->hqk",
        heads_view(query_rows),
        heads_view(key_rows),
        preferred_element_type=jnp.float32,
    ) * HEAD ** (-0.5)
    return jnp.where(key_live[None, None, :], scores, NEGATIVE)


def attend_clip(items):
    query_rows, pair_rows, key_live = items
    width = query_rows.shape[1]
    scores = score_block(query_rows, pair_rows[:, :width], key_live)
    highest = jnp.max(scores, axis=-1, keepdims=True)
    logsum = highest + jnp.log(jnp.sum(jnp.exp(scores - highest), axis=-1, keepdims=True))
    probs_low = jnp.exp(scores - logsum).astype(jnp.bfloat16)
    attended = jnp.einsum(
        "hqk,khd->qhd",
        probs_low,
        heads_view(pair_rows[:, width:]),
        preferred_element_type=jnp.float32,
    )
    return (attended.reshape(query_rows.shape[0], width).astype(jnp.bfloat16), logsum[:, :, 0].T)


def score_grads(query_rows, dattended, logsum, delta, pair_rows, key_live):
    width = query_rows.shape[1]
    scores = score_block(query_rows, pair_rows[:, :width], key_live)
    probs = jnp.exp(scores - logsum.T[:, :, None])
    dprob = jnp.einsum(
        "qhd,khd->hqk",
        heads_view(dattended),
        heads_view(pair_rows[:, width:]),
        preferred_element_type=jnp.float32,
    )
    dscore = (probs * (dprob - delta.T[:, :, None]) * HEAD ** (-0.5)).astype(jnp.bfloat16)
    return (probs.astype(jnp.bfloat16), dscore)


def both_grads(items):
    query_rows, dattended, logsum, delta, pair_rows, key_live = items
    width = query_rows.shape[1]
    probs_low, dscore = score_grads(query_rows, dattended, logsum, delta, pair_rows, key_live)
    dqueries = jnp.einsum(
        "hqk,khd->qhd", dscore, heads_view(pair_rows[:, :width]), preferred_element_type=jnp.float32
    ).reshape(query_rows.shape[0], width)
    dkeys = jnp.einsum(
        "hqk,qhd->khd", dscore, heads_view(query_rows), preferred_element_type=jnp.float32
    )
    dvalues = jnp.einsum(
        "hqk,qhd->khd", probs_low, heads_view(dattended), preferred_element_type=jnp.float32
    )
    key_count = pair_rows.shape[0]
    return (
        dqueries,
        jnp.concatenate(
            [dkeys.reshape(key_count, width), dvalues.reshape(key_count, width)], axis=1
        ),
    )


def local(
    tokens,
    lengths,
    cotangent,
    attention_weight,
    output_weight,
    expand_weight,
    contract_weight,
    first_gain,
    first_shift,
    query_bias,
    value_bias,
    output_bias,
    second_gain,
    second_shift,
    expand_bias,
    contract_bias,
):
    clip_count, slot_count, width = tokens.shape
    parts = lax.axis_size("shard")
    frame_count = slot_count * parts
    place = lax.axis_index("shard")
    row_total = clip_count * slot_count
    gathered = (
        lax.all_gather(attention_weight, "shard", axis=0, tiled=True),
        lax.all_gather(output_weight, "shard", axis=0, tiled=True),
        lax.all_gather(expand_weight, "shard", axis=0, tiled=True),
        lax.all_gather(contract_weight, "shard", axis=0, tiled=True),
        lax.all_gather(first_gain, "shard", axis=0, tiled=True),
        lax.all_gather(first_shift, "shard", axis=0, tiled=True),
        lax.all_gather(query_bias, "shard", axis=0, tiled=True),
        lax.all_gather(value_bias, "shard", axis=0, tiled=True),
        lax.all_gather(output_bias, "shard", axis=0, tiled=True),
        lax.all_gather(second_gain, "shard", axis=0, tiled=True),
        lax.all_gather(second_shift, "shard", axis=0, tiled=True),
        lax.all_gather(expand_bias, "shard", axis=0, tiled=True),
        lax.all_gather(contract_bias, "shard", axis=0, tiled=True),
    )
    vectors = [entry.astype(jnp.float32) for entry in gathered[4:]]
    own_length = jnp.sum(jnp.where(jnp.arange(parts)[None, :] == place, lengths, 0), axis=1)
    row_live = jnp.arange(slot_count)[None, :] < own_length[:, None]
    key_live = (jnp.arange(slot_count)[None, None, :] < lengths[:, :, None]).reshape(
        clip_count, frame_count
    )
    inputs = tokens.reshape(row_total, width).astype(jnp.float32)
    first_normed, first_inverse, first_act = norm_forward(inputs, vectors[0], vectors[1])
    mixed = jnp.dot(first_act, gathered[0], preferred_element_type=jnp.float32)
    mixed = mixed + jnp.concatenate([vectors[2], jnp.zeros_like(vectors[2]), vectors[3]])
    mixed_low = mixed.astype(jnp.bfloat16)
    query_rows = mixed_low[:, :width].reshape(clip_count, slot_count, width)
    pair_own = mixed_low[:, width:].reshape(clip_count, slot_count, 2 * width)
    pair_all = lax.all_gather(pair_own, "shard", axis=1, tiled=True)
    attended, logsum = lax.map(attend_clip, (query_rows, pair_all, key_live))
    attended_flat = attended.reshape(row_total, width)
    residual = (
        inputs
        + jnp.dot(attended_flat, gathered[1], preferred_element_type=jnp.float32)
        + vectors[4]
    )
    second_normed, second_inverse, second_act = norm_forward(residual, vectors[5], vectors[6])
    pre = jnp.dot(second_act, gathered[2], preferred_element_type=jnp.float32) + vectors[7]
    hidden_act = jax.nn.gelu(pre, approximate=False).astype(jnp.bfloat16)
    block_output = (
        residual + jnp.dot(hidden_act, gathered[3], preferred_element_type=jnp.float32) + vectors[8]
    )
    backward = (
        lax.all_gather(attention_weight, "shard", axis=0, tiled=True),
        lax.all_gather(output_weight, "shard", axis=0, tiled=True),
        lax.all_gather(expand_weight, "shard", axis=0, tiled=True),
        lax.all_gather(contract_weight, "shard", axis=0, tiled=True),
        lax.all_gather(first_gain, "shard", axis=0, tiled=True),
        lax.all_gather(first_shift, "shard", axis=0, tiled=True),
        lax.all_gather(query_bias, "shard", axis=0, tiled=True),
        lax.all_gather(value_bias, "shard", axis=0, tiled=True),
        lax.all_gather(output_bias, "shard", axis=0, tiled=True),
        lax.all_gather(second_gain, "shard", axis=0, tiled=True),
        lax.all_gather(second_shift, "shard", axis=0, tiled=True),
        lax.all_gather(expand_bias, "shard", axis=0, tiled=True),
        lax.all_gather(contract_bias, "shard", axis=0, tiled=True),
    )
    back_vectors = [entry.astype(jnp.float32) for entry in backward[4:]]
    error = cotangent.reshape(row_total, width) * row_live.reshape(row_total, 1).astype(jnp.float32)
    error_low = error.astype(jnp.bfloat16)
    contract_bias_grad = jnp.sum(error, axis=0)
    contract_grad = inner_rows(hidden_act, error_low)
    dpre = lax.dot_general(
        error_low, backward[3], (((1,), (1,)), ((), ())), preferred_element_type=jnp.float32
    ) * gelu_slope(pre)
    expand_bias_grad = jnp.sum(dpre, axis=0)
    dpre_low = dpre.astype(jnp.bfloat16)
    expand_grad = inner_rows(second_act, dpre_low)
    dsecond = lax.dot_general(
        dpre_low, backward[2], (((1,), (1,)), ((), ())), preferred_element_type=jnp.float32
    )
    second_gain_grad = jnp.sum(dsecond * second_normed, axis=0)
    second_shift_grad = jnp.sum(dsecond, axis=0)
    dresidual = error + norm_backward(dsecond, second_normed, second_inverse, back_vectors[5])
    output_bias_grad = jnp.sum(dresidual, axis=0)
    dresidual_low = dresidual.astype(jnp.bfloat16)
    output_grad = inner_rows(attended_flat, dresidual_low)
    dattended = lax.dot_general(
        dresidual_low, backward[1], (((1,), (1,)), ((), ())), preferred_element_type=jnp.float32
    ).astype(jnp.bfloat16)
    delta = jnp.sum(
        heads_view(dattended.astype(jnp.float32)) * heads_view(attended_flat.astype(jnp.float32)),
        axis=-1,
    )
    delta = delta.reshape(clip_count, slot_count, HEADS)
    dattended_clips = dattended.reshape(clip_count, slot_count, width)
    dqueries, pair_terms = lax.map(
        both_grads, (query_rows, dattended_clips, logsum, delta, pair_all, key_live)
    )
    pair_grads = lax.psum_scatter(pair_terms, "shard", scatter_dimension=1, tiled=True)
    dqueries_flat = dqueries.reshape(row_total, width)
    pair_flat = pair_grads.reshape(row_total, 2 * width)
    dmixed = jnp.concatenate([dqueries_flat, pair_flat], axis=1)
    query_bias_grad = jnp.sum(dqueries_flat, axis=0)
    value_bias_grad = jnp.sum(pair_flat[:, width:], axis=0)
    dmixed_low = dmixed.astype(jnp.bfloat16)
    attention_grad = inner_rows(first_act, dmixed_low)
    dfirst = lax.dot_general(
        dmixed_low, backward[0], (((1,), (1,)), ((), ())), preferred_element_type=jnp.float32
    )
    first_gain_grad = jnp.sum(dfirst * first_normed, axis=0)
    first_shift_grad = jnp.sum(dfirst, axis=0)
    input_grad = dresidual + norm_backward(dfirst, first_normed, first_inverse, back_vectors[0])
    shares = (
        lax.psum_scatter(attention_grad, "shard", scatter_dimension=0, tiled=True),
        lax.psum_scatter(output_grad, "shard", scatter_dimension=0, tiled=True),
        lax.psum_scatter(expand_grad, "shard", scatter_dimension=0, tiled=True),
        lax.psum_scatter(contract_grad, "shard", scatter_dimension=0, tiled=True),
        lax.psum_scatter(first_gain_grad, "shard", scatter_dimension=0, tiled=True),
        lax.psum_scatter(first_shift_grad, "shard", scatter_dimension=0, tiled=True),
        lax.psum_scatter(query_bias_grad, "shard", scatter_dimension=0, tiled=True),
        lax.psum_scatter(value_bias_grad, "shard", scatter_dimension=0, tiled=True),
        lax.psum_scatter(output_bias_grad, "shard", scatter_dimension=0, tiled=True),
        lax.psum_scatter(second_gain_grad, "shard", scatter_dimension=0, tiled=True),
        lax.psum_scatter(second_shift_grad, "shard", scatter_dimension=0, tiled=True),
        lax.psum_scatter(expand_bias_grad, "shard", scatter_dimension=0, tiled=True),
        lax.psum_scatter(contract_bias_grad, "shard", scatter_dimension=0, tiled=True),
    )
    totals = lax.psum(
        (
            shares[0],
            shares[1],
            shares[2],
            shares[3],
            shares[4],
            shares[5],
            shares[6],
            shares[7],
            shares[8],
            shares[9],
            shares[10],
            shares[11],
            shares[12],
        ),
        "rep",
    )
    return (
        block_output.reshape(clip_count, slot_count, width),
        input_grad.reshape(clip_count, slot_count, width),
        totals[0],
        totals[1],
        totals[2],
        totals[3],
        totals[4],
        totals[5],
        totals[6],
        totals[7],
        totals[8],
        totals[9],
        totals[10],
        totals[11],
        totals[12],
    )


def clip_layer(tokens, lengths, cotangent_of, weights, vectors, reduce):
    attention_weight, output_weight, later_weights = weights
    (first_gain, first_shift, query_bias, value_bias, output_bias, second_gain, second_shift,
     expand_bias, contract_bias) = vectors
    clip_count, frame_count, width = tokens.shape
    block_count = lengths.shape[1]
    slot_count = frame_count // block_count
    rows = clip_count * frame_count
    live = (jnp.arange(slot_count)[None, None, :] < lengths[:, :, None]).reshape(clip_count, frame_count)
    scale = HEAD ** (-0.5)
    inputs = tokens.reshape(rows, width).astype(jnp.float32)
    first_normed, first_inverse, first_act = norm_forward(inputs, first_gain, first_shift)
    mixed = jnp.dot(first_act, attention_weight, preferred_element_type=jnp.float32)
    mixed = mixed + jnp.concatenate([query_bias, jnp.zeros_like(query_bias), value_bias])
    mixed_low = mixed.astype(jnp.bfloat16).reshape(clip_count, frame_count, 3, HEADS, HEAD)
    expand_weight, contract_weight = later_weights(mixed_low[0, 0, 0, 0, :1])
    queries = mixed_low[:, :, 0]
    keys = mixed_low[:, :, 1]
    values = mixed_low[:, :, 2]
    scores = jnp.einsum("cqhd,ckhd->chqk", queries, keys, preferred_element_type=jnp.float32) * scale
    scores = jnp.where(live[:, None, None, :], scores, NEGATIVE)
    highest = jnp.max(scores, axis=-1, keepdims=True)
    logsum = highest + jnp.log(jnp.sum(jnp.exp(scores - highest), axis=-1, keepdims=True))
    probs = jnp.exp(scores - logsum)
    probs_low = probs.astype(jnp.bfloat16)
    attended = jnp.einsum("chqk,ckhd->cqhd", probs_low, values, preferred_element_type=jnp.float32)
    attended_flat = attended.reshape(rows, width).astype(jnp.bfloat16)
    residual = inputs + jnp.dot(attended_flat, output_weight, preferred_element_type=jnp.float32) + output_bias
    second_normed, second_inverse, second_act = norm_forward(residual, second_gain, second_shift)
    pre = jnp.dot(second_act, expand_weight, preferred_element_type=jnp.float32) + expand_bias
    hidden_act = jax.nn.gelu(pre, approximate=False).astype(jnp.bfloat16)
    block_output = residual + jnp.dot(hidden_act, contract_weight, preferred_element_type=jnp.float32) + contract_bias
    cotangent = cotangent_of(pre[0, :1])
    error = cotangent.reshape(rows, width) * live.reshape(rows, 1).astype(jnp.float32)
    error_low = error.astype(jnp.bfloat16)
    contract_bias_grad = jnp.sum(error, axis=0)
    contract_grad = inner_rows(hidden_act, error_low)
    contract_grad, error_low = lax.optimization_barrier((contract_grad, error_low))
    contract_total = reduce(contract_grad)
    dpre = lax.dot_general(
        error_low, contract_weight, (((1,), (1,)), ((), ())), preferred_element_type=jnp.float32
    ) * gelu_slope(pre)
    expand_bias_grad = jnp.sum(dpre, axis=0)
    dpre_low = dpre.astype(jnp.bfloat16)
    expand_grad = inner_rows(second_act, dpre_low)
    expand_grad, dpre_low = lax.optimization_barrier((expand_grad, dpre_low))
    expand_total = reduce(expand_grad)
    dsecond = lax.dot_general(
        dpre_low, expand_weight, (((1,), (1,)), ((), ())), preferred_element_type=jnp.float32
    )
    second_gain_grad = jnp.sum(dsecond * second_normed, axis=0)
    second_shift_grad = jnp.sum(dsecond, axis=0)
    dresidual = error + norm_backward(dsecond, second_normed, second_inverse, second_gain)
    output_bias_grad = jnp.sum(dresidual, axis=0)
    dresidual_low = dresidual.astype(jnp.bfloat16)
    output_grad = inner_rows(attended_flat, dresidual_low)
    output_grad, dresidual_low = lax.optimization_barrier((output_grad, dresidual_low))
    output_total = reduce(output_grad)
    dattended = lax.dot_general(
        dresidual_low, output_weight, (((1,), (1,)), ((), ())), preferred_element_type=jnp.float32
    ).astype(jnp.bfloat16)
    dattended_heads = dattended.reshape(clip_count, frame_count, HEADS, HEAD)
    attended_heads = attended_flat.reshape(clip_count, frame_count, HEADS, HEAD)
    delta = jnp.sum(
        dattended_heads.astype(jnp.float32) * attended_heads.astype(jnp.float32), axis=-1
    )
    dprob = jnp.einsum("cqhd,ckhd->chqk", dattended_heads, values, preferred_element_type=jnp.float32)
    dscore = (probs * (dprob - jnp.transpose(delta, (0, 2, 1))[:, :, :, None]) * scale).astype(jnp.bfloat16)
    dqueries = jnp.einsum("chqk,ckhd->cqhd", dscore, keys, preferred_element_type=jnp.float32)
    dkeys = jnp.einsum("chqk,cqhd->ckhd", dscore, queries, preferred_element_type=jnp.float32)
    dvalues = jnp.einsum("chqk,cqhd->ckhd", probs_low, dattended_heads, preferred_element_type=jnp.float32)
    dmixed = jnp.concatenate(
        [dqueries.reshape(rows, width), dkeys.reshape(rows, width), dvalues.reshape(rows, width)], axis=1
    )
    query_bias_grad = jnp.sum(dmixed[:, :width], axis=0)
    value_bias_grad = jnp.sum(dmixed[:, 2 * width:], axis=0)
    dmixed_low = dmixed.astype(jnp.bfloat16)
    dmixed_low, contract_total, expand_total = lax.optimization_barrier(
        (dmixed_low, contract_total, expand_total)
    )
    attention_grad = inner_rows(first_act, dmixed_low)
    dfirst = lax.dot_general(
        dmixed_low, attention_weight, (((1,), (1,)), ((), ())), preferred_element_type=jnp.float32
    )
    dfirst, output_total = lax.optimization_barrier((dfirst, output_total))
    first_gain_grad = jnp.sum(dfirst * first_normed, axis=0)
    first_shift_grad = jnp.sum(dfirst, axis=0)
    input_grad = dresidual + norm_backward(dfirst, first_normed, first_inverse, first_gain)
    weight_grads = (attention_grad, output_total, expand_total, contract_total)
    vector_grads = (first_gain_grad, first_shift_grad, query_bias_grad, value_bias_grad, output_bias_grad,
                    second_gain_grad, second_shift_grad, expand_bias_grad, contract_bias_grad)
    return (
        block_output.reshape(clip_count, frame_count, width),
        input_grad.reshape(clip_count, frame_count, width),
        weight_grads,
        vector_grads,
    )


PAIR = [(0, 1), (1, 0)]
OUTER = ("outer", "inner")


def core_pick(core, first, second):
    return jnp.where(core == 0, first, second)


def gather_weight(shard_rows, extra=None):
    parts = lax.axis_size("shard")
    core = lax.axis_index("core")
    rows, width = shard_rows.shape
    half = rows // 2
    mine = lax.dynamic_slice_in_dim(shard_rows, core * half, half, axis=0)
    if extra is not None:
        mine = jnp.concatenate([mine, extra], axis=0)
    mine = lax.all_gather(mine, "shard", axis=0, tiled=False)
    other = lax.ppermute(mine, "core", PAIR)
    first = core_pick(core, mine, other)
    second = core_pick(core, other, mine)
    full = jnp.stack([first[:, :half], second[:, :half]], axis=1).reshape(parts * rows, width)
    if extra is None:
        return full, None
    return full, first[:, half:]


def reduce_weight(grad, extra=None):
    parts = lax.axis_size("shard")
    core = lax.axis_index("core")
    width = grad.shape[1]
    rows = grad.shape[0] // parts
    half = rows // 2
    quarters = grad.reshape(parts, 2, half, width)
    keep = lax.dynamic_index_in_dim(quarters, core, axis=1, keepdims=False)
    send = lax.dynamic_index_in_dim(quarters, 1 - core, axis=1, keepdims=False)
    if extra is not None:
        on_first = (core == 0).astype(extra.dtype)
        keep = jnp.concatenate([keep, extra * on_first], axis=1)
        send = jnp.concatenate([send, extra * (1 - on_first)], axis=1)
    chip = keep + lax.ppermute(send, "core", PAIR)
    part = lax.psum_scatter(chip, "shard", scatter_dimension=0, tiled=False)
    if lax.axis_size("inner") > 1:
        part = lax.psum(part, "inner")
    total = line_sum(part)
    other = lax.ppermute(total, "core", PAIR)
    first = core_pick(core, total, other)
    second = core_pick(core, other, total)
    out = jnp.concatenate([first[:half], second[:half]], axis=0)
    if extra is None:
        return out, None
    return out, first[half:]


def line_sum(values):
    groups = lax.axis_size("outer")
    if groups == 1:
        return values
    if groups & (groups - 1):
        return lax.psum(values, "outer")
    here = lax.axis_index("outer")
    length = values.shape[0]
    padded = -(-length // groups) * groups
    held = jnp.pad(values, ((0, padded - length),) + ((0, 0),) * (values.ndim - 1))
    held = held.reshape((groups, padded // groups) + values.shape[1:])
    step = 1
    while step < groups:
        held = held.reshape((held.shape[0] // 2, 2) + held.shape[1:])
        bit = (here // step) % 2
        keep = lax.dynamic_index_in_dim(held, bit, axis=1, keepdims=False)
        send = lax.dynamic_index_in_dim(held, 1 - bit, axis=1, keepdims=False)
        held = keep + lax.ppermute(send, "outer", [(j, j ^ step) for j in range(groups)])
        step *= 2
    step = groups // 2
    while step >= 1:
        bit = (here // step) % 2
        other = lax.ppermute(held, "outer", [(j, j ^ step) for j in range(groups)])
        low = jnp.where(bit == 0, held, other)
        high = jnp.where(bit == 0, other, held)
        held = jnp.stack([low, high], axis=1)
        held = held.reshape((held.shape[0] * 2,) + held.shape[2:])
        step //= 2
    return held.reshape((padded,) + values.shape[1:])[:length]


def gather_packed(blocks, after=None):
    core = lax.axis_index("core")
    mine = lax.all_gather(jnp.concatenate(blocks, axis=0), "shard", axis=0, tiled=False)
    if after is not None:
        mine = mine + (after * 0).astype(mine.dtype)
    other = lax.ppermute(mine, "core", PAIR)
    return core_pick(core, mine, other), core_pick(core, other, mine)


def unpack_rows(first, second, begin, count, shape):
    parts = first.shape[0]
    rows, width = shape
    low = first[:, begin:begin + count].reshape(parts, -1, width)
    high = second[:, begin:begin + count].reshape(parts, -1, width)
    return jnp.stack([low, high], axis=1).reshape(rows, width)


def core_half(shard_rows):
    core = lax.axis_index("core")
    half = shard_rows.shape[0] // 2
    return lax.dynamic_slice_in_dim(shard_rows, core * half, half, axis=0)


def clip_local(tokens, lengths, cotangent, *params):
    clip_count, slot_count, width = tokens.shape
    parts = lax.axis_size("shard")
    place = lax.axis_index("shard")
    own = clip_count // parts
    weight_shards = params[:4]
    vector_shards = params[4:]
    wide = weight_shards[0].shape[1]
    vector_row = jnp.concatenate([entry.reshape(-1) for entry in vector_shards])
    pad = (-vector_row.shape[0]) % wide
    vector_rows = jnp.pad(vector_row, (0, pad)).reshape(-1, wide)
    attention_half = core_half(weight_shards[0])
    output_half = core_half(weight_shards[1]).reshape(-1, wide)
    first, second = gather_packed([attention_half, output_half, vector_rows])
    a_rows = attention_half.shape[0]
    o_rows = output_half.shape[0]
    attention_weight = unpack_rows(first, second, 0, a_rows, (parts * weight_shards[0].shape[0], wide))
    output_weight = unpack_rows(
        first, second, a_rows, o_rows, (parts * weight_shards[1].shape[0], weight_shards[1].shape[1])
    )
    vector_all = first[:, a_rows + o_rows:].reshape(parts, -1)[:, : vector_row.shape[0]]
    vectors = []
    offset = 0
    for entry in vector_shards:
        size = entry.shape[0]
        vectors.append(vector_all[:, offset:offset + size].reshape(parts * size).astype(jnp.float32))
        offset += size
    late = weight_shards[2].shape[1]
    expand_half = core_half(weight_shards[2])
    contract_half = core_half(weight_shards[3]).reshape(-1, late)

    def later_weights(after):
        first_b, second_b = gather_packed([expand_half, contract_half], after)
        e_rows = expand_half.shape[0]
        expand_weight = unpack_rows(first_b, second_b, 0, e_rows, (parts * weight_shards[2].shape[0], late))
        contract_weight = unpack_rows(
            first_b, second_b, e_rows, contract_half.shape[0],
            (parts * weight_shards[3].shape[0], weight_shards[3].shape[1]),
        )
        return expand_weight, contract_weight

    weights = (attention_weight, output_weight, later_weights)
    tokens_clip = lax.all_to_all(tokens, "shard", 0, 1, tiled=True)

    def cotangent_of(after):
        late = cotangent + (after * 0).astype(cotangent.dtype)
        return lax.all_to_all(late, "shard", 0, 1, tiled=True)

    lengths_clip = lax.dynamic_slice_in_dim(lengths, place * own, own, axis=0)
    block_output, input_grad, weight_grads, vector_grads = clip_layer(
        tokens_clip, lengths_clip, cotangent_of, weights, vectors, lambda grad: reduce_weight(grad)[0]
    )
    block_output = lax.all_to_all(block_output, "shard", 1, 0, tiled=True)
    input_grad = lax.all_to_all(input_grad, "shard", 1, 0, tiled=True)
    attention_grad = weight_grads[0]
    attention_width = attention_grad.shape[1]
    vector_parts = jnp.concatenate([entry.reshape(parts, -1) for entry in vector_grads], axis=1)
    vector_size = vector_parts.shape[1]
    vpad = (-vector_size) % attention_width
    vector_parts = jnp.pad(vector_parts, ((0, 0), (0, vpad))).reshape(parts, -1, attention_width)
    attention_total, vector_total = reduce_weight(attention_grad, vector_parts)
    totals = (attention_total,) + tuple(weight_grads[1:])
    vector_total = vector_total.reshape(-1)[:vector_size]
    vector_outs = []
    offset = 0
    for entry in vector_shards:
        size = entry.shape[0]
        vector_outs.append(vector_total[offset:offset + size])
        offset += size
    return (block_output, input_grad) + totals + tuple(vector_outs)


def split_rep(mesh):
    devices = mesh.devices
    rep, parts = devices.shape
    first = devices[0, 0]
    stride = None
    for index in range(1, rep):
        other = devices[index, 0]
        if tuple(other.coords) == tuple(first.coords) and other.core_on_chip != first.core_on_chip:
            stride = index
            break
    if stride is None or rep % (2 * stride):
        return None
    grid = devices.reshape(rep // (2 * stride), 2, stride, parts)
    for spot in np.ndindex(grid.shape[0], grid.shape[2], grid.shape[3]):
        low = grid[spot[0], 0, spot[1], spot[2]]
        high = grid[spot[0], 1, spot[1], spot[2]]
        if tuple(low.coords) != tuple(high.coords) or low.core_on_chip == high.core_on_chip:
            return None
    return Mesh(grid, ("outer", "core", "inner", "shard"))


def solution(mesh):
    def specs(rep):
        ins = (P(rep, "shard", None), P(rep, None), P(rep, "shard", None)) + (P("shard", None),) * 4 + (
            P("shard"),
        ) * 9
        outs = (P(rep, "shard", None), P(rep, "shard", None)) + (P("shard", None),) * 4 + (P("shard"),) * 9
        return ins, outs

    ins, outs = specs("rep")
    plain = jax.shard_map(local, mesh=mesh, in_specs=ins, out_specs=outs, check_vma=False)
    split = split_rep(mesh)
    if split is None:
        return plain
    ins, outs = specs(("outer", "core", "inner"))
    fast = jax.shard_map(clip_local, mesh=split, in_specs=ins, out_specs=outs, check_vma=False)
    rep, parts = mesh.devices.shape

    def run(*args):
        if (args[0].shape[0] // rep) % parts == 0:
            return fast(*args)
        return plain(*args)

    return run
```

```python
import jax
import jax.numpy as jnp
from jax import lax
from jax.sharding import Mesh, PartitionSpec as P
import numpy as np

HEADS = 12
HEAD = 64


EPSILON = 1e-05
NEGATIVE = -1e30


def norm_forward(values, gain, shift):
    centred = values - jnp.mean(values, axis=-1, keepdims=True)
    inverse = lax.rsqrt(jnp.mean(centred * centred, axis=-1, keepdims=True) + EPSILON)
    normed = centred * inverse
    return (normed, inverse, (normed * gain + shift).astype(jnp.bfloat16))


def norm_backward(upstream, normed, inverse, gain):
    scaled = upstream * gain
    return inverse * (
        scaled
        - jnp.mean(scaled, axis=-1, keepdims=True)
        - normed * jnp.mean(scaled * normed, axis=-1, keepdims=True)
    )


def gelu_slope(values):
    return (
        0.5 * (1.0 + jax.scipy.special.erf(values * 0.7071067811865476))
        + values * jnp.exp(-0.5 * values * values) * 0.3989422804014327
    )


def inner_rows(left, right):
    return lax.dot_general(
        left, right, (((0,), (0,)), ((), ())), preferred_element_type=jnp.float32
    )


def heads_view(matrix):
    return matrix.reshape(matrix.shape[0], HEADS, HEAD)


def score_block(query_rows, key_rows, key_live):
    scores = jnp.einsum(
        "qhd,khd->hqk",
        heads_view(query_rows),
        heads_view(key_rows),
        preferred_element_type=jnp.float32,
    ) * HEAD ** (-0.5)
    return jnp.where(key_live[None, None, :], scores, NEGATIVE)


def attend_clip(items):
    query_rows, pair_rows, key_live = items
    width = query_rows.shape[1]
    scores = score_block(query_rows, pair_rows[:, :width], key_live)
    highest = jnp.max(scores, axis=-1, keepdims=True)
    logsum = highest + jnp.log(jnp.sum(jnp.exp(scores - highest), axis=-1, keepdims=True))
    probs_low = jnp.exp(scores - logsum).astype(jnp.bfloat16)
    attended = jnp.einsum(
        "hqk,khd->qhd",
        probs_low,
        heads_view(pair_rows[:, width:]),
        preferred_element_type=jnp.float32,
    )
    return (attended.reshape(query_rows.shape[0], width).astype(jnp.bfloat16), logsum[:, :, 0].T)


def score_grads(query_rows, dattended, logsum, delta, pair_rows, key_live):
    width = query_rows.shape[1]
    scores = score_block(query_rows, pair_rows[:, :width], key_live)
    probs = jnp.exp(scores - logsum.T[:, :, None])
    dprob = jnp.einsum(
        "qhd,khd->hqk",
        heads_view(dattended),
        heads_view(pair_rows[:, width:]),
        preferred_element_type=jnp.float32,
    )
    dscore = (probs * (dprob - delta.T[:, :, None]) * HEAD ** (-0.5)).astype(jnp.bfloat16)
    return (probs.astype(jnp.bfloat16), dscore)


def both_grads(items):
    query_rows, dattended, logsum, delta, pair_rows, key_live = items
    width = query_rows.shape[1]
    probs_low, dscore = score_grads(query_rows, dattended, logsum, delta, pair_rows, key_live)
    dqueries = jnp.einsum(
        "hqk,khd->qhd", dscore, heads_view(pair_rows[:, :width]), preferred_element_type=jnp.float32
    ).reshape(query_rows.shape[0], width)
    dkeys = jnp.einsum(
        "hqk,qhd->khd", dscore, heads_view(query_rows), preferred_element_type=jnp.float32
    )
    dvalues = jnp.einsum(
        "hqk,qhd->khd", probs_low, heads_view(dattended), preferred_element_type=jnp.float32
    )
    key_count = pair_rows.shape[0]
    return (
        dqueries,
        jnp.concatenate(
            [dkeys.reshape(key_count, width), dvalues.reshape(key_count, width)], axis=1
        ),
    )


def local(
    tokens,
    lengths,
    cotangent,
    attention_weight,
    output_weight,
    expand_weight,
    contract_weight,
    first_gain,
    first_shift,
    query_bias,
    value_bias,
    output_bias,
    second_gain,
    second_shift,
    expand_bias,
    contract_bias,
):
    clip_count, slot_count, width = tokens.shape
    parts = lax.axis_size("shard")
    frame_count = slot_count * parts
    place = lax.axis_index("shard")
    row_total = clip_count * slot_count
    gathered = (
        lax.all_gather(attention_weight, "shard", axis=0, tiled=True),
        lax.all_gather(output_weight, "shard", axis=0, tiled=True),
        lax.all_gather(expand_weight, "shard", axis=0, tiled=True),
        lax.all_gather(contract_weight, "shard", axis=0, tiled=True),
        lax.all_gather(first_gain, "shard", axis=0, tiled=True),
        lax.all_gather(first_shift, "shard", axis=0, tiled=True),
        lax.all_gather(query_bias, "shard", axis=0, tiled=True),
        lax.all_gather(value_bias, "shard", axis=0, tiled=True),
        lax.all_gather(output_bias, "shard", axis=0, tiled=True),
        lax.all_gather(second_gain, "shard", axis=0, tiled=True),
        lax.all_gather(second_shift, "shard", axis=0, tiled=True),
        lax.all_gather(expand_bias, "shard", axis=0, tiled=True),
        lax.all_gather(contract_bias, "shard", axis=0, tiled=True),
    )
    vectors = [entry.astype(jnp.float32) for entry in gathered[4:]]
    own_length = jnp.sum(jnp.where(jnp.arange(parts)[None, :] == place, lengths, 0), axis=1)
    row_live = jnp.arange(slot_count)[None, :] < own_length[:, None]
    key_live = (jnp.arange(slot_count)[None, None, :] < lengths[:, :, None]).reshape(
        clip_count, frame_count
    )
    inputs = tokens.reshape(row_total, width).astype(jnp.float32)
    first_normed, first_inverse, first_act = norm_forward(inputs, vectors[0], vectors[1])
    mixed = jnp.dot(first_act, gathered[0], preferred_element_type=jnp.float32)
    mixed = mixed + jnp.concatenate([vectors[2], jnp.zeros_like(vectors[2]), vectors[3]])
    mixed_low = mixed.astype(jnp.bfloat16)
    query_rows = mixed_low[:, :width].reshape(clip_count, slot_count, width)
    pair_own = mixed_low[:, width:].reshape(clip_count, slot_count, 2 * width)
    pair_all = lax.all_gather(pair_own, "shard", axis=1, tiled=True)
    attended, logsum = lax.map(attend_clip, (query_rows, pair_all, key_live))
    attended_flat = attended.reshape(row_total, width)
    residual = (
        inputs
        + jnp.dot(attended_flat, gathered[1], preferred_element_type=jnp.float32)
        + vectors[4]
    )
    second_normed, second_inverse, second_act = norm_forward(residual, vectors[5], vectors[6])
    pre = jnp.dot(second_act, gathered[2], preferred_element_type=jnp.float32) + vectors[7]
    hidden_act = jax.nn.gelu(pre, approximate=False).astype(jnp.bfloat16)
    block_output = (
        residual + jnp.dot(hidden_act, gathered[3], preferred_element_type=jnp.float32) + vectors[8]
    )
    backward = (
        lax.all_gather(attention_weight, "shard", axis=0, tiled=True),
        lax.all_gather(output_weight, "shard", axis=0, tiled=True),
        lax.all_gather(expand_weight, "shard", axis=0, tiled=True),
        lax.all_gather(contract_weight, "shard", axis=0, tiled=True),
        lax.all_gather(first_gain, "shard", axis=0, tiled=True),
        lax.all_gather(first_shift, "shard", axis=0, tiled=True),
        lax.all_gather(query_bias, "shard", axis=0, tiled=True),
        lax.all_gather(value_bias, "shard", axis=0, tiled=True),
        lax.all_gather(output_bias, "shard", axis=0, tiled=True),
        lax.all_gather(second_gain, "shard", axis=0, tiled=True),
        lax.all_gather(second_shift, "shard", axis=0, tiled=True),
        lax.all_gather(expand_bias, "shard", axis=0, tiled=True),
        lax.all_gather(contract_bias, "shard", axis=0, tiled=True),
    )
    back_vectors = [entry.astype(jnp.float32) for entry in backward[4:]]
    error = cotangent.reshape(row_total, width) * row_live.reshape(row_total, 1).astype(jnp.float32)
    error_low = error.astype(jnp.bfloat16)
    contract_bias_grad = jnp.sum(error, axis=0)
    contract_grad = inner_rows(hidden_act, error_low)
    dpre = lax.dot_general(
        error_low, backward[3], (((1,), (1,)), ((), ())), preferred_element_type=jnp.float32
    ) * gelu_slope(pre)
    expand_bias_grad = jnp.sum(dpre, axis=0)
    dpre_low = dpre.astype(jnp.bfloat16)
    expand_grad = inner_rows(second_act, dpre_low)
    dsecond = lax.dot_general(
        dpre_low, backward[2], (((1,), (1,)), ((), ())), preferred_element_type=jnp.float32
    )
    second_gain_grad = jnp.sum(dsecond * second_normed, axis=0)
    second_shift_grad = jnp.sum(dsecond, axis=0)
    dresidual = error + norm_backward(dsecond, second_normed, second_inverse, back_vectors[5])
    output_bias_grad = jnp.sum(dresidual, axis=0)
    dresidual_low = dresidual.astype(jnp.bfloat16)
    output_grad = inner_rows(attended_flat, dresidual_low)
    dattended = lax.dot_general(
        dresidual_low, backward[1], (((1,), (1,)), ((), ())), preferred_element_type=jnp.float32
    ).astype(jnp.bfloat16)
    delta = jnp.sum(
        heads_view(dattended.astype(jnp.float32)) * heads_view(attended_flat.astype(jnp.float32)),
        axis=-1,
    )
    delta = delta.reshape(clip_count, slot_count, HEADS)
    dattended_clips = dattended.reshape(clip_count, slot_count, width)
    dqueries, pair_terms = lax.map(
        both_grads, (query_rows, dattended_clips, logsum, delta, pair_all, key_live)
    )
    pair_grads = lax.psum_scatter(pair_terms, "shard", scatter_dimension=1, tiled=True)
    dqueries_flat = dqueries.reshape(row_total, width)
    pair_flat = pair_grads.reshape(row_total, 2 * width)
    dmixed = jnp.concatenate([dqueries_flat, pair_flat], axis=1)
    query_bias_grad = jnp.sum(dqueries_flat, axis=0)
    value_bias_grad = jnp.sum(pair_flat[:, width:], axis=0)
    dmixed_low = dmixed.astype(jnp.bfloat16)
    attention_grad = inner_rows(first_act, dmixed_low)
    dfirst = lax.dot_general(
        dmixed_low, backward[0], (((1,), (1,)), ((), ())), preferred_element_type=jnp.float32
    )
    first_gain_grad = jnp.sum(dfirst * first_normed, axis=0)
    first_shift_grad = jnp.sum(dfirst, axis=0)
    input_grad = dresidual + norm_backward(dfirst, first_normed, first_inverse, back_vectors[0])
    shares = (
        lax.psum_scatter(attention_grad, "shard", scatter_dimension=0, tiled=True),
        lax.psum_scatter(output_grad, "shard", scatter_dimension=0, tiled=True),
        lax.psum_scatter(expand_grad, "shard", scatter_dimension=0, tiled=True),
        lax.psum_scatter(contract_grad, "shard", scatter_dimension=0, tiled=True),
        lax.psum_scatter(first_gain_grad, "shard", scatter_dimension=0, tiled=True),
        lax.psum_scatter(first_shift_grad, "shard", scatter_dimension=0, tiled=True),
        lax.psum_scatter(query_bias_grad, "shard", scatter_dimension=0, tiled=True),
        lax.psum_scatter(value_bias_grad, "shard", scatter_dimension=0, tiled=True),
        lax.psum_scatter(output_bias_grad, "shard", scatter_dimension=0, tiled=True),
        lax.psum_scatter(second_gain_grad, "shard", scatter_dimension=0, tiled=True),
        lax.psum_scatter(second_shift_grad, "shard", scatter_dimension=0, tiled=True),
        lax.psum_scatter(expand_bias_grad, "shard", scatter_dimension=0, tiled=True),
        lax.psum_scatter(contract_bias_grad, "shard", scatter_dimension=0, tiled=True),
    )
    totals = lax.psum(
        (
            shares[0],
            shares[1],
            shares[2],
            shares[3],
            shares[4],
            shares[5],
            shares[6],
            shares[7],
            shares[8],
            shares[9],
            shares[10],
            shares[11],
            shares[12],
        ),
        "rep",
    )
    return (
        block_output.reshape(clip_count, slot_count, width),
        input_grad.reshape(clip_count, slot_count, width),
        totals[0],
        totals[1],
        totals[2],
        totals[3],
        totals[4],
        totals[5],
        totals[6],
        totals[7],
        totals[8],
        totals[9],
        totals[10],
        totals[11],
        totals[12],
    )


def clip_layer(tokens, lengths, cotangent_of, weights, vectors, reduce):
    attention_weight, output_weight, later_weights = weights
    (first_gain, first_shift, query_bias, value_bias, output_bias, second_gain, second_shift,
     expand_bias, contract_bias) = vectors
    clip_count, frame_count, width = tokens.shape
    block_count = lengths.shape[1]
    slot_count = frame_count // block_count
    rows = clip_count * frame_count
    live = (jnp.arange(slot_count)[None, None, :] < lengths[:, :, None]).reshape(clip_count, frame_count)
    scale = HEAD ** (-0.5)
    inputs = tokens.reshape(rows, width).astype(jnp.float32)
    first_normed, first_inverse, first_act = norm_forward(inputs, first_gain, first_shift)
    mixed = jnp.dot(first_act, attention_weight, preferred_element_type=jnp.float32)
    mixed = mixed + jnp.concatenate([query_bias, jnp.zeros_like(query_bias), value_bias])
    mixed_low = mixed.astype(jnp.bfloat16).reshape(clip_count, frame_count, 3, HEADS, HEAD)
    expand_weight, contract_weight = later_weights(mixed_low[0, 0, 0, 0, :1])
    queries = mixed_low[:, :, 0]
    keys = mixed_low[:, :, 1]
    values = mixed_low[:, :, 2]
    scores = jnp.einsum("cqhd,ckhd->chqk", queries, keys, preferred_element_type=jnp.float32) * scale
    scores = jnp.where(live[:, None, None, :], scores, NEGATIVE)
    highest = jnp.max(scores, axis=-1, keepdims=True)
    logsum = highest + jnp.log(jnp.sum(jnp.exp(scores - highest), axis=-1, keepdims=True))
    probs = jnp.exp(scores - logsum)
    probs_low = probs.astype(jnp.bfloat16)
    attended = jnp.einsum("chqk,ckhd->cqhd", probs_low, values, preferred_element_type=jnp.float32)
    attended_flat = attended.reshape(rows, width).astype(jnp.bfloat16)
    residual = inputs + jnp.dot(attended_flat, output_weight, preferred_element_type=jnp.float32) + output_bias
    second_normed, second_inverse, second_act = norm_forward(residual, second_gain, second_shift)
    pre = jnp.dot(second_act, expand_weight, preferred_element_type=jnp.float32) + expand_bias
    hidden_act = jax.nn.gelu(pre, approximate=False).astype(jnp.bfloat16)
    block_output = residual + jnp.dot(hidden_act, contract_weight, preferred_element_type=jnp.float32) + contract_bias
    cotangent = cotangent_of(pre[0, :1])
    error = cotangent.reshape(rows, width) * live.reshape(rows, 1).astype(jnp.float32)
    error_low = error.astype(jnp.bfloat16)
    contract_bias_grad = jnp.sum(error, axis=0)
    contract_grad = inner_rows(hidden_act, error_low)
    contract_chip = chip_sum(contract_grad)
    dpre = lax.dot_general(
        error_low, contract_weight, (((1,), (1,)), ((), ())), preferred_element_type=jnp.float32
    ) * gelu_slope(pre)
    expand_bias_grad = jnp.sum(dpre, axis=0)
    dpre_low = dpre.astype(jnp.bfloat16)
    contract_chip, dpre_low = lax.optimization_barrier((contract_chip, dpre_low))
    contract_part = shard_sum(contract_chip)
    expand_grad = inner_rows(second_act, dpre_low)
    expand_chip = chip_sum(expand_grad)
    dsecond = lax.dot_general(
        dpre_low, expand_weight, (((1,), (1,)), ((), ())), preferred_element_type=jnp.float32
    )
    second_gain_grad = jnp.sum(dsecond * second_normed, axis=0)
    second_shift_grad = jnp.sum(dsecond, axis=0)
    dresidual = error + norm_backward(dsecond, second_normed, second_inverse, second_gain)
    output_bias_grad = jnp.sum(dresidual, axis=0)
    dresidual_low = dresidual.astype(jnp.bfloat16)
    expand_chip, dresidual_low = lax.optimization_barrier((expand_chip, dresidual_low))
    expand_part = shard_sum(expand_chip)
    output_grad = inner_rows(attended_flat, dresidual_low)
    output_chip = chip_sum(output_grad)
    dattended = lax.dot_general(
        dresidual_low, output_weight, (((1,), (1,)), ((), ())), preferred_element_type=jnp.float32
    ).astype(jnp.bfloat16)
    contract_part, dattended = lax.optimization_barrier((contract_part, dattended))
    dattended_heads = dattended.reshape(clip_count, frame_count, HEADS, HEAD)
    attended_heads = attended_flat.reshape(clip_count, frame_count, HEADS, HEAD)
    delta = jnp.sum(
        dattended_heads.astype(jnp.float32) * attended_heads.astype(jnp.float32), axis=-1
    )
    dprob = jnp.einsum("cqhd,ckhd->chqk", dattended_heads, values, preferred_element_type=jnp.float32)
    dscore = (probs * (dprob - jnp.transpose(delta, (0, 2, 1))[:, :, :, None]) * scale).astype(jnp.bfloat16)
    dqueries = jnp.einsum("chqk,ckhd->cqhd", dscore, keys, preferred_element_type=jnp.float32)
    dkeys = jnp.einsum("chqk,cqhd->ckhd", dscore, queries, preferred_element_type=jnp.float32)
    dvalues = jnp.einsum("chqk,cqhd->ckhd", probs_low, dattended_heads, preferred_element_type=jnp.float32)
    dmixed = jnp.concatenate(
        [dqueries.reshape(rows, width), dkeys.reshape(rows, width), dvalues.reshape(rows, width)], axis=1
    )
    query_bias_grad = jnp.sum(dmixed[:, :width], axis=0)
    value_bias_grad = jnp.sum(dmixed[:, 2 * width:], axis=0)
    dmixed_low = dmixed.astype(jnp.bfloat16)
    output_chip, expand_part, dmixed_low = lax.optimization_barrier((output_chip, expand_part, dmixed_low))
    output_part = shard_sum(output_chip)
    attention_grad = inner_rows(first_act, dmixed_low)
    dfirst = lax.dot_general(
        dmixed_low, attention_weight, (((1,), (1,)), ((), ())), preferred_element_type=jnp.float32
    )
    first_gain_grad = jnp.sum(dfirst * first_normed, axis=0)
    first_shift_grad = jnp.sum(dfirst, axis=0)
    input_grad = dresidual + norm_backward(dfirst, first_normed, first_inverse, first_gain)
    output_part, input_grad = lax.optimization_barrier((output_part, input_grad))
    output_total = reduce(output_part, output_grad.shape[0])
    expand_total = reduce(expand_part, expand_grad.shape[0])
    contract_total = reduce(contract_part, contract_grad.shape[0])
    weight_grads = (attention_grad, output_total, expand_total, contract_total)
    vector_grads = (first_gain_grad, first_shift_grad, query_bias_grad, value_bias_grad, output_bias_grad,
                    second_gain_grad, second_shift_grad, expand_bias_grad, contract_bias_grad)
    return (
        block_output.reshape(clip_count, frame_count, width),
        input_grad.reshape(clip_count, frame_count, width),
        weight_grads,
        vector_grads,
    )


PAIR = [(0, 1), (1, 0)]
OUTER = ("outer", "inner")


def core_pick(core, first, second):
    return jnp.where(core == 0, first, second)


def gather_weight(shard_rows, extra=None):
    parts = lax.axis_size("shard")
    core = lax.axis_index("core")
    rows, width = shard_rows.shape
    half = rows // 2
    mine = lax.dynamic_slice_in_dim(shard_rows, core * half, half, axis=0)
    if extra is not None:
        mine = jnp.concatenate([mine, extra], axis=0)
    mine = lax.all_gather(mine, "shard", axis=0, tiled=False)
    other = lax.ppermute(mine, "core", PAIR)
    first = core_pick(core, mine, other)
    second = core_pick(core, other, mine)
    full = jnp.stack([first[:, :half], second[:, :half]], axis=1).reshape(parts * rows, width)
    if extra is None:
        return full, None
    return full, first[:, half:]


def chip_sum(grad, extra=None):
    parts = lax.axis_size("shard")
    core = lax.axis_index("core")
    width = grad.shape[1]
    rows = grad.shape[0] // parts
    half = rows // 2
    quarters = grad.reshape(parts, 2, half, width)
    keep = lax.dynamic_index_in_dim(quarters, core, axis=1, keepdims=False)
    send = lax.dynamic_index_in_dim(quarters, 1 - core, axis=1, keepdims=False)
    if extra is not None:
        on_first = (core == 0).astype(extra.dtype)
        keep = jnp.concatenate([keep, extra * on_first], axis=1)
        send = jnp.concatenate([send, extra * (1 - on_first)], axis=1)
    return keep + lax.ppermute(send, "core", PAIR)


def shard_sum(chip):
    part = lax.psum_scatter(chip, "shard", scatter_dimension=0, tiled=False)
    if lax.axis_size("inner") > 1:
        part = lax.psum(part, "inner")
    return part


def finish_sum(part, half):
    core = lax.axis_index("core")
    total = line_sum(part)
    other = lax.ppermute(total, "core", PAIR)
    first = core_pick(core, total, other)
    second = core_pick(core, other, total)
    return jnp.concatenate([first[:half], second[:half]], axis=0), first[half:]


def reduce_weight(grad, extra=None):
    half = grad.shape[0] // lax.axis_size("shard") // 2
    return finish_sum(shard_sum(chip_sum(grad, extra)), half)


def line_sum(values):
    groups = lax.axis_size("outer")
    if groups == 1:
        return values
    if groups & (groups - 1):
        return lax.psum(values, "outer")
    here = lax.axis_index("outer")
    length = values.shape[0]
    padded = -(-length // groups) * groups
    held = jnp.pad(values, ((0, padded - length),) + ((0, 0),) * (values.ndim - 1))
    held = held.reshape((groups, padded // groups) + values.shape[1:])
    step = 1
    while step < groups:
        held = held.reshape((held.shape[0] // 2, 2) + held.shape[1:])
        bit = (here // step) % 2
        keep = lax.dynamic_index_in_dim(held, bit, axis=1, keepdims=False)
        send = lax.dynamic_index_in_dim(held, 1 - bit, axis=1, keepdims=False)
        held = keep + lax.ppermute(send, "outer", [(j, j ^ step) for j in range(groups)])
        step *= 2
    step = groups // 2
    while step >= 1:
        bit = (here // step) % 2
        other = lax.ppermute(held, "outer", [(j, j ^ step) for j in range(groups)])
        low = jnp.where(bit == 0, held, other)
        high = jnp.where(bit == 0, other, held)
        held = jnp.stack([low, high], axis=1)
        held = held.reshape((held.shape[0] * 2,) + held.shape[2:])
        step //= 2
    return held.reshape((padded,) + values.shape[1:])[:length]


def gather_packed(blocks, after=None):
    core = lax.axis_index("core")
    mine = lax.all_gather(jnp.concatenate(blocks, axis=0), "shard", axis=0, tiled=False)
    if after is not None:
        mine = mine + (after * 0).astype(mine.dtype)
    other = lax.ppermute(mine, "core", PAIR)
    return core_pick(core, mine, other), core_pick(core, other, mine)


def unpack_rows(first, second, begin, count, shape):
    parts = first.shape[0]
    rows, width = shape
    low = first[:, begin:begin + count].reshape(parts, -1, width)
    high = second[:, begin:begin + count].reshape(parts, -1, width)
    return jnp.stack([low, high], axis=1).reshape(rows, width)


def core_half(shard_rows):
    core = lax.axis_index("core")
    half = shard_rows.shape[0] // 2
    return lax.dynamic_slice_in_dim(shard_rows, core * half, half, axis=0)


def clip_local(tokens, lengths, cotangent, *params):
    clip_count, slot_count, width = tokens.shape
    parts = lax.axis_size("shard")
    place = lax.axis_index("shard")
    own = clip_count // parts
    weight_shards = params[:4]
    vector_shards = params[4:]
    wide = weight_shards[0].shape[1]
    vector_row = jnp.concatenate([entry.reshape(-1) for entry in vector_shards])
    pad = (-vector_row.shape[0]) % wide
    vector_rows = jnp.pad(vector_row, (0, pad)).reshape(-1, wide)
    attention_half = core_half(weight_shards[0])
    output_half = core_half(weight_shards[1]).reshape(-1, wide)
    first, second = gather_packed([attention_half, output_half, vector_rows])
    a_rows = attention_half.shape[0]
    o_rows = output_half.shape[0]
    attention_weight = unpack_rows(first, second, 0, a_rows, (parts * weight_shards[0].shape[0], wide))
    output_weight = unpack_rows(
        first, second, a_rows, o_rows, (parts * weight_shards[1].shape[0], weight_shards[1].shape[1])
    )
    vector_all = first[:, a_rows + o_rows:].reshape(parts, -1)[:, : vector_row.shape[0]]
    vectors = []
    offset = 0
    for entry in vector_shards:
        size = entry.shape[0]
        vectors.append(vector_all[:, offset:offset + size].reshape(parts * size).astype(jnp.float32))
        offset += size
    late = weight_shards[2].shape[1]
    expand_half = core_half(weight_shards[2])
    contract_half = core_half(weight_shards[3]).reshape(-1, late)

    def later_weights(after):
        first_b, second_b = gather_packed([expand_half, contract_half], after)
        e_rows = expand_half.shape[0]
        expand_weight = unpack_rows(first_b, second_b, 0, e_rows, (parts * weight_shards[2].shape[0], late))
        contract_weight = unpack_rows(
            first_b, second_b, e_rows, contract_half.shape[0],
            (parts * weight_shards[3].shape[0], weight_shards[3].shape[1]),
        )
        return expand_weight, contract_weight

    weights = (attention_weight, output_weight, later_weights)
    tokens_clip = lax.all_to_all(tokens, "shard", 0, 1, tiled=True)

    def cotangent_of(after):
        late = cotangent + (after * 0).astype(cotangent.dtype)
        return lax.all_to_all(late, "shard", 0, 1, tiled=True)

    lengths_clip = lax.dynamic_slice_in_dim(lengths, place * own, own, axis=0)
    block_output, input_grad, weight_grads, vector_grads = clip_layer(
        tokens_clip, lengths_clip, cotangent_of, weights, vectors, lambda part, rows: finish_sum(part, rows // parts // 2)[0]
    )
    block_output = lax.all_to_all(block_output, "shard", 1, 0, tiled=True)
    input_grad = lax.all_to_all(input_grad, "shard", 1, 0, tiled=True)
    attention_grad = weight_grads[0]
    attention_width = attention_grad.shape[1]
    vector_parts = jnp.concatenate([entry.reshape(parts, -1) for entry in vector_grads], axis=1)
    vector_size = vector_parts.shape[1]
    vpad = (-vector_size) % attention_width
    vector_parts = jnp.pad(vector_parts, ((0, 0), (0, vpad))).reshape(parts, -1, attention_width)
    attention_total, vector_total = reduce_weight(attention_grad, vector_parts)
    totals = (attention_total,) + tuple(weight_grads[1:])
    vector_total = vector_total.reshape(-1)[:vector_size]
    vector_outs = []
    offset = 0
    for entry in vector_shards:
        size = entry.shape[0]
        vector_outs.append(vector_total[offset:offset + size])
        offset += size
    return (block_output, input_grad) + totals + tuple(vector_outs)


def split_rep(mesh):
    devices = mesh.devices
    rep, parts = devices.shape
    first = devices[0, 0]
    stride = None
    for index in range(1, rep):
        other = devices[index, 0]
        if tuple(other.coords) == tuple(first.coords) and other.core_on_chip != first.core_on_chip:
            stride = index
            break
    if stride is None or rep % (2 * stride):
        return None
    grid = devices.reshape(rep // (2 * stride), 2, stride, parts)
    for spot in np.ndindex(grid.shape[0], grid.shape[2], grid.shape[3]):
        low = grid[spot[0], 0, spot[1], spot[2]]
        high = grid[spot[0], 1, spot[1], spot[2]]
        if tuple(low.coords) != tuple(high.coords) or low.core_on_chip == high.core_on_chip:
            return None
    return Mesh(grid, ("outer", "core", "inner", "shard"))


def solution(mesh):
    def specs(rep):
        ins = (P(rep, "shard", None), P(rep, None), P(rep, "shard", None)) + (P("shard", None),) * 4 + (
            P("shard"),
        ) * 9
        outs = (P(rep, "shard", None), P(rep, "shard", None)) + (P("shard", None),) * 4 + (P("shard"),) * 9
        return ins, outs

    ins, outs = specs("rep")
    plain = jax.shard_map(local, mesh=mesh, in_specs=ins, out_specs=outs, check_vma=False)
    split = split_rep(mesh)
    if split is None:
        return plain
    ins, outs = specs(("outer", "core", "inner"))
    fast = jax.shard_map(clip_local, mesh=split, in_specs=ins, out_specs=outs, check_vma=False)
    rep, parts = mesh.devices.shape

    def run(*args):
        if (args[0].shape[0] // rep) % parts == 0:
            return fast(*args)
        return plain(*args)

    return run
```

```python
import jax
import jax.numpy as jnp
from jax import lax
from jax.sharding import Mesh, PartitionSpec as P
import numpy as np

HEADS = 12
HEAD = 64


EPSILON = 1e-05
NEGATIVE = -1e30


def norm_forward(values, gain, shift):
    centred = values - jnp.mean(values, axis=-1, keepdims=True)
    inverse = lax.rsqrt(jnp.mean(centred * centred, axis=-1, keepdims=True) + EPSILON)
    normed = centred * inverse
    return (normed, inverse, (normed * gain + shift).astype(jnp.bfloat16))


def norm_backward(upstream, normed, inverse, gain):
    scaled = upstream * gain
    return inverse * (
        scaled
        - jnp.mean(scaled, axis=-1, keepdims=True)
        - normed * jnp.mean(scaled * normed, axis=-1, keepdims=True)
    )


def gelu_slope(values):
    return (
        0.5 * (1.0 + jax.scipy.special.erf(values * 0.7071067811865476))
        + values * jnp.exp(-0.5 * values * values) * 0.3989422804014327
    )


def inner_rows(left, right):
    return lax.dot_general(
        left, right, (((0,), (0,)), ((), ())), preferred_element_type=jnp.float32
    )


def heads_view(matrix):
    return matrix.reshape(matrix.shape[0], HEADS, HEAD)


def score_block(query_rows, key_rows, key_live):
    scores = jnp.einsum(
        "qhd,khd->hqk",
        heads_view(query_rows),
        heads_view(key_rows),
        preferred_element_type=jnp.float32,
    ) * HEAD ** (-0.5)
    return jnp.where(key_live[None, None, :], scores, NEGATIVE)


def attend_clip(items):
    query_rows, pair_rows, key_live = items
    width = query_rows.shape[1]
    scores = score_block(query_rows, pair_rows[:, :width], key_live)
    highest = jnp.max(scores, axis=-1, keepdims=True)
    logsum = highest + jnp.log(jnp.sum(jnp.exp(scores - highest), axis=-1, keepdims=True))
    probs_low = jnp.exp(scores - logsum).astype(jnp.bfloat16)
    attended = jnp.einsum(
        "hqk,khd->qhd",
        probs_low,
        heads_view(pair_rows[:, width:]),
        preferred_element_type=jnp.float32,
    )
    return (attended.reshape(query_rows.shape[0], width).astype(jnp.bfloat16), logsum[:, :, 0].T)


def score_grads(query_rows, dattended, logsum, delta, pair_rows, key_live):
    width = query_rows.shape[1]
    scores = score_block(query_rows, pair_rows[:, :width], key_live)
    probs = jnp.exp(scores - logsum.T[:, :, None])
    dprob = jnp.einsum(
        "qhd,khd->hqk",
        heads_view(dattended),
        heads_view(pair_rows[:, width:]),
        preferred_element_type=jnp.float32,
    )
    dscore = (probs * (dprob - delta.T[:, :, None]) * HEAD ** (-0.5)).astype(jnp.bfloat16)
    return (probs.astype(jnp.bfloat16), dscore)


def both_grads(items):
    query_rows, dattended, logsum, delta, pair_rows, key_live = items
    width = query_rows.shape[1]
    probs_low, dscore = score_grads(query_rows, dattended, logsum, delta, pair_rows, key_live)
    dqueries = jnp.einsum(
        "hqk,khd->qhd", dscore, heads_view(pair_rows[:, :width]), preferred_element_type=jnp.float32
    ).reshape(query_rows.shape[0], width)
    dkeys = jnp.einsum(
        "hqk,qhd->khd", dscore, heads_view(query_rows), preferred_element_type=jnp.float32
    )
    dvalues = jnp.einsum(
        "hqk,qhd->khd", probs_low, heads_view(dattended), preferred_element_type=jnp.float32
    )
    key_count = pair_rows.shape[0]
    return (
        dqueries,
        jnp.concatenate(
            [dkeys.reshape(key_count, width), dvalues.reshape(key_count, width)], axis=1
        ),
    )


def local(
    tokens,
    lengths,
    cotangent,
    attention_weight,
    output_weight,
    expand_weight,
    contract_weight,
    first_gain,
    first_shift,
    query_bias,
    value_bias,
    output_bias,
    second_gain,
    second_shift,
    expand_bias,
    contract_bias,
):
    clip_count, slot_count, width = tokens.shape
    parts = lax.axis_size("shard")
    frame_count = slot_count * parts
    place = lax.axis_index("shard")
    row_total = clip_count * slot_count
    gathered = (
        lax.all_gather(attention_weight, "shard", axis=0, tiled=True),
        lax.all_gather(output_weight, "shard", axis=0, tiled=True),
        lax.all_gather(expand_weight, "shard", axis=0, tiled=True),
        lax.all_gather(contract_weight, "shard", axis=0, tiled=True),
        lax.all_gather(first_gain, "shard", axis=0, tiled=True),
        lax.all_gather(first_shift, "shard", axis=0, tiled=True),
        lax.all_gather(query_bias, "shard", axis=0, tiled=True),
        lax.all_gather(value_bias, "shard", axis=0, tiled=True),
        lax.all_gather(output_bias, "shard", axis=0, tiled=True),
        lax.all_gather(second_gain, "shard", axis=0, tiled=True),
        lax.all_gather(second_shift, "shard", axis=0, tiled=True),
        lax.all_gather(expand_bias, "shard", axis=0, tiled=True),
        lax.all_gather(contract_bias, "shard", axis=0, tiled=True),
    )
    vectors = [entry.astype(jnp.float32) for entry in gathered[4:]]
    own_length = jnp.sum(jnp.where(jnp.arange(parts)[None, :] == place, lengths, 0), axis=1)
    row_live = jnp.arange(slot_count)[None, :] < own_length[:, None]
    key_live = (jnp.arange(slot_count)[None, None, :] < lengths[:, :, None]).reshape(
        clip_count, frame_count
    )
    inputs = tokens.reshape(row_total, width).astype(jnp.float32)
    first_normed, first_inverse, first_act = norm_forward(inputs, vectors[0], vectors[1])
    mixed = jnp.dot(first_act, gathered[0], preferred_element_type=jnp.float32)
    mixed = mixed + jnp.concatenate([vectors[2], jnp.zeros_like(vectors[2]), vectors[3]])
    mixed_low = mixed.astype(jnp.bfloat16)
    query_rows = mixed_low[:, :width].reshape(clip_count, slot_count, width)
    pair_own = mixed_low[:, width:].reshape(clip_count, slot_count, 2 * width)
    pair_all = lax.all_gather(pair_own, "shard", axis=1, tiled=True)
    attended, logsum = lax.map(attend_clip, (query_rows, pair_all, key_live))
    attended_flat = attended.reshape(row_total, width)
    residual = (
        inputs
        + jnp.dot(attended_flat, gathered[1], preferred_element_type=jnp.float32)
        + vectors[4]
    )
    second_normed, second_inverse, second_act = norm_forward(residual, vectors[5], vectors[6])
    pre = jnp.dot(second_act, gathered[2], preferred_element_type=jnp.float32) + vectors[7]
    hidden_act = jax.nn.gelu(pre, approximate=False).astype(jnp.bfloat16)
    block_output = (
        residual + jnp.dot(hidden_act, gathered[3], preferred_element_type=jnp.float32) + vectors[8]
    )
    backward = (
        lax.all_gather(attention_weight, "shard", axis=0, tiled=True),
        lax.all_gather(output_weight, "shard", axis=0, tiled=True),
        lax.all_gather(expand_weight, "shard", axis=0, tiled=True),
        lax.all_gather(contract_weight, "shard", axis=0, tiled=True),
        lax.all_gather(first_gain, "shard", axis=0, tiled=True),
        lax.all_gather(first_shift, "shard", axis=0, tiled=True),
        lax.all_gather(query_bias, "shard", axis=0, tiled=True),
        lax.all_gather(value_bias, "shard", axis=0, tiled=True),
        lax.all_gather(output_bias, "shard", axis=0, tiled=True),
        lax.all_gather(second_gain, "shard", axis=0, tiled=True),
        lax.all_gather(second_shift, "shard", axis=0, tiled=True),
        lax.all_gather(expand_bias, "shard", axis=0, tiled=True),
        lax.all_gather(contract_bias, "shard", axis=0, tiled=True),
    )
    back_vectors = [entry.astype(jnp.float32) for entry in backward[4:]]
    error = cotangent.reshape(row_total, width) * row_live.reshape(row_total, 1).astype(jnp.float32)
    error_low = error.astype(jnp.bfloat16)
    contract_bias_grad = jnp.sum(error, axis=0)
    contract_grad = inner_rows(hidden_act, error_low)
    dpre = lax.dot_general(
        error_low, backward[3], (((1,), (1,)), ((), ())), preferred_element_type=jnp.float32
    ) * gelu_slope(pre)
    expand_bias_grad = jnp.sum(dpre, axis=0)
    dpre_low = dpre.astype(jnp.bfloat16)
    expand_grad = inner_rows(second_act, dpre_low)
    dsecond = lax.dot_general(
        dpre_low, backward[2], (((1,), (1,)), ((), ())), preferred_element_type=jnp.float32
    )
    second_gain_grad = jnp.sum(dsecond * second_normed, axis=0)
    second_shift_grad = jnp.sum(dsecond, axis=0)
    dresidual = error + norm_backward(dsecond, second_normed, second_inverse, back_vectors[5])
    output_bias_grad = jnp.sum(dresidual, axis=0)
    dresidual_low = dresidual.astype(jnp.bfloat16)
    output_grad = inner_rows(attended_flat, dresidual_low)
    dattended = lax.dot_general(
        dresidual_low, backward[1], (((1,), (1,)), ((), ())), preferred_element_type=jnp.float32
    ).astype(jnp.bfloat16)
    delta = jnp.sum(
        heads_view(dattended.astype(jnp.float32)) * heads_view(attended_flat.astype(jnp.float32)),
        axis=-1,
    )
    delta = delta.reshape(clip_count, slot_count, HEADS)
    dattended_clips = dattended.reshape(clip_count, slot_count, width)
    dqueries, pair_terms = lax.map(
        both_grads, (query_rows, dattended_clips, logsum, delta, pair_all, key_live)
    )
    pair_grads = lax.psum_scatter(pair_terms, "shard", scatter_dimension=1, tiled=True)
    dqueries_flat = dqueries.reshape(row_total, width)
    pair_flat = pair_grads.reshape(row_total, 2 * width)
    dmixed = jnp.concatenate([dqueries_flat, pair_flat], axis=1)
    query_bias_grad = jnp.sum(dqueries_flat, axis=0)
    value_bias_grad = jnp.sum(pair_flat[:, width:], axis=0)
    dmixed_low = dmixed.astype(jnp.bfloat16)
    attention_grad = inner_rows(first_act, dmixed_low)
    dfirst = lax.dot_general(
        dmixed_low, backward[0], (((1,), (1,)), ((), ())), preferred_element_type=jnp.float32
    )
    first_gain_grad = jnp.sum(dfirst * first_normed, axis=0)
    first_shift_grad = jnp.sum(dfirst, axis=0)
    input_grad = dresidual + norm_backward(dfirst, first_normed, first_inverse, back_vectors[0])
    shares = (
        lax.psum_scatter(attention_grad, "shard", scatter_dimension=0, tiled=True),
        lax.psum_scatter(output_grad, "shard", scatter_dimension=0, tiled=True),
        lax.psum_scatter(expand_grad, "shard", scatter_dimension=0, tiled=True),
        lax.psum_scatter(contract_grad, "shard", scatter_dimension=0, tiled=True),
        lax.psum_scatter(first_gain_grad, "shard", scatter_dimension=0, tiled=True),
        lax.psum_scatter(first_shift_grad, "shard", scatter_dimension=0, tiled=True),
        lax.psum_scatter(query_bias_grad, "shard", scatter_dimension=0, tiled=True),
        lax.psum_scatter(value_bias_grad, "shard", scatter_dimension=0, tiled=True),
        lax.psum_scatter(output_bias_grad, "shard", scatter_dimension=0, tiled=True),
        lax.psum_scatter(second_gain_grad, "shard", scatter_dimension=0, tiled=True),
        lax.psum_scatter(second_shift_grad, "shard", scatter_dimension=0, tiled=True),
        lax.psum_scatter(expand_bias_grad, "shard", scatter_dimension=0, tiled=True),
        lax.psum_scatter(contract_bias_grad, "shard", scatter_dimension=0, tiled=True),
    )
    totals = lax.psum(
        (
            shares[0],
            shares[1],
            shares[2],
            shares[3],
            shares[4],
            shares[5],
            shares[6],
            shares[7],
            shares[8],
            shares[9],
            shares[10],
            shares[11],
            shares[12],
        ),
        "rep",
    )
    return (
        block_output.reshape(clip_count, slot_count, width),
        input_grad.reshape(clip_count, slot_count, width),
        totals[0],
        totals[1],
        totals[2],
        totals[3],
        totals[4],
        totals[5],
        totals[6],
        totals[7],
        totals[8],
        totals[9],
        totals[10],
        totals[11],
        totals[12],
    )


def clip_layer(tokens, lengths, cotangent_of, weights, vectors, reduce, send_out):
    attention_weight, output_weight, later_weights = weights
    (first_gain, first_shift, query_bias, value_bias, output_bias, second_gain, second_shift,
     expand_bias, contract_bias) = vectors
    clip_count, frame_count, width = tokens.shape
    block_count = lengths.shape[1]
    slot_count = frame_count // block_count
    rows = clip_count * frame_count
    live = (jnp.arange(slot_count)[None, None, :] < lengths[:, :, None]).reshape(clip_count, frame_count)
    scale = HEAD ** (-0.5)
    inputs = tokens.reshape(rows, width).astype(jnp.float32)
    first_normed, first_inverse, first_act = norm_forward(inputs, first_gain, first_shift)
    mixed = jnp.dot(first_act, attention_weight, preferred_element_type=jnp.float32)
    mixed = mixed + jnp.concatenate([query_bias, jnp.zeros_like(query_bias), value_bias])
    mixed_low = mixed.astype(jnp.bfloat16).reshape(clip_count, frame_count, 3, HEADS, HEAD)
    expand_weight, contract_weight = later_weights(mixed_low[0, 0, 0, 0, :1])
    queries = mixed_low[:, :, 0]
    keys = mixed_low[:, :, 1]
    values = mixed_low[:, :, 2]
    scores = jnp.einsum("cqhd,ckhd->chqk", queries, keys, preferred_element_type=jnp.float32) * scale
    scores = jnp.where(live[:, None, None, :], scores, NEGATIVE)
    highest = jnp.max(scores, axis=-1, keepdims=True)
    logsum = highest + jnp.log(jnp.sum(jnp.exp(scores - highest), axis=-1, keepdims=True))
    probs = jnp.exp(scores - logsum)
    probs_low = probs.astype(jnp.bfloat16)
    attended = jnp.einsum("chqk,ckhd->cqhd", probs_low, values, preferred_element_type=jnp.float32)
    attended_flat = attended.reshape(rows, width).astype(jnp.bfloat16)
    residual = inputs + jnp.dot(attended_flat, output_weight, preferred_element_type=jnp.float32) + output_bias
    second_normed, second_inverse, second_act = norm_forward(residual, second_gain, second_shift)
    pre = jnp.dot(second_act, expand_weight, preferred_element_type=jnp.float32) + expand_bias
    hidden_act = jax.nn.gelu(pre, approximate=False).astype(jnp.bfloat16)
    block_output = residual + jnp.dot(hidden_act, contract_weight, preferred_element_type=jnp.float32) + contract_bias
    cotangent = cotangent_of(pre[0, :1])
    error = cotangent.reshape(rows, width) * live.reshape(rows, 1).astype(jnp.float32)
    error_low = error.astype(jnp.bfloat16)
    contract_bias_grad = jnp.sum(error, axis=0)
    contract_grad = inner_rows(hidden_act, error_low)
    contract_chip = chip_sum(contract_grad)
    dpre = lax.dot_general(
        error_low, contract_weight, (((1,), (1,)), ((), ())), preferred_element_type=jnp.float32
    ) * gelu_slope(pre)
    expand_bias_grad = jnp.sum(dpre, axis=0)
    dpre_low = dpre.astype(jnp.bfloat16)
    contract_chip, dpre_low = lax.optimization_barrier((contract_chip, dpre_low))
    contract_part = shard_sum(contract_chip)
    expand_grad = inner_rows(second_act, dpre_low)
    expand_chip = chip_sum(expand_grad)
    dsecond = lax.dot_general(
        dpre_low, expand_weight, (((1,), (1,)), ((), ())), preferred_element_type=jnp.float32
    )
    second_gain_grad = jnp.sum(dsecond * second_normed, axis=0)
    second_shift_grad = jnp.sum(dsecond, axis=0)
    dresidual = error + norm_backward(dsecond, second_normed, second_inverse, second_gain)
    output_bias_grad = jnp.sum(dresidual, axis=0)
    dresidual_low = dresidual.astype(jnp.bfloat16)
    sent_output = send_out(block_output.reshape(clip_count, frame_count, width))
    expand_chip, sent_output, dresidual_low = lax.optimization_barrier((expand_chip, sent_output, dresidual_low))
    expand_part = shard_sum(expand_chip)
    output_grad = inner_rows(attended_flat, dresidual_low)
    output_chip = chip_sum(output_grad)
    dattended = lax.dot_general(
        dresidual_low, output_weight, (((1,), (1,)), ((), ())), preferred_element_type=jnp.float32
    ).astype(jnp.bfloat16)
    contract_part, dattended = lax.optimization_barrier((contract_part, dattended))
    dattended_heads = dattended.reshape(clip_count, frame_count, HEADS, HEAD)
    attended_heads = attended_flat.reshape(clip_count, frame_count, HEADS, HEAD)
    delta = jnp.sum(
        dattended_heads.astype(jnp.float32) * attended_heads.astype(jnp.float32), axis=-1
    )
    dprob = jnp.einsum("cqhd,ckhd->chqk", dattended_heads, values, preferred_element_type=jnp.float32)
    dscore = (probs * (dprob - jnp.transpose(delta, (0, 2, 1))[:, :, :, None]) * scale).astype(jnp.bfloat16)
    dqueries = jnp.einsum("chqk,ckhd->cqhd", dscore, keys, preferred_element_type=jnp.float32)
    dkeys = jnp.einsum("chqk,cqhd->ckhd", dscore, queries, preferred_element_type=jnp.float32)
    dvalues = jnp.einsum("chqk,cqhd->ckhd", probs_low, dattended_heads, preferred_element_type=jnp.float32)
    dmixed = jnp.concatenate(
        [dqueries.reshape(rows, width), dkeys.reshape(rows, width), dvalues.reshape(rows, width)], axis=1
    )
    query_bias_grad = jnp.sum(dmixed[:, :width], axis=0)
    value_bias_grad = jnp.sum(dmixed[:, 2 * width:], axis=0)
    dmixed_low = dmixed.astype(jnp.bfloat16)
    contract_total = reduce(contract_part, contract_grad.shape[0])
    output_chip, expand_part, contract_total, dmixed_low = lax.optimization_barrier(
        (output_chip, expand_part, contract_total, dmixed_low)
    )
    output_part = shard_sum(output_chip)
    expand_total = reduce(expand_part, expand_grad.shape[0])
    attention_grad = inner_rows(first_act, dmixed_low)
    dfirst = lax.optimization_barrier(lax.dot_general(
        dmixed_low, attention_weight, (((1,), (1,)), ((), ())), preferred_element_type=jnp.float32
    ))
    first_gain_grad = jnp.sum(dfirst * first_normed, axis=0)
    first_shift_grad = jnp.sum(dfirst, axis=0)
    input_grad = dresidual + norm_backward(dfirst, first_normed, first_inverse, first_gain)
    output_part, expand_total, input_grad = lax.optimization_barrier((output_part, expand_total, input_grad))
    output_total = reduce(output_part, output_grad.shape[0])
    weight_grads = (attention_grad, output_total, expand_total, contract_total)
    vector_grads = (first_gain_grad, first_shift_grad, query_bias_grad, value_bias_grad, output_bias_grad,
                    second_gain_grad, second_shift_grad, expand_bias_grad, contract_bias_grad)
    return (
        sent_output,
        input_grad.reshape(clip_count, frame_count, width),
        weight_grads,
        vector_grads,
    )


PAIR = [(0, 1), (1, 0)]
OUTER = ("outer", "inner")


def core_pick(core, first, second):
    return jnp.where(core == 0, first, second)


def gather_weight(shard_rows, extra=None):
    parts = lax.axis_size("shard")
    core = lax.axis_index("core")
    rows, width = shard_rows.shape
    half = rows // 2
    mine = lax.dynamic_slice_in_dim(shard_rows, core * half, half, axis=0)
    if extra is not None:
        mine = jnp.concatenate([mine, extra], axis=0)
    mine = lax.all_gather(mine, "shard", axis=0, tiled=False)
    other = lax.ppermute(mine, "core", PAIR)
    first = core_pick(core, mine, other)
    second = core_pick(core, other, mine)
    full = jnp.stack([first[:, :half], second[:, :half]], axis=1).reshape(parts * rows, width)
    if extra is None:
        return full, None
    return full, first[:, half:]


def chip_sum(grad, extra=None):
    parts = lax.axis_size("shard")
    core = lax.axis_index("core")
    width = grad.shape[1]
    rows = grad.shape[0] // parts
    half = rows // 2
    quarters = grad.reshape(parts, 2, half, width)
    keep = lax.dynamic_index_in_dim(quarters, core, axis=1, keepdims=False)
    send = lax.dynamic_index_in_dim(quarters, 1 - core, axis=1, keepdims=False)
    if extra is not None:
        on_first = (core == 0).astype(extra.dtype)
        keep = jnp.concatenate([keep, extra * on_first], axis=1)
        send = jnp.concatenate([send, extra * (1 - on_first)], axis=1)
    return keep + lax.ppermute(send, "core", PAIR)


def shard_sum(chip):
    part = lax.psum_scatter(chip, "shard", scatter_dimension=0, tiled=False)
    if lax.axis_size("inner") > 1:
        part = lax.psum(part, "inner")
    return part


def finish_sum(part, half):
    core = lax.axis_index("core")
    total = line_sum(part)
    other = lax.ppermute(total, "core", PAIR)
    first = core_pick(core, total, other)
    second = core_pick(core, other, total)
    return jnp.concatenate([first[:half], second[:half]], axis=0), first[half:]


def reduce_weight(grad, extra=None):
    half = grad.shape[0] // lax.axis_size("shard") // 2
    return finish_sum(shard_sum(chip_sum(grad, extra)), half)


def line_sum(values):
    groups = lax.axis_size("outer")
    if groups == 1:
        return values
    if groups & (groups - 1):
        return lax.psum(values, "outer")
    here = lax.axis_index("outer")
    length = values.shape[0]
    padded = -(-length // groups) * groups
    held = jnp.pad(values, ((0, padded - length),) + ((0, 0),) * (values.ndim - 1))
    held = held.reshape((groups, padded // groups) + values.shape[1:])
    step = 1
    while step < groups:
        held = held.reshape((held.shape[0] // 2, 2) + held.shape[1:])
        bit = (here // step) % 2
        keep = lax.dynamic_index_in_dim(held, bit, axis=1, keepdims=False)
        send = lax.dynamic_index_in_dim(held, 1 - bit, axis=1, keepdims=False)
        held = keep + lax.ppermute(send, "outer", [(j, j ^ step) for j in range(groups)])
        step *= 2
    step = groups // 2
    while step >= 1:
        bit = (here // step) % 2
        other = lax.ppermute(held, "outer", [(j, j ^ step) for j in range(groups)])
        low = jnp.where(bit == 0, held, other)
        high = jnp.where(bit == 0, other, held)
        held = jnp.stack([low, high], axis=1)
        held = held.reshape((held.shape[0] * 2,) + held.shape[2:])
        step //= 2
    return held.reshape((padded,) + values.shape[1:])[:length]


def gather_packed(blocks, after=None):
    core = lax.axis_index("core")
    mine = lax.all_gather(jnp.concatenate(blocks, axis=0), "shard", axis=0, tiled=False)
    if after is not None:
        mine = mine + (after * 0).astype(mine.dtype)
    other = lax.ppermute(mine, "core", PAIR)
    return core_pick(core, mine, other), core_pick(core, other, mine)


def unpack_rows(first, second, begin, count, shape):
    parts = first.shape[0]
    rows, width = shape
    low = first[:, begin:begin + count].reshape(parts, -1, width)
    high = second[:, begin:begin + count].reshape(parts, -1, width)
    return jnp.stack([low, high], axis=1).reshape(rows, width)


def core_half(shard_rows):
    core = lax.axis_index("core")
    half = shard_rows.shape[0] // 2
    return lax.dynamic_slice_in_dim(shard_rows, core * half, half, axis=0)


def clip_local(tokens, lengths, cotangent, *params):
    clip_count, slot_count, width = tokens.shape
    parts = lax.axis_size("shard")
    place = lax.axis_index("shard")
    own = clip_count // parts
    weight_shards = params[:4]
    vector_shards = params[4:]
    wide = weight_shards[0].shape[1]
    vector_row = jnp.concatenate([entry.reshape(-1) for entry in vector_shards])
    pad = (-vector_row.shape[0]) % wide
    vector_rows = jnp.pad(vector_row, (0, pad)).reshape(-1, wide)
    attention_half = core_half(weight_shards[0])
    output_half = core_half(weight_shards[1]).reshape(-1, wide)
    first, second = gather_packed([attention_half, output_half, vector_rows])
    a_rows = attention_half.shape[0]
    o_rows = output_half.shape[0]
    attention_weight = unpack_rows(first, second, 0, a_rows, (parts * weight_shards[0].shape[0], wide))
    output_weight = unpack_rows(
        first, second, a_rows, o_rows, (parts * weight_shards[1].shape[0], weight_shards[1].shape[1])
    )
    vector_all = first[:, a_rows + o_rows:].reshape(parts, -1)[:, : vector_row.shape[0]]
    vectors = []
    offset = 0
    for entry in vector_shards:
        size = entry.shape[0]
        vectors.append(vector_all[:, offset:offset + size].reshape(parts * size).astype(jnp.float32))
        offset += size
    late = weight_shards[2].shape[1]
    expand_half = core_half(weight_shards[2])
    contract_half = core_half(weight_shards[3]).reshape(-1, late)

    def later_weights(after):
        first_b, second_b = gather_packed([expand_half, contract_half], after)
        e_rows = expand_half.shape[0]
        expand_weight = unpack_rows(first_b, second_b, 0, e_rows, (parts * weight_shards[2].shape[0], late))
        contract_weight = unpack_rows(
            first_b, second_b, e_rows, contract_half.shape[0],
            (parts * weight_shards[3].shape[0], weight_shards[3].shape[1]),
        )
        return expand_weight, contract_weight

    weights = (attention_weight, output_weight, later_weights)
    tokens_clip = lax.all_to_all(tokens, "shard", 0, 1, tiled=True)

    def cotangent_of(after):
        late = cotangent + (after * 0).astype(cotangent.dtype)
        return lax.all_to_all(late, "shard", 0, 1, tiled=True)

    lengths_clip = lax.dynamic_slice_in_dim(lengths, place * own, own, axis=0)
    block_output, input_grad, weight_grads, vector_grads = clip_layer(
        tokens_clip, lengths_clip, cotangent_of, weights, vectors, lambda part, rows: finish_sum(part, rows // parts // 2)[0],
        lambda values: lax.all_to_all(values, "shard", 1, 0, tiled=True),
    )
    input_grad = lax.all_to_all(input_grad, "shard", 1, 0, tiled=True)
    attention_grad = weight_grads[0]
    attention_width = attention_grad.shape[1]
    vector_parts = jnp.concatenate([entry.reshape(parts, -1) for entry in vector_grads], axis=1)
    vector_size = vector_parts.shape[1]
    vpad = (-vector_size) % attention_width
    vector_parts = jnp.pad(vector_parts, ((0, 0), (0, vpad))).reshape(parts, -1, attention_width)
    attention_total, vector_total = reduce_weight(attention_grad, vector_parts)
    totals = (attention_total,) + tuple(weight_grads[1:])
    vector_total = vector_total.reshape(-1)[:vector_size]
    vector_outs = []
    offset = 0
    for entry in vector_shards:
        size = entry.shape[0]
        vector_outs.append(vector_total[offset:offset + size])
        offset += size
    return (block_output, input_grad) + totals + tuple(vector_outs)


def split_rep(mesh):
    devices = mesh.devices
    rep, parts = devices.shape
    first = devices[0, 0]
    stride = None
    for index in range(1, rep):
        other = devices[index, 0]
        if tuple(other.coords) == tuple(first.coords) and other.core_on_chip != first.core_on_chip:
            stride = index
            break
    if stride is None or rep % (2 * stride):
        return None
    grid = devices.reshape(rep // (2 * stride), 2, stride, parts)
    for spot in np.ndindex(grid.shape[0], grid.shape[2], grid.shape[3]):
        low = grid[spot[0], 0, spot[1], spot[2]]
        high = grid[spot[0], 1, spot[1], spot[2]]
        if tuple(low.coords) != tuple(high.coords) or low.core_on_chip == high.core_on_chip:
            return None
    return Mesh(grid, ("outer", "core", "inner", "shard"))


def solution(mesh):
    def specs(rep):
        ins = (P(rep, "shard", None), P(rep, None), P(rep, "shard", None)) + (P("shard", None),) * 4 + (
            P("shard"),
        ) * 9
        outs = (P(rep, "shard", None), P(rep, "shard", None)) + (P("shard", None),) * 4 + (P("shard"),) * 9
        return ins, outs

    ins, outs = specs("rep")
    plain = jax.shard_map(local, mesh=mesh, in_specs=ins, out_specs=outs, check_vma=False)
    split = split_rep(mesh)
    if split is None:
        return plain
    ins, outs = specs(("outer", "core", "inner"))
    fast = jax.shard_map(clip_local, mesh=split, in_specs=ins, out_specs=outs, check_vma=False)
    rep, parts = mesh.devices.shape

    def run(*args):
        if (args[0].shape[0] // rep) % parts == 0:
            return fast(*args)
        return plain(*args)

    return run
```

```python
import jax
import jax.numpy as jnp
from jax import lax
from jax.sharding import Mesh, PartitionSpec as P
import numpy as np

HEADS = 12
HEAD = 64


EPSILON = 1e-05
NEGATIVE = -1e30


def norm_forward(values, gain, shift):
    centred = values - jnp.mean(values, axis=-1, keepdims=True)
    inverse = lax.rsqrt(jnp.mean(centred * centred, axis=-1, keepdims=True) + EPSILON)
    normed = centred * inverse
    return (normed, inverse, (normed * gain + shift).astype(jnp.bfloat16))


def norm_backward(upstream, normed, inverse, gain):
    scaled = upstream * gain
    return inverse * (
        scaled
        - jnp.mean(scaled, axis=-1, keepdims=True)
        - normed * jnp.mean(scaled * normed, axis=-1, keepdims=True)
    )


def gelu_slope(values):
    return (
        0.5 * (1.0 + jax.scipy.special.erf(values * 0.7071067811865476))
        + values * jnp.exp(-0.5 * values * values) * 0.3989422804014327
    )


def inner_rows(left, right):
    return lax.dot_general(
        left, right, (((0,), (0,)), ((), ())), preferred_element_type=jnp.float32
    )


def heads_view(matrix):
    return matrix.reshape(matrix.shape[0], HEADS, HEAD)


def score_block(query_rows, key_rows, key_live):
    scores = jnp.einsum(
        "qhd,khd->hqk",
        heads_view(query_rows),
        heads_view(key_rows),
        preferred_element_type=jnp.float32,
    ) * HEAD ** (-0.5)
    return jnp.where(key_live[None, None, :], scores, NEGATIVE)


def attend_clip(items):
    query_rows, pair_rows, key_live = items
    width = query_rows.shape[1]
    scores = score_block(query_rows, pair_rows[:, :width], key_live)
    highest = jnp.max(scores, axis=-1, keepdims=True)
    logsum = highest + jnp.log(jnp.sum(jnp.exp(scores - highest), axis=-1, keepdims=True))
    probs_low = jnp.exp(scores - logsum).astype(jnp.bfloat16)
    attended = jnp.einsum(
        "hqk,khd->qhd",
        probs_low,
        heads_view(pair_rows[:, width:]),
        preferred_element_type=jnp.float32,
    )
    return (attended.reshape(query_rows.shape[0], width).astype(jnp.bfloat16), logsum[:, :, 0].T)


def score_grads(query_rows, dattended, logsum, delta, pair_rows, key_live):
    width = query_rows.shape[1]
    scores = score_block(query_rows, pair_rows[:, :width], key_live)
    probs = jnp.exp(scores - logsum.T[:, :, None])
    dprob = jnp.einsum(
        "qhd,khd->hqk",
        heads_view(dattended),
        heads_view(pair_rows[:, width:]),
        preferred_element_type=jnp.float32,
    )
    dscore = (probs * (dprob - delta.T[:, :, None]) * HEAD ** (-0.5)).astype(jnp.bfloat16)
    return (probs.astype(jnp.bfloat16), dscore)


def both_grads(items):
    query_rows, dattended, logsum, delta, pair_rows, key_live = items
    width = query_rows.shape[1]
    probs_low, dscore = score_grads(query_rows, dattended, logsum, delta, pair_rows, key_live)
    dqueries = jnp.einsum(
        "hqk,khd->qhd", dscore, heads_view(pair_rows[:, :width]), preferred_element_type=jnp.float32
    ).reshape(query_rows.shape[0], width)
    dkeys = jnp.einsum(
        "hqk,qhd->khd", dscore, heads_view(query_rows), preferred_element_type=jnp.float32
    )
    dvalues = jnp.einsum(
        "hqk,qhd->khd", probs_low, heads_view(dattended), preferred_element_type=jnp.float32
    )
    key_count = pair_rows.shape[0]
    return (
        dqueries,
        jnp.concatenate(
            [dkeys.reshape(key_count, width), dvalues.reshape(key_count, width)], axis=1
        ),
    )


def local(
    tokens,
    lengths,
    cotangent,
    attention_weight,
    output_weight,
    expand_weight,
    contract_weight,
    first_gain,
    first_shift,
    query_bias,
    value_bias,
    output_bias,
    second_gain,
    second_shift,
    expand_bias,
    contract_bias,
):
    clip_count, slot_count, width = tokens.shape
    parts = lax.axis_size("shard")
    frame_count = slot_count * parts
    place = lax.axis_index("shard")
    row_total = clip_count * slot_count
    gathered = (
        lax.all_gather(attention_weight, "shard", axis=0, tiled=True),
        lax.all_gather(output_weight, "shard", axis=0, tiled=True),
        lax.all_gather(expand_weight, "shard", axis=0, tiled=True),
        lax.all_gather(contract_weight, "shard", axis=0, tiled=True),
        lax.all_gather(first_gain, "shard", axis=0, tiled=True),
        lax.all_gather(first_shift, "shard", axis=0, tiled=True),
        lax.all_gather(query_bias, "shard", axis=0, tiled=True),
        lax.all_gather(value_bias, "shard", axis=0, tiled=True),
        lax.all_gather(output_bias, "shard", axis=0, tiled=True),
        lax.all_gather(second_gain, "shard", axis=0, tiled=True),
        lax.all_gather(second_shift, "shard", axis=0, tiled=True),
        lax.all_gather(expand_bias, "shard", axis=0, tiled=True),
        lax.all_gather(contract_bias, "shard", axis=0, tiled=True),
    )
    vectors = [entry.astype(jnp.float32) for entry in gathered[4:]]
    own_length = jnp.sum(jnp.where(jnp.arange(parts)[None, :] == place, lengths, 0), axis=1)
    row_live = jnp.arange(slot_count)[None, :] < own_length[:, None]
    key_live = (jnp.arange(slot_count)[None, None, :] < lengths[:, :, None]).reshape(
        clip_count, frame_count
    )
    inputs = tokens.reshape(row_total, width).astype(jnp.float32)
    first_normed, first_inverse, first_act = norm_forward(inputs, vectors[0], vectors[1])
    mixed = jnp.dot(first_act, gathered[0], preferred_element_type=jnp.float32)
    mixed = mixed + jnp.concatenate([vectors[2], jnp.zeros_like(vectors[2]), vectors[3]])
    mixed_low = mixed.astype(jnp.bfloat16)
    query_rows = mixed_low[:, :width].reshape(clip_count, slot_count, width)
    pair_own = mixed_low[:, width:].reshape(clip_count, slot_count, 2 * width)
    pair_all = lax.all_gather(pair_own, "shard", axis=1, tiled=True)
    attended, logsum = lax.map(attend_clip, (query_rows, pair_all, key_live))
    attended_flat = attended.reshape(row_total, width)
    residual = (
        inputs
        + jnp.dot(attended_flat, gathered[1], preferred_element_type=jnp.float32)
        + vectors[4]
    )
    second_normed, second_inverse, second_act = norm_forward(residual, vectors[5], vectors[6])
    pre = jnp.dot(second_act, gathered[2], preferred_element_type=jnp.float32) + vectors[7]
    hidden_act = jax.nn.gelu(pre, approximate=False).astype(jnp.bfloat16)
    block_output = (
        residual + jnp.dot(hidden_act, gathered[3], preferred_element_type=jnp.float32) + vectors[8]
    )
    backward = (
        lax.all_gather(attention_weight, "shard", axis=0, tiled=True),
        lax.all_gather(output_weight, "shard", axis=0, tiled=True),
        lax.all_gather(expand_weight, "shard", axis=0, tiled=True),
        lax.all_gather(contract_weight, "shard", axis=0, tiled=True),
        lax.all_gather(first_gain, "shard", axis=0, tiled=True),
        lax.all_gather(first_shift, "shard", axis=0, tiled=True),
        lax.all_gather(query_bias, "shard", axis=0, tiled=True),
        lax.all_gather(value_bias, "shard", axis=0, tiled=True),
        lax.all_gather(output_bias, "shard", axis=0, tiled=True),
        lax.all_gather(second_gain, "shard", axis=0, tiled=True),
        lax.all_gather(second_shift, "shard", axis=0, tiled=True),
        lax.all_gather(expand_bias, "shard", axis=0, tiled=True),
        lax.all_gather(contract_bias, "shard", axis=0, tiled=True),
    )
    back_vectors = [entry.astype(jnp.float32) for entry in backward[4:]]
    error = cotangent.reshape(row_total, width) * row_live.reshape(row_total, 1).astype(jnp.float32)
    error_low = error.astype(jnp.bfloat16)
    contract_bias_grad = jnp.sum(error, axis=0)
    contract_grad = inner_rows(hidden_act, error_low)
    dpre = lax.dot_general(
        error_low, backward[3], (((1,), (1,)), ((), ())), preferred_element_type=jnp.float32
    ) * gelu_slope(pre)
    expand_bias_grad = jnp.sum(dpre, axis=0)
    dpre_low = dpre.astype(jnp.bfloat16)
    expand_grad = inner_rows(second_act, dpre_low)
    dsecond = lax.dot_general(
        dpre_low, backward[2], (((1,), (1,)), ((), ())), preferred_element_type=jnp.float32
    )
    second_gain_grad = jnp.sum(dsecond * second_normed, axis=0)
    second_shift_grad = jnp.sum(dsecond, axis=0)
    dresidual = error + norm_backward(dsecond, second_normed, second_inverse, back_vectors[5])
    output_bias_grad = jnp.sum(dresidual, axis=0)
    dresidual_low = dresidual.astype(jnp.bfloat16)
    output_grad = inner_rows(attended_flat, dresidual_low)
    dattended = lax.dot_general(
        dresidual_low, backward[1], (((1,), (1,)), ((), ())), preferred_element_type=jnp.float32
    ).astype(jnp.bfloat16)
    delta = jnp.sum(
        heads_view(dattended.astype(jnp.float32)) * heads_view(attended_flat.astype(jnp.float32)),
        axis=-1,
    )
    delta = delta.reshape(clip_count, slot_count, HEADS)
    dattended_clips = dattended.reshape(clip_count, slot_count, width)
    dqueries, pair_terms = lax.map(
        both_grads, (query_rows, dattended_clips, logsum, delta, pair_all, key_live)
    )
    pair_grads = lax.psum_scatter(pair_terms, "shard", scatter_dimension=1, tiled=True)
    dqueries_flat = dqueries.reshape(row_total, width)
    pair_flat = pair_grads.reshape(row_total, 2 * width)
    dmixed = jnp.concatenate([dqueries_flat, pair_flat], axis=1)
    query_bias_grad = jnp.sum(dqueries_flat, axis=0)
    value_bias_grad = jnp.sum(pair_flat[:, width:], axis=0)
    dmixed_low = dmixed.astype(jnp.bfloat16)
    attention_grad = inner_rows(first_act, dmixed_low)
    dfirst = lax.dot_general(
        dmixed_low, backward[0], (((1,), (1,)), ((), ())), preferred_element_type=jnp.float32
    )
    first_gain_grad = jnp.sum(dfirst * first_normed, axis=0)
    first_shift_grad = jnp.sum(dfirst, axis=0)
    input_grad = dresidual + norm_backward(dfirst, first_normed, first_inverse, back_vectors[0])
    shares = (
        lax.psum_scatter(attention_grad, "shard", scatter_dimension=0, tiled=True),
        lax.psum_scatter(output_grad, "shard", scatter_dimension=0, tiled=True),
        lax.psum_scatter(expand_grad, "shard", scatter_dimension=0, tiled=True),
        lax.psum_scatter(contract_grad, "shard", scatter_dimension=0, tiled=True),
        lax.psum_scatter(first_gain_grad, "shard", scatter_dimension=0, tiled=True),
        lax.psum_scatter(first_shift_grad, "shard", scatter_dimension=0, tiled=True),
        lax.psum_scatter(query_bias_grad, "shard", scatter_dimension=0, tiled=True),
        lax.psum_scatter(value_bias_grad, "shard", scatter_dimension=0, tiled=True),
        lax.psum_scatter(output_bias_grad, "shard", scatter_dimension=0, tiled=True),
        lax.psum_scatter(second_gain_grad, "shard", scatter_dimension=0, tiled=True),
        lax.psum_scatter(second_shift_grad, "shard", scatter_dimension=0, tiled=True),
        lax.psum_scatter(expand_bias_grad, "shard", scatter_dimension=0, tiled=True),
        lax.psum_scatter(contract_bias_grad, "shard", scatter_dimension=0, tiled=True),
    )
    totals = lax.psum(
        (
            shares[0],
            shares[1],
            shares[2],
            shares[3],
            shares[4],
            shares[5],
            shares[6],
            shares[7],
            shares[8],
            shares[9],
            shares[10],
            shares[11],
            shares[12],
        ),
        "rep",
    )
    return (
        block_output.reshape(clip_count, slot_count, width),
        input_grad.reshape(clip_count, slot_count, width),
        totals[0],
        totals[1],
        totals[2],
        totals[3],
        totals[4],
        totals[5],
        totals[6],
        totals[7],
        totals[8],
        totals[9],
        totals[10],
        totals[11],
        totals[12],
    )


def clip_layer(tokens, lengths, cotangent_of, weights, vectors, reduce, send_out):
    attention_weight, output_weight, later_weights = weights
    (first_gain, first_shift, query_bias, value_bias, output_bias, second_gain, second_shift,
     expand_bias, contract_bias) = vectors
    clip_count, frame_count, width = tokens.shape
    block_count = lengths.shape[1]
    slot_count = frame_count // block_count
    rows = clip_count * frame_count
    live = (jnp.arange(slot_count)[None, None, :] < lengths[:, :, None]).reshape(clip_count, frame_count)
    scale = HEAD ** (-0.5)
    inputs = tokens.reshape(rows, width).astype(jnp.float32)
    first_normed, first_inverse, first_act = norm_forward(inputs, first_gain, first_shift)
    mixed = jnp.dot(first_act, attention_weight, preferred_element_type=jnp.float32)
    mixed = mixed + jnp.concatenate([query_bias, jnp.zeros_like(query_bias), value_bias])
    mixed_low = mixed.astype(jnp.bfloat16).reshape(clip_count, frame_count, 3, HEADS, HEAD)
    expand_weight, contract_weight = later_weights(mixed_low[0, 0, 0, 0, :1])
    queries = mixed_low[:, :, 0]
    keys = mixed_low[:, :, 1]
    values = mixed_low[:, :, 2]
    scores = jnp.einsum("cqhd,ckhd->chqk", queries, keys, preferred_element_type=jnp.float32) * scale
    scores = jnp.where(live[:, None, None, :], scores, NEGATIVE)
    highest = jnp.max(scores, axis=-1, keepdims=True)
    logsum = highest + jnp.log(jnp.sum(jnp.exp(scores - highest), axis=-1, keepdims=True))
    probs = jnp.exp(scores - logsum)
    probs_low = probs.astype(jnp.bfloat16)
    attended = jnp.einsum("chqk,ckhd->cqhd", probs_low, values, preferred_element_type=jnp.float32)
    attended_flat = attended.reshape(rows, width).astype(jnp.bfloat16)
    residual = inputs + jnp.dot(attended_flat, output_weight, preferred_element_type=jnp.float32) + output_bias
    second_normed, second_inverse, second_act = norm_forward(residual, second_gain, second_shift)
    pre = jnp.dot(second_act, expand_weight, preferred_element_type=jnp.float32) + expand_bias
    hidden_act = jax.nn.gelu(pre, approximate=False).astype(jnp.bfloat16)
    block_output = residual + jnp.dot(hidden_act, contract_weight, preferred_element_type=jnp.float32) + contract_bias
    cotangent = cotangent_of(pre[0, :1])
    error = cotangent.reshape(rows, width) * live.reshape(rows, 1).astype(jnp.float32)
    error_low = error.astype(jnp.bfloat16)
    contract_bias_grad = jnp.sum(error, axis=0)
    contract_grad = inner_rows(hidden_act, error_low)
    contract_chip = chip_sum(contract_grad)
    dpre = lax.dot_general(
        error_low, contract_weight, (((1,), (1,)), ((), ())), preferred_element_type=jnp.float32
    ) * gelu_slope(pre)
    expand_bias_grad = jnp.sum(dpre, axis=0)
    dpre_low = dpre.astype(jnp.bfloat16)
    contract_chip, dpre_low = lax.optimization_barrier((contract_chip, dpre_low))
    contract_part = shard_sum(contract_chip)
    expand_grad = inner_rows(second_act, dpre_low)
    expand_chip = chip_sum(expand_grad)
    dsecond = lax.dot_general(
        dpre_low, expand_weight, (((1,), (1,)), ((), ())), preferred_element_type=jnp.float32
    )
    second_gain_grad = jnp.sum(dsecond * second_normed, axis=0)
    second_shift_grad = jnp.sum(dsecond, axis=0)
    dresidual = error + norm_backward(dsecond, second_normed, second_inverse, second_gain)
    output_bias_grad = jnp.sum(dresidual, axis=0)
    dresidual_low = dresidual.astype(jnp.bfloat16)
    sent_output = send_out(block_output)
    expand_chip, dresidual_low = lax.optimization_barrier((expand_chip, dresidual_low))
    expand_part = shard_sum(expand_chip)
    output_grad = inner_rows(attended_flat, dresidual_low)
    output_chip = chip_sum(output_grad)
    dattended = lax.dot_general(
        dresidual_low, output_weight, (((1,), (1,)), ((), ())), preferred_element_type=jnp.float32
    ).astype(jnp.bfloat16)
    contract_part, dattended = lax.optimization_barrier((contract_part, dattended))
    dattended_heads = dattended.reshape(clip_count, frame_count, HEADS, HEAD)
    attended_heads = attended_flat.reshape(clip_count, frame_count, HEADS, HEAD)
    delta = jnp.sum(
        dattended_heads.astype(jnp.float32) * attended_heads.astype(jnp.float32), axis=-1
    )
    dprob = jnp.einsum("cqhd,ckhd->chqk", dattended_heads, values, preferred_element_type=jnp.float32)
    dscore = (probs * (dprob - jnp.transpose(delta, (0, 2, 1))[:, :, :, None]) * scale).astype(jnp.bfloat16)
    dqueries = jnp.einsum("chqk,ckhd->cqhd", dscore, keys, preferred_element_type=jnp.float32)
    dkeys = jnp.einsum("chqk,cqhd->ckhd", dscore, queries, preferred_element_type=jnp.float32)
    dvalues = jnp.einsum("chqk,cqhd->ckhd", probs_low, dattended_heads, preferred_element_type=jnp.float32)
    dmixed = jnp.concatenate(
        [dqueries.reshape(rows, width), dkeys.reshape(rows, width), dvalues.reshape(rows, width)], axis=1
    )
    query_bias_grad = jnp.sum(dmixed[:, :width], axis=0)
    value_bias_grad = jnp.sum(dmixed[:, 2 * width:], axis=0)
    dmixed_low = dmixed.astype(jnp.bfloat16)
    contract_total = reduce(contract_part, contract_grad.shape[0])
    output_chip, expand_part, contract_total, sent_output, dmixed_low = lax.optimization_barrier(
        (output_chip, expand_part, contract_total, sent_output, dmixed_low)
    )
    output_part = shard_sum(output_chip)
    expand_total = reduce(expand_part, expand_grad.shape[0])
    attention_grad = inner_rows(first_act, dmixed_low)
    dfirst = lax.optimization_barrier(lax.dot_general(
        dmixed_low, attention_weight, (((1,), (1,)), ((), ())), preferred_element_type=jnp.float32
    ))
    first_gain_grad = jnp.sum(dfirst * first_normed, axis=0)
    first_shift_grad = jnp.sum(dfirst, axis=0)
    input_grad = dresidual + norm_backward(dfirst, first_normed, first_inverse, first_gain)
    output_part, expand_total, input_grad = lax.optimization_barrier((output_part, expand_total, input_grad))
    weight_grads = (attention_grad, output_part, expand_total, contract_total)
    vector_grads = (first_gain_grad, first_shift_grad, query_bias_grad, value_bias_grad, output_bias_grad,
                    second_gain_grad, second_shift_grad, expand_bias_grad, contract_bias_grad)
    return (
        sent_output,
        input_grad,
        weight_grads,
        vector_grads,
    )


PAIR = [(0, 1), (1, 0)]
OUTER = ("outer", "inner")


def core_pick(core, first, second):
    return jnp.where(core == 0, first, second)


def gather_weight(shard_rows, extra=None):
    parts = lax.axis_size("shard")
    core = lax.axis_index("core")
    rows, width = shard_rows.shape
    half = rows // 2
    mine = lax.dynamic_slice_in_dim(shard_rows, core * half, half, axis=0)
    if extra is not None:
        mine = jnp.concatenate([mine, extra], axis=0)
    mine = lax.all_gather(mine, "shard", axis=0, tiled=False)
    other = lax.ppermute(mine, "core", PAIR)
    first = core_pick(core, mine, other)
    second = core_pick(core, other, mine)
    full = jnp.stack([first[:, :half], second[:, :half]], axis=1).reshape(parts * rows, width)
    if extra is None:
        return full, None
    return full, first[:, half:]


def chip_sum(grad, extra=None):
    parts = lax.axis_size("shard")
    core = lax.axis_index("core")
    width = grad.shape[1]
    rows = grad.shape[0] // parts
    half = rows // 2
    quarters = grad.reshape(parts, 2, half, width)
    keep = lax.dynamic_index_in_dim(quarters, core, axis=1, keepdims=False)
    send = lax.dynamic_index_in_dim(quarters, 1 - core, axis=1, keepdims=False)
    if extra is not None:
        on_first = (core == 0).astype(extra.dtype)
        keep = jnp.concatenate([keep, extra * on_first], axis=1)
        send = jnp.concatenate([send, extra * (1 - on_first)], axis=1)
    return keep + lax.ppermute(send, "core", PAIR)


def shard_sum(chip):
    part = lax.psum_scatter(chip, "shard", scatter_dimension=0, tiled=False)
    if lax.axis_size("inner") > 1:
        part = lax.psum(part, "inner")
    return part


def finish_sum(part, half):
    core = lax.axis_index("core")
    total = line_sum(part)
    other = lax.ppermute(total, "core", PAIR)
    first = core_pick(core, total, other)
    second = core_pick(core, other, total)
    return jnp.concatenate([first[:half], second[:half]], axis=0), first[half:]


def finish_many(parts, halves):
    core = lax.axis_index("core")
    flat = jnp.concatenate([part.reshape(-1) for part in parts])
    total = line_sum(flat)
    other = lax.ppermute(total, "core", PAIR)
    first = core_pick(core, total, other)
    second = core_pick(core, other, total)
    outs = []
    offset = 0
    for part, half in zip(parts, halves):
        size = part.size
        low = first[offset:offset + size].reshape(part.shape)
        high = second[offset:offset + size].reshape(part.shape)
        outs.append((jnp.concatenate([low[:half], high[:half]], axis=0), low[half:]))
        offset += size
    return outs


def reduce_weight(grad, extra=None):
    half = grad.shape[0] // lax.axis_size("shard") // 2
    return finish_sum(shard_sum(chip_sum(grad, extra)), half)


def line_sum(values):
    groups = lax.axis_size("outer")
    if groups == 1:
        return values
    if groups & (groups - 1):
        return lax.psum(values, "outer")
    here = lax.axis_index("outer")
    length = values.shape[0]
    padded = -(-length // groups) * groups
    held = jnp.pad(values, ((0, padded - length),) + ((0, 0),) * (values.ndim - 1))
    held = held.reshape((groups, padded // groups) + values.shape[1:])
    step = 1
    while step < groups:
        held = held.reshape((held.shape[0] // 2, 2) + held.shape[1:])
        bit = (here // step) % 2
        keep = lax.dynamic_index_in_dim(held, bit, axis=1, keepdims=False)
        send = lax.dynamic_index_in_dim(held, 1 - bit, axis=1, keepdims=False)
        held = keep + lax.ppermute(send, "outer", [(j, j ^ step) for j in range(groups)])
        step *= 2
    step = groups // 2
    while step >= 1:
        bit = (here // step) % 2
        other = lax.ppermute(held, "outer", [(j, j ^ step) for j in range(groups)])
        low = jnp.where(bit == 0, held, other)
        high = jnp.where(bit == 0, other, held)
        held = jnp.stack([low, high], axis=1)
        held = held.reshape((held.shape[0] * 2,) + held.shape[2:])
        step //= 2
    return held.reshape((padded,) + values.shape[1:])[:length]


def gather_packed(blocks, after=None):
    core = lax.axis_index("core")
    mine = lax.all_gather(jnp.concatenate(blocks, axis=0), "shard", axis=0, tiled=False)
    if after is not None:
        mine = mine + (after * 0).astype(mine.dtype)
    other = lax.ppermute(mine, "core", PAIR)
    return core_pick(core, mine, other), core_pick(core, other, mine)


def unpack_rows(first, second, begin, count, shape):
    parts = first.shape[0]
    rows, width = shape
    low = first[:, begin:begin + count].reshape(parts, -1, width)
    high = second[:, begin:begin + count].reshape(parts, -1, width)
    return jnp.stack([low, high], axis=1).reshape(rows, width)


def core_half(shard_rows):
    core = lax.axis_index("core")
    half = shard_rows.shape[0] // 2
    return lax.dynamic_slice_in_dim(shard_rows, core * half, half, axis=0)


def clip_local(tokens, lengths, cotangent, *params):
    clip_count, slot_count, width = tokens.shape
    parts = lax.axis_size("shard")
    place = lax.axis_index("shard")
    own = clip_count // parts
    weight_shards = params[:4]
    vector_shards = params[4:]
    wide = weight_shards[0].shape[1]
    vector_row = jnp.concatenate([entry.reshape(-1) for entry in vector_shards])
    pad = (-vector_row.shape[0]) % wide
    vector_rows = jnp.pad(vector_row, (0, pad)).reshape(-1, wide)
    attention_half = core_half(weight_shards[0])
    output_half = core_half(weight_shards[1]).reshape(-1, wide)
    first, second = gather_packed([attention_half, output_half, vector_rows])
    a_rows = attention_half.shape[0]
    o_rows = output_half.shape[0]
    attention_weight = unpack_rows(first, second, 0, a_rows, (parts * weight_shards[0].shape[0], wide))
    output_weight = unpack_rows(
        first, second, a_rows, o_rows, (parts * weight_shards[1].shape[0], weight_shards[1].shape[1])
    )
    vector_all = first[:, a_rows + o_rows:].reshape(parts, -1)[:, : vector_row.shape[0]]
    vectors = []
    offset = 0
    for entry in vector_shards:
        size = entry.shape[0]
        vectors.append(vector_all[:, offset:offset + size].reshape(parts * size).astype(jnp.float32))
        offset += size
    late = weight_shards[2].shape[1]
    expand_half = core_half(weight_shards[2])
    contract_half = core_half(weight_shards[3]).reshape(-1, late)

    def later_weights(after):
        first_b, second_b = gather_packed([expand_half, contract_half], after)
        e_rows = expand_half.shape[0]
        expand_weight = unpack_rows(first_b, second_b, 0, e_rows, (parts * weight_shards[2].shape[0], late))
        contract_weight = unpack_rows(
            first_b, second_b, e_rows, contract_half.shape[0],
            (parts * weight_shards[3].shape[0], weight_shards[3].shape[1]),
        )
        return expand_weight, contract_weight

    weights = (attention_weight, output_weight, later_weights)
    def gather_rows(values):
        moved = lax.all_to_all(values.reshape(clip_count * slot_count, width), "shard", 0, 0, tiled=True)
        moved = moved.reshape(parts, own, slot_count, width)
        return jnp.transpose(moved, (1, 0, 2, 3)).reshape(own, parts * slot_count, width) if own > 1 else moved.reshape(own, parts * slot_count, width)

    def scatter_rows(values):
        rows = values.reshape(own, parts, slot_count, width)
        if own > 1:
            rows = jnp.transpose(rows, (1, 0, 2, 3))
        moved = lax.all_to_all(rows.reshape(own * parts * slot_count, width), "shard", 0, 0, tiled=True)
        return moved.reshape(clip_count, slot_count, width)

    tokens_clip = gather_rows(tokens)

    def cotangent_of(after):
        late = cotangent + (after * 0).astype(cotangent.dtype)
        return gather_rows(late)

    lengths_clip = lax.dynamic_slice_in_dim(lengths, place * own, own, axis=0)
    block_output, input_grad, weight_grads, vector_grads = clip_layer(
        tokens_clip, lengths_clip, cotangent_of, weights, vectors, lambda part, rows: finish_sum(part, rows // parts // 2)[0],
        scatter_rows,
    )
    input_grad = scatter_rows(input_grad)
    attention_grad = weight_grads[0]
    attention_width = attention_grad.shape[1]
    vector_parts = jnp.concatenate([entry.reshape(parts, -1) for entry in vector_grads], axis=1)
    vector_size = vector_parts.shape[1]
    vpad = (-vector_size) % attention_width
    vector_parts = jnp.pad(vector_parts, ((0, 0), (0, vpad))).reshape(parts, -1, attention_width)
    attention_part = shard_sum(chip_sum(attention_grad, vector_parts))
    output_part = weight_grads[1]
    (attention_total, vector_total), (output_total, _) = finish_many(
        [attention_part, output_part],
        [attention_grad.shape[0] // parts // 2, params[1].shape[0] // 2],
    )
    totals = (attention_total, output_total) + tuple(weight_grads[2:])
    vector_total = vector_total.reshape(-1)[:vector_size]
    vector_outs = []
    offset = 0
    for entry in vector_shards:
        size = entry.shape[0]
        vector_outs.append(vector_total[offset:offset + size])
        offset += size
    return (block_output, input_grad) + totals + tuple(vector_outs)


def split_rep(mesh):
    devices = mesh.devices
    rep, parts = devices.shape
    first = devices[0, 0]
    stride = None
    for index in range(1, rep):
        other = devices[index, 0]
        if tuple(other.coords) == tuple(first.coords) and other.core_on_chip != first.core_on_chip:
            stride = index
            break
    if stride is None or rep % (2 * stride):
        return None
    grid = devices.reshape(rep // (2 * stride), 2, stride, parts)
    for spot in np.ndindex(grid.shape[0], grid.shape[2], grid.shape[3]):
        low = grid[spot[0], 0, spot[1], spot[2]]
        high = grid[spot[0], 1, spot[1], spot[2]]
        if tuple(low.coords) != tuple(high.coords) or low.core_on_chip == high.core_on_chip:
            return None
    return Mesh(grid, ("outer", "core", "inner", "shard"))


def solution(mesh):
    def specs(rep):
        ins = (P(rep, "shard", None), P(rep, None), P(rep, "shard", None)) + (P("shard", None),) * 4 + (
            P("shard"),
        ) * 9
        outs = (P(rep, "shard", None), P(rep, "shard", None)) + (P("shard", None),) * 4 + (P("shard"),) * 9
        return ins, outs

    ins, outs = specs("rep")
    plain = jax.shard_map(local, mesh=mesh, in_specs=ins, out_specs=outs, check_vma=False)
    split = split_rep(mesh)
    if split is None:
        return plain
    ins, outs = specs(("outer", "core", "inner"))
    fast = jax.shard_map(clip_local, mesh=split, in_specs=ins, out_specs=outs, check_vma=False)
    rep, parts = mesh.devices.shape

    def run(*args):
        if (args[0].shape[0] // rep) % parts == 0:
            return fast(*args)
        return plain(*args)

    return run
```

```python
import jax
import jax.numpy as jnp
from jax import lax
from jax.sharding import Mesh, PartitionSpec as P
import numpy as np

HEADS = 12
HEAD = 64


EPSILON = 1e-05
NEGATIVE = -1e30


def norm_forward(values, gain, shift):
    centred = values - jnp.mean(values, axis=-1, keepdims=True)
    inverse = lax.rsqrt(jnp.mean(centred * centred, axis=-1, keepdims=True) + EPSILON)
    normed = centred * inverse
    return (normed, inverse, (normed * gain + shift).astype(jnp.bfloat16))


def norm_backward(upstream, normed, inverse, gain):
    scaled = upstream * gain
    return inverse * (
        scaled
        - jnp.mean(scaled, axis=-1, keepdims=True)
        - normed * jnp.mean(scaled * normed, axis=-1, keepdims=True)
    )


def gelu_slope(values):
    return (
        0.5 * (1.0 + jax.scipy.special.erf(values * 0.7071067811865476))
        + values * jnp.exp(-0.5 * values * values) * 0.3989422804014327
    )


def inner_rows(left, right):
    return lax.dot_general(
        left, right, (((0,), (0,)), ((), ())), preferred_element_type=jnp.float32
    )


def heads_view(matrix):
    return matrix.reshape(matrix.shape[0], HEADS, HEAD)


def score_block(query_rows, key_rows, key_live):
    scores = jnp.einsum(
        "qhd,khd->hqk",
        heads_view(query_rows),
        heads_view(key_rows),
        preferred_element_type=jnp.float32,
    ) * HEAD ** (-0.5)
    return jnp.where(key_live[None, None, :], scores, NEGATIVE)


def attend_clip(items):
    query_rows, pair_rows, key_live = items
    width = query_rows.shape[1]
    scores = score_block(query_rows, pair_rows[:, :width], key_live)
    highest = jnp.max(scores, axis=-1, keepdims=True)
    logsum = highest + jnp.log(jnp.sum(jnp.exp(scores - highest), axis=-1, keepdims=True))
    probs_low = jnp.exp(scores - logsum).astype(jnp.bfloat16)
    attended = jnp.einsum(
        "hqk,khd->qhd",
        probs_low,
        heads_view(pair_rows[:, width:]),
        preferred_element_type=jnp.float32,
    )
    return (attended.reshape(query_rows.shape[0], width).astype(jnp.bfloat16), logsum[:, :, 0].T)


def score_grads(query_rows, dattended, logsum, delta, pair_rows, key_live):
    width = query_rows.shape[1]
    scores = score_block(query_rows, pair_rows[:, :width], key_live)
    probs = jnp.exp(scores - logsum.T[:, :, None])
    dprob = jnp.einsum(
        "qhd,khd->hqk",
        heads_view(dattended),
        heads_view(pair_rows[:, width:]),
        preferred_element_type=jnp.float32,
    )
    dscore = (probs * (dprob - delta.T[:, :, None]) * HEAD ** (-0.5)).astype(jnp.bfloat16)
    return (probs.astype(jnp.bfloat16), dscore)


def both_grads(items):
    query_rows, dattended, logsum, delta, pair_rows, key_live = items
    width = query_rows.shape[1]
    probs_low, dscore = score_grads(query_rows, dattended, logsum, delta, pair_rows, key_live)
    dqueries = jnp.einsum(
        "hqk,khd->qhd", dscore, heads_view(pair_rows[:, :width]), preferred_element_type=jnp.float32
    ).reshape(query_rows.shape[0], width)
    dkeys = jnp.einsum(
        "hqk,qhd->khd", dscore, heads_view(query_rows), preferred_element_type=jnp.float32
    )
    dvalues = jnp.einsum(
        "hqk,qhd->khd", probs_low, heads_view(dattended), preferred_element_type=jnp.float32
    )
    key_count = pair_rows.shape[0]
    return (
        dqueries,
        jnp.concatenate(
            [dkeys.reshape(key_count, width), dvalues.reshape(key_count, width)], axis=1
        ),
    )


def local(
    tokens,
    lengths,
    cotangent,
    attention_weight,
    output_weight,
    expand_weight,
    contract_weight,
    first_gain,
    first_shift,
    query_bias,
    value_bias,
    output_bias,
    second_gain,
    second_shift,
    expand_bias,
    contract_bias,
):
    clip_count, slot_count, width = tokens.shape
    parts = lax.axis_size("shard")
    frame_count = slot_count * parts
    place = lax.axis_index("shard")
    row_total = clip_count * slot_count
    gathered = (
        lax.all_gather(attention_weight, "shard", axis=0, tiled=True),
        lax.all_gather(output_weight, "shard", axis=0, tiled=True),
        lax.all_gather(expand_weight, "shard", axis=0, tiled=True),
        lax.all_gather(contract_weight, "shard", axis=0, tiled=True),
        lax.all_gather(first_gain, "shard", axis=0, tiled=True),
        lax.all_gather(first_shift, "shard", axis=0, tiled=True),
        lax.all_gather(query_bias, "shard", axis=0, tiled=True),
        lax.all_gather(value_bias, "shard", axis=0, tiled=True),
        lax.all_gather(output_bias, "shard", axis=0, tiled=True),
        lax.all_gather(second_gain, "shard", axis=0, tiled=True),
        lax.all_gather(second_shift, "shard", axis=0, tiled=True),
        lax.all_gather(expand_bias, "shard", axis=0, tiled=True),
        lax.all_gather(contract_bias, "shard", axis=0, tiled=True),
    )
    vectors = [entry.astype(jnp.float32) for entry in gathered[4:]]
    own_length = jnp.sum(jnp.where(jnp.arange(parts)[None, :] == place, lengths, 0), axis=1)
    row_live = jnp.arange(slot_count)[None, :] < own_length[:, None]
    key_live = (jnp.arange(slot_count)[None, None, :] < lengths[:, :, None]).reshape(
        clip_count, frame_count
    )
    inputs = tokens.reshape(row_total, width).astype(jnp.float32)
    first_normed, first_inverse, first_act = norm_forward(inputs, vectors[0], vectors[1])
    mixed = jnp.dot(first_act, gathered[0], preferred_element_type=jnp.float32)
    mixed = mixed + jnp.concatenate([vectors[2], jnp.zeros_like(vectors[2]), vectors[3]])
    mixed_low = mixed.astype(jnp.bfloat16)
    query_rows = mixed_low[:, :width].reshape(clip_count, slot_count, width)
    pair_own = mixed_low[:, width:].reshape(clip_count, slot_count, 2 * width)
    pair_all = lax.all_gather(pair_own, "shard", axis=1, tiled=True)
    attended, logsum = lax.map(attend_clip, (query_rows, pair_all, key_live))
    attended_flat = attended.reshape(row_total, width)
    residual = (
        inputs
        + jnp.dot(attended_flat, gathered[1], preferred_element_type=jnp.float32)
        + vectors[4]
    )
    second_normed, second_inverse, second_act = norm_forward(residual, vectors[5], vectors[6])
    pre = jnp.dot(second_act, gathered[2], preferred_element_type=jnp.float32) + vectors[7]
    hidden_act = jax.nn.gelu(pre, approximate=False).astype(jnp.bfloat16)
    block_output = (
        residual + jnp.dot(hidden_act, gathered[3], preferred_element_type=jnp.float32) + vectors[8]
    )
    backward = (
        lax.all_gather(attention_weight, "shard", axis=0, tiled=True),
        lax.all_gather(output_weight, "shard", axis=0, tiled=True),
        lax.all_gather(expand_weight, "shard", axis=0, tiled=True),
        lax.all_gather(contract_weight, "shard", axis=0, tiled=True),
        lax.all_gather(first_gain, "shard", axis=0, tiled=True),
        lax.all_gather(first_shift, "shard", axis=0, tiled=True),
        lax.all_gather(query_bias, "shard", axis=0, tiled=True),
        lax.all_gather(value_bias, "shard", axis=0, tiled=True),
        lax.all_gather(output_bias, "shard", axis=0, tiled=True),
        lax.all_gather(second_gain, "shard", axis=0, tiled=True),
        lax.all_gather(second_shift, "shard", axis=0, tiled=True),
        lax.all_gather(expand_bias, "shard", axis=0, tiled=True),
        lax.all_gather(contract_bias, "shard", axis=0, tiled=True),
    )
    back_vectors = [entry.astype(jnp.float32) for entry in backward[4:]]
    error = cotangent.reshape(row_total, width) * row_live.reshape(row_total, 1).astype(jnp.float32)
    error_low = error.astype(jnp.bfloat16)
    contract_bias_grad = jnp.sum(error, axis=0)
    contract_grad = inner_rows(hidden_act, error_low)
    dpre = lax.dot_general(
        error_low, backward[3], (((1,), (1,)), ((), ())), preferred_element_type=jnp.float32
    ) * gelu_slope(pre)
    expand_bias_grad = jnp.sum(dpre, axis=0)
    dpre_low = dpre.astype(jnp.bfloat16)
    expand_grad = inner_rows(second_act, dpre_low)
    dsecond = lax.dot_general(
        dpre_low, backward[2], (((1,), (1,)), ((), ())), preferred_element_type=jnp.float32
    )
    second_gain_grad = jnp.sum(dsecond * second_normed, axis=0)
    second_shift_grad = jnp.sum(dsecond, axis=0)
    dresidual = error + norm_backward(dsecond, second_normed, second_inverse, back_vectors[5])
    output_bias_grad = jnp.sum(dresidual, axis=0)
    dresidual_low = dresidual.astype(jnp.bfloat16)
    output_grad = inner_rows(attended_flat, dresidual_low)
    dattended = lax.dot_general(
        dresidual_low, backward[1], (((1,), (1,)), ((), ())), preferred_element_type=jnp.float32
    ).astype(jnp.bfloat16)
    delta = jnp.sum(
        heads_view(dattended.astype(jnp.float32)) * heads_view(attended_flat.astype(jnp.float32)),
        axis=-1,
    )
    delta = delta.reshape(clip_count, slot_count, HEADS)
    dattended_clips = dattended.reshape(clip_count, slot_count, width)
    dqueries, pair_terms = lax.map(
        both_grads, (query_rows, dattended_clips, logsum, delta, pair_all, key_live)
    )
    pair_grads = lax.psum_scatter(pair_terms, "shard", scatter_dimension=1, tiled=True)
    dqueries_flat = dqueries.reshape(row_total, width)
    pair_flat = pair_grads.reshape(row_total, 2 * width)
    dmixed = jnp.concatenate([dqueries_flat, pair_flat], axis=1)
    query_bias_grad = jnp.sum(dqueries_flat, axis=0)
    value_bias_grad = jnp.sum(pair_flat[:, width:], axis=0)
    dmixed_low = dmixed.astype(jnp.bfloat16)
    attention_grad = inner_rows(first_act, dmixed_low)
    dfirst = lax.dot_general(
        dmixed_low, backward[0], (((1,), (1,)), ((), ())), preferred_element_type=jnp.float32
    )
    first_gain_grad = jnp.sum(dfirst * first_normed, axis=0)
    first_shift_grad = jnp.sum(dfirst, axis=0)
    input_grad = dresidual + norm_backward(dfirst, first_normed, first_inverse, back_vectors[0])
    shares = (
        lax.psum_scatter(attention_grad, "shard", scatter_dimension=0, tiled=True),
        lax.psum_scatter(output_grad, "shard", scatter_dimension=0, tiled=True),
        lax.psum_scatter(expand_grad, "shard", scatter_dimension=0, tiled=True),
        lax.psum_scatter(contract_grad, "shard", scatter_dimension=0, tiled=True),
        lax.psum_scatter(first_gain_grad, "shard", scatter_dimension=0, tiled=True),
        lax.psum_scatter(first_shift_grad, "shard", scatter_dimension=0, tiled=True),
        lax.psum_scatter(query_bias_grad, "shard", scatter_dimension=0, tiled=True),
        lax.psum_scatter(value_bias_grad, "shard", scatter_dimension=0, tiled=True),
        lax.psum_scatter(output_bias_grad, "shard", scatter_dimension=0, tiled=True),
        lax.psum_scatter(second_gain_grad, "shard", scatter_dimension=0, tiled=True),
        lax.psum_scatter(second_shift_grad, "shard", scatter_dimension=0, tiled=True),
        lax.psum_scatter(expand_bias_grad, "shard", scatter_dimension=0, tiled=True),
        lax.psum_scatter(contract_bias_grad, "shard", scatter_dimension=0, tiled=True),
    )
    totals = lax.psum(
        (
            shares[0],
            shares[1],
            shares[2],
            shares[3],
            shares[4],
            shares[5],
            shares[6],
            shares[7],
            shares[8],
            shares[9],
            shares[10],
            shares[11],
            shares[12],
        ),
        "rep",
    )
    return (
        block_output.reshape(clip_count, slot_count, width),
        input_grad.reshape(clip_count, slot_count, width),
        totals[0],
        totals[1],
        totals[2],
        totals[3],
        totals[4],
        totals[5],
        totals[6],
        totals[7],
        totals[8],
        totals[9],
        totals[10],
        totals[11],
        totals[12],
    )


def clip_layer(tokens, lengths, cotangent_of, weights, vectors, reduce, send_out):
    attention_weight, later_weights = weights
    (first_gain, first_shift, query_bias, value_bias, output_bias, second_gain, second_shift,
     expand_bias, contract_bias) = vectors
    clip_count, frame_count, width = tokens.shape
    block_count = lengths.shape[1]
    slot_count = frame_count // block_count
    rows = clip_count * frame_count
    live = (jnp.arange(slot_count)[None, None, :] < lengths[:, :, None]).reshape(clip_count, frame_count)
    scale = HEAD ** (-0.5)
    inputs = tokens.reshape(rows, width).astype(jnp.float32)
    first_normed, first_inverse, first_act = norm_forward(inputs, first_gain, first_shift)
    mixed = jnp.dot(first_act, attention_weight, preferred_element_type=jnp.float32)
    mixed = mixed + jnp.concatenate([query_bias, jnp.zeros_like(query_bias), value_bias])
    mixed_low = mixed.astype(jnp.bfloat16).reshape(clip_count, frame_count, 3, HEADS, HEAD)
    output_weight, expand_weight, contract_weight = later_weights(mixed_low[0, 0, 0, 0, :1])
    queries = mixed_low[:, :, 0]
    keys = mixed_low[:, :, 1]
    values = mixed_low[:, :, 2]
    scores = jnp.einsum("cqhd,ckhd->chqk", queries, keys, preferred_element_type=jnp.float32) * scale
    scores = jnp.where(live[:, None, None, :], scores, NEGATIVE)
    highest = jnp.max(scores, axis=-1, keepdims=True)
    logsum = highest + jnp.log(jnp.sum(jnp.exp(scores - highest), axis=-1, keepdims=True))
    probs = jnp.exp(scores - logsum)
    probs_low = probs.astype(jnp.bfloat16)
    attended = jnp.einsum("chqk,ckhd->cqhd", probs_low, values, preferred_element_type=jnp.float32)
    attended_flat = attended.reshape(rows, width).astype(jnp.bfloat16)
    residual = inputs + jnp.dot(attended_flat, output_weight, preferred_element_type=jnp.float32) + output_bias
    second_normed, second_inverse, second_act = norm_forward(residual, second_gain, second_shift)
    pre = jnp.dot(second_act, expand_weight, preferred_element_type=jnp.float32) + expand_bias
    hidden_act = jax.nn.gelu(pre, approximate=False).astype(jnp.bfloat16)
    block_output = residual + jnp.dot(hidden_act, contract_weight, preferred_element_type=jnp.float32) + contract_bias
    cotangent = cotangent_of(attended_flat[0, :1])
    error = cotangent.reshape(rows, width) * live.reshape(rows, 1).astype(jnp.float32)
    error_low = error.astype(jnp.bfloat16)
    contract_bias_grad = jnp.sum(error, axis=0)
    contract_grad = inner_rows(hidden_act, error_low)
    contract_chip = chip_sum(contract_grad)
    dpre = lax.dot_general(
        error_low, contract_weight, (((1,), (1,)), ((), ())), preferred_element_type=jnp.float32
    ) * gelu_slope(pre)
    expand_bias_grad = jnp.sum(dpre, axis=0)
    dpre_low = dpre.astype(jnp.bfloat16)
    contract_chip, dpre_low = lax.optimization_barrier((contract_chip, dpre_low))
    contract_part = shard_sum(contract_chip)
    expand_grad = inner_rows(second_act, dpre_low)
    expand_chip = chip_sum(expand_grad)
    dsecond = lax.dot_general(
        dpre_low, expand_weight, (((1,), (1,)), ((), ())), preferred_element_type=jnp.float32
    )
    second_gain_grad = jnp.sum(dsecond * second_normed, axis=0)
    second_shift_grad = jnp.sum(dsecond, axis=0)
    dresidual = error + norm_backward(dsecond, second_normed, second_inverse, second_gain)
    output_bias_grad = jnp.sum(dresidual, axis=0)
    dresidual_low = dresidual.astype(jnp.bfloat16)
    sent_output = send_out(block_output)
    expand_chip, dresidual_low = lax.optimization_barrier((expand_chip, dresidual_low))
    expand_part = shard_sum(expand_chip)
    output_grad = inner_rows(attended_flat, dresidual_low)
    output_chip = chip_sum(output_grad)
    dattended = lax.dot_general(
        dresidual_low, output_weight, (((1,), (1,)), ((), ())), preferred_element_type=jnp.float32
    ).astype(jnp.bfloat16)
    dattended_heads = dattended.reshape(clip_count, frame_count, HEADS, HEAD)
    attended_heads = attended_flat.reshape(clip_count, frame_count, HEADS, HEAD)
    delta = jnp.sum(
        dattended_heads.astype(jnp.float32) * attended_heads.astype(jnp.float32), axis=-1
    )
    dprob = jnp.einsum("cqhd,ckhd->chqk", dattended_heads, values, preferred_element_type=jnp.float32)
    dscore = (probs * (dprob - jnp.transpose(delta, (0, 2, 1))[:, :, :, None]) * scale).astype(jnp.bfloat16)
    dqueries = jnp.einsum("chqk,ckhd->cqhd", dscore, keys, preferred_element_type=jnp.float32)
    dkeys = jnp.einsum("chqk,cqhd->ckhd", dscore, queries, preferred_element_type=jnp.float32)
    dvalues = jnp.einsum("chqk,cqhd->ckhd", probs_low, dattended_heads, preferred_element_type=jnp.float32)
    dmixed = jnp.concatenate(
        [dqueries.reshape(rows, width), dkeys.reshape(rows, width), dvalues.reshape(rows, width)], axis=1
    )
    query_bias_grad = jnp.sum(dmixed[:, :width], axis=0)
    value_bias_grad = jnp.sum(dmixed[:, 2 * width:], axis=0)
    dmixed_low = dmixed.astype(jnp.bfloat16)
    contract_total = reduce(contract_part, contract_grad.shape[0])
    output_chip, expand_part, contract_total, sent_output, dmixed_low = lax.optimization_barrier(
        (output_chip, expand_part, contract_total, sent_output, dmixed_low)
    )
    output_part = shard_sum(output_chip)
    expand_total = reduce(expand_part, expand_grad.shape[0])
    attention_grad = inner_rows(first_act, dmixed_low)
    dfirst, expand_total = lax.optimization_barrier((lax.dot_general(
        dmixed_low, attention_weight, (((1,), (1,)), ((), ())), preferred_element_type=jnp.float32
    ), expand_total))
    first_gain_grad = jnp.sum(dfirst * first_normed, axis=0)
    first_shift_grad = jnp.sum(dfirst, axis=0)
    input_grad = dresidual + norm_backward(dfirst, first_normed, first_inverse, first_gain)
    output_part, input_grad = lax.optimization_barrier((output_part, input_grad))
    weight_grads = (attention_grad, output_part, expand_total, contract_total)
    vector_grads = (first_gain_grad, first_shift_grad, query_bias_grad, value_bias_grad, output_bias_grad,
                    second_gain_grad, second_shift_grad, expand_bias_grad, contract_bias_grad)
    return (
        sent_output,
        input_grad,
        weight_grads,
        vector_grads,
    )


PAIR = [(0, 1), (1, 0)]
OUTER = ("outer", "inner")


def core_pick(core, first, second):
    return jnp.where(core == 0, first, second)


def gather_weight(shard_rows, extra=None):
    parts = lax.axis_size("shard")
    core = lax.axis_index("core")
    rows, width = shard_rows.shape
    half = rows // 2
    mine = lax.dynamic_slice_in_dim(shard_rows, core * half, half, axis=0)
    if extra is not None:
        mine = jnp.concatenate([mine, extra], axis=0)
    mine = lax.all_gather(mine, "shard", axis=0, tiled=False)
    other = lax.ppermute(mine, "core", PAIR)
    first = core_pick(core, mine, other)
    second = core_pick(core, other, mine)
    full = jnp.stack([first[:, :half], second[:, :half]], axis=1).reshape(parts * rows, width)
    if extra is None:
        return full, None
    return full, first[:, half:]


def chip_sum(grad, extra=None):
    parts = lax.axis_size("shard")
    core = lax.axis_index("core")
    width = grad.shape[1]
    rows = grad.shape[0] // parts
    half = rows // 2
    quarters = grad.reshape(parts, 2, half, width)
    keep = lax.dynamic_index_in_dim(quarters, core, axis=1, keepdims=False)
    send = lax.dynamic_index_in_dim(quarters, 1 - core, axis=1, keepdims=False)
    if extra is not None:
        on_first = (core == 0).astype(extra.dtype)
        keep = jnp.concatenate([keep, extra * on_first], axis=1)
        send = jnp.concatenate([send, extra * (1 - on_first)], axis=1)
    return keep + lax.ppermute(send, "core", PAIR)


def shard_sum(chip):
    part = lax.psum_scatter(chip, "shard", scatter_dimension=0, tiled=False)
    if lax.axis_size("inner") > 1:
        part = lax.psum(part, "inner")
    return part


def finish_sum(part, half):
    core = lax.axis_index("core")
    total = line_sum(part)
    other = lax.ppermute(total, "core", PAIR)
    first = core_pick(core, total, other)
    second = core_pick(core, other, total)
    return jnp.concatenate([first[:half], second[:half]], axis=0), first[half:]


def finish_many(parts, halves):
    core = lax.axis_index("core")
    flat = jnp.concatenate([part.reshape(-1) for part in parts])
    total = line_sum(flat)
    other = lax.ppermute(total, "core", PAIR)
    first = core_pick(core, total, other)
    second = core_pick(core, other, total)
    outs = []
    offset = 0
    for part, half in zip(parts, halves):
        size = part.size
        low = first[offset:offset + size].reshape(part.shape)
        high = second[offset:offset + size].reshape(part.shape)
        outs.append((jnp.concatenate([low[:half], high[:half]], axis=0), low[half:]))
        offset += size
    return outs


def reduce_weight(grad, extra=None):
    half = grad.shape[0] // lax.axis_size("shard") // 2
    return finish_sum(shard_sum(chip_sum(grad, extra)), half)


def line_sum(values):
    groups = lax.axis_size("outer")
    if groups == 1:
        return values
    if groups & (groups - 1):
        return lax.psum(values, "outer")
    here = lax.axis_index("outer")
    length = values.shape[0]
    padded = -(-length // groups) * groups
    held = jnp.pad(values, ((0, padded - length),) + ((0, 0),) * (values.ndim - 1))
    held = held.reshape((groups, padded // groups) + values.shape[1:])
    step = 1
    while step < groups:
        held = held.reshape((held.shape[0] // 2, 2) + held.shape[1:])
        bit = (here // step) % 2
        keep = lax.dynamic_index_in_dim(held, bit, axis=1, keepdims=False)
        send = lax.dynamic_index_in_dim(held, 1 - bit, axis=1, keepdims=False)
        held = keep + lax.ppermute(send, "outer", [(j, j ^ step) for j in range(groups)])
        step *= 2
    step = groups // 2
    while step >= 1:
        bit = (here // step) % 2
        other = lax.ppermute(held, "outer", [(j, j ^ step) for j in range(groups)])
        low = jnp.where(bit == 0, held, other)
        high = jnp.where(bit == 0, other, held)
        held = jnp.stack([low, high], axis=1)
        held = held.reshape((held.shape[0] * 2,) + held.shape[2:])
        step //= 2
    return held.reshape((padded,) + values.shape[1:])[:length]


def gather_packed(blocks, after=None):
    core = lax.axis_index("core")
    mine = lax.all_gather(jnp.concatenate(blocks, axis=0), "shard", axis=0, tiled=False)
    if after is not None:
        mine = mine + (after * 0).astype(mine.dtype)
    other = lax.ppermute(mine, "core", PAIR)
    return core_pick(core, mine, other), core_pick(core, other, mine)


def unpack_rows(first, second, begin, count, shape):
    parts = first.shape[0]
    rows, width = shape
    low = first[:, begin:begin + count].reshape(parts, -1, width)
    high = second[:, begin:begin + count].reshape(parts, -1, width)
    return jnp.stack([low, high], axis=1).reshape(rows, width)


def core_half(shard_rows):
    core = lax.axis_index("core")
    half = shard_rows.shape[0] // 2
    return lax.dynamic_slice_in_dim(shard_rows, core * half, half, axis=0)


def clip_local(tokens, lengths, cotangent, *params):
    clip_count, slot_count, width = tokens.shape
    parts = lax.axis_size("shard")
    place = lax.axis_index("shard")
    own = clip_count // parts
    weight_shards = params[:4]
    vector_shards = params[4:]
    wide = weight_shards[0].shape[1]
    vector_row = jnp.concatenate([entry.reshape(-1) for entry in vector_shards])
    pad = (-vector_row.shape[0]) % wide
    vector_rows = jnp.pad(vector_row, (0, pad)).reshape(-1, wide)
    attention_half = core_half(weight_shards[0])
    first, second = gather_packed([attention_half, vector_rows])
    a_rows = attention_half.shape[0]
    attention_weight = unpack_rows(first, second, 0, a_rows, (parts * weight_shards[0].shape[0], wide))
    vector_all = first[:, a_rows:].reshape(parts, -1)[:, : vector_row.shape[0]]
    vectors = []
    offset = 0
    for entry in vector_shards:
        size = entry.shape[0]
        vectors.append(vector_all[:, offset:offset + size].reshape(parts * size).astype(jnp.float32))
        offset += size
    late = weight_shards[2].shape[1]
    expand_half = core_half(weight_shards[2])
    contract_half = core_half(weight_shards[3]).reshape(-1, late)
    output_half = core_half(weight_shards[1]).reshape(-1, late)

    def later_weights(after):
        first_b, second_b = gather_packed([output_half, expand_half, contract_half], after)
        o_rows = output_half.shape[0]
        e_rows = expand_half.shape[0]
        output_weight = unpack_rows(
            first_b, second_b, 0, o_rows, (parts * weight_shards[1].shape[0], weight_shards[1].shape[1])
        )
        expand_weight = unpack_rows(first_b, second_b, o_rows, e_rows, (parts * weight_shards[2].shape[0], late))
        contract_weight = unpack_rows(
            first_b, second_b, o_rows + e_rows, contract_half.shape[0],
            (parts * weight_shards[3].shape[0], weight_shards[3].shape[1]),
        )
        return output_weight, expand_weight, contract_weight

    weights = (attention_weight, later_weights)
    def gather_rows(values):
        moved = lax.all_to_all(values.reshape(clip_count * slot_count, width), "shard", 0, 0, tiled=True)
        moved = moved.reshape(parts, own, slot_count, width)
        return jnp.transpose(moved, (1, 0, 2, 3)).reshape(own, parts * slot_count, width) if own > 1 else moved.reshape(own, parts * slot_count, width)

    def scatter_rows(values):
        rows = values.reshape(own, parts, slot_count, width)
        if own > 1:
            rows = jnp.transpose(rows, (1, 0, 2, 3))
        moved = lax.all_to_all(rows.reshape(own * parts * slot_count, width), "shard", 0, 0, tiled=True)
        return moved.reshape(clip_count, slot_count, width)

    tokens_clip = gather_rows(tokens)

    def cotangent_of(after):
        late = cotangent + (after * 0).astype(cotangent.dtype)
        return gather_rows(late)

    lengths_clip = lax.dynamic_slice_in_dim(lengths, place * own, own, axis=0)
    block_output, input_grad, weight_grads, vector_grads = clip_layer(
        tokens_clip, lengths_clip, cotangent_of, weights, vectors, lambda part, rows: finish_sum(part, rows // parts // 2)[0],
        scatter_rows,
    )
    input_grad = scatter_rows(input_grad)
    attention_grad = weight_grads[0]
    attention_width = attention_grad.shape[1]
    vector_parts = jnp.concatenate([entry.reshape(parts, -1) for entry in vector_grads], axis=1)
    vector_size = vector_parts.shape[1]
    vpad = (-vector_size) % attention_width
    vector_parts = jnp.pad(vector_parts, ((0, 0), (0, vpad))).reshape(parts, -1, attention_width)
    attention_part = shard_sum(chip_sum(attention_grad, vector_parts))
    output_part = weight_grads[1]
    (attention_total, vector_total), (output_total, _) = finish_many(
        [attention_part, output_part],
        [attention_grad.shape[0] // parts // 2, params[1].shape[0] // 2],
    )
    totals = (attention_total, output_total) + tuple(weight_grads[2:])
    vector_total = vector_total.reshape(-1)[:vector_size]
    vector_outs = []
    offset = 0
    for entry in vector_shards:
        size = entry.shape[0]
        vector_outs.append(vector_total[offset:offset + size])
        offset += size
    return (block_output, input_grad) + totals + tuple(vector_outs)


def split_rep(mesh):
    devices = mesh.devices
    rep, parts = devices.shape
    first = devices[0, 0]
    stride = None
    for index in range(1, rep):
        other = devices[index, 0]
        if tuple(other.coords) == tuple(first.coords) and other.core_on_chip != first.core_on_chip:
            stride = index
            break
    if stride is None or rep % (2 * stride):
        return None
    grid = devices.reshape(rep // (2 * stride), 2, stride, parts)
    for spot in np.ndindex(grid.shape[0], grid.shape[2], grid.shape[3]):
        low = grid[spot[0], 0, spot[1], spot[2]]
        high = grid[spot[0], 1, spot[1], spot[2]]
        if tuple(low.coords) != tuple(high.coords) or low.core_on_chip == high.core_on_chip:
            return None
    return Mesh(grid, ("outer", "core", "inner", "shard"))


def solution(mesh):
    def specs(rep):
        ins = (P(rep, "shard", None), P(rep, None), P(rep, "shard", None)) + (P("shard", None),) * 4 + (
            P("shard"),
        ) * 9
        outs = (P(rep, "shard", None), P(rep, "shard", None)) + (P("shard", None),) * 4 + (P("shard"),) * 9
        return ins, outs

    ins, outs = specs("rep")
    plain = jax.shard_map(local, mesh=mesh, in_specs=ins, out_specs=outs, check_vma=False)
    split = split_rep(mesh)
    if split is None:
        return plain
    ins, outs = specs(("outer", "core", "inner"))
    fast = jax.shard_map(clip_local, mesh=split, in_specs=ins, out_specs=outs, check_vma=False)
    rep, parts = mesh.devices.shape

    def run(*args):
        if (args[0].shape[0] // rep) % parts == 0:
            return fast(*args)
        return plain(*args)

    return run
```

```python
import jax
import jax.numpy as jnp
from jax import lax
from jax.sharding import Mesh, PartitionSpec as P
import numpy as np

HEADS = 12
HEAD = 64


EPSILON = 1e-05
NEGATIVE = -1e30


def norm_forward(values, gain, shift):
    centred = values - jnp.mean(values, axis=-1, keepdims=True)
    inverse = lax.rsqrt(jnp.mean(centred * centred, axis=-1, keepdims=True) + EPSILON)
    normed = centred * inverse
    return (normed, inverse, (normed * gain + shift).astype(jnp.bfloat16))


def norm_backward(upstream, normed, inverse, gain):
    scaled = upstream * gain
    return inverse * (
        scaled
        - jnp.mean(scaled, axis=-1, keepdims=True)
        - normed * jnp.mean(scaled * normed, axis=-1, keepdims=True)
    )


def gelu_slope(values):
    return (
        0.5 * (1.0 + jax.scipy.special.erf(values * 0.7071067811865476))
        + values * jnp.exp(-0.5 * values * values) * 0.3989422804014327
    )


def inner_rows(left, right):
    return lax.dot_general(
        left, right, (((0,), (0,)), ((), ())), preferred_element_type=jnp.float32
    )


def heads_view(matrix):
    return matrix.reshape(matrix.shape[0], HEADS, HEAD)


def score_block(query_rows, key_rows, key_live):
    scores = jnp.einsum(
        "qhd,khd->hqk",
        heads_view(query_rows),
        heads_view(key_rows),
        preferred_element_type=jnp.float32,
    ) * HEAD ** (-0.5)
    return jnp.where(key_live[None, None, :], scores, NEGATIVE)


def attend_clip(items):
    query_rows, pair_rows, key_live = items
    width = query_rows.shape[1]
    scores = score_block(query_rows, pair_rows[:, :width], key_live)
    highest = jnp.max(scores, axis=-1, keepdims=True)
    logsum = highest + jnp.log(jnp.sum(jnp.exp(scores - highest), axis=-1, keepdims=True))
    probs_low = jnp.exp(scores - logsum).astype(jnp.bfloat16)
    attended = jnp.einsum(
        "hqk,khd->qhd",
        probs_low,
        heads_view(pair_rows[:, width:]),
        preferred_element_type=jnp.float32,
    )
    return (attended.reshape(query_rows.shape[0], width).astype(jnp.bfloat16), logsum[:, :, 0].T)


def score_grads(query_rows, dattended, logsum, delta, pair_rows, key_live):
    width = query_rows.shape[1]
    scores = score_block(query_rows, pair_rows[:, :width], key_live)
    probs = jnp.exp(scores - logsum.T[:, :, None])
    dprob = jnp.einsum(
        "qhd,khd->hqk",
        heads_view(dattended),
        heads_view(pair_rows[:, width:]),
        preferred_element_type=jnp.float32,
    )
    dscore = (probs * (dprob - delta.T[:, :, None]) * HEAD ** (-0.5)).astype(jnp.bfloat16)
    return (probs.astype(jnp.bfloat16), dscore)


def both_grads(items):
    query_rows, dattended, logsum, delta, pair_rows, key_live = items
    width = query_rows.shape[1]
    probs_low, dscore = score_grads(query_rows, dattended, logsum, delta, pair_rows, key_live)
    dqueries = jnp.einsum(
        "hqk,khd->qhd", dscore, heads_view(pair_rows[:, :width]), preferred_element_type=jnp.float32
    ).reshape(query_rows.shape[0], width)
    dkeys = jnp.einsum(
        "hqk,qhd->khd", dscore, heads_view(query_rows), preferred_element_type=jnp.float32
    )
    dvalues = jnp.einsum(
        "hqk,qhd->khd", probs_low, heads_view(dattended), preferred_element_type=jnp.float32
    )
    key_count = pair_rows.shape[0]
    return (
        dqueries,
        jnp.concatenate(
            [dkeys.reshape(key_count, width), dvalues.reshape(key_count, width)], axis=1
        ),
    )


def local(
    tokens,
    lengths,
    cotangent,
    attention_weight,
    output_weight,
    expand_weight,
    contract_weight,
    first_gain,
    first_shift,
    query_bias,
    value_bias,
    output_bias,
    second_gain,
    second_shift,
    expand_bias,
    contract_bias,
):
    clip_count, slot_count, width = tokens.shape
    parts = lax.axis_size("shard")
    frame_count = slot_count * parts
    place = lax.axis_index("shard")
    row_total = clip_count * slot_count
    gathered = (
        lax.all_gather(attention_weight, "shard", axis=0, tiled=True),
        lax.all_gather(output_weight, "shard", axis=0, tiled=True),
        lax.all_gather(expand_weight, "shard", axis=0, tiled=True),
        lax.all_gather(contract_weight, "shard", axis=0, tiled=True),
        lax.all_gather(first_gain, "shard", axis=0, tiled=True),
        lax.all_gather(first_shift, "shard", axis=0, tiled=True),
        lax.all_gather(query_bias, "shard", axis=0, tiled=True),
        lax.all_gather(value_bias, "shard", axis=0, tiled=True),
        lax.all_gather(output_bias, "shard", axis=0, tiled=True),
        lax.all_gather(second_gain, "shard", axis=0, tiled=True),
        lax.all_gather(second_shift, "shard", axis=0, tiled=True),
        lax.all_gather(expand_bias, "shard", axis=0, tiled=True),
        lax.all_gather(contract_bias, "shard", axis=0, tiled=True),
    )
    vectors = [entry.astype(jnp.float32) for entry in gathered[4:]]
    own_length = jnp.sum(jnp.where(jnp.arange(parts)[None, :] == place, lengths, 0), axis=1)
    row_live = jnp.arange(slot_count)[None, :] < own_length[:, None]
    key_live = (jnp.arange(slot_count)[None, None, :] < lengths[:, :, None]).reshape(
        clip_count, frame_count
    )
    inputs = tokens.reshape(row_total, width).astype(jnp.float32)
    first_normed, first_inverse, first_act = norm_forward(inputs, vectors[0], vectors[1])
    mixed = jnp.dot(first_act, gathered[0], preferred_element_type=jnp.float32)
    mixed = mixed + jnp.concatenate([vectors[2], jnp.zeros_like(vectors[2]), vectors[3]])
    mixed_low = mixed.astype(jnp.bfloat16)
    query_rows = mixed_low[:, :width].reshape(clip_count, slot_count, width)
    pair_own = mixed_low[:, width:].reshape(clip_count, slot_count, 2 * width)
    pair_all = lax.all_gather(pair_own, "shard", axis=1, tiled=True)
    attended, logsum = lax.map(attend_clip, (query_rows, pair_all, key_live))
    attended_flat = attended.reshape(row_total, width)
    residual = (
        inputs
        + jnp.dot(attended_flat, gathered[1], preferred_element_type=jnp.float32)
        + vectors[4]
    )
    second_normed, second_inverse, second_act = norm_forward(residual, vectors[5], vectors[6])
    pre = jnp.dot(second_act, gathered[2], preferred_element_type=jnp.float32) + vectors[7]
    hidden_act = jax.nn.gelu(pre, approximate=False).astype(jnp.bfloat16)
    block_output = (
        residual + jnp.dot(hidden_act, gathered[3], preferred_element_type=jnp.float32) + vectors[8]
    )
    backward = (
        lax.all_gather(attention_weight, "shard", axis=0, tiled=True),
        lax.all_gather(output_weight, "shard", axis=0, tiled=True),
        lax.all_gather(expand_weight, "shard", axis=0, tiled=True),
        lax.all_gather(contract_weight, "shard", axis=0, tiled=True),
        lax.all_gather(first_gain, "shard", axis=0, tiled=True),
        lax.all_gather(first_shift, "shard", axis=0, tiled=True),
        lax.all_gather(query_bias, "shard", axis=0, tiled=True),
        lax.all_gather(value_bias, "shard", axis=0, tiled=True),
        lax.all_gather(output_bias, "shard", axis=0, tiled=True),
        lax.all_gather(second_gain, "shard", axis=0, tiled=True),
        lax.all_gather(second_shift, "shard", axis=0, tiled=True),
        lax.all_gather(expand_bias, "shard", axis=0, tiled=True),
        lax.all_gather(contract_bias, "shard", axis=0, tiled=True),
    )
    back_vectors = [entry.astype(jnp.float32) for entry in backward[4:]]
    error = cotangent.reshape(row_total, width) * row_live.reshape(row_total, 1).astype(jnp.float32)
    error_low = error.astype(jnp.bfloat16)
    contract_bias_grad = jnp.sum(error, axis=0)
    contract_grad = inner_rows(hidden_act, error_low)
    dpre = lax.dot_general(
        error_low, backward[3], (((1,), (1,)), ((), ())), preferred_element_type=jnp.float32
    ) * gelu_slope(pre)
    expand_bias_grad = jnp.sum(dpre, axis=0)
    dpre_low = dpre.astype(jnp.bfloat16)
    expand_grad = inner_rows(second_act, dpre_low)
    dsecond = lax.dot_general(
        dpre_low, backward[2], (((1,), (1,)), ((), ())), preferred_element_type=jnp.float32
    )
    second_gain_grad = jnp.sum(dsecond * second_normed, axis=0)
    second_shift_grad = jnp.sum(dsecond, axis=0)
    dresidual = error + norm_backward(dsecond, second_normed, second_inverse, back_vectors[5])
    output_bias_grad = jnp.sum(dresidual, axis=0)
    dresidual_low = dresidual.astype(jnp.bfloat16)
    output_grad = inner_rows(attended_flat, dresidual_low)
    dattended = lax.dot_general(
        dresidual_low, backward[1], (((1,), (1,)), ((), ())), preferred_element_type=jnp.float32
    ).astype(jnp.bfloat16)
    delta = jnp.sum(
        heads_view(dattended.astype(jnp.float32)) * heads_view(attended_flat.astype(jnp.float32)),
        axis=-1,
    )
    delta = delta.reshape(clip_count, slot_count, HEADS)
    dattended_clips = dattended.reshape(clip_count, slot_count, width)
    dqueries, pair_terms = lax.map(
        both_grads, (query_rows, dattended_clips, logsum, delta, pair_all, key_live)
    )
    pair_grads = lax.psum_scatter(pair_terms, "shard", scatter_dimension=1, tiled=True)
    dqueries_flat = dqueries.reshape(row_total, width)
    pair_flat = pair_grads.reshape(row_total, 2 * width)
    dmixed = jnp.concatenate([dqueries_flat, pair_flat], axis=1)
    query_bias_grad = jnp.sum(dqueries_flat, axis=0)
    value_bias_grad = jnp.sum(pair_flat[:, width:], axis=0)
    dmixed_low = dmixed.astype(jnp.bfloat16)
    attention_grad = inner_rows(first_act, dmixed_low)
    dfirst = lax.dot_general(
        dmixed_low, backward[0], (((1,), (1,)), ((), ())), preferred_element_type=jnp.float32
    )
    first_gain_grad = jnp.sum(dfirst * first_normed, axis=0)
    first_shift_grad = jnp.sum(dfirst, axis=0)
    input_grad = dresidual + norm_backward(dfirst, first_normed, first_inverse, back_vectors[0])
    shares = (
        lax.psum_scatter(attention_grad, "shard", scatter_dimension=0, tiled=True),
        lax.psum_scatter(output_grad, "shard", scatter_dimension=0, tiled=True),
        lax.psum_scatter(expand_grad, "shard", scatter_dimension=0, tiled=True),
        lax.psum_scatter(contract_grad, "shard", scatter_dimension=0, tiled=True),
        lax.psum_scatter(first_gain_grad, "shard", scatter_dimension=0, tiled=True),
        lax.psum_scatter(first_shift_grad, "shard", scatter_dimension=0, tiled=True),
        lax.psum_scatter(query_bias_grad, "shard", scatter_dimension=0, tiled=True),
        lax.psum_scatter(value_bias_grad, "shard", scatter_dimension=0, tiled=True),
        lax.psum_scatter(output_bias_grad, "shard", scatter_dimension=0, tiled=True),
        lax.psum_scatter(second_gain_grad, "shard", scatter_dimension=0, tiled=True),
        lax.psum_scatter(second_shift_grad, "shard", scatter_dimension=0, tiled=True),
        lax.psum_scatter(expand_bias_grad, "shard", scatter_dimension=0, tiled=True),
        lax.psum_scatter(contract_bias_grad, "shard", scatter_dimension=0, tiled=True),
    )
    totals = lax.psum(
        (
            shares[0],
            shares[1],
            shares[2],
            shares[3],
            shares[4],
            shares[5],
            shares[6],
            shares[7],
            shares[8],
            shares[9],
            shares[10],
            shares[11],
            shares[12],
        ),
        "rep",
    )
    return (
        block_output.reshape(clip_count, slot_count, width),
        input_grad.reshape(clip_count, slot_count, width),
        totals[0],
        totals[1],
        totals[2],
        totals[3],
        totals[4],
        totals[5],
        totals[6],
        totals[7],
        totals[8],
        totals[9],
        totals[10],
        totals[11],
        totals[12],
    )


def clip_layer(tokens, lengths, cotangent_of, weights, vectors, reduce, send_out):
    attention_weight, output_weight, later_weights = weights
    (first_gain, first_shift, query_bias, value_bias, output_bias, second_gain, second_shift,
     expand_bias, contract_bias) = vectors
    clip_count, frame_count, width = tokens.shape
    block_count = lengths.shape[1]
    slot_count = frame_count // block_count
    rows = clip_count * frame_count
    live = (jnp.arange(slot_count)[None, None, :] < lengths[:, :, None]).reshape(clip_count, frame_count)
    scale = HEAD ** (-0.5)
    inputs = tokens.reshape(rows, width).astype(jnp.float32)
    first_normed, first_inverse, first_act = norm_forward(inputs, first_gain, first_shift)
    mixed = jnp.dot(first_act, attention_weight, preferred_element_type=jnp.float32)
    mixed = mixed + jnp.concatenate([query_bias, jnp.zeros_like(query_bias), value_bias])
    mixed_low = mixed.astype(jnp.bfloat16).reshape(clip_count, frame_count, 3, HEADS, HEAD)
    expand_weight, contract_weight = later_weights(mixed_low[0, 0, 0, 0, :1])
    queries = mixed_low[:, :, 0]
    keys = mixed_low[:, :, 1]
    values = mixed_low[:, :, 2]
    scores = jnp.einsum("cqhd,ckhd->chqk", queries, keys, preferred_element_type=jnp.float32) * scale
    scores = jnp.where(live[:, None, None, :], scores, NEGATIVE)
    highest = jnp.max(scores, axis=-1, keepdims=True)
    logsum = highest + jnp.log(jnp.sum(jnp.exp(scores - highest), axis=-1, keepdims=True))
    probs = jnp.exp(scores - logsum)
    probs_low = probs.astype(jnp.bfloat16)
    attended = jnp.einsum("chqk,ckhd->cqhd", probs_low, values, preferred_element_type=jnp.float32)
    attended_flat = attended.reshape(rows, width).astype(jnp.bfloat16)
    residual = inputs + jnp.dot(attended_flat, output_weight, preferred_element_type=jnp.float32) + output_bias
    second_normed, second_inverse, second_act = norm_forward(residual, second_gain, second_shift)
    pre = jnp.dot(second_act, expand_weight, preferred_element_type=jnp.float32) + expand_bias
    hidden_act = jax.nn.gelu(pre, approximate=False).astype(jnp.bfloat16)
    block_output = residual + jnp.dot(hidden_act, contract_weight, preferred_element_type=jnp.float32) + contract_bias
    cotangent = cotangent_of(pre[0, :1])
    error = cotangent.reshape(rows, width) * live.reshape(rows, 1).astype(jnp.float32)
    error_low = error.astype(jnp.bfloat16)
    contract_bias_grad = jnp.sum(error, axis=0)
    contract_grad = inner_rows(hidden_act, error_low)
    contract_chip = chip_sum(contract_grad)
    dpre = lax.dot_general(
        error_low, contract_weight, (((1,), (1,)), ((), ())), preferred_element_type=jnp.float32
    ) * gelu_slope(pre)
    expand_bias_grad = jnp.sum(dpre, axis=0)
    dpre_low = dpre.astype(jnp.bfloat16)
    contract_chip, dpre_low = lax.optimization_barrier((contract_chip, dpre_low))
    contract_part = shard_sum(contract_chip)
    expand_grad = inner_rows(second_act, dpre_low)
    expand_chip = chip_sum(expand_grad)
    dsecond = lax.dot_general(
        dpre_low, expand_weight, (((1,), (1,)), ((), ())), preferred_element_type=jnp.float32
    )
    second_gain_grad = jnp.sum(dsecond * second_normed, axis=0)
    second_shift_grad = jnp.sum(dsecond, axis=0)
    dresidual = error + norm_backward(dsecond, second_normed, second_inverse, second_gain)
    output_bias_grad = jnp.sum(dresidual, axis=0)
    dresidual_low = dresidual.astype(jnp.bfloat16)
    sent_output = send_out(block_output)
    expand_chip, dresidual_low = lax.optimization_barrier((expand_chip, dresidual_low))
    expand_part = shard_sum(expand_chip)
    output_grad = inner_rows(attended_flat, dresidual_low)
    output_chip = chip_sum(output_grad)
    dattended = lax.dot_general(
        dresidual_low, output_weight, (((1,), (1,)), ((), ())), preferred_element_type=jnp.float32
    ).astype(jnp.bfloat16)
    contract_part, dattended = lax.optimization_barrier((contract_part, dattended))
    dattended_heads = dattended.reshape(clip_count, frame_count, HEADS, HEAD)
    attended_heads = attended_flat.reshape(clip_count, frame_count, HEADS, HEAD)
    delta = jnp.sum(
        dattended_heads.astype(jnp.float32) * attended_heads.astype(jnp.float32), axis=-1
    )
    dprob = jnp.einsum("cqhd,ckhd->chqk", dattended_heads, values, preferred_element_type=jnp.float32)
    dscore = (probs * (dprob - jnp.transpose(delta, (0, 2, 1))[:, :, :, None]) * scale).astype(jnp.bfloat16)
    dqueries = jnp.einsum("chqk,ckhd->cqhd", dscore, keys, preferred_element_type=jnp.float32)
    dkeys = jnp.einsum("chqk,cqhd->ckhd", dscore, queries, preferred_element_type=jnp.float32)
    dvalues = jnp.einsum("chqk,cqhd->ckhd", probs_low, dattended_heads, preferred_element_type=jnp.float32)
    dmixed = jnp.concatenate(
        [dqueries.reshape(rows, width), dkeys.reshape(rows, width), dvalues.reshape(rows, width)], axis=1
    )
    query_bias_grad = jnp.sum(dmixed[:, :width], axis=0)
    value_bias_grad = jnp.sum(dmixed[:, 2 * width:], axis=0)
    dmixed_low = dmixed.astype(jnp.bfloat16)
    contract_total = reduce(contract_part, contract_grad.shape[0])
    output_chip, expand_part, contract_total, sent_output, dmixed_low = lax.optimization_barrier(
        (output_chip, expand_part, contract_total, sent_output, dmixed_low)
    )
    output_part = shard_sum(output_chip)
    expand_total = reduce(expand_part, expand_grad.shape[0])
    attention_grad = inner_rows(first_act, dmixed_low)
    dfirst = lax.optimization_barrier(lax.dot_general(
        dmixed_low, attention_weight, (((1,), (1,)), ((), ())), preferred_element_type=jnp.float32
    ))
    first_gain_grad = jnp.sum(dfirst * first_normed, axis=0)
    first_shift_grad = jnp.sum(dfirst, axis=0)
    input_grad = dresidual + norm_backward(dfirst, first_normed, first_inverse, first_gain)
    output_part, expand_total, input_grad = lax.optimization_barrier((output_part, expand_total, input_grad))
    weight_grads = (attention_grad, output_part, expand_total, contract_total)
    vector_grads = (first_gain_grad, first_shift_grad, query_bias_grad, value_bias_grad, output_bias_grad,
                    second_gain_grad, second_shift_grad, expand_bias_grad, contract_bias_grad)
    return (
        sent_output,
        input_grad,
        weight_grads,
        vector_grads,
    )


PAIR = [(0, 1), (1, 0)]
OUTER = ("outer", "inner")


def core_pick(core, first, second):
    return jnp.where(core == 0, first, second)


def gather_weight(shard_rows, extra=None):
    parts = lax.axis_size("shard")
    core = lax.axis_index("core")
    rows, width = shard_rows.shape
    half = rows // 2
    mine = lax.dynamic_slice_in_dim(shard_rows, core * half, half, axis=0)
    if extra is not None:
        mine = jnp.concatenate([mine, extra], axis=0)
    mine = lax.all_gather(mine, "shard", axis=0, tiled=False)
    other = lax.ppermute(mine, "core", PAIR)
    first = core_pick(core, mine, other)
    second = core_pick(core, other, mine)
    full = jnp.stack([first[:, :half], second[:, :half]], axis=1).reshape(parts * rows, width)
    if extra is None:
        return full, None
    return full, first[:, half:]


def chip_sum(grad, extra=None):
    parts = lax.axis_size("shard")
    core = lax.axis_index("core")
    width = grad.shape[1]
    rows = grad.shape[0] // parts
    half = rows // 2
    quarters = grad.reshape(parts, 2, half, width)
    keep = lax.dynamic_index_in_dim(quarters, core, axis=1, keepdims=False)
    send = lax.dynamic_index_in_dim(quarters, 1 - core, axis=1, keepdims=False)
    if extra is not None:
        on_first = (core == 0).astype(extra.dtype)
        keep = jnp.concatenate([keep, extra * on_first], axis=1)
        send = jnp.concatenate([send, extra * (1 - on_first)], axis=1)
    return keep + lax.ppermute(send, "core", PAIR)


def shard_sum(chip):
    part = lax.psum_scatter(chip.astype(jnp.bfloat16), "shard", scatter_dimension=0, tiled=False)
    part = part.astype(jnp.float32)
    if lax.axis_size("inner") > 1:
        part = lax.psum(part, "inner")
    return part


def finish_sum(part, half):
    core = lax.axis_index("core")
    total = line_sum(part)
    other = lax.ppermute(total, "core", PAIR)
    first = core_pick(core, total, other)
    second = core_pick(core, other, total)
    return jnp.concatenate([first[:half], second[:half]], axis=0), first[half:]


def finish_many(parts, halves):
    core = lax.axis_index("core")
    flat = jnp.concatenate([part.reshape(-1) for part in parts])
    total = line_sum(flat)
    other = lax.ppermute(total, "core", PAIR)
    first = core_pick(core, total, other)
    second = core_pick(core, other, total)
    outs = []
    offset = 0
    for part, half in zip(parts, halves):
        size = part.size
        low = first[offset:offset + size].reshape(part.shape)
        high = second[offset:offset + size].reshape(part.shape)
        outs.append((jnp.concatenate([low[:half], high[:half]], axis=0), low[half:]))
        offset += size
    return outs


def reduce_weight(grad, extra=None):
    half = grad.shape[0] // lax.axis_size("shard") // 2
    return finish_sum(shard_sum(chip_sum(grad, extra)), half)


def line_sum(values):
    groups = lax.axis_size("outer")
    if groups == 1:
        return values
    if groups & (groups - 1):
        return lax.psum(values, "outer")
    here = lax.axis_index("outer")
    length = values.shape[0]
    padded = -(-length // groups) * groups
    held = jnp.pad(values, ((0, padded - length),) + ((0, 0),) * (values.ndim - 1))
    held = held.reshape((groups, padded // groups) + values.shape[1:])
    step = 1
    while step < groups:
        held = held.reshape((held.shape[0] // 2, 2) + held.shape[1:])
        bit = (here // step) % 2
        keep = lax.dynamic_index_in_dim(held, bit, axis=1, keepdims=False)
        send = lax.dynamic_index_in_dim(held, 1 - bit, axis=1, keepdims=False)
        held = keep + lax.ppermute(send, "outer", [(j, j ^ step) for j in range(groups)])
        step *= 2
    step = groups // 2
    while step >= 1:
        bit = (here // step) % 2
        other = lax.ppermute(held, "outer", [(j, j ^ step) for j in range(groups)])
        low = jnp.where(bit == 0, held, other)
        high = jnp.where(bit == 0, other, held)
        held = jnp.stack([low, high], axis=1)
        held = held.reshape((held.shape[0] * 2,) + held.shape[2:])
        step //= 2
    return held.reshape((padded,) + values.shape[1:])[:length]


def gather_packed(blocks, after=None):
    core = lax.axis_index("core")
    mine = lax.all_gather(jnp.concatenate(blocks, axis=0), "shard", axis=0, tiled=False)
    if after is not None:
        mine = mine + (after * 0).astype(mine.dtype)
    other = lax.ppermute(mine, "core", PAIR)
    return core_pick(core, mine, other), core_pick(core, other, mine)


def unpack_rows(first, second, begin, count, shape):
    parts = first.shape[0]
    rows, width = shape
    low = first[:, begin:begin + count].reshape(parts, -1, width)
    high = second[:, begin:begin + count].reshape(parts, -1, width)
    return jnp.stack([low, high], axis=1).reshape(rows, width)


def core_half(shard_rows):
    core = lax.axis_index("core")
    half = shard_rows.shape[0] // 2
    return lax.dynamic_slice_in_dim(shard_rows, core * half, half, axis=0)


def clip_local(tokens, lengths, cotangent, *params):
    clip_count, slot_count, width = tokens.shape
    parts = lax.axis_size("shard")
    place = lax.axis_index("shard")
    own = clip_count // parts
    weight_shards = params[:4]
    vector_shards = params[4:]
    wide = weight_shards[0].shape[1]
    vector_row = jnp.concatenate([entry.reshape(-1) for entry in vector_shards])
    pad = (-vector_row.shape[0]) % wide
    vector_rows = jnp.pad(vector_row, (0, pad)).reshape(-1, wide)
    attention_half = core_half(weight_shards[0])
    output_half = core_half(weight_shards[1]).reshape(-1, wide)
    first, second = gather_packed([attention_half, output_half, vector_rows])
    a_rows = attention_half.shape[0]
    o_rows = output_half.shape[0]
    attention_weight = unpack_rows(first, second, 0, a_rows, (parts * weight_shards[0].shape[0], wide))
    output_weight = unpack_rows(
        first, second, a_rows, o_rows, (parts * weight_shards[1].shape[0], weight_shards[1].shape[1])
    )
    vector_all = first[:, a_rows + o_rows:].reshape(parts, -1)[:, : vector_row.shape[0]]
    vectors = []
    offset = 0
    for entry in vector_shards:
        size = entry.shape[0]
        vectors.append(vector_all[:, offset:offset + size].reshape(parts * size).astype(jnp.float32))
        offset += size
    late = weight_shards[2].shape[1]
    expand_half = core_half(weight_shards[2])
    contract_half = core_half(weight_shards[3]).reshape(-1, late)

    def later_weights(after):
        first_b, second_b = gather_packed([expand_half, contract_half], after)
        e_rows = expand_half.shape[0]
        expand_weight = unpack_rows(first_b, second_b, 0, e_rows, (parts * weight_shards[2].shape[0], late))
        contract_weight = unpack_rows(
            first_b, second_b, e_rows, contract_half.shape[0],
            (parts * weight_shards[3].shape[0], weight_shards[3].shape[1]),
        )
        return expand_weight, contract_weight

    weights = (attention_weight, output_weight, later_weights)
    def gather_rows(values):
        moved = lax.all_to_all(values.reshape(clip_count * slot_count, width), "shard", 0, 0, tiled=True)
        moved = moved.reshape(parts, own, slot_count, width)
        return jnp.transpose(moved, (1, 0, 2, 3)).reshape(own, parts * slot_count, width) if own > 1 else moved.reshape(own, parts * slot_count, width)

    def scatter_rows(values):
        rows = values.reshape(own, parts, slot_count, width)
        if own > 1:
            rows = jnp.transpose(rows, (1, 0, 2, 3))
        moved = lax.all_to_all(rows.reshape(own * parts * slot_count, width), "shard", 0, 0, tiled=True)
        return moved.reshape(clip_count, slot_count, width)

    tokens_clip = gather_rows(tokens)

    def cotangent_of(after):
        late = cotangent + (after * 0).astype(cotangent.dtype)
        return gather_rows(late)

    lengths_clip = lax.dynamic_slice_in_dim(lengths, place * own, own, axis=0)
    block_output, input_grad, weight_grads, vector_grads = clip_layer(
        tokens_clip, lengths_clip, cotangent_of, weights, vectors, lambda part, rows: finish_sum(part, rows // parts // 2)[0],
        scatter_rows,
    )
    input_grad = scatter_rows(input_grad)
    attention_grad = weight_grads[0]
    attention_width = attention_grad.shape[1]
    vector_parts = jnp.concatenate([entry.reshape(parts, -1) for entry in vector_grads], axis=1)
    vector_size = vector_parts.shape[1]
    vpad = (-vector_size) % attention_width
    vector_parts = jnp.pad(vector_parts, ((0, 0), (0, vpad))).reshape(parts, -1, attention_width)
    attention_part = shard_sum(chip_sum(attention_grad, vector_parts))
    output_part = weight_grads[1]
    (attention_total, vector_total), (output_total, _) = finish_many(
        [attention_part, output_part],
        [attention_grad.shape[0] // parts // 2, params[1].shape[0] // 2],
    )
    totals = (attention_total, output_total) + tuple(weight_grads[2:])
    vector_total = vector_total.reshape(-1)[:vector_size]
    vector_outs = []
    offset = 0
    for entry in vector_shards:
        size = entry.shape[0]
        vector_outs.append(vector_total[offset:offset + size])
        offset += size
    return (block_output, input_grad) + totals + tuple(vector_outs)


def split_rep(mesh):
    devices = mesh.devices
    rep, parts = devices.shape
    first = devices[0, 0]
    stride = None
    for index in range(1, rep):
        other = devices[index, 0]
        if tuple(other.coords) == tuple(first.coords) and other.core_on_chip != first.core_on_chip:
            stride = index
            break
    if stride is None or rep % (2 * stride):
        return None
    grid = devices.reshape(rep // (2 * stride), 2, stride, parts)
    for spot in np.ndindex(grid.shape[0], grid.shape[2], grid.shape[3]):
        low = grid[spot[0], 0, spot[1], spot[2]]
        high = grid[spot[0], 1, spot[1], spot[2]]
        if tuple(low.coords) != tuple(high.coords) or low.core_on_chip == high.core_on_chip:
            return None
    return Mesh(grid, ("outer", "core", "inner", "shard"))


def solution(mesh):
    def specs(rep):
        ins = (P(rep, "shard", None), P(rep, None), P(rep, "shard", None)) + (P("shard", None),) * 4 + (
            P("shard"),
        ) * 9
        outs = (P(rep, "shard", None), P(rep, "shard", None)) + (P("shard", None),) * 4 + (P("shard"),) * 9
        return ins, outs

    ins, outs = specs("rep")
    plain = jax.shard_map(local, mesh=mesh, in_specs=ins, out_specs=outs, check_vma=False)
    split = split_rep(mesh)
    if split is None:
        return plain
    ins, outs = specs(("outer", "core", "inner"))
    fast = jax.shard_map(clip_local, mesh=split, in_specs=ins, out_specs=outs, check_vma=False)
    rep, parts = mesh.devices.shape

    def run(*args):
        if (args[0].shape[0] // rep) % parts == 0:
            return fast(*args)
        return plain(*args)

    return run
```

```python
import jax
import jax.numpy as jnp
from jax import lax
from jax.sharding import Mesh, PartitionSpec as P
import numpy as np

HEADS = 12
HEAD = 64


EPSILON = 1e-05
NEGATIVE = -1e30


def norm_forward(values, gain, shift):
    centred = values - jnp.mean(values, axis=-1, keepdims=True)
    inverse = lax.rsqrt(jnp.mean(centred * centred, axis=-1, keepdims=True) + EPSILON)
    normed = centred * inverse
    return (normed, inverse, (normed * gain + shift).astype(jnp.bfloat16))


def norm_backward(upstream, normed, inverse, gain):
    scaled = upstream * gain
    return inverse * (
        scaled
        - jnp.mean(scaled, axis=-1, keepdims=True)
        - normed * jnp.mean(scaled * normed, axis=-1, keepdims=True)
    )


def gelu_slope(values):
    return (
        0.5 * (1.0 + jax.scipy.special.erf(values * 0.7071067811865476))
        + values * jnp.exp(-0.5 * values * values) * 0.3989422804014327
    )


def inner_rows(left, right):
    return lax.dot_general(
        left, right, (((0,), (0,)), ((), ())), preferred_element_type=jnp.float32
    )


def heads_view(matrix):
    return matrix.reshape(matrix.shape[0], HEADS, HEAD)


def score_block(query_rows, key_rows, key_live):
    scores = jnp.einsum(
        "qhd,khd->hqk",
        heads_view(query_rows),
        heads_view(key_rows),
        preferred_element_type=jnp.float32,
    ) * HEAD ** (-0.5)
    return jnp.where(key_live[None, None, :], scores, NEGATIVE)


def attend_clip(items):
    query_rows, pair_rows, key_live = items
    width = query_rows.shape[1]
    scores = score_block(query_rows, pair_rows[:, :width], key_live)
    highest = jnp.max(scores, axis=-1, keepdims=True)
    logsum = highest + jnp.log(jnp.sum(jnp.exp(scores - highest), axis=-1, keepdims=True))
    probs_low = jnp.exp(scores - logsum).astype(jnp.bfloat16)
    attended = jnp.einsum(
        "hqk,khd->qhd",
        probs_low,
        heads_view(pair_rows[:, width:]),
        preferred_element_type=jnp.float32,
    )
    return (attended.reshape(query_rows.shape[0], width).astype(jnp.bfloat16), logsum[:, :, 0].T)


def score_grads(query_rows, dattended, logsum, delta, pair_rows, key_live):
    width = query_rows.shape[1]
    scores = score_block(query_rows, pair_rows[:, :width], key_live)
    probs = jnp.exp(scores - logsum.T[:, :, None])
    dprob = jnp.einsum(
        "qhd,khd->hqk",
        heads_view(dattended),
        heads_view(pair_rows[:, width:]),
        preferred_element_type=jnp.float32,
    )
    dscore = (probs * (dprob - delta.T[:, :, None]) * HEAD ** (-0.5)).astype(jnp.bfloat16)
    return (probs.astype(jnp.bfloat16), dscore)


def both_grads(items):
    query_rows, dattended, logsum, delta, pair_rows, key_live = items
    width = query_rows.shape[1]
    probs_low, dscore = score_grads(query_rows, dattended, logsum, delta, pair_rows, key_live)
    dqueries = jnp.einsum(
        "hqk,khd->qhd", dscore, heads_view(pair_rows[:, :width]), preferred_element_type=jnp.float32
    ).reshape(query_rows.shape[0], width)
    dkeys = jnp.einsum(
        "hqk,qhd->khd", dscore, heads_view(query_rows), preferred_element_type=jnp.float32
    )
    dvalues = jnp.einsum(
        "hqk,qhd->khd", probs_low, heads_view(dattended), preferred_element_type=jnp.float32
    )
    key_count = pair_rows.shape[0]
    return (
        dqueries,
        jnp.concatenate(
            [dkeys.reshape(key_count, width), dvalues.reshape(key_count, width)], axis=1
        ),
    )


def local(
    tokens,
    lengths,
    cotangent,
    attention_weight,
    output_weight,
    expand_weight,
    contract_weight,
    first_gain,
    first_shift,
    query_bias,
    value_bias,
    output_bias,
    second_gain,
    second_shift,
    expand_bias,
    contract_bias,
):
    clip_count, slot_count, width = tokens.shape
    parts = lax.axis_size("shard")
    frame_count = slot_count * parts
    place = lax.axis_index("shard")
    row_total = clip_count * slot_count
    gathered = (
        lax.all_gather(attention_weight, "shard", axis=0, tiled=True),
        lax.all_gather(output_weight, "shard", axis=0, tiled=True),
        lax.all_gather(expand_weight, "shard", axis=0, tiled=True),
        lax.all_gather(contract_weight, "shard", axis=0, tiled=True),
        lax.all_gather(first_gain, "shard", axis=0, tiled=True),
        lax.all_gather(first_shift, "shard", axis=0, tiled=True),
        lax.all_gather(query_bias, "shard", axis=0, tiled=True),
        lax.all_gather(value_bias, "shard", axis=0, tiled=True),
        lax.all_gather(output_bias, "shard", axis=0, tiled=True),
        lax.all_gather(second_gain, "shard", axis=0, tiled=True),
        lax.all_gather(second_shift, "shard", axis=0, tiled=True),
        lax.all_gather(expand_bias, "shard", axis=0, tiled=True),
        lax.all_gather(contract_bias, "shard", axis=0, tiled=True),
    )
    vectors = [entry.astype(jnp.float32) for entry in gathered[4:]]
    own_length = jnp.sum(jnp.where(jnp.arange(parts)[None, :] == place, lengths, 0), axis=1)
    row_live = jnp.arange(slot_count)[None, :] < own_length[:, None]
    key_live = (jnp.arange(slot_count)[None, None, :] < lengths[:, :, None]).reshape(
        clip_count, frame_count
    )
    inputs = tokens.reshape(row_total, width).astype(jnp.float32)
    first_normed, first_inverse, first_act = norm_forward(inputs, vectors[0], vectors[1])
    mixed = jnp.dot(first_act, gathered[0], preferred_element_type=jnp.float32)
    mixed = mixed + jnp.concatenate([vectors[2], jnp.zeros_like(vectors[2]), vectors[3]])
    mixed_low = mixed.astype(jnp.bfloat16)
    query_rows = mixed_low[:, :width].reshape(clip_count, slot_count, width)
    pair_own = mixed_low[:, width:].reshape(clip_count, slot_count, 2 * width)
    pair_all = lax.all_gather(pair_own, "shard", axis=1, tiled=True)
    attended, logsum = lax.map(attend_clip, (query_rows, pair_all, key_live))
    attended_flat = attended.reshape(row_total, width)
    residual = (
        inputs
        + jnp.dot(attended_flat, gathered[1], preferred_element_type=jnp.float32)
        + vectors[4]
    )
    second_normed, second_inverse, second_act = norm_forward(residual, vectors[5], vectors[6])
    pre = jnp.dot(second_act, gathered[2], preferred_element_type=jnp.float32) + vectors[7]
    hidden_act = jax.nn.gelu(pre, approximate=False).astype(jnp.bfloat16)
    block_output = (
        residual + jnp.dot(hidden_act, gathered[3], preferred_element_type=jnp.float32) + vectors[8]
    )
    backward = (
        lax.all_gather(attention_weight, "shard", axis=0, tiled=True),
        lax.all_gather(output_weight, "shard", axis=0, tiled=True),
        lax.all_gather(expand_weight, "shard", axis=0, tiled=True),
        lax.all_gather(contract_weight, "shard", axis=0, tiled=True),
        lax.all_gather(first_gain, "shard", axis=0, tiled=True),
        lax.all_gather(first_shift, "shard", axis=0, tiled=True),
        lax.all_gather(query_bias, "shard", axis=0, tiled=True),
        lax.all_gather(value_bias, "shard", axis=0, tiled=True),
        lax.all_gather(output_bias, "shard", axis=0, tiled=True),
        lax.all_gather(second_gain, "shard", axis=0, tiled=True),
        lax.all_gather(second_shift, "shard", axis=0, tiled=True),
        lax.all_gather(expand_bias, "shard", axis=0, tiled=True),
        lax.all_gather(contract_bias, "shard", axis=0, tiled=True),
    )
    back_vectors = [entry.astype(jnp.float32) for entry in backward[4:]]
    error = cotangent.reshape(row_total, width) * row_live.reshape(row_total, 1).astype(jnp.float32)
    error_low = error.astype(jnp.bfloat16)
    contract_bias_grad = jnp.sum(error, axis=0)
    contract_grad = inner_rows(hidden_act, error_low)
    dpre = lax.dot_general(
        error_low, backward[3], (((1,), (1,)), ((), ())), preferred_element_type=jnp.float32
    ) * gelu_slope(pre)
    expand_bias_grad = jnp.sum(dpre, axis=0)
    dpre_low = dpre.astype(jnp.bfloat16)
    expand_grad = inner_rows(second_act, dpre_low)
    dsecond = lax.dot_general(
        dpre_low, backward[2], (((1,), (1,)), ((), ())), preferred_element_type=jnp.float32
    )
    second_gain_grad = jnp.sum(dsecond * second_normed, axis=0)
    second_shift_grad = jnp.sum(dsecond, axis=0)
    dresidual = error + norm_backward(dsecond, second_normed, second_inverse, back_vectors[5])
    output_bias_grad = jnp.sum(dresidual, axis=0)
    dresidual_low = dresidual.astype(jnp.bfloat16)
    output_grad = inner_rows(attended_flat, dresidual_low)
    dattended = lax.dot_general(
        dresidual_low, backward[1], (((1,), (1,)), ((), ())), preferred_element_type=jnp.float32
    ).astype(jnp.bfloat16)
    delta = jnp.sum(
        heads_view(dattended.astype(jnp.float32)) * heads_view(attended_flat.astype(jnp.float32)),
        axis=-1,
    )
    delta = delta.reshape(clip_count, slot_count, HEADS)
    dattended_clips = dattended.reshape(clip_count, slot_count, width)
    dqueries, pair_terms = lax.map(
        both_grads, (query_rows, dattended_clips, logsum, delta, pair_all, key_live)
    )
    pair_grads = lax.psum_scatter(pair_terms, "shard", scatter_dimension=1, tiled=True)
    dqueries_flat = dqueries.reshape(row_total, width)
    pair_flat = pair_grads.reshape(row_total, 2 * width)
    dmixed = jnp.concatenate([dqueries_flat, pair_flat], axis=1)
    query_bias_grad = jnp.sum(dqueries_flat, axis=0)
    value_bias_grad = jnp.sum(pair_flat[:, width:], axis=0)
    dmixed_low = dmixed.astype(jnp.bfloat16)
    attention_grad = inner_rows(first_act, dmixed_low)
    dfirst = lax.dot_general(
        dmixed_low, backward[0], (((1,), (1,)), ((), ())), preferred_element_type=jnp.float32
    )
    first_gain_grad = jnp.sum(dfirst * first_normed, axis=0)
    first_shift_grad = jnp.sum(dfirst, axis=0)
    input_grad = dresidual + norm_backward(dfirst, first_normed, first_inverse, back_vectors[0])
    shares = (
        lax.psum_scatter(attention_grad, "shard", scatter_dimension=0, tiled=True),
        lax.psum_scatter(output_grad, "shard", scatter_dimension=0, tiled=True),
        lax.psum_scatter(expand_grad, "shard", scatter_dimension=0, tiled=True),
        lax.psum_scatter(contract_grad, "shard", scatter_dimension=0, tiled=True),
        lax.psum_scatter(first_gain_grad, "shard", scatter_dimension=0, tiled=True),
        lax.psum_scatter(first_shift_grad, "shard", scatter_dimension=0, tiled=True),
        lax.psum_scatter(query_bias_grad, "shard", scatter_dimension=0, tiled=True),
        lax.psum_scatter(value_bias_grad, "shard", scatter_dimension=0, tiled=True),
        lax.psum_scatter(output_bias_grad, "shard", scatter_dimension=0, tiled=True),
        lax.psum_scatter(second_gain_grad, "shard", scatter_dimension=0, tiled=True),
        lax.psum_scatter(second_shift_grad, "shard", scatter_dimension=0, tiled=True),
        lax.psum_scatter(expand_bias_grad, "shard", scatter_dimension=0, tiled=True),
        lax.psum_scatter(contract_bias_grad, "shard", scatter_dimension=0, tiled=True),
    )
    totals = lax.psum(
        (
            shares[0],
            shares[1],
            shares[2],
            shares[3],
            shares[4],
            shares[5],
            shares[6],
            shares[7],
            shares[8],
            shares[9],
            shares[10],
            shares[11],
            shares[12],
        ),
        "rep",
    )
    return (
        block_output.reshape(clip_count, slot_count, width),
        input_grad.reshape(clip_count, slot_count, width),
        totals[0],
        totals[1],
        totals[2],
        totals[3],
        totals[4],
        totals[5],
        totals[6],
        totals[7],
        totals[8],
        totals[9],
        totals[10],
        totals[11],
        totals[12],
    )


def clip_layer(tokens, lengths, cotangent_of, weights, vectors, reduce, send_out):
    attention_weight, output_weight, later_weights = weights
    (first_gain, first_shift, query_bias, value_bias, output_bias, second_gain, second_shift,
     expand_bias, contract_bias) = vectors
    clip_count, frame_count, width = tokens.shape
    block_count = lengths.shape[1]
    slot_count = frame_count // block_count
    rows = clip_count * frame_count
    live = (jnp.arange(slot_count)[None, None, :] < lengths[:, :, None]).reshape(clip_count, frame_count)
    scale = HEAD ** (-0.5)
    inputs = tokens.reshape(rows, width).astype(jnp.float32)
    first_normed, first_inverse, first_act = norm_forward(inputs, first_gain, first_shift)
    mixed = jnp.dot(first_act, attention_weight, preferred_element_type=jnp.float32)
    mixed = mixed + jnp.concatenate([query_bias, jnp.zeros_like(query_bias), value_bias])
    mixed_low = mixed.astype(jnp.bfloat16).reshape(clip_count, frame_count, 3, HEADS, HEAD)
    expand_weight, contract_weight = later_weights(mixed_low[0, 0, 0, 0, :1])
    queries = mixed_low[:, :, 0]
    keys = mixed_low[:, :, 1]
    values = mixed_low[:, :, 2]
    scores = jnp.einsum("cqhd,ckhd->chqk", queries, keys, preferred_element_type=jnp.float32) * scale
    scores = jnp.where(live[:, None, None, :], scores, NEGATIVE)
    highest = jnp.max(scores, axis=-1, keepdims=True)
    logsum = highest + jnp.log(jnp.sum(jnp.exp(scores - highest), axis=-1, keepdims=True))
    probs = jnp.exp(scores - logsum)
    probs_low = probs.astype(jnp.bfloat16)
    attended = jnp.einsum("chqk,ckhd->cqhd", probs_low, values, preferred_element_type=jnp.float32)
    attended_flat = attended.reshape(rows, width).astype(jnp.bfloat16)
    residual = inputs + jnp.dot(attended_flat, output_weight, preferred_element_type=jnp.float32) + output_bias
    second_normed, second_inverse, second_act = norm_forward(residual, second_gain, second_shift)
    pre = jnp.dot(second_act, expand_weight, preferred_element_type=jnp.float32) + expand_bias
    hidden_act = jax.nn.gelu(pre, approximate=False).astype(jnp.bfloat16)
    block_output = residual + jnp.dot(hidden_act, contract_weight, preferred_element_type=jnp.float32) + contract_bias
    cotangent = cotangent_of(pre[0, :1])
    error = cotangent.reshape(rows, width) * live.reshape(rows, 1).astype(jnp.float32)
    error_low = error.astype(jnp.bfloat16)
    contract_bias_grad = jnp.sum(error, axis=0)
    contract_grad = inner_rows(hidden_act, error_low)
    contract_chip = chip_sum(contract_grad)
    dpre = lax.dot_general(
        error_low, contract_weight, (((1,), (1,)), ((), ())), preferred_element_type=jnp.float32
    ) * gelu_slope(pre)
    expand_bias_grad = jnp.sum(dpre, axis=0)
    dpre_low = dpre.astype(jnp.bfloat16)
    contract_chip, dpre_low = lax.optimization_barrier((contract_chip, dpre_low))
    contract_part = shard_sum(contract_chip)
    expand_grad = inner_rows(second_act, dpre_low)
    expand_chip = chip_sum(expand_grad)
    dsecond = lax.dot_general(
        dpre_low, expand_weight, (((1,), (1,)), ((), ())), preferred_element_type=jnp.float32
    )
    second_gain_grad = jnp.sum(dsecond * second_normed, axis=0)
    second_shift_grad = jnp.sum(dsecond, axis=0)
    dresidual = error + norm_backward(dsecond, second_normed, second_inverse, second_gain)
    output_bias_grad = jnp.sum(dresidual, axis=0)
    dresidual_low = dresidual.astype(jnp.bfloat16)
    sent_output = send_out(block_output)
    expand_chip, dresidual_low = lax.optimization_barrier((expand_chip, dresidual_low))
    expand_part = shard_sum(expand_chip)
    output_grad = inner_rows(attended_flat, dresidual_low)
    output_chip = chip_sum(output_grad)
    dattended = lax.dot_general(
        dresidual_low, output_weight, (((1,), (1,)), ((), ())), preferred_element_type=jnp.float32
    ).astype(jnp.bfloat16)
    contract_part, dattended = lax.optimization_barrier((contract_part, dattended))
    dattended_heads = dattended.reshape(clip_count, frame_count, HEADS, HEAD)
    attended_heads = attended_flat.reshape(clip_count, frame_count, HEADS, HEAD)
    delta = jnp.sum(
        dattended_heads.astype(jnp.float32) * attended_heads.astype(jnp.float32), axis=-1
    )
    dprob = jnp.einsum("cqhd,ckhd->chqk", dattended_heads, values, preferred_element_type=jnp.float32)
    dscore = (probs * (dprob - jnp.transpose(delta, (0, 2, 1))[:, :, :, None]) * scale).astype(jnp.bfloat16)
    dqueries = jnp.einsum("chqk,ckhd->cqhd", dscore, keys, preferred_element_type=jnp.float32)
    dkeys = jnp.einsum("chqk,cqhd->ckhd", dscore, queries, preferred_element_type=jnp.float32)
    dvalues = jnp.einsum("chqk,cqhd->ckhd", probs_low, dattended_heads, preferred_element_type=jnp.float32)
    dmixed = jnp.concatenate(
        [dqueries.reshape(rows, width), dkeys.reshape(rows, width), dvalues.reshape(rows, width)], axis=1
    )
    query_bias_grad = jnp.sum(dmixed[:, :width], axis=0)
    value_bias_grad = jnp.sum(dmixed[:, 2 * width:], axis=0)
    dmixed_low = dmixed.astype(jnp.bfloat16)
    contract_total = reduce(contract_part, contract_grad.shape[0])
    output_chip, expand_part, contract_total, sent_output, dmixed_low = lax.optimization_barrier(
        (output_chip, expand_part, contract_total, sent_output, dmixed_low)
    )
    output_part = shard_sum(output_chip)
    expand_total = reduce(expand_part, expand_grad.shape[0])
    attention_grad = inner_rows(first_act, dmixed_low)
    dfirst = lax.optimization_barrier(lax.dot_general(
        dmixed_low, attention_weight, (((1,), (1,)), ((), ())), preferred_element_type=jnp.float32
    ))
    first_gain_grad = jnp.sum(dfirst * first_normed, axis=0)
    first_shift_grad = jnp.sum(dfirst, axis=0)
    input_grad = dresidual + norm_backward(dfirst, first_normed, first_inverse, first_gain)
    output_part, expand_total, input_grad = lax.optimization_barrier((output_part, expand_total, input_grad))
    weight_grads = (attention_grad, output_part, expand_total, contract_total)
    vector_grads = (first_gain_grad, first_shift_grad, query_bias_grad, value_bias_grad, output_bias_grad,
                    second_gain_grad, second_shift_grad, expand_bias_grad, contract_bias_grad)
    return (
        sent_output,
        input_grad,
        weight_grads,
        vector_grads,
    )


PAIR = [(0, 1), (1, 0)]
OUTER = ("outer", "inner")


def core_pick(core, first, second):
    return jnp.where(core == 0, first, second)


def gather_weight(shard_rows, extra=None):
    parts = lax.axis_size("shard")
    core = lax.axis_index("core")
    rows, width = shard_rows.shape
    half = rows // 2
    mine = lax.dynamic_slice_in_dim(shard_rows, core * half, half, axis=0)
    if extra is not None:
        mine = jnp.concatenate([mine, extra], axis=0)
    mine = lax.all_gather(mine, "shard", axis=0, tiled=False)
    other = lax.ppermute(mine, "core", PAIR)
    first = core_pick(core, mine, other)
    second = core_pick(core, other, mine)
    full = jnp.stack([first[:, :half], second[:, :half]], axis=1).reshape(parts * rows, width)
    if extra is None:
        return full, None
    return full, first[:, half:]


def chip_sum(grad, extra=None):
    parts = lax.axis_size("shard")
    core = lax.axis_index("core")
    width = grad.shape[1]
    rows = grad.shape[0] // parts
    half = rows // 2
    quarters = grad.reshape(parts, 2, half, width)
    keep = lax.dynamic_index_in_dim(quarters, core, axis=1, keepdims=False)
    send = lax.dynamic_index_in_dim(quarters, 1 - core, axis=1, keepdims=False)
    if extra is not None:
        on_first = (core == 0).astype(extra.dtype)
        keep = jnp.concatenate([keep, extra * on_first], axis=1)
        send = jnp.concatenate([send, extra * (1 - on_first)], axis=1)
    return keep + lax.ppermute(send, "core", PAIR)


def shard_sum(chip):
    part = lax.psum_scatter(chip, "shard", scatter_dimension=0, tiled=False)
    if lax.axis_size("inner") > 1:
        part = lax.psum(part, "inner")
    return part


def finish_sum(part, half, queued=False):
    core = lax.axis_index("core")
    total = lax.psum(part, "outer") if queued else line_sum(part)
    other = lax.ppermute(total, "core", PAIR)
    first = core_pick(core, total, other)
    second = core_pick(core, other, total)
    return jnp.concatenate([first[:half], second[:half]], axis=0), first[half:]


def finish_many(parts, halves):
    core = lax.axis_index("core")
    flat = jnp.concatenate([part.reshape(-1) for part in parts])
    total = line_sum(flat)
    other = lax.ppermute(total, "core", PAIR)
    first = core_pick(core, total, other)
    second = core_pick(core, other, total)
    outs = []
    offset = 0
    for part, half in zip(parts, halves):
        size = part.size
        low = first[offset:offset + size].reshape(part.shape)
        high = second[offset:offset + size].reshape(part.shape)
        outs.append((jnp.concatenate([low[:half], high[:half]], axis=0), low[half:]))
        offset += size
    return outs


def reduce_weight(grad, extra=None):
    half = grad.shape[0] // lax.axis_size("shard") // 2
    return finish_sum(shard_sum(chip_sum(grad, extra)), half)


def line_sum(values):
    groups = lax.axis_size("outer")
    if groups == 1:
        return values
    if groups & (groups - 1):
        return lax.psum(values, "outer")
    here = lax.axis_index("outer")
    length = values.shape[0]
    padded = -(-length // groups) * groups
    held = jnp.pad(values, ((0, padded - length),) + ((0, 0),) * (values.ndim - 1))
    held = held.reshape((groups, padded // groups) + values.shape[1:])
    step = 1
    while step < groups:
        held = held.reshape((held.shape[0] // 2, 2) + held.shape[1:])
        bit = (here // step) % 2
        keep = lax.dynamic_index_in_dim(held, bit, axis=1, keepdims=False)
        send = lax.dynamic_index_in_dim(held, 1 - bit, axis=1, keepdims=False)
        held = keep + lax.ppermute(send, "outer", [(j, j ^ step) for j in range(groups)])
        step *= 2
    step = groups // 2
    while step >= 1:
        bit = (here // step) % 2
        other = lax.ppermute(held, "outer", [(j, j ^ step) for j in range(groups)])
        low = jnp.where(bit == 0, held, other)
        high = jnp.where(bit == 0, other, held)
        held = jnp.stack([low, high], axis=1)
        held = held.reshape((held.shape[0] * 2,) + held.shape[2:])
        step //= 2
    return held.reshape((padded,) + values.shape[1:])[:length]


def gather_packed(blocks, after=None):
    core = lax.axis_index("core")
    mine = lax.all_gather(jnp.concatenate(blocks, axis=0), "shard", axis=0, tiled=False)
    if after is not None:
        mine = mine + (after * 0).astype(mine.dtype)
    other = lax.ppermute(mine, "core", PAIR)
    return core_pick(core, mine, other), core_pick(core, other, mine)


def unpack_rows(first, second, begin, count, shape):
    parts = first.shape[0]
    rows, width = shape
    low = first[:, begin:begin + count].reshape(parts, -1, width)
    high = second[:, begin:begin + count].reshape(parts, -1, width)
    return jnp.stack([low, high], axis=1).reshape(rows, width)


def core_half(shard_rows):
    core = lax.axis_index("core")
    half = shard_rows.shape[0] // 2
    return lax.dynamic_slice_in_dim(shard_rows, core * half, half, axis=0)


def clip_local(tokens, lengths, cotangent, *params):
    clip_count, slot_count, width = tokens.shape
    parts = lax.axis_size("shard")
    place = lax.axis_index("shard")
    own = clip_count // parts
    weight_shards = params[:4]
    vector_shards = params[4:]
    wide = weight_shards[0].shape[1]
    vector_row = jnp.concatenate([entry.reshape(-1) for entry in vector_shards])
    pad = (-vector_row.shape[0]) % wide
    vector_rows = jnp.pad(vector_row, (0, pad)).reshape(-1, wide)
    attention_half = core_half(weight_shards[0])
    output_half = core_half(weight_shards[1]).reshape(-1, wide)
    first, second = gather_packed([attention_half, output_half, vector_rows])
    a_rows = attention_half.shape[0]
    o_rows = output_half.shape[0]
    attention_weight = unpack_rows(first, second, 0, a_rows, (parts * weight_shards[0].shape[0], wide))
    output_weight = unpack_rows(
        first, second, a_rows, o_rows, (parts * weight_shards[1].shape[0], weight_shards[1].shape[1])
    )
    vector_all = first[:, a_rows + o_rows:].reshape(parts, -1)[:, : vector_row.shape[0]]
    vectors = []
    offset = 0
    for entry in vector_shards:
        size = entry.shape[0]
        vectors.append(vector_all[:, offset:offset + size].reshape(parts * size).astype(jnp.float32))
        offset += size
    late = weight_shards[2].shape[1]
    expand_half = core_half(weight_shards[2])
    contract_half = core_half(weight_shards[3]).reshape(-1, late)

    def later_weights(after):
        first_b, second_b = gather_packed([expand_half, contract_half], after)
        e_rows = expand_half.shape[0]
        expand_weight = unpack_rows(first_b, second_b, 0, e_rows, (parts * weight_shards[2].shape[0], late))
        contract_weight = unpack_rows(
            first_b, second_b, e_rows, contract_half.shape[0],
            (parts * weight_shards[3].shape[0], weight_shards[3].shape[1]),
        )
        return expand_weight, contract_weight

    weights = (attention_weight, output_weight, later_weights)
    def gather_rows(values):
        moved = lax.all_to_all(values.reshape(clip_count * slot_count, width), "shard", 0, 0, tiled=True)
        moved = moved.reshape(parts, own, slot_count, width)
        return jnp.transpose(moved, (1, 0, 2, 3)).reshape(own, parts * slot_count, width) if own > 1 else moved.reshape(own, parts * slot_count, width)

    def scatter_rows(values):
        rows = values.reshape(own, parts, slot_count, width)
        if own > 1:
            rows = jnp.transpose(rows, (1, 0, 2, 3))
        moved = lax.all_to_all(rows.reshape(own * parts * slot_count, width), "shard", 0, 0, tiled=True)
        return moved.reshape(clip_count, slot_count, width)

    tokens_clip = gather_rows(tokens)

    def cotangent_of(after):
        late = cotangent + (after * 0).astype(cotangent.dtype)
        return gather_rows(late)

    lengths_clip = lax.dynamic_slice_in_dim(lengths, place * own, own, axis=0)
    block_output, input_grad, weight_grads, vector_grads = clip_layer(
        tokens_clip, lengths_clip, cotangent_of, weights, vectors, lambda part, rows: finish_sum(part, rows // parts // 2, True)[0],
        scatter_rows,
    )
    input_grad = scatter_rows(input_grad)
    attention_grad = weight_grads[0]
    attention_width = attention_grad.shape[1]
    vector_parts = jnp.concatenate([entry.reshape(parts, -1) for entry in vector_grads], axis=1)
    vector_size = vector_parts.shape[1]
    vpad = (-vector_size) % attention_width
    vector_parts = jnp.pad(vector_parts, ((0, 0), (0, vpad))).reshape(parts, -1, attention_width)
    attention_part = shard_sum(chip_sum(attention_grad, vector_parts))
    output_part = weight_grads[1]
    (attention_total, vector_total), (output_total, _) = finish_many(
        [attention_part, output_part],
        [attention_grad.shape[0] // parts // 2, params[1].shape[0] // 2],
    )
    totals = (attention_total, output_total) + tuple(weight_grads[2:])
    vector_total = vector_total.reshape(-1)[:vector_size]
    vector_outs = []
    offset = 0
    for entry in vector_shards:
        size = entry.shape[0]
        vector_outs.append(vector_total[offset:offset + size])
        offset += size
    return (block_output, input_grad) + totals + tuple(vector_outs)


def split_rep(mesh):
    devices = mesh.devices
    rep, parts = devices.shape
    first = devices[0, 0]
    stride = None
    for index in range(1, rep):
        other = devices[index, 0]
        if tuple(other.coords) == tuple(first.coords) and other.core_on_chip != first.core_on_chip:
            stride = index
            break
    if stride is None or rep % (2 * stride):
        return None
    grid = devices.reshape(rep // (2 * stride), 2, stride, parts)
    for spot in np.ndindex(grid.shape[0], grid.shape[2], grid.shape[3]):
        low = grid[spot[0], 0, spot[1], spot[2]]
        high = grid[spot[0], 1, spot[1], spot[2]]
        if tuple(low.coords) != tuple(high.coords) or low.core_on_chip == high.core_on_chip:
            return None
    return Mesh(grid, ("outer", "core", "inner", "shard"))


def solution(mesh):
    def specs(rep):
        ins = (P(rep, "shard", None), P(rep, None), P(rep, "shard", None)) + (P("shard", None),) * 4 + (
            P("shard"),
        ) * 9
        outs = (P(rep, "shard", None), P(rep, "shard", None)) + (P("shard", None),) * 4 + (P("shard"),) * 9
        return ins, outs

    ins, outs = specs("rep")
    plain = jax.shard_map(local, mesh=mesh, in_specs=ins, out_specs=outs, check_vma=False)
    split = split_rep(mesh)
    if split is None:
        return plain
    ins, outs = specs(("outer", "core", "inner"))
    fast = jax.shard_map(clip_local, mesh=split, in_specs=ins, out_specs=outs, check_vma=False)
    rep, parts = mesh.devices.shape

    def run(*args):
        if (args[0].shape[0] // rep) % parts == 0:
            return fast(*args)
        return plain(*args)

    return run
```

```python
import jax
import jax.numpy as jnp
from jax import lax
from jax.sharding import Mesh, PartitionSpec as P
import numpy as np

HEADS = 12
HEAD = 64


EPSILON = 1e-05
NEGATIVE = -1e30


def norm_forward(values, gain, shift):
    centred = values - jnp.mean(values, axis=-1, keepdims=True)
    inverse = lax.rsqrt(jnp.mean(centred * centred, axis=-1, keepdims=True) + EPSILON)
    normed = centred * inverse
    return (normed, inverse, (normed * gain + shift).astype(jnp.bfloat16))


def norm_backward(upstream, normed, inverse, gain):
    scaled = upstream * gain
    return inverse * (
        scaled
        - jnp.mean(scaled, axis=-1, keepdims=True)
        - normed * jnp.mean(scaled * normed, axis=-1, keepdims=True)
    )


def gelu_slope(values):
    return (
        0.5 * (1.0 + jax.scipy.special.erf(values * 0.7071067811865476))
        + values * jnp.exp(-0.5 * values * values) * 0.3989422804014327
    )


def inner_rows(left, right):
    return lax.dot_general(
        left, right, (((0,), (0,)), ((), ())), preferred_element_type=jnp.float32
    )


def heads_view(matrix):
    return matrix.reshape(matrix.shape[0], HEADS, HEAD)


def score_block(query_rows, key_rows, key_live):
    scores = jnp.einsum(
        "qhd,khd->hqk",
        heads_view(query_rows),
        heads_view(key_rows),
        preferred_element_type=jnp.float32,
    ) * HEAD ** (-0.5)
    return jnp.where(key_live[None, None, :], scores, NEGATIVE)


def attend_clip(items):
    query_rows, pair_rows, key_live = items
    width = query_rows.shape[1]
    scores = score_block(query_rows, pair_rows[:, :width], key_live)
    highest = jnp.max(scores, axis=-1, keepdims=True)
    logsum = highest + jnp.log(jnp.sum(jnp.exp(scores - highest), axis=-1, keepdims=True))
    probs_low = jnp.exp(scores - logsum).astype(jnp.bfloat16)
    attended = jnp.einsum(
        "hqk,khd->qhd",
        probs_low,
        heads_view(pair_rows[:, width:]),
        preferred_element_type=jnp.float32,
    )
    return (attended.reshape(query_rows.shape[0], width).astype(jnp.bfloat16), logsum[:, :, 0].T)


def score_grads(query_rows, dattended, logsum, delta, pair_rows, key_live):
    width = query_rows.shape[1]
    scores = score_block(query_rows, pair_rows[:, :width], key_live)
    probs = jnp.exp(scores - logsum.T[:, :, None])
    dprob = jnp.einsum(
        "qhd,khd->hqk",
        heads_view(dattended),
        heads_view(pair_rows[:, width:]),
        preferred_element_type=jnp.float32,
    )
    dscore = (probs * (dprob - delta.T[:, :, None]) * HEAD ** (-0.5)).astype(jnp.bfloat16)
    return (probs.astype(jnp.bfloat16), dscore)


def both_grads(items):
    query_rows, dattended, logsum, delta, pair_rows, key_live = items
    width = query_rows.shape[1]
    probs_low, dscore = score_grads(query_rows, dattended, logsum, delta, pair_rows, key_live)
    dqueries = jnp.einsum(
        "hqk,khd->qhd", dscore, heads_view(pair_rows[:, :width]), preferred_element_type=jnp.float32
    ).reshape(query_rows.shape[0], width)
    dkeys = jnp.einsum(
        "hqk,qhd->khd", dscore, heads_view(query_rows), preferred_element_type=jnp.float32
    )
    dvalues = jnp.einsum(
        "hqk,qhd->khd", probs_low, heads_view(dattended), preferred_element_type=jnp.float32
    )
    key_count = pair_rows.shape[0]
    return (
        dqueries,
        jnp.concatenate(
            [dkeys.reshape(key_count, width), dvalues.reshape(key_count, width)], axis=1
        ),
    )


def local(
    tokens,
    lengths,
    cotangent,
    attention_weight,
    output_weight,
    expand_weight,
    contract_weight,
    first_gain,
    first_shift,
    query_bias,
    value_bias,
    output_bias,
    second_gain,
    second_shift,
    expand_bias,
    contract_bias,
):
    clip_count, slot_count, width = tokens.shape
    parts = lax.axis_size("shard")
    frame_count = slot_count * parts
    place = lax.axis_index("shard")
    row_total = clip_count * slot_count
    gathered = (
        lax.all_gather(attention_weight, "shard", axis=0, tiled=True),
        lax.all_gather(output_weight, "shard", axis=0, tiled=True),
        lax.all_gather(expand_weight, "shard", axis=0, tiled=True),
        lax.all_gather(contract_weight, "shard", axis=0, tiled=True),
        lax.all_gather(first_gain, "shard", axis=0, tiled=True),
        lax.all_gather(first_shift, "shard", axis=0, tiled=True),
        lax.all_gather(query_bias, "shard", axis=0, tiled=True),
        lax.all_gather(value_bias, "shard", axis=0, tiled=True),
        lax.all_gather(output_bias, "shard", axis=0, tiled=True),
        lax.all_gather(second_gain, "shard", axis=0, tiled=True),
        lax.all_gather(second_shift, "shard", axis=0, tiled=True),
        lax.all_gather(expand_bias, "shard", axis=0, tiled=True),
        lax.all_gather(contract_bias, "shard", axis=0, tiled=True),
    )
    vectors = [entry.astype(jnp.float32) for entry in gathered[4:]]
    own_length = jnp.sum(jnp.where(jnp.arange(parts)[None, :] == place, lengths, 0), axis=1)
    row_live = jnp.arange(slot_count)[None, :] < own_length[:, None]
    key_live = (jnp.arange(slot_count)[None, None, :] < lengths[:, :, None]).reshape(
        clip_count, frame_count
    )
    inputs = tokens.reshape(row_total, width).astype(jnp.float32)
    first_normed, first_inverse, first_act = norm_forward(inputs, vectors[0], vectors[1])
    mixed = jnp.dot(first_act, gathered[0], preferred_element_type=jnp.float32)
    mixed = mixed + jnp.concatenate([vectors[2], jnp.zeros_like(vectors[2]), vectors[3]])
    mixed_low = mixed.astype(jnp.bfloat16)
    query_rows = mixed_low[:, :width].reshape(clip_count, slot_count, width)
    pair_own = mixed_low[:, width:].reshape(clip_count, slot_count, 2 * width)
    pair_all = lax.all_gather(pair_own, "shard", axis=1, tiled=True)
    attended, logsum = lax.map(attend_clip, (query_rows, pair_all, key_live))
    attended_flat = attended.reshape(row_total, width)
    residual = (
        inputs
        + jnp.dot(attended_flat, gathered[1], preferred_element_type=jnp.float32)
        + vectors[4]
    )
    second_normed, second_inverse, second_act = norm_forward(residual, vectors[5], vectors[6])
    pre = jnp.dot(second_act, gathered[2], preferred_element_type=jnp.float32) + vectors[7]
    hidden_act = jax.nn.gelu(pre, approximate=False).astype(jnp.bfloat16)
    block_output = (
        residual + jnp.dot(hidden_act, gathered[3], preferred_element_type=jnp.float32) + vectors[8]
    )
    backward = (
        lax.all_gather(attention_weight, "shard", axis=0, tiled=True),
        lax.all_gather(output_weight, "shard", axis=0, tiled=True),
        lax.all_gather(expand_weight, "shard", axis=0, tiled=True),
        lax.all_gather(contract_weight, "shard", axis=0, tiled=True),
        lax.all_gather(first_gain, "shard", axis=0, tiled=True),
        lax.all_gather(first_shift, "shard", axis=0, tiled=True),
        lax.all_gather(query_bias, "shard", axis=0, tiled=True),
        lax.all_gather(value_bias, "shard", axis=0, tiled=True),
        lax.all_gather(output_bias, "shard", axis=0, tiled=True),
        lax.all_gather(second_gain, "shard", axis=0, tiled=True),
        lax.all_gather(second_shift, "shard", axis=0, tiled=True),
        lax.all_gather(expand_bias, "shard", axis=0, tiled=True),
        lax.all_gather(contract_bias, "shard", axis=0, tiled=True),
    )
    back_vectors = [entry.astype(jnp.float32) for entry in backward[4:]]
    error = cotangent.reshape(row_total, width) * row_live.reshape(row_total, 1).astype(jnp.float32)
    error_low = error.astype(jnp.bfloat16)
    contract_bias_grad = jnp.sum(error, axis=0)
    contract_grad = inner_rows(hidden_act, error_low)
    dpre = lax.dot_general(
        error_low, backward[3], (((1,), (1,)), ((), ())), preferred_element_type=jnp.float32
    ) * gelu_slope(pre)
    expand_bias_grad = jnp.sum(dpre, axis=0)
    dpre_low = dpre.astype(jnp.bfloat16)
    expand_grad = inner_rows(second_act, dpre_low)
    dsecond = lax.dot_general(
        dpre_low, backward[2], (((1,), (1,)), ((), ())), preferred_element_type=jnp.float32
    )
    second_gain_grad = jnp.sum(dsecond * second_normed, axis=0)
    second_shift_grad = jnp.sum(dsecond, axis=0)
    dresidual = error + norm_backward(dsecond, second_normed, second_inverse, back_vectors[5])
    output_bias_grad = jnp.sum(dresidual, axis=0)
    dresidual_low = dresidual.astype(jnp.bfloat16)
    output_grad = inner_rows(attended_flat, dresidual_low)
    dattended = lax.dot_general(
        dresidual_low, backward[1], (((1,), (1,)), ((), ())), preferred_element_type=jnp.float32
    ).astype(jnp.bfloat16)
    delta = jnp.sum(
        heads_view(dattended.astype(jnp.float32)) * heads_view(attended_flat.astype(jnp.float32)),
        axis=-1,
    )
    delta = delta.reshape(clip_count, slot_count, HEADS)
    dattended_clips = dattended.reshape(clip_count, slot_count, width)
    dqueries, pair_terms = lax.map(
        both_grads, (query_rows, dattended_clips, logsum, delta, pair_all, key_live)
    )
    pair_grads = lax.psum_scatter(pair_terms, "shard", scatter_dimension=1, tiled=True)
    dqueries_flat = dqueries.reshape(row_total, width)
    pair_flat = pair_grads.reshape(row_total, 2 * width)
    dmixed = jnp.concatenate([dqueries_flat, pair_flat], axis=1)
    query_bias_grad = jnp.sum(dqueries_flat, axis=0)
    value_bias_grad = jnp.sum(pair_flat[:, width:], axis=0)
    dmixed_low = dmixed.astype(jnp.bfloat16)
    attention_grad = inner_rows(first_act, dmixed_low)
    dfirst = lax.dot_general(
        dmixed_low, backward[0], (((1,), (1,)), ((), ())), preferred_element_type=jnp.float32
    )
    first_gain_grad = jnp.sum(dfirst * first_normed, axis=0)
    first_shift_grad = jnp.sum(dfirst, axis=0)
    input_grad = dresidual + norm_backward(dfirst, first_normed, first_inverse, back_vectors[0])
    shares = (
        lax.psum_scatter(attention_grad, "shard", scatter_dimension=0, tiled=True),
        lax.psum_scatter(output_grad, "shard", scatter_dimension=0, tiled=True),
        lax.psum_scatter(expand_grad, "shard", scatter_dimension=0, tiled=True),
        lax.psum_scatter(contract_grad, "shard", scatter_dimension=0, tiled=True),
        lax.psum_scatter(first_gain_grad, "shard", scatter_dimension=0, tiled=True),
        lax.psum_scatter(first_shift_grad, "shard", scatter_dimension=0, tiled=True),
        lax.psum_scatter(query_bias_grad, "shard", scatter_dimension=0, tiled=True),
        lax.psum_scatter(value_bias_grad, "shard", scatter_dimension=0, tiled=True),
        lax.psum_scatter(output_bias_grad, "shard", scatter_dimension=0, tiled=True),
        lax.psum_scatter(second_gain_grad, "shard", scatter_dimension=0, tiled=True),
        lax.psum_scatter(second_shift_grad, "shard", scatter_dimension=0, tiled=True),
        lax.psum_scatter(expand_bias_grad, "shard", scatter_dimension=0, tiled=True),
        lax.psum_scatter(contract_bias_grad, "shard", scatter_dimension=0, tiled=True),
    )
    totals = lax.psum(
        (
            shares[0],
            shares[1],
            shares[2],
            shares[3],
            shares[4],
            shares[5],
            shares[6],
            shares[7],
            shares[8],
            shares[9],
            shares[10],
            shares[11],
            shares[12],
        ),
        "rep",
    )
    return (
        block_output.reshape(clip_count, slot_count, width),
        input_grad.reshape(clip_count, slot_count, width),
        totals[0],
        totals[1],
        totals[2],
        totals[3],
        totals[4],
        totals[5],
        totals[6],
        totals[7],
        totals[8],
        totals[9],
        totals[10],
        totals[11],
        totals[12],
    )


def clip_layer(tokens, lengths, cotangent_of, weights, vectors, reduce, send_out):
    attention_weight, output_weight, later_weights = weights
    (first_gain, first_shift, query_bias, value_bias, output_bias, second_gain, second_shift,
     expand_bias, contract_bias) = vectors
    clip_count, frame_count, width = tokens.shape
    block_count = lengths.shape[1]
    slot_count = frame_count // block_count
    rows = clip_count * frame_count
    live = (jnp.arange(slot_count)[None, None, :] < lengths[:, :, None]).reshape(clip_count, frame_count)
    scale = HEAD ** (-0.5)
    inputs = tokens.reshape(rows, width).astype(jnp.float32)
    first_normed, first_inverse, first_act = norm_forward(inputs, first_gain, first_shift)
    mixed = jnp.dot(first_act, attention_weight, preferred_element_type=jnp.float32)
    mixed = mixed + jnp.concatenate([query_bias, jnp.zeros_like(query_bias), value_bias])
    mixed_low = mixed.astype(jnp.bfloat16).reshape(clip_count, frame_count, 3, HEADS, HEAD)
    expand_weight, contract_weight = later_weights(mixed_low[0, 0, 0, 0, :1])
    queries = mixed_low[:, :, 0]
    keys = mixed_low[:, :, 1]
    values = mixed_low[:, :, 2]
    scores = jnp.einsum("cqhd,ckhd->chqk", queries, keys, preferred_element_type=jnp.float32) * scale
    scores = jnp.where(live[:, None, None, :], scores, NEGATIVE)
    highest = jnp.max(scores, axis=-1, keepdims=True)
    logsum = highest + jnp.log(jnp.sum(jnp.exp(scores - highest), axis=-1, keepdims=True))
    probs = jnp.exp(scores - logsum)
    probs_low = probs.astype(jnp.bfloat16)
    attended = jnp.einsum("chqk,ckhd->cqhd", probs_low, values, preferred_element_type=jnp.float32)
    attended_flat = attended.reshape(rows, width).astype(jnp.bfloat16)
    residual = inputs + jnp.dot(attended_flat, output_weight, preferred_element_type=jnp.float32) + output_bias
    second_normed, second_inverse, second_act = norm_forward(residual, second_gain, second_shift)
    pre = jnp.dot(second_act, expand_weight, preferred_element_type=jnp.float32) + expand_bias
    hidden_act = jax.nn.gelu(pre, approximate=False).astype(jnp.bfloat16)
    block_output = residual + jnp.dot(hidden_act, contract_weight, preferred_element_type=jnp.float32) + contract_bias
    cotangent = cotangent_of(pre[0, :1])
    error = cotangent.reshape(rows, width) * live.reshape(rows, 1).astype(jnp.float32)
    error_low = error.astype(jnp.bfloat16)
    contract_bias_grad = jnp.sum(error, axis=0)
    contract_grad = inner_rows(hidden_act, error_low)
    contract_chip = chip_sum(contract_grad)
    dpre = lax.dot_general(
        error_low, contract_weight, (((1,), (1,)), ((), ())), preferred_element_type=jnp.float32
    ) * gelu_slope(pre)
    expand_bias_grad = jnp.sum(dpre, axis=0)
    dpre_low = dpre.astype(jnp.bfloat16)
    contract_chip, dpre_low = lax.optimization_barrier((contract_chip, dpre_low))
    contract_part = shard_sum(contract_chip)
    expand_grad = inner_rows(second_act, dpre_low)
    expand_chip = chip_sum(expand_grad)
    dsecond = lax.dot_general(
        dpre_low, expand_weight, (((1,), (1,)), ((), ())), preferred_element_type=jnp.float32
    )
    second_gain_grad = jnp.sum(dsecond * second_normed, axis=0)
    second_shift_grad = jnp.sum(dsecond, axis=0)
    dresidual = error + norm_backward(dsecond, second_normed, second_inverse, second_gain)
    output_bias_grad = jnp.sum(dresidual, axis=0)
    dresidual_low = dresidual.astype(jnp.bfloat16)
    sent_output = send_out(block_output)
    expand_chip, dresidual_low = lax.optimization_barrier((expand_chip, dresidual_low))
    expand_part = shard_sum(expand_chip)
    output_grad = inner_rows(attended_flat, dresidual_low)
    output_chip = chip_sum(output_grad)
    dattended = lax.dot_general(
        dresidual_low, output_weight, (((1,), (1,)), ((), ())), preferred_element_type=jnp.float32
    ).astype(jnp.bfloat16)
    contract_part, dattended = lax.optimization_barrier((contract_part, dattended))
    dattended_heads = dattended.reshape(clip_count, frame_count, HEADS, HEAD)
    attended_heads = attended_flat.reshape(clip_count, frame_count, HEADS, HEAD)
    delta = jnp.sum(
        dattended_heads.astype(jnp.float32) * attended_heads.astype(jnp.float32), axis=-1
    )
    dprob = jnp.einsum("cqhd,ckhd->chqk", dattended_heads, values, preferred_element_type=jnp.float32)
    dscore = (probs * (dprob - jnp.transpose(delta, (0, 2, 1))[:, :, :, None]) * scale).astype(jnp.bfloat16)
    dqueries = jnp.einsum("chqk,ckhd->cqhd", dscore, keys, preferred_element_type=jnp.float32)
    dkeys = jnp.einsum("chqk,cqhd->ckhd", dscore, queries, preferred_element_type=jnp.float32)
    dvalues = jnp.einsum("chqk,cqhd->ckhd", probs_low, dattended_heads, preferred_element_type=jnp.float32)
    dmixed = jnp.concatenate(
        [dqueries.reshape(rows, width), dkeys.reshape(rows, width), dvalues.reshape(rows, width)], axis=1
    )
    query_bias_grad = jnp.sum(dmixed[:, :width], axis=0)
    value_bias_grad = jnp.sum(dmixed[:, 2 * width:], axis=0)
    dmixed_low = dmixed.astype(jnp.bfloat16)
    contract_total = reduce(contract_part, contract_grad.shape[0])
    output_chip, expand_part, contract_total, sent_output, dmixed_low = lax.optimization_barrier(
        (output_chip, expand_part, contract_total, sent_output, dmixed_low)
    )
    output_part = shard_sum(output_chip)
    expand_total = reduce(expand_part, expand_grad.shape[0])
    attention_grad = inner_rows(first_act, dmixed_low)
    dfirst = lax.optimization_barrier(lax.dot_general(
        dmixed_low, attention_weight, (((1,), (1,)), ((), ())), preferred_element_type=jnp.float32
    ))
    first_gain_grad = jnp.sum(dfirst * first_normed, axis=0)
    first_shift_grad = jnp.sum(dfirst, axis=0)
    input_grad = dresidual + norm_backward(dfirst, first_normed, first_inverse, first_gain)
    output_part, expand_total, input_grad = lax.optimization_barrier((output_part, expand_total, input_grad))
    weight_grads = (attention_grad, output_part, expand_total, contract_total)
    vector_grads = (first_gain_grad, first_shift_grad, query_bias_grad, value_bias_grad, output_bias_grad,
                    second_gain_grad, second_shift_grad, expand_bias_grad, contract_bias_grad)
    return (
        sent_output,
        input_grad,
        weight_grads,
        vector_grads,
    )


PAIR = [(0, 1), (1, 0)]
OUTER = ("outer", "inner")


def core_pick(core, first, second):
    return jnp.where(core == 0, first, second)


def gather_weight(shard_rows, extra=None):
    parts = lax.axis_size("shard")
    core = lax.axis_index("core")
    rows, width = shard_rows.shape
    half = rows // 2
    mine = lax.dynamic_slice_in_dim(shard_rows, core * half, half, axis=0)
    if extra is not None:
        mine = jnp.concatenate([mine, extra], axis=0)
    mine = lax.all_gather(mine, "shard", axis=0, tiled=False)
    other = lax.ppermute(mine, "core", PAIR)
    first = core_pick(core, mine, other)
    second = core_pick(core, other, mine)
    full = jnp.stack([first[:, :half], second[:, :half]], axis=1).reshape(parts * rows, width)
    if extra is None:
        return full, None
    return full, first[:, half:]


def chip_sum(grad, extra=None):
    parts = lax.axis_size("shard")
    core = lax.axis_index("core")
    width = grad.shape[1]
    rows = grad.shape[0] // parts
    half = rows // 2
    quarters = grad.reshape(parts, 2, half, width)
    keep = lax.dynamic_index_in_dim(quarters, core, axis=1, keepdims=False)
    send = lax.dynamic_index_in_dim(quarters, 1 - core, axis=1, keepdims=False)
    if extra is not None:
        on_first = (core == 0).astype(extra.dtype)
        keep = jnp.concatenate([keep, extra * on_first], axis=1)
        send = jnp.concatenate([send, extra * (1 - on_first)], axis=1)
    return keep + lax.ppermute(send, "core", PAIR)


def shard_sum(chip):
    part = lax.psum_scatter(chip, "shard", scatter_dimension=0, tiled=False)
    if lax.axis_size("inner") > 1:
        part = lax.psum(part, "inner")
    return part


def finish_sum(part, half):
    core = lax.axis_index("core")
    total = line_sum(part)
    other = lax.ppermute(total, "core", PAIR)
    first = core_pick(core, total, other)
    second = core_pick(core, other, total)
    return jnp.concatenate([first[:half], second[:half]], axis=0), first[half:]


def finish_many(parts, halves):
    core = lax.axis_index("core")
    flat = jnp.concatenate([part.reshape(-1) for part in parts])
    total = line_sum(flat)
    other = lax.ppermute(total, "core", PAIR)
    first = core_pick(core, total, other)
    second = core_pick(core, other, total)
    outs = []
    offset = 0
    for part, half in zip(parts, halves):
        size = part.size
        low = first[offset:offset + size].reshape(part.shape)
        high = second[offset:offset + size].reshape(part.shape)
        outs.append((jnp.concatenate([low[:half], high[:half]], axis=0), low[half:]))
        offset += size
    return outs


def reduce_weight(grad, extra=None):
    half = grad.shape[0] // lax.axis_size("shard") // 2
    return finish_sum(shard_sum(chip_sum(grad, extra)), half)


def line_sum(values):
    groups = lax.axis_size("outer")
    if groups == 1:
        return values
    if groups & (groups - 1):
        return lax.psum(values, "outer")
    here = lax.axis_index("outer")
    length = values.shape[0]
    padded = -(-length // groups) * groups
    held = jnp.pad(values, ((0, padded - length),) + ((0, 0),) * (values.ndim - 1))
    held = held.reshape((groups, padded // groups) + values.shape[1:])
    step = 1
    while step < groups:
        held = held.reshape((held.shape[0] // 2, 2) + held.shape[1:])
        bit = (here // step) % 2
        keep = lax.dynamic_index_in_dim(held, bit, axis=1, keepdims=False)
        send = lax.dynamic_index_in_dim(held, 1 - bit, axis=1, keepdims=False)
        held = keep + lax.ppermute(send, "outer", [(j, j ^ step) for j in range(groups)])
        step *= 2
    step = groups // 2
    while step >= 1:
        bit = (here // step) % 2
        other = lax.ppermute(held, "outer", [(j, j ^ step) for j in range(groups)])
        low = jnp.where(bit == 0, held, other)
        high = jnp.where(bit == 0, other, held)
        held = jnp.stack([low, high], axis=1)
        held = held.reshape((held.shape[0] * 2,) + held.shape[2:])
        step //= 2
    return held.reshape((padded,) + values.shape[1:])[:length]


def gather_packed(blocks, after=None):
    core = lax.axis_index("core")
    mine = lax.all_gather(jnp.concatenate(blocks, axis=0), "shard", axis=0, tiled=False)
    if after is not None:
        mine = mine + (after * 0).astype(mine.dtype)
    other = lax.ppermute(mine, "core", PAIR)
    return core_pick(core, mine, other), core_pick(core, other, mine)


def unpack_rows(first, second, begin, count, shape):
    parts = first.shape[0]
    rows, width = shape
    low = first[:, begin:begin + count].reshape(parts, -1, width)
    high = second[:, begin:begin + count].reshape(parts, -1, width)
    return jnp.stack([low, high], axis=1).reshape(rows, width)


def core_half(shard_rows):
    core = lax.axis_index("core")
    half = shard_rows.shape[0] // 2
    return lax.dynamic_slice_in_dim(shard_rows, core * half, half, axis=0)


def clip_local(tokens, lengths, cotangent, *params):
    clip_count, slot_count, width = tokens.shape
    parts = lax.axis_size("shard")
    place = lax.axis_index("shard")
    own = clip_count // parts
    weight_shards = params[:4]
    vector_shards = params[4:]
    wide = weight_shards[0].shape[1]
    vector_row = jnp.concatenate([entry.reshape(-1) for entry in vector_shards])
    pad = (-vector_row.shape[0]) % wide
    vector_rows = jnp.pad(vector_row, (0, pad)).reshape(-1, wide)
    attention_half = core_half(weight_shards[0])
    output_half = core_half(weight_shards[1]).reshape(-1, wide)
    first, second = gather_packed([attention_half, output_half, vector_rows])
    a_rows = attention_half.shape[0]
    o_rows = output_half.shape[0]
    attention_weight = unpack_rows(first, second, 0, a_rows, (parts * weight_shards[0].shape[0], wide))
    output_weight = unpack_rows(
        first, second, a_rows, o_rows, (parts * weight_shards[1].shape[0], weight_shards[1].shape[1])
    )
    vector_all = first[:, a_rows + o_rows:].reshape(parts, -1)[:, : vector_row.shape[0]]
    vectors = []
    offset = 0
    for entry in vector_shards:
        size = entry.shape[0]
        vectors.append(vector_all[:, offset:offset + size].reshape(parts * size).astype(jnp.float32))
        offset += size
    late = weight_shards[2].shape[1]
    expand_half = core_half(weight_shards[2])
    contract_half = core_half(weight_shards[3]).reshape(-1, late)

    def later_weights(after):
        first_b, second_b = gather_packed([expand_half, contract_half], after)
        e_rows = expand_half.shape[0]
        expand_weight = unpack_rows(first_b, second_b, 0, e_rows, (parts * weight_shards[2].shape[0], late))
        contract_weight = unpack_rows(
            first_b, second_b, e_rows, contract_half.shape[0],
            (parts * weight_shards[3].shape[0], weight_shards[3].shape[1]),
        )
        return expand_weight, contract_weight

    weights = (attention_weight, output_weight, later_weights)
    def exchange(rows):
        blocks = rows.reshape((parts, rows.shape[0] // parts) + rows.shape[1:])
        held = [lax.dynamic_index_in_dim(blocks, place, axis=0, keepdims=False)]
        for shift in range(1, parts):
            outgoing = lax.dynamic_index_in_dim(blocks, (place + shift) % parts, axis=0, keepdims=False)
            held.append(lax.ppermute(outgoing, "shard", [(i, (i + shift) % parts) for i in range(parts)]))
        stacked = jnp.stack(held[::-1], axis=0)
        doubled = jnp.concatenate([stacked, stacked], axis=0)
        start = (parts - (place + 1) % parts) % parts
        return lax.dynamic_slice_in_dim(doubled, start, parts, axis=0).reshape(rows.shape)

    def gather_rows(values):
        moved = exchange(values.reshape(clip_count * slot_count, width))
        moved = moved.reshape(parts, own, slot_count, width)
        return jnp.transpose(moved, (1, 0, 2, 3)).reshape(own, parts * slot_count, width) if own > 1 else moved.reshape(own, parts * slot_count, width)

    def scatter_rows(values):
        rows = values.reshape(own, parts, slot_count, width)
        if own > 1:
            rows = jnp.transpose(rows, (1, 0, 2, 3))
        moved = exchange(rows.reshape(own * parts * slot_count, width))
        return moved.reshape(clip_count, slot_count, width)

    tokens_clip = gather_rows(tokens)

    def cotangent_of(after):
        late = cotangent + (after * 0).astype(cotangent.dtype)
        return gather_rows(late)

    lengths_clip = lax.dynamic_slice_in_dim(lengths, place * own, own, axis=0)
    block_output, input_grad, weight_grads, vector_grads = clip_layer(
        tokens_clip, lengths_clip, cotangent_of, weights, vectors, lambda part, rows: finish_sum(part, rows // parts // 2)[0],
        scatter_rows,
    )
    input_grad = scatter_rows(input_grad)
    attention_grad = weight_grads[0]
    attention_width = attention_grad.shape[1]
    vector_parts = jnp.concatenate([entry.reshape(parts, -1) for entry in vector_grads], axis=1)
    vector_size = vector_parts.shape[1]
    vpad = (-vector_size) % attention_width
    vector_parts = jnp.pad(vector_parts, ((0, 0), (0, vpad))).reshape(parts, -1, attention_width)
    attention_part = shard_sum(chip_sum(attention_grad, vector_parts))
    output_part = weight_grads[1]
    (attention_total, vector_total), (output_total, _) = finish_many(
        [attention_part, output_part],
        [attention_grad.shape[0] // parts // 2, params[1].shape[0] // 2],
    )
    totals = (attention_total, output_total) + tuple(weight_grads[2:])
    vector_total = vector_total.reshape(-1)[:vector_size]
    vector_outs = []
    offset = 0
    for entry in vector_shards:
        size = entry.shape[0]
        vector_outs.append(vector_total[offset:offset + size])
        offset += size
    return (block_output, input_grad) + totals + tuple(vector_outs)


def split_rep(mesh):
    devices = mesh.devices
    rep, parts = devices.shape
    first = devices[0, 0]
    stride = None
    for index in range(1, rep):
        other = devices[index, 0]
        if tuple(other.coords) == tuple(first.coords) and other.core_on_chip != first.core_on_chip:
            stride = index
            break
    if stride is None or rep % (2 * stride):
        return None
    grid = devices.reshape(rep // (2 * stride), 2, stride, parts)
    for spot in np.ndindex(grid.shape[0], grid.shape[2], grid.shape[3]):
        low = grid[spot[0], 0, spot[1], spot[2]]
        high = grid[spot[0], 1, spot[1], spot[2]]
        if tuple(low.coords) != tuple(high.coords) or low.core_on_chip == high.core_on_chip:
            return None
    return Mesh(grid, ("outer", "core", "inner", "shard"))


def solution(mesh):
    def specs(rep):
        ins = (P(rep, "shard", None), P(rep, None), P(rep, "shard", None)) + (P("shard", None),) * 4 + (
            P("shard"),
        ) * 9
        outs = (P(rep, "shard", None), P(rep, "shard", None)) + (P("shard", None),) * 4 + (P("shard"),) * 9
        return ins, outs

    ins, outs = specs("rep")
    plain = jax.shard_map(local, mesh=mesh, in_specs=ins, out_specs=outs, check_vma=False)
    split = split_rep(mesh)
    if split is None:
        return plain
    ins, outs = specs(("outer", "core", "inner"))
    fast = jax.shard_map(clip_local, mesh=split, in_specs=ins, out_specs=outs, check_vma=False)
    rep, parts = mesh.devices.shape

    def run(*args):
        if (args[0].shape[0] // rep) % parts == 0:
            return fast(*args)
        return plain(*args)

    return run
```

```python
import jax
import jax.numpy as jnp
from jax import lax
from jax.sharding import Mesh, PartitionSpec as P
import numpy as np

HEADS = 12
HEAD = 64


EPSILON = 1e-05
NEGATIVE = -1e30


def norm_forward(values, gain, shift):
    centred = values - jnp.mean(values, axis=-1, keepdims=True)
    inverse = lax.rsqrt(jnp.mean(centred * centred, axis=-1, keepdims=True) + EPSILON)
    normed = centred * inverse
    return (normed, inverse, (normed * gain + shift).astype(jnp.bfloat16))


def norm_backward(upstream, normed, inverse, gain):
    scaled = upstream * gain
    return inverse * (
        scaled
        - jnp.mean(scaled, axis=-1, keepdims=True)
        - normed * jnp.mean(scaled * normed, axis=-1, keepdims=True)
    )


def gelu_slope(values):
    return (
        0.5 * (1.0 + jax.scipy.special.erf(values * 0.7071067811865476))
        + values * jnp.exp(-0.5 * values * values) * 0.3989422804014327
    )


def inner_rows(left, right):
    return lax.dot_general(
        left, right, (((0,), (0,)), ((), ())), preferred_element_type=jnp.float32
    )


def heads_view(matrix):
    return matrix.reshape(matrix.shape[0], HEADS, HEAD)


def score_block(query_rows, key_rows, key_live):
    scores = jnp.einsum(
        "qhd,khd->hqk",
        heads_view(query_rows),
        heads_view(key_rows),
        preferred_element_type=jnp.float32,
    ) * HEAD ** (-0.5)
    return jnp.where(key_live[None, None, :], scores, NEGATIVE)


def attend_clip(items):
    query_rows, pair_rows, key_live = items
    width = query_rows.shape[1]
    scores = score_block(query_rows, pair_rows[:, :width], key_live)
    highest = jnp.max(scores, axis=-1, keepdims=True)
    logsum = highest + jnp.log(jnp.sum(jnp.exp(scores - highest), axis=-1, keepdims=True))
    probs_low = jnp.exp(scores - logsum).astype(jnp.bfloat16)
    attended = jnp.einsum(
        "hqk,khd->qhd",
        probs_low,
        heads_view(pair_rows[:, width:]),
        preferred_element_type=jnp.float32,
    )
    return (attended.reshape(query_rows.shape[0], width).astype(jnp.bfloat16), logsum[:, :, 0].T)


def score_grads(query_rows, dattended, logsum, delta, pair_rows, key_live):
    width = query_rows.shape[1]
    scores = score_block(query_rows, pair_rows[:, :width], key_live)
    probs = jnp.exp(scores - logsum.T[:, :, None])
    dprob = jnp.einsum(
        "qhd,khd->hqk",
        heads_view(dattended),
        heads_view(pair_rows[:, width:]),
        preferred_element_type=jnp.float32,
    )
    dscore = (probs * (dprob - delta.T[:, :, None]) * HEAD ** (-0.5)).astype(jnp.bfloat16)
    return (probs.astype(jnp.bfloat16), dscore)


def both_grads(items):
    query_rows, dattended, logsum, delta, pair_rows, key_live = items
    width = query_rows.shape[1]
    probs_low, dscore = score_grads(query_rows, dattended, logsum, delta, pair_rows, key_live)
    dqueries = jnp.einsum(
        "hqk,khd->qhd", dscore, heads_view(pair_rows[:, :width]), preferred_element_type=jnp.float32
    ).reshape(query_rows.shape[0], width)
    dkeys = jnp.einsum(
        "hqk,qhd->khd", dscore, heads_view(query_rows), preferred_element_type=jnp.float32
    )
    dvalues = jnp.einsum(
        "hqk,qhd->khd", probs_low, heads_view(dattended), preferred_element_type=jnp.float32
    )
    key_count = pair_rows.shape[0]
    return (
        dqueries,
        jnp.concatenate(
            [dkeys.reshape(key_count, width), dvalues.reshape(key_count, width)], axis=1
        ),
    )


def local(
    tokens,
    lengths,
    cotangent,
    attention_weight,
    output_weight,
    expand_weight,
    contract_weight,
    first_gain,
    first_shift,
    query_bias,
    value_bias,
    output_bias,
    second_gain,
    second_shift,
    expand_bias,
    contract_bias,
):
    clip_count, slot_count, width = tokens.shape
    parts = lax.axis_size("shard")
    frame_count = slot_count * parts
    place = lax.axis_index("shard")
    row_total = clip_count * slot_count
    gathered = (
        lax.all_gather(attention_weight, "shard", axis=0, tiled=True),
        lax.all_gather(output_weight, "shard", axis=0, tiled=True),
        lax.all_gather(expand_weight, "shard", axis=0, tiled=True),
        lax.all_gather(contract_weight, "shard", axis=0, tiled=True),
        lax.all_gather(first_gain, "shard", axis=0, tiled=True),
        lax.all_gather(first_shift, "shard", axis=0, tiled=True),
        lax.all_gather(query_bias, "shard", axis=0, tiled=True),
        lax.all_gather(value_bias, "shard", axis=0, tiled=True),
        lax.all_gather(output_bias, "shard", axis=0, tiled=True),
        lax.all_gather(second_gain, "shard", axis=0, tiled=True),
        lax.all_gather(second_shift, "shard", axis=0, tiled=True),
        lax.all_gather(expand_bias, "shard", axis=0, tiled=True),
        lax.all_gather(contract_bias, "shard", axis=0, tiled=True),
    )
    vectors = [entry.astype(jnp.float32) for entry in gathered[4:]]
    own_length = jnp.sum(jnp.where(jnp.arange(parts)[None, :] == place, lengths, 0), axis=1)
    row_live = jnp.arange(slot_count)[None, :] < own_length[:, None]
    key_live = (jnp.arange(slot_count)[None, None, :] < lengths[:, :, None]).reshape(
        clip_count, frame_count
    )
    inputs = tokens.reshape(row_total, width).astype(jnp.float32)
    first_normed, first_inverse, first_act = norm_forward(inputs, vectors[0], vectors[1])
    mixed = jnp.dot(first_act, gathered[0], preferred_element_type=jnp.float32)
    mixed = mixed + jnp.concatenate([vectors[2], jnp.zeros_like(vectors[2]), vectors[3]])
    mixed_low = mixed.astype(jnp.bfloat16)
    query_rows = mixed_low[:, :width].reshape(clip_count, slot_count, width)
    pair_own = mixed_low[:, width:].reshape(clip_count, slot_count, 2 * width)
    pair_all = lax.all_gather(pair_own, "shard", axis=1, tiled=True)
    attended, logsum = lax.map(attend_clip, (query_rows, pair_all, key_live))
    attended_flat = attended.reshape(row_total, width)
    residual = (
        inputs
        + jnp.dot(attended_flat, gathered[1], preferred_element_type=jnp.float32)
        + vectors[4]
    )
    second_normed, second_inverse, second_act = norm_forward(residual, vectors[5], vectors[6])
    pre = jnp.dot(second_act, gathered[2], preferred_element_type=jnp.float32) + vectors[7]
    hidden_act = jax.nn.gelu(pre, approximate=False).astype(jnp.bfloat16)
    block_output = (
        residual + jnp.dot(hidden_act, gathered[3], preferred_element_type=jnp.float32) + vectors[8]
    )
    backward = (
        lax.all_gather(attention_weight, "shard", axis=0, tiled=True),
        lax.all_gather(output_weight, "shard", axis=0, tiled=True),
        lax.all_gather(expand_weight, "shard", axis=0, tiled=True),
        lax.all_gather(contract_weight, "shard", axis=0, tiled=True),
        lax.all_gather(first_gain, "shard", axis=0, tiled=True),
        lax.all_gather(first_shift, "shard", axis=0, tiled=True),
        lax.all_gather(query_bias, "shard", axis=0, tiled=True),
        lax.all_gather(value_bias, "shard", axis=0, tiled=True),
        lax.all_gather(output_bias, "shard", axis=0, tiled=True),
        lax.all_gather(second_gain, "shard", axis=0, tiled=True),
        lax.all_gather(second_shift, "shard", axis=0, tiled=True),
        lax.all_gather(expand_bias, "shard", axis=0, tiled=True),
        lax.all_gather(contract_bias, "shard", axis=0, tiled=True),
    )
    back_vectors = [entry.astype(jnp.float32) for entry in backward[4:]]
    error = cotangent.reshape(row_total, width) * row_live.reshape(row_total, 1).astype(jnp.float32)
    error_low = error.astype(jnp.bfloat16)
    contract_bias_grad = jnp.sum(error, axis=0)
    contract_grad = inner_rows(hidden_act, error_low)
    dpre = lax.dot_general(
        error_low, backward[3], (((1,), (1,)), ((), ())), preferred_element_type=jnp.float32
    ) * gelu_slope(pre)
    expand_bias_grad = jnp.sum(dpre, axis=0)
    dpre_low = dpre.astype(jnp.bfloat16)
    expand_grad = inner_rows(second_act, dpre_low)
    dsecond = lax.dot_general(
        dpre_low, backward[2], (((1,), (1,)), ((), ())), preferred_element_type=jnp.float32
    )
    second_gain_grad = jnp.sum(dsecond * second_normed, axis=0)
    second_shift_grad = jnp.sum(dsecond, axis=0)
    dresidual = error + norm_backward(dsecond, second_normed, second_inverse, back_vectors[5])
    output_bias_grad = jnp.sum(dresidual, axis=0)
    dresidual_low = dresidual.astype(jnp.bfloat16)
    output_grad = inner_rows(attended_flat, dresidual_low)
    dattended = lax.dot_general(
        dresidual_low, backward[1], (((1,), (1,)), ((), ())), preferred_element_type=jnp.float32
    ).astype(jnp.bfloat16)
    delta = jnp.sum(
        heads_view(dattended.astype(jnp.float32)) * heads_view(attended_flat.astype(jnp.float32)),
        axis=-1,
    )
    delta = delta.reshape(clip_count, slot_count, HEADS)
    dattended_clips = dattended.reshape(clip_count, slot_count, width)
    dqueries, pair_terms = lax.map(
        both_grads, (query_rows, dattended_clips, logsum, delta, pair_all, key_live)
    )
    pair_grads = lax.psum_scatter(pair_terms, "shard", scatter_dimension=1, tiled=True)
    dqueries_flat = dqueries.reshape(row_total, width)
    pair_flat = pair_grads.reshape(row_total, 2 * width)
    dmixed = jnp.concatenate([dqueries_flat, pair_flat], axis=1)
    query_bias_grad = jnp.sum(dqueries_flat, axis=0)
    value_bias_grad = jnp.sum(pair_flat[:, width:], axis=0)
    dmixed_low = dmixed.astype(jnp.bfloat16)
    attention_grad = inner_rows(first_act, dmixed_low)
    dfirst = lax.dot_general(
        dmixed_low, backward[0], (((1,), (1,)), ((), ())), preferred_element_type=jnp.float32
    )
    first_gain_grad = jnp.sum(dfirst * first_normed, axis=0)
    first_shift_grad = jnp.sum(dfirst, axis=0)
    input_grad = dresidual + norm_backward(dfirst, first_normed, first_inverse, back_vectors[0])
    shares = (
        lax.psum_scatter(attention_grad, "shard", scatter_dimension=0, tiled=True),
        lax.psum_scatter(output_grad, "shard", scatter_dimension=0, tiled=True),
        lax.psum_scatter(expand_grad, "shard", scatter_dimension=0, tiled=True),
        lax.psum_scatter(contract_grad, "shard", scatter_dimension=0, tiled=True),
        lax.psum_scatter(first_gain_grad, "shard", scatter_dimension=0, tiled=True),
        lax.psum_scatter(first_shift_grad, "shard", scatter_dimension=0, tiled=True),
        lax.psum_scatter(query_bias_grad, "shard", scatter_dimension=0, tiled=True),
        lax.psum_scatter(value_bias_grad, "shard", scatter_dimension=0, tiled=True),
        lax.psum_scatter(output_bias_grad, "shard", scatter_dimension=0, tiled=True),
        lax.psum_scatter(second_gain_grad, "shard", scatter_dimension=0, tiled=True),
        lax.psum_scatter(second_shift_grad, "shard", scatter_dimension=0, tiled=True),
        lax.psum_scatter(expand_bias_grad, "shard", scatter_dimension=0, tiled=True),
        lax.psum_scatter(contract_bias_grad, "shard", scatter_dimension=0, tiled=True),
    )
    totals = lax.psum(
        (
            shares[0],
            shares[1],
            shares[2],
            shares[3],
            shares[4],
            shares[5],
            shares[6],
            shares[7],
            shares[8],
            shares[9],
            shares[10],
            shares[11],
            shares[12],
        ),
        "rep",
    )
    return (
        block_output.reshape(clip_count, slot_count, width),
        input_grad.reshape(clip_count, slot_count, width),
        totals[0],
        totals[1],
        totals[2],
        totals[3],
        totals[4],
        totals[5],
        totals[6],
        totals[7],
        totals[8],
        totals[9],
        totals[10],
        totals[11],
        totals[12],
    )


def clip_layer(tokens, lengths, cotangent_of, weights, vectors, reduce, send_out):
    attention_weight, output_weight, later_weights = weights
    (first_gain, first_shift, query_bias, value_bias, output_bias, second_gain, second_shift,
     expand_bias, contract_bias) = vectors
    clip_count, frame_count, width = tokens.shape
    block_count = lengths.shape[1]
    slot_count = frame_count // block_count
    rows = clip_count * frame_count
    live = (jnp.arange(slot_count)[None, None, :] < lengths[:, :, None]).reshape(clip_count, frame_count)
    scale = HEAD ** (-0.5)
    inputs = tokens.reshape(rows, width).astype(jnp.float32)
    first_normed, first_inverse, first_act = norm_forward(inputs, first_gain, first_shift)
    mixed = jnp.dot(first_act, attention_weight, preferred_element_type=jnp.float32)
    mixed = mixed + jnp.concatenate([query_bias, jnp.zeros_like(query_bias), value_bias])
    mixed_low = mixed.astype(jnp.bfloat16).reshape(clip_count, frame_count, 3, HEADS, HEAD)
    expand_weight, contract_weight = later_weights(mixed_low[0, 0, 0, 0, :1])
    queries = mixed_low[:, :, 0]
    keys = mixed_low[:, :, 1]
    values = mixed_low[:, :, 2]
    scores = jnp.einsum("cqhd,ckhd->chqk", queries, keys, preferred_element_type=jnp.float32) * scale
    scores = jnp.where(live[:, None, None, :], scores, NEGATIVE)
    highest = jnp.max(scores, axis=-1, keepdims=True)
    logsum = highest + jnp.log(jnp.sum(jnp.exp(scores - highest), axis=-1, keepdims=True))
    probs = jnp.exp(scores - logsum)
    probs_low = probs.astype(jnp.bfloat16)
    attended = jnp.einsum("chqk,ckhd->cqhd", probs_low, values, preferred_element_type=jnp.float32)
    attended_flat = attended.reshape(rows, width).astype(jnp.bfloat16)
    residual = inputs + jnp.dot(attended_flat, output_weight, preferred_element_type=jnp.float32) + output_bias
    second_normed, second_inverse, second_act = norm_forward(residual, second_gain, second_shift)
    pre = jnp.dot(second_act, expand_weight, preferred_element_type=jnp.float32) + expand_bias
    hidden_act = jax.nn.gelu(pre, approximate=False).astype(jnp.bfloat16)
    block_output = residual + jnp.dot(hidden_act, contract_weight, preferred_element_type=jnp.float32) + contract_bias
    cotangent = cotangent_of(pre[0, :1])
    error = cotangent.reshape(rows, width) * live.reshape(rows, 1).astype(jnp.float32)
    error_low = error.astype(jnp.bfloat16)
    contract_bias_grad = jnp.sum(error, axis=0)
    contract_grad = inner_rows(hidden_act, error_low)
    contract_chip = chip_sum(contract_grad)
    dpre = lax.dot_general(
        error_low, contract_weight, (((1,), (1,)), ((), ())), preferred_element_type=jnp.float32
    ) * gelu_slope(pre)
    expand_bias_grad = jnp.sum(dpre, axis=0)
    dpre_low = dpre.astype(jnp.bfloat16)
    contract_chip, dpre_low = lax.optimization_barrier((contract_chip, dpre_low))
    contract_part = shard_sum(contract_chip)
    expand_grad = inner_rows(second_act, dpre_low)
    expand_chip = chip_sum(expand_grad)
    dsecond = lax.dot_general(
        dpre_low, expand_weight, (((1,), (1,)), ((), ())), preferred_element_type=jnp.float32
    )
    second_gain_grad = jnp.sum(dsecond * second_normed, axis=0)
    second_shift_grad = jnp.sum(dsecond, axis=0)
    dresidual = error + norm_backward(dsecond, second_normed, second_inverse, second_gain)
    output_bias_grad = jnp.sum(dresidual, axis=0)
    dresidual_low = dresidual.astype(jnp.bfloat16)
    sent_output = send_out(block_output)
    expand_chip, dresidual_low = lax.optimization_barrier((expand_chip, dresidual_low))
    expand_part = shard_sum(expand_chip)
    output_grad = inner_rows(attended_flat, dresidual_low)
    output_chip = chip_sum(output_grad)
    dattended = lax.dot_general(
        dresidual_low, output_weight, (((1,), (1,)), ((), ())), preferred_element_type=jnp.float32
    ).astype(jnp.bfloat16)
    contract_part, dattended = lax.optimization_barrier((contract_part, dattended))
    dattended_heads = dattended.reshape(clip_count, frame_count, HEADS, HEAD)
    attended_heads = attended_flat.reshape(clip_count, frame_count, HEADS, HEAD)
    delta = jnp.sum(
        dattended_heads.astype(jnp.float32) * attended_heads.astype(jnp.float32), axis=-1
    )
    dprob = jnp.einsum("cqhd,ckhd->chqk", dattended_heads, values, preferred_element_type=jnp.float32)
    dscore = (probs * (dprob - jnp.transpose(delta, (0, 2, 1))[:, :, :, None]) * scale).astype(jnp.bfloat16)
    dqueries = jnp.einsum("chqk,ckhd->cqhd", dscore, keys, preferred_element_type=jnp.float32)
    dkeys = jnp.einsum("chqk,cqhd->ckhd", dscore, queries, preferred_element_type=jnp.float32)
    dvalues = jnp.einsum("chqk,cqhd->ckhd", probs_low, dattended_heads, preferred_element_type=jnp.float32)
    dmixed = jnp.concatenate(
        [dqueries.reshape(rows, width), dkeys.reshape(rows, width), dvalues.reshape(rows, width)], axis=1
    )
    query_bias_grad = jnp.sum(dmixed[:, :width], axis=0)
    value_bias_grad = jnp.sum(dmixed[:, 2 * width:], axis=0)
    dmixed_low = dmixed.astype(jnp.bfloat16)
    contract_total = reduce(contract_part, contract_grad.shape[0])
    output_chip, expand_part, contract_total, sent_output, dmixed_low = lax.optimization_barrier(
        (output_chip, expand_part, contract_total, sent_output, dmixed_low)
    )
    output_part = shard_sum(output_chip)
    expand_total = reduce(expand_part, expand_grad.shape[0])
    attention_grad = inner_rows(first_act, dmixed_low)
    dfirst = lax.optimization_barrier(lax.dot_general(
        dmixed_low, attention_weight, (((1,), (1,)), ((), ())), preferred_element_type=jnp.float32
    ))
    first_gain_grad = jnp.sum(dfirst * first_normed, axis=0)
    first_shift_grad = jnp.sum(dfirst, axis=0)
    input_grad = dresidual + norm_backward(dfirst, first_normed, first_inverse, first_gain)
    output_part, expand_total, input_grad = lax.optimization_barrier((output_part, expand_total, input_grad))
    weight_grads = (attention_grad, output_part, expand_total, contract_total)
    vector_grads = (first_gain_grad, first_shift_grad, query_bias_grad, value_bias_grad, output_bias_grad,
                    second_gain_grad, second_shift_grad, expand_bias_grad, contract_bias_grad)
    return (
        sent_output,
        input_grad,
        weight_grads,
        vector_grads,
    )


PAIR = [(0, 1), (1, 0)]
OUTER = ("outer", "inner")


def core_pick(core, first, second):
    return jnp.where(core == 0, first, second)


def gather_weight(shard_rows, extra=None):
    parts = lax.axis_size("shard")
    core = lax.axis_index("core")
    rows, width = shard_rows.shape
    half = rows // 2
    mine = lax.dynamic_slice_in_dim(shard_rows, core * half, half, axis=0)
    if extra is not None:
        mine = jnp.concatenate([mine, extra], axis=0)
    mine = lax.all_gather(mine, "shard", axis=0, tiled=False)
    other = lax.ppermute(mine, "core", PAIR)
    first = core_pick(core, mine, other)
    second = core_pick(core, other, mine)
    full = jnp.stack([first[:, :half], second[:, :half]], axis=1).reshape(parts * rows, width)
    if extra is None:
        return full, None
    return full, first[:, half:]


def chip_sum(grad, extra=None):
    parts = lax.axis_size("shard")
    core = lax.axis_index("core")
    width = grad.shape[1]
    rows = grad.shape[0] // parts
    half = rows // 2
    quarters = grad.reshape(parts, 2, half, width)
    keep = lax.dynamic_index_in_dim(quarters, core, axis=1, keepdims=False)
    send = lax.dynamic_index_in_dim(quarters, 1 - core, axis=1, keepdims=False)
    if extra is not None:
        on_first = (core == 0).astype(extra.dtype)
        keep = jnp.concatenate([keep, extra * on_first], axis=1)
        send = jnp.concatenate([send, extra * (1 - on_first)], axis=1)
    return keep + lax.ppermute(send, "core", PAIR)


def shard_sum(chip):
    part = lax.psum_scatter(chip, "shard", scatter_dimension=0, tiled=False)
    if lax.axis_size("inner") > 1:
        part = lax.psum(part, "inner")
    return part


def finish_sum(part, half):
    core = lax.axis_index("core")
    total = line_sum(part)
    other = lax.ppermute(total, "core", PAIR)
    first = core_pick(core, total, other)
    second = core_pick(core, other, total)
    return jnp.concatenate([first[:half], second[:half]], axis=0), first[half:]


def finish_many(parts, halves):
    core = lax.axis_index("core")
    flat = jnp.concatenate([part.reshape(-1) for part in parts])
    total = line_sum(flat)
    other = lax.ppermute(total, "core", PAIR)
    first = core_pick(core, total, other)
    second = core_pick(core, other, total)
    outs = []
    offset = 0
    for part, half in zip(parts, halves):
        size = part.size
        low = first[offset:offset + size].reshape(part.shape)
        high = second[offset:offset + size].reshape(part.shape)
        outs.append((jnp.concatenate([low[:half], high[:half]], axis=0), low[half:]))
        offset += size
    return outs


def reduce_weight(grad, extra=None):
    half = grad.shape[0] // lax.axis_size("shard") // 2
    return finish_sum(shard_sum(chip_sum(grad, extra)), half)


def line_sum(values):
    groups = lax.axis_size("outer")
    if groups == 1:
        return values
    if groups & (groups - 1):
        return lax.psum(values, "outer")
    here = lax.axis_index("outer")
    length = values.shape[0]
    padded = -(-length // groups) * groups
    held = jnp.pad(values, ((0, padded - length),) + ((0, 0),) * (values.ndim - 1))
    held = held.reshape((groups, padded // groups) + values.shape[1:])
    step = 1
    while step < groups:
        held = held.reshape((held.shape[0] // 2, 2) + held.shape[1:])
        bit = (here // step) % 2
        keep = lax.dynamic_index_in_dim(held, bit, axis=1, keepdims=False)
        send = lax.dynamic_index_in_dim(held, 1 - bit, axis=1, keepdims=False)
        held = keep + lax.ppermute(send, "outer", [(j, j ^ step) for j in range(groups)])
        step *= 2
    step = groups // 2
    while step >= 1:
        bit = (here // step) % 2
        other = lax.ppermute(held, "outer", [(j, j ^ step) for j in range(groups)])
        low = jnp.where(bit == 0, held, other)
        high = jnp.where(bit == 0, other, held)
        held = jnp.stack([low, high], axis=1)
        held = held.reshape((held.shape[0] * 2,) + held.shape[2:])
        step //= 2
    return held.reshape((padded,) + values.shape[1:])[:length]


def gather_packed(blocks, after=None):
    core = lax.axis_index("core")
    mine = lax.all_gather(jnp.concatenate(blocks, axis=0), "shard", axis=0, tiled=False)
    if after is not None:
        mine = mine + (after * 0).astype(mine.dtype)
    other = lax.ppermute(mine, "core", PAIR)
    return core_pick(core, mine, other), core_pick(core, other, mine)


def unpack_rows(first, second, begin, count, shape):
    parts = first.shape[0]
    rows, width = shape
    low = first[:, begin:begin + count].reshape(parts, -1, width)
    high = second[:, begin:begin + count].reshape(parts, -1, width)
    return jnp.stack([low, high], axis=1).reshape(rows, width)


def core_half(shard_rows):
    core = lax.axis_index("core")
    half = shard_rows.shape[0] // 2
    return lax.dynamic_slice_in_dim(shard_rows, core * half, half, axis=0)


def clip_local(tokens, lengths, cotangent, *params):
    clip_count, slot_count, width = tokens.shape
    parts = lax.axis_size("shard")
    place = lax.axis_index("shard")
    own = clip_count // parts
    weight_shards = params[:4]
    vector_shards = params[4:]
    wide = weight_shards[0].shape[1]
    vector_row = jnp.concatenate([entry.reshape(-1) for entry in vector_shards])
    pad = (-vector_row.shape[0]) % wide
    vector_rows = jnp.pad(vector_row, (0, pad)).reshape(-1, wide)
    attention_half = core_half(weight_shards[0])
    output_half = core_half(weight_shards[1]).reshape(-1, wide)
    first, second = gather_packed([attention_half, output_half, vector_rows])
    a_rows = attention_half.shape[0]
    o_rows = output_half.shape[0]
    attention_weight = unpack_rows(first, second, 0, a_rows, (parts * weight_shards[0].shape[0], wide))
    output_weight = unpack_rows(
        first, second, a_rows, o_rows, (parts * weight_shards[1].shape[0], weight_shards[1].shape[1])
    )
    vector_all = first[:, a_rows + o_rows:].reshape(parts, -1)[:, : vector_row.shape[0]]
    vectors = []
    offset = 0
    for entry in vector_shards:
        size = entry.shape[0]
        vectors.append(vector_all[:, offset:offset + size].reshape(parts * size).astype(jnp.float32))
        offset += size
    late = weight_shards[2].shape[1]
    expand_half = core_half(weight_shards[2])
    contract_half = core_half(weight_shards[3]).reshape(-1, late)

    def later_weights(after):
        first_b, second_b = gather_packed([expand_half, contract_half], after)
        e_rows = expand_half.shape[0]
        expand_weight = unpack_rows(first_b, second_b, 0, e_rows, (parts * weight_shards[2].shape[0], late))
        contract_weight = unpack_rows(
            first_b, second_b, e_rows, contract_half.shape[0],
            (parts * weight_shards[3].shape[0], weight_shards[3].shape[1]),
        )
        return expand_weight, contract_weight

    weights = (attention_weight, output_weight, later_weights)
    def exchange(rows):
        blocks = rows.reshape((parts, rows.shape[0] // parts) + rows.shape[1:])
        held = [lax.dynamic_index_in_dim(blocks, place, axis=0, keepdims=False)]
        for shift in range(1, parts):
            outgoing = lax.dynamic_index_in_dim(blocks, (place + shift) % parts, axis=0, keepdims=False)
            held.append(lax.ppermute(outgoing, "shard", [(i, (i + shift) % parts) for i in range(parts)]))
        stacked = jnp.stack(held[::-1], axis=0)
        doubled = jnp.concatenate([stacked, stacked], axis=0)
        start = (parts - (place + 1) % parts) % parts
        return lax.dynamic_slice_in_dim(doubled, start, parts, axis=0).reshape(rows.shape)

    def gather_rows(values, early=False):
        flat = values.reshape(clip_count * slot_count, width)
        moved = exchange(flat) if early else lax.all_to_all(flat, "shard", 0, 0, tiled=True)
        moved = moved.reshape(parts, own, slot_count, width)
        return jnp.transpose(moved, (1, 0, 2, 3)).reshape(own, parts * slot_count, width) if own > 1 else moved.reshape(own, parts * slot_count, width)

    def scatter_rows(values):
        rows = values.reshape(own, parts, slot_count, width)
        if own > 1:
            rows = jnp.transpose(rows, (1, 0, 2, 3))
        moved = lax.all_to_all(rows.reshape(own * parts * slot_count, width), "shard", 0, 0, tiled=True)
        return moved.reshape(clip_count, slot_count, width)

    tokens_clip = gather_rows(tokens, True)

    def cotangent_of(after):
        late = cotangent + (after * 0).astype(cotangent.dtype)
        return gather_rows(late)

    lengths_clip = lax.dynamic_slice_in_dim(lengths, place * own, own, axis=0)
    block_output, input_grad, weight_grads, vector_grads = clip_layer(
        tokens_clip, lengths_clip, cotangent_of, weights, vectors, lambda part, rows: finish_sum(part, rows // parts // 2)[0],
        scatter_rows,
    )
    input_grad = scatter_rows(input_grad)
    attention_grad = weight_grads[0]
    attention_width = attention_grad.shape[1]
    vector_parts = jnp.concatenate([entry.reshape(parts, -1) for entry in vector_grads], axis=1)
    vector_size = vector_parts.shape[1]
    vpad = (-vector_size) % attention_width
    vector_parts = jnp.pad(vector_parts, ((0, 0), (0, vpad))).reshape(parts, -1, attention_width)
    attention_part = shard_sum(chip_sum(attention_grad, vector_parts))
    output_part = weight_grads[1]
    (attention_total, vector_total), (output_total, _) = finish_many(
        [attention_part, output_part],
        [attention_grad.shape[0] // parts // 2, params[1].shape[0] // 2],
    )
    totals = (attention_total, output_total) + tuple(weight_grads[2:])
    vector_total = vector_total.reshape(-1)[:vector_size]
    vector_outs = []
    offset = 0
    for entry in vector_shards:
        size = entry.shape[0]
        vector_outs.append(vector_total[offset:offset + size])
        offset += size
    return (block_output, input_grad) + totals + tuple(vector_outs)


def split_rep(mesh):
    devices = mesh.devices
    rep, parts = devices.shape
    first = devices[0, 0]
    stride = None
    for index in range(1, rep):
        other = devices[index, 0]
        if tuple(other.coords) == tuple(first.coords) and other.core_on_chip != first.core_on_chip:
            stride = index
            break
    if stride is None or rep % (2 * stride):
        return None
    grid = devices.reshape(rep // (2 * stride), 2, stride, parts)
    for spot in np.ndindex(grid.shape[0], grid.shape[2], grid.shape[3]):
        low = grid[spot[0], 0, spot[1], spot[2]]
        high = grid[spot[0], 1, spot[1], spot[2]]
        if tuple(low.coords) != tuple(high.coords) or low.core_on_chip == high.core_on_chip:
            return None
    return Mesh(grid, ("outer", "core", "inner", "shard"))


def solution(mesh):
    def specs(rep):
        ins = (P(rep, "shard", None), P(rep, None), P(rep, "shard", None)) + (P("shard", None),) * 4 + (
            P("shard"),
        ) * 9
        outs = (P(rep, "shard", None), P(rep, "shard", None)) + (P("shard", None),) * 4 + (P("shard"),) * 9
        return ins, outs

    ins, outs = specs("rep")
    plain = jax.shard_map(local, mesh=mesh, in_specs=ins, out_specs=outs, check_vma=False)
    split = split_rep(mesh)
    if split is None:
        return plain
    ins, outs = specs(("outer", "core", "inner"))
    fast = jax.shard_map(clip_local, mesh=split, in_specs=ins, out_specs=outs, check_vma=False)
    rep, parts = mesh.devices.shape

    def run(*args):
        if (args[0].shape[0] // rep) % parts == 0:
            return fast(*args)
        return plain(*args)

    return run
```

```python
import jax
import jax.numpy as jnp
from jax import lax
from jax.sharding import Mesh, PartitionSpec as P
import numpy as np

HEADS = 12
HEAD = 64


EPSILON = 1e-05
NEGATIVE = -1e30


def norm_forward(values, gain, shift):
    centred = values - jnp.mean(values, axis=-1, keepdims=True)
    inverse = lax.rsqrt(jnp.mean(centred * centred, axis=-1, keepdims=True) + EPSILON)
    normed = centred * inverse
    return (normed, inverse, (normed * gain + shift).astype(jnp.bfloat16))


def norm_backward(upstream, normed, inverse, gain):
    scaled = upstream * gain
    return inverse * (
        scaled
        - jnp.mean(scaled, axis=-1, keepdims=True)
        - normed * jnp.mean(scaled * normed, axis=-1, keepdims=True)
    )


def gelu_slope(values):
    return (
        0.5 * (1.0 + jax.scipy.special.erf(values * 0.7071067811865476))
        + values * jnp.exp(-0.5 * values * values) * 0.3989422804014327
    )


def inner_rows(left, right):
    return lax.dot_general(
        left, right, (((0,), (0,)), ((), ())), preferred_element_type=jnp.float32
    )


def heads_view(matrix):
    return matrix.reshape(matrix.shape[0], HEADS, HEAD)


def score_block(query_rows, key_rows, key_live):
    scores = jnp.einsum(
        "qhd,khd->hqk",
        heads_view(query_rows),
        heads_view(key_rows),
        preferred_element_type=jnp.float32,
    ) * HEAD ** (-0.5)
    return jnp.where(key_live[None, None, :], scores, NEGATIVE)


def attend_clip(items):
    query_rows, pair_rows, key_live = items
    width = query_rows.shape[1]
    scores = score_block(query_rows, pair_rows[:, :width], key_live)
    highest = jnp.max(scores, axis=-1, keepdims=True)
    logsum = highest + jnp.log(jnp.sum(jnp.exp(scores - highest), axis=-1, keepdims=True))
    probs_low = jnp.exp(scores - logsum).astype(jnp.bfloat16)
    attended = jnp.einsum(
        "hqk,khd->qhd",
        probs_low,
        heads_view(pair_rows[:, width:]),
        preferred_element_type=jnp.float32,
    )
    return (attended.reshape(query_rows.shape[0], width).astype(jnp.bfloat16), logsum[:, :, 0].T)


def score_grads(query_rows, dattended, logsum, delta, pair_rows, key_live):
    width = query_rows.shape[1]
    scores = score_block(query_rows, pair_rows[:, :width], key_live)
    probs = jnp.exp(scores - logsum.T[:, :, None])
    dprob = jnp.einsum(
        "qhd,khd->hqk",
        heads_view(dattended),
        heads_view(pair_rows[:, width:]),
        preferred_element_type=jnp.float32,
    )
    dscore = (probs * (dprob - delta.T[:, :, None]) * HEAD ** (-0.5)).astype(jnp.bfloat16)
    return (probs.astype(jnp.bfloat16), dscore)


def both_grads(items):
    query_rows, dattended, logsum, delta, pair_rows, key_live = items
    width = query_rows.shape[1]
    probs_low, dscore = score_grads(query_rows, dattended, logsum, delta, pair_rows, key_live)
    dqueries = jnp.einsum(
        "hqk,khd->qhd", dscore, heads_view(pair_rows[:, :width]), preferred_element_type=jnp.float32
    ).reshape(query_rows.shape[0], width)
    dkeys = jnp.einsum(
        "hqk,qhd->khd", dscore, heads_view(query_rows), preferred_element_type=jnp.float32
    )
    dvalues = jnp.einsum(
        "hqk,qhd->khd", probs_low, heads_view(dattended), preferred_element_type=jnp.float32
    )
    key_count = pair_rows.shape[0]
    return (
        dqueries,
        jnp.concatenate(
            [dkeys.reshape(key_count, width), dvalues.reshape(key_count, width)], axis=1
        ),
    )


def local(
    tokens,
    lengths,
    cotangent,
    attention_weight,
    output_weight,
    expand_weight,
    contract_weight,
    first_gain,
    first_shift,
    query_bias,
    value_bias,
    output_bias,
    second_gain,
    second_shift,
    expand_bias,
    contract_bias,
):
    clip_count, slot_count, width = tokens.shape
    parts = lax.axis_size("shard")
    frame_count = slot_count * parts
    place = lax.axis_index("shard")
    row_total = clip_count * slot_count
    gathered = (
        lax.all_gather(attention_weight, "shard", axis=0, tiled=True),
        lax.all_gather(output_weight, "shard", axis=0, tiled=True),
        lax.all_gather(expand_weight, "shard", axis=0, tiled=True),
        lax.all_gather(contract_weight, "shard", axis=0, tiled=True),
        lax.all_gather(first_gain, "shard", axis=0, tiled=True),
        lax.all_gather(first_shift, "shard", axis=0, tiled=True),
        lax.all_gather(query_bias, "shard", axis=0, tiled=True),
        lax.all_gather(value_bias, "shard", axis=0, tiled=True),
        lax.all_gather(output_bias, "shard", axis=0, tiled=True),
        lax.all_gather(second_gain, "shard", axis=0, tiled=True),
        lax.all_gather(second_shift, "shard", axis=0, tiled=True),
        lax.all_gather(expand_bias, "shard", axis=0, tiled=True),
        lax.all_gather(contract_bias, "shard", axis=0, tiled=True),
    )
    vectors = [entry.astype(jnp.float32) for entry in gathered[4:]]
    own_length = jnp.sum(jnp.where(jnp.arange(parts)[None, :] == place, lengths, 0), axis=1)
    row_live = jnp.arange(slot_count)[None, :] < own_length[:, None]
    key_live = (jnp.arange(slot_count)[None, None, :] < lengths[:, :, None]).reshape(
        clip_count, frame_count
    )
    inputs = tokens.reshape(row_total, width).astype(jnp.float32)
    first_normed, first_inverse, first_act = norm_forward(inputs, vectors[0], vectors[1])
    mixed = jnp.dot(first_act, gathered[0], preferred_element_type=jnp.float32)
    mixed = mixed + jnp.concatenate([vectors[2], jnp.zeros_like(vectors[2]), vectors[3]])
    mixed_low = mixed.astype(jnp.bfloat16)
    query_rows = mixed_low[:, :width].reshape(clip_count, slot_count, width)
    pair_own = mixed_low[:, width:].reshape(clip_count, slot_count, 2 * width)
    pair_all = lax.all_gather(pair_own, "shard", axis=1, tiled=True)
    attended, logsum = lax.map(attend_clip, (query_rows, pair_all, key_live))
    attended_flat = attended.reshape(row_total, width)
    residual = (
        inputs
        + jnp.dot(attended_flat, gathered[1], preferred_element_type=jnp.float32)
        + vectors[4]
    )
    second_normed, second_inverse, second_act = norm_forward(residual, vectors[5], vectors[6])
    pre = jnp.dot(second_act, gathered[2], preferred_element_type=jnp.float32) + vectors[7]
    hidden_act = jax.nn.gelu(pre, approximate=False).astype(jnp.bfloat16)
    block_output = (
        residual + jnp.dot(hidden_act, gathered[3], preferred_element_type=jnp.float32) + vectors[8]
    )
    backward = (
        lax.all_gather(attention_weight, "shard", axis=0, tiled=True),
        lax.all_gather(output_weight, "shard", axis=0, tiled=True),
        lax.all_gather(expand_weight, "shard", axis=0, tiled=True),
        lax.all_gather(contract_weight, "shard", axis=0, tiled=True),
        lax.all_gather(first_gain, "shard", axis=0, tiled=True),
        lax.all_gather(first_shift, "shard", axis=0, tiled=True),
        lax.all_gather(query_bias, "shard", axis=0, tiled=True),
        lax.all_gather(value_bias, "shard", axis=0, tiled=True),
        lax.all_gather(output_bias, "shard", axis=0, tiled=True),
        lax.all_gather(second_gain, "shard", axis=0, tiled=True),
        lax.all_gather(second_shift, "shard", axis=0, tiled=True),
        lax.all_gather(expand_bias, "shard", axis=0, tiled=True),
        lax.all_gather(contract_bias, "shard", axis=0, tiled=True),
    )
    back_vectors = [entry.astype(jnp.float32) for entry in backward[4:]]
    error = cotangent.reshape(row_total, width) * row_live.reshape(row_total, 1).astype(jnp.float32)
    error_low = error.astype(jnp.bfloat16)
    contract_bias_grad = jnp.sum(error, axis=0)
    contract_grad = inner_rows(hidden_act, error_low)
    dpre = lax.dot_general(
        error_low, backward[3], (((1,), (1,)), ((), ())), preferred_element_type=jnp.float32
    ) * gelu_slope(pre)
    expand_bias_grad = jnp.sum(dpre, axis=0)
    dpre_low = dpre.astype(jnp.bfloat16)
    expand_grad = inner_rows(second_act, dpre_low)
    dsecond = lax.dot_general(
        dpre_low, backward[2], (((1,), (1,)), ((), ())), preferred_element_type=jnp.float32
    )
    second_gain_grad = jnp.sum(dsecond * second_normed, axis=0)
    second_shift_grad = jnp.sum(dsecond, axis=0)
    dresidual = error + norm_backward(dsecond, second_normed, second_inverse, back_vectors[5])
    output_bias_grad = jnp.sum(dresidual, axis=0)
    dresidual_low = dresidual.astype(jnp.bfloat16)
    output_grad = inner_rows(attended_flat, dresidual_low)
    dattended = lax.dot_general(
        dresidual_low, backward[1], (((1,), (1,)), ((), ())), preferred_element_type=jnp.float32
    ).astype(jnp.bfloat16)
    delta = jnp.sum(
        heads_view(dattended.astype(jnp.float32)) * heads_view(attended_flat.astype(jnp.float32)),
        axis=-1,
    )
    delta = delta.reshape(clip_count, slot_count, HEADS)
    dattended_clips = dattended.reshape(clip_count, slot_count, width)
    dqueries, pair_terms = lax.map(
        both_grads, (query_rows, dattended_clips, logsum, delta, pair_all, key_live)
    )
    pair_grads = lax.psum_scatter(pair_terms, "shard", scatter_dimension=1, tiled=True)
    dqueries_flat = dqueries.reshape(row_total, width)
    pair_flat = pair_grads.reshape(row_total, 2 * width)
    dmixed = jnp.concatenate([dqueries_flat, pair_flat], axis=1)
    query_bias_grad = jnp.sum(dqueries_flat, axis=0)
    value_bias_grad = jnp.sum(pair_flat[:, width:], axis=0)
    dmixed_low = dmixed.astype(jnp.bfloat16)
    attention_grad = inner_rows(first_act, dmixed_low)
    dfirst = lax.dot_general(
        dmixed_low, backward[0], (((1,), (1,)), ((), ())), preferred_element_type=jnp.float32
    )
    first_gain_grad = jnp.sum(dfirst * first_normed, axis=0)
    first_shift_grad = jnp.sum(dfirst, axis=0)
    input_grad = dresidual + norm_backward(dfirst, first_normed, first_inverse, back_vectors[0])
    shares = (
        lax.psum_scatter(attention_grad, "shard", scatter_dimension=0, tiled=True),
        lax.psum_scatter(output_grad, "shard", scatter_dimension=0, tiled=True),
        lax.psum_scatter(expand_grad, "shard", scatter_dimension=0, tiled=True),
        lax.psum_scatter(contract_grad, "shard", scatter_dimension=0, tiled=True),
        lax.psum_scatter(first_gain_grad, "shard", scatter_dimension=0, tiled=True),
        lax.psum_scatter(first_shift_grad, "shard", scatter_dimension=0, tiled=True),
        lax.psum_scatter(query_bias_grad, "shard", scatter_dimension=0, tiled=True),
        lax.psum_scatter(value_bias_grad, "shard", scatter_dimension=0, tiled=True),
        lax.psum_scatter(output_bias_grad, "shard", scatter_dimension=0, tiled=True),
        lax.psum_scatter(second_gain_grad, "shard", scatter_dimension=0, tiled=True),
        lax.psum_scatter(second_shift_grad, "shard", scatter_dimension=0, tiled=True),
        lax.psum_scatter(expand_bias_grad, "shard", scatter_dimension=0, tiled=True),
        lax.psum_scatter(contract_bias_grad, "shard", scatter_dimension=0, tiled=True),
    )
    totals = lax.psum(
        (
            shares[0],
            shares[1],
            shares[2],
            shares[3],
            shares[4],
            shares[5],
            shares[6],
            shares[7],
            shares[8],
            shares[9],
            shares[10],
            shares[11],
            shares[12],
        ),
        "rep",
    )
    return (
        block_output.reshape(clip_count, slot_count, width),
        input_grad.reshape(clip_count, slot_count, width),
        totals[0],
        totals[1],
        totals[2],
        totals[3],
        totals[4],
        totals[5],
        totals[6],
        totals[7],
        totals[8],
        totals[9],
        totals[10],
        totals[11],
        totals[12],
    )


def clip_layer(tokens, lengths, cotangent_of, weights, vectors, reduce, send_out):
    attention_weight, output_weight, later_weights = weights
    (first_gain, first_shift, query_bias, value_bias, output_bias, second_gain, second_shift,
     expand_bias, contract_bias) = vectors
    clip_count, frame_count, width = tokens.shape
    block_count = lengths.shape[1]
    slot_count = frame_count // block_count
    rows = clip_count * frame_count
    live = (jnp.arange(slot_count)[None, None, :] < lengths[:, :, None]).reshape(clip_count, frame_count)
    scale = HEAD ** (-0.5)
    inputs = tokens.reshape(rows, width).astype(jnp.float32)
    first_normed, first_inverse, first_act = norm_forward(inputs, first_gain, first_shift)
    mixed = jnp.dot(first_act, attention_weight, preferred_element_type=jnp.float32)
    mixed = mixed + jnp.concatenate([query_bias, jnp.zeros_like(query_bias), value_bias])
    mixed_low = mixed.astype(jnp.bfloat16).reshape(clip_count, frame_count, 3, HEADS, HEAD)
    queries = mixed_low[:, :, 0]
    keys = mixed_low[:, :, 1]
    values = mixed_low[:, :, 2]
    scores = jnp.einsum("cqhd,ckhd->chqk", queries, keys, preferred_element_type=jnp.float32) * scale
    scores = jnp.where(live[:, None, None, :], scores, NEGATIVE)
    highest = jnp.max(scores, axis=-1, keepdims=True)
    logsum = highest + jnp.log(jnp.sum(jnp.exp(scores - highest), axis=-1, keepdims=True))
    probs = jnp.exp(scores - logsum)
    expand_weight, contract_weight = later_weights(logsum[0, 0, 0, :1])
    probs_low = probs.astype(jnp.bfloat16)
    attended = jnp.einsum("chqk,ckhd->cqhd", probs_low, values, preferred_element_type=jnp.float32)
    attended_flat = attended.reshape(rows, width).astype(jnp.bfloat16)
    residual = inputs + jnp.dot(attended_flat, output_weight, preferred_element_type=jnp.float32) + output_bias
    second_normed, second_inverse, second_act = norm_forward(residual, second_gain, second_shift)
    pre = jnp.dot(second_act, expand_weight, preferred_element_type=jnp.float32) + expand_bias
    hidden_act = jax.nn.gelu(pre, approximate=False).astype(jnp.bfloat16)
    block_output = residual + jnp.dot(hidden_act, contract_weight, preferred_element_type=jnp.float32) + contract_bias
    cotangent = cotangent_of(pre[0, :1])
    error = cotangent.reshape(rows, width) * live.reshape(rows, 1).astype(jnp.float32)
    error_low = error.astype(jnp.bfloat16)
    contract_bias_grad = jnp.sum(error, axis=0)
    contract_grad = inner_rows(hidden_act, error_low)
    contract_chip = chip_sum(contract_grad)
    dpre = lax.dot_general(
        error_low, contract_weight, (((1,), (1,)), ((), ())), preferred_element_type=jnp.float32
    ) * gelu_slope(pre)
    expand_bias_grad = jnp.sum(dpre, axis=0)
    dpre_low = dpre.astype(jnp.bfloat16)
    contract_chip, dpre_low = lax.optimization_barrier((contract_chip, dpre_low))
    contract_part = shard_sum(contract_chip)
    expand_grad = inner_rows(second_act, dpre_low)
    expand_chip = chip_sum(expand_grad)
    dsecond = lax.optimization_barrier(lax.dot_general(
        dpre_low, expand_weight, (((1,), (1,)), ((), ())), preferred_element_type=jnp.float32
    ))
    second_gain_grad = jnp.sum(dsecond * second_normed, axis=0)
    second_shift_grad = jnp.sum(dsecond, axis=0)
    dresidual = error + norm_backward(dsecond, second_normed, second_inverse, second_gain)
    output_bias_grad = jnp.sum(dresidual, axis=0)
    dresidual_low = dresidual.astype(jnp.bfloat16)
    sent_output = send_out(block_output)
    expand_chip, dresidual_low = lax.optimization_barrier((expand_chip, dresidual_low))
    expand_part = shard_sum(expand_chip)
    output_grad = inner_rows(attended_flat, dresidual_low)
    output_chip = chip_sum(output_grad)
    dattended = lax.dot_general(
        dresidual_low, output_weight, (((1,), (1,)), ((), ())), preferred_element_type=jnp.float32
    ).astype(jnp.bfloat16)
    contract_part, dattended = lax.optimization_barrier((contract_part, dattended))
    dattended_heads = dattended.reshape(clip_count, frame_count, HEADS, HEAD)
    attended_heads = attended_flat.reshape(clip_count, frame_count, HEADS, HEAD)
    delta = jnp.sum(
        dattended_heads.astype(jnp.float32) * attended_heads.astype(jnp.float32), axis=-1
    )
    dprob = jnp.einsum("cqhd,ckhd->chqk", dattended_heads, values, preferred_element_type=jnp.float32)
    dscore = (probs * (dprob - jnp.transpose(delta, (0, 2, 1))[:, :, :, None]) * scale).astype(jnp.bfloat16)
    dqueries = jnp.einsum("chqk,ckhd->cqhd", dscore, keys, preferred_element_type=jnp.float32)
    dkeys = jnp.einsum("chqk,cqhd->ckhd", dscore, queries, preferred_element_type=jnp.float32)
    dvalues = jnp.einsum("chqk,cqhd->ckhd", probs_low, dattended_heads, preferred_element_type=jnp.float32)
    dmixed = jnp.concatenate(
        [dqueries.reshape(rows, width), dkeys.reshape(rows, width), dvalues.reshape(rows, width)], axis=1
    )
    query_bias_grad = jnp.sum(dmixed[:, :width], axis=0)
    value_bias_grad = jnp.sum(dmixed[:, 2 * width:], axis=0)
    dmixed_low = dmixed.astype(jnp.bfloat16)
    contract_total = reduce(contract_part, contract_grad.shape[0])
    output_chip, expand_part, contract_total, sent_output, dmixed_low = lax.optimization_barrier(
        (output_chip, expand_part, contract_total, sent_output, dmixed_low)
    )
    output_part = shard_sum(output_chip)
    expand_total = reduce(expand_part, expand_grad.shape[0])
    attention_grad = inner_rows(first_act, dmixed_low)
    dfirst = lax.optimization_barrier(lax.dot_general(
        dmixed_low, attention_weight, (((1,), (1,)), ((), ())), preferred_element_type=jnp.float32
    ))
    first_gain_grad = jnp.sum(dfirst * first_normed, axis=0)
    first_shift_grad = jnp.sum(dfirst, axis=0)
    input_grad = dresidual + norm_backward(dfirst, first_normed, first_inverse, first_gain)
    output_part, expand_total, input_grad = lax.optimization_barrier((output_part, expand_total, input_grad))
    weight_grads = (attention_grad, output_part, expand_total, contract_total)
    vector_grads = (first_gain_grad, first_shift_grad, query_bias_grad, value_bias_grad, output_bias_grad,
                    second_gain_grad, second_shift_grad, expand_bias_grad, contract_bias_grad)
    return (
        sent_output,
        input_grad,
        weight_grads,
        vector_grads,
    )


PAIR = [(0, 1), (1, 0)]
OUTER = ("outer", "inner")


def core_pick(core, first, second):
    return jnp.where(core == 0, first, second)


def gather_weight(shard_rows, extra=None):
    parts = lax.axis_size("shard")
    core = lax.axis_index("core")
    rows, width = shard_rows.shape
    half = rows // 2
    mine = lax.dynamic_slice_in_dim(shard_rows, core * half, half, axis=0)
    if extra is not None:
        mine = jnp.concatenate([mine, extra], axis=0)
    mine = lax.all_gather(mine, "shard", axis=0, tiled=False)
    other = lax.ppermute(mine, "core", PAIR)
    first = core_pick(core, mine, other)
    second = core_pick(core, other, mine)
    full = jnp.stack([first[:, :half], second[:, :half]], axis=1).reshape(parts * rows, width)
    if extra is None:
        return full, None
    return full, first[:, half:]


def chip_sum(grad, extra=None):
    parts = lax.axis_size("shard")
    core = lax.axis_index("core")
    width = grad.shape[1]
    rows = grad.shape[0] // parts
    half = rows // 2
    quarters = grad.reshape(parts, 2, half, width)
    keep = lax.dynamic_index_in_dim(quarters, core, axis=1, keepdims=False)
    send = lax.dynamic_index_in_dim(quarters, 1 - core, axis=1, keepdims=False)
    if extra is not None:
        on_first = (core == 0).astype(extra.dtype)
        keep = jnp.concatenate([keep, extra * on_first], axis=1)
        send = jnp.concatenate([send, extra * (1 - on_first)], axis=1)
    return keep + lax.ppermute(send, "core", PAIR)


def shard_sum(chip):
    part = lax.psum_scatter(chip, "shard", scatter_dimension=0, tiled=False)
    if lax.axis_size("inner") > 1:
        part = lax.psum(part, "inner")
    return part


def finish_sum(part, half):
    core = lax.axis_index("core")
    total = line_sum(part)
    other = lax.ppermute(total, "core", PAIR)
    first = core_pick(core, total, other)
    second = core_pick(core, other, total)
    return jnp.concatenate([first[:half], second[:half]], axis=0), first[half:]


def finish_many(parts, halves):
    core = lax.axis_index("core")
    flat = jnp.concatenate([part.reshape(-1) for part in parts])
    total = line_sum(flat)
    other = lax.ppermute(total, "core", PAIR)
    first = core_pick(core, total, other)
    second = core_pick(core, other, total)
    outs = []
    offset = 0
    for part, half in zip(parts, halves):
        size = part.size
        low = first[offset:offset + size].reshape(part.shape)
        high = second[offset:offset + size].reshape(part.shape)
        outs.append((jnp.concatenate([low[:half], high[:half]], axis=0), low[half:]))
        offset += size
    return outs


def reduce_weight(grad, extra=None):
    half = grad.shape[0] // lax.axis_size("shard") // 2
    return finish_sum(shard_sum(chip_sum(grad, extra)), half)


def line_sum(values):
    groups = lax.axis_size("outer")
    if groups == 1:
        return values
    if groups & (groups - 1):
        return lax.psum(values, "outer")
    here = lax.axis_index("outer")
    length = values.shape[0]
    padded = -(-length // groups) * groups
    held = jnp.pad(values, ((0, padded - length),) + ((0, 0),) * (values.ndim - 1))
    held = held.reshape((groups, padded // groups) + values.shape[1:])
    step = 1
    while step < groups:
        held = held.reshape((held.shape[0] // 2, 2) + held.shape[1:])
        bit = (here // step) % 2
        keep = lax.dynamic_index_in_dim(held, bit, axis=1, keepdims=False)
        send = lax.dynamic_index_in_dim(held, 1 - bit, axis=1, keepdims=False)
        held = keep + lax.ppermute(send, "outer", [(j, j ^ step) for j in range(groups)])
        step *= 2
    step = groups // 2
    while step >= 1:
        bit = (here // step) % 2
        other = lax.ppermute(held, "outer", [(j, j ^ step) for j in range(groups)])
        low = jnp.where(bit == 0, held, other)
        high = jnp.where(bit == 0, other, held)
        held = jnp.stack([low, high], axis=1)
        held = held.reshape((held.shape[0] * 2,) + held.shape[2:])
        step //= 2
    return held.reshape((padded,) + values.shape[1:])[:length]


def gather_packed(blocks, after=None):
    core = lax.axis_index("core")
    mine = lax.all_gather(jnp.concatenate(blocks, axis=0), "shard", axis=0, tiled=False)
    if after is not None:
        mine = mine + (after * 0).astype(mine.dtype)
    other = lax.ppermute(mine, "core", PAIR)
    return core_pick(core, mine, other), core_pick(core, other, mine)


def unpack_rows(first, second, begin, count, shape):
    parts = first.shape[0]
    rows, width = shape
    low = first[:, begin:begin + count].reshape(parts, -1, width)
    high = second[:, begin:begin + count].reshape(parts, -1, width)
    return jnp.stack([low, high], axis=1).reshape(rows, width)


def core_half(shard_rows):
    core = lax.axis_index("core")
    half = shard_rows.shape[0] // 2
    return lax.dynamic_slice_in_dim(shard_rows, core * half, half, axis=0)


def clip_local(tokens, lengths, cotangent, *params):
    clip_count, slot_count, width = tokens.shape
    parts = lax.axis_size("shard")
    place = lax.axis_index("shard")
    own = clip_count // parts
    weight_shards = params[:4]
    vector_shards = params[4:]
    wide = weight_shards[0].shape[1]
    vector_row = jnp.concatenate([entry.reshape(-1) for entry in vector_shards])
    pad = (-vector_row.shape[0]) % wide
    vector_rows = jnp.pad(vector_row, (0, pad)).reshape(-1, wide)
    attention_half = core_half(weight_shards[0])
    output_half = core_half(weight_shards[1]).reshape(-1, wide)
    first, second = gather_packed([attention_half, output_half, vector_rows])
    a_rows = attention_half.shape[0]
    o_rows = output_half.shape[0]
    attention_weight = unpack_rows(first, second, 0, a_rows, (parts * weight_shards[0].shape[0], wide))
    output_weight = unpack_rows(
        first, second, a_rows, o_rows, (parts * weight_shards[1].shape[0], weight_shards[1].shape[1])
    )
    vector_all = first[:, a_rows + o_rows:].reshape(parts, -1)[:, : vector_row.shape[0]]
    vectors = []
    offset = 0
    for entry in vector_shards:
        size = entry.shape[0]
        vectors.append(vector_all[:, offset:offset + size].reshape(parts * size).astype(jnp.float32))
        offset += size
    late = weight_shards[2].shape[1]
    expand_half = core_half(weight_shards[2])
    contract_half = core_half(weight_shards[3]).reshape(-1, late)

    def later_weights(after):
        first_b, second_b = gather_packed([expand_half, contract_half], after)
        e_rows = expand_half.shape[0]
        expand_weight = unpack_rows(first_b, second_b, 0, e_rows, (parts * weight_shards[2].shape[0], late))
        contract_weight = unpack_rows(
            first_b, second_b, e_rows, contract_half.shape[0],
            (parts * weight_shards[3].shape[0], weight_shards[3].shape[1]),
        )
        return expand_weight, contract_weight

    weights = (attention_weight, output_weight, later_weights)
    def exchange(rows):
        blocks = rows.reshape((parts, rows.shape[0] // parts) + rows.shape[1:])
        held = [lax.dynamic_index_in_dim(blocks, place, axis=0, keepdims=False)]
        for shift in range(1, parts):
            outgoing = lax.dynamic_index_in_dim(blocks, (place + shift) % parts, axis=0, keepdims=False)
            held.append(lax.ppermute(outgoing, "shard", [(i, (i + shift) % parts) for i in range(parts)]))
        stacked = jnp.stack(held[::-1], axis=0)
        doubled = jnp.concatenate([stacked, stacked], axis=0)
        start = (parts - (place + 1) % parts) % parts
        return lax.dynamic_slice_in_dim(doubled, start, parts, axis=0).reshape(rows.shape)

    def gather_rows(values, early=False):
        flat = values.reshape(clip_count * slot_count, width)
        moved = exchange(flat) if early else lax.all_to_all(flat, "shard", 0, 0, tiled=True)
        moved = moved.reshape(parts, own, slot_count, width)
        return jnp.transpose(moved, (1, 0, 2, 3)).reshape(own, parts * slot_count, width) if own > 1 else moved.reshape(own, parts * slot_count, width)

    def scatter_rows(values):
        rows = values.reshape(own, parts, slot_count, width)
        if own > 1:
            rows = jnp.transpose(rows, (1, 0, 2, 3))
        moved = lax.all_to_all(rows.reshape(own * parts * slot_count, width), "shard", 0, 0, tiled=True)
        return moved.reshape(clip_count, slot_count, width)

    tokens_clip = gather_rows(tokens, True)

    def cotangent_of(after):
        late = cotangent + (after * 0).astype(cotangent.dtype)
        return gather_rows(late)

    lengths_clip = lax.dynamic_slice_in_dim(lengths, place * own, own, axis=0)
    block_output, input_grad, weight_grads, vector_grads = clip_layer(
        tokens_clip, lengths_clip, cotangent_of, weights, vectors, lambda part, rows: finish_sum(part, rows // parts // 2)[0],
        scatter_rows,
    )
    input_grad = scatter_rows(input_grad)
    attention_grad = weight_grads[0]
    attention_width = attention_grad.shape[1]
    vector_parts = jnp.concatenate([entry.reshape(parts, -1) for entry in vector_grads], axis=1)
    vector_size = vector_parts.shape[1]
    vpad = (-vector_size) % attention_width
    vector_parts = jnp.pad(vector_parts, ((0, 0), (0, vpad))).reshape(parts, -1, attention_width)
    attention_part = shard_sum(chip_sum(attention_grad, vector_parts))
    output_part = weight_grads[1]
    (attention_total, vector_total), (output_total, _) = finish_many(
        [attention_part, output_part],
        [attention_grad.shape[0] // parts // 2, params[1].shape[0] // 2],
    )
    totals = (attention_total, output_total) + tuple(weight_grads[2:])
    vector_total = vector_total.reshape(-1)[:vector_size]
    vector_outs = []
    offset = 0
    for entry in vector_shards:
        size = entry.shape[0]
        vector_outs.append(vector_total[offset:offset + size])
        offset += size
    return (block_output, input_grad) + totals + tuple(vector_outs)


def split_rep(mesh):
    devices = mesh.devices
    rep, parts = devices.shape
    first = devices[0, 0]
    stride = None
    for index in range(1, rep):
        other = devices[index, 0]
        if tuple(other.coords) == tuple(first.coords) and other.core_on_chip != first.core_on_chip:
            stride = index
            break
    if stride is None or rep % (2 * stride):
        return None
    grid = devices.reshape(rep // (2 * stride), 2, stride, parts)
    for spot in np.ndindex(grid.shape[0], grid.shape[2], grid.shape[3]):
        low = grid[spot[0], 0, spot[1], spot[2]]
        high = grid[spot[0], 1, spot[1], spot[2]]
        if tuple(low.coords) != tuple(high.coords) or low.core_on_chip == high.core_on_chip:
            return None
    return Mesh(grid, ("outer", "core", "inner", "shard"))


def solution(mesh):
    def specs(rep):
        ins = (P(rep, "shard", None), P(rep, None), P(rep, "shard", None)) + (P("shard", None),) * 4 + (
            P("shard"),
        ) * 9
        outs = (P(rep, "shard", None), P(rep, "shard", None)) + (P("shard", None),) * 4 + (P("shard"),) * 9
        return ins, outs

    ins, outs = specs("rep")
    plain = jax.shard_map(local, mesh=mesh, in_specs=ins, out_specs=outs, check_vma=False)
    split = split_rep(mesh)
    if split is None:
        return plain
    ins, outs = specs(("outer", "core", "inner"))
    fast = jax.shard_map(clip_local, mesh=split, in_specs=ins, out_specs=outs, check_vma=False)
    rep, parts = mesh.devices.shape

    def run(*args):
        if (args[0].shape[0] // rep) % parts == 0:
            return fast(*args)
        return plain(*args)

    return run
```

```python
import jax
import jax.numpy as jnp
from jax import lax
from jax.sharding import Mesh, PartitionSpec as P
import numpy as np

HEADS = 12
HEAD = 64


EPSILON = 1e-05
NEGATIVE = -1e30


def norm_forward(values, gain, shift):
    centred = values - jnp.mean(values, axis=-1, keepdims=True)
    inverse = lax.rsqrt(jnp.mean(centred * centred, axis=-1, keepdims=True) + EPSILON)
    normed = centred * inverse
    return (normed, inverse, (normed * gain + shift).astype(jnp.bfloat16))


def norm_backward(upstream, normed, inverse, gain):
    scaled = upstream * gain
    return inverse * (
        scaled
        - jnp.mean(scaled, axis=-1, keepdims=True)
        - normed * jnp.mean(scaled * normed, axis=-1, keepdims=True)
    )


def gelu_slope(values):
    return (
        0.5 * (1.0 + jax.scipy.special.erf(values * 0.7071067811865476))
        + values * jnp.exp(-0.5 * values * values) * 0.3989422804014327
    )


def inner_rows(left, right):
    return lax.dot_general(
        left, right, (((0,), (0,)), ((), ())), preferred_element_type=jnp.float32
    )


def heads_view(matrix):
    return matrix.reshape(matrix.shape[0], HEADS, HEAD)


def score_block(query_rows, key_rows, key_live):
    scores = jnp.einsum(
        "qhd,khd->hqk",
        heads_view(query_rows),
        heads_view(key_rows),
        preferred_element_type=jnp.float32,
    ) * HEAD ** (-0.5)
    return jnp.where(key_live[None, None, :], scores, NEGATIVE)


def attend_clip(items):
    query_rows, pair_rows, key_live = items
    width = query_rows.shape[1]
    scores = score_block(query_rows, pair_rows[:, :width], key_live)
    highest = jnp.max(scores, axis=-1, keepdims=True)
    logsum = highest + jnp.log(jnp.sum(jnp.exp(scores - highest), axis=-1, keepdims=True))
    probs_low = jnp.exp(scores - logsum).astype(jnp.bfloat16)
    attended = jnp.einsum(
        "hqk,khd->qhd",
        probs_low,
        heads_view(pair_rows[:, width:]),
        preferred_element_type=jnp.float32,
    )
    return (attended.reshape(query_rows.shape[0], width).astype(jnp.bfloat16), logsum[:, :, 0].T)


def score_grads(query_rows, dattended, logsum, delta, pair_rows, key_live):
    width = query_rows.shape[1]
    scores = score_block(query_rows, pair_rows[:, :width], key_live)
    probs = jnp.exp(scores - logsum.T[:, :, None])
    dprob = jnp.einsum(
        "qhd,khd->hqk",
        heads_view(dattended),
        heads_view(pair_rows[:, width:]),
        preferred_element_type=jnp.float32,
    )
    dscore = (probs * (dprob - delta.T[:, :, None]) * HEAD ** (-0.5)).astype(jnp.bfloat16)
    return (probs.astype(jnp.bfloat16), dscore)


def both_grads(items):
    query_rows, dattended, logsum, delta, pair_rows, key_live = items
    width = query_rows.shape[1]
    probs_low, dscore = score_grads(query_rows, dattended, logsum, delta, pair_rows, key_live)
    dqueries = jnp.einsum(
        "hqk,khd->qhd", dscore, heads_view(pair_rows[:, :width]), preferred_element_type=jnp.float32
    ).reshape(query_rows.shape[0], width)
    dkeys = jnp.einsum(
        "hqk,qhd->khd", dscore, heads_view(query_rows), preferred_element_type=jnp.float32
    )
    dvalues = jnp.einsum(
        "hqk,qhd->khd", probs_low, heads_view(dattended), preferred_element_type=jnp.float32
    )
    key_count = pair_rows.shape[0]
    return (
        dqueries,
        jnp.concatenate(
            [dkeys.reshape(key_count, width), dvalues.reshape(key_count, width)], axis=1
        ),
    )


def local(
    tokens,
    lengths,
    cotangent,
    attention_weight,
    output_weight,
    expand_weight,
    contract_weight,
    first_gain,
    first_shift,
    query_bias,
    value_bias,
    output_bias,
    second_gain,
    second_shift,
    expand_bias,
    contract_bias,
):
    clip_count, slot_count, width = tokens.shape
    parts = lax.axis_size("shard")
    frame_count = slot_count * parts
    place = lax.axis_index("shard")
    row_total = clip_count * slot_count
    gathered = (
        lax.all_gather(attention_weight, "shard", axis=0, tiled=True),
        lax.all_gather(output_weight, "shard", axis=0, tiled=True),
        lax.all_gather(expand_weight, "shard", axis=0, tiled=True),
        lax.all_gather(contract_weight, "shard", axis=0, tiled=True),
        lax.all_gather(first_gain, "shard", axis=0, tiled=True),
        lax.all_gather(first_shift, "shard", axis=0, tiled=True),
        lax.all_gather(query_bias, "shard", axis=0, tiled=True),
        lax.all_gather(value_bias, "shard", axis=0, tiled=True),
        lax.all_gather(output_bias, "shard", axis=0, tiled=True),
        lax.all_gather(second_gain, "shard", axis=0, tiled=True),
        lax.all_gather(second_shift, "shard", axis=0, tiled=True),
        lax.all_gather(expand_bias, "shard", axis=0, tiled=True),
        lax.all_gather(contract_bias, "shard", axis=0, tiled=True),
    )
    vectors = [entry.astype(jnp.float32) for entry in gathered[4:]]
    own_length = jnp.sum(jnp.where(jnp.arange(parts)[None, :] == place, lengths, 0), axis=1)
    row_live = jnp.arange(slot_count)[None, :] < own_length[:, None]
    key_live = (jnp.arange(slot_count)[None, None, :] < lengths[:, :, None]).reshape(
        clip_count, frame_count
    )
    inputs = tokens.reshape(row_total, width).astype(jnp.float32)
    first_normed, first_inverse, first_act = norm_forward(inputs, vectors[0], vectors[1])
    mixed = jnp.dot(first_act, gathered[0], preferred_element_type=jnp.float32)
    mixed = mixed + jnp.concatenate([vectors[2], jnp.zeros_like(vectors[2]), vectors[3]])
    mixed_low = mixed.astype(jnp.bfloat16)
    query_rows = mixed_low[:, :width].reshape(clip_count, slot_count, width)
    pair_own = mixed_low[:, width:].reshape(clip_count, slot_count, 2 * width)
    pair_all = lax.all_gather(pair_own, "shard", axis=1, tiled=True)
    attended, logsum = lax.map(attend_clip, (query_rows, pair_all, key_live))
    attended_flat = attended.reshape(row_total, width)
    residual = (
        inputs
        + jnp.dot(attended_flat, gathered[1], preferred_element_type=jnp.float32)
        + vectors[4]
    )
    second_normed, second_inverse, second_act = norm_forward(residual, vectors[5], vectors[6])
    pre = jnp.dot(second_act, gathered[2], preferred_element_type=jnp.float32) + vectors[7]
    hidden_act = jax.nn.gelu(pre, approximate=False).astype(jnp.bfloat16)
    block_output = (
        residual + jnp.dot(hidden_act, gathered[3], preferred_element_type=jnp.float32) + vectors[8]
    )
    backward = (
        lax.all_gather(attention_weight, "shard", axis=0, tiled=True),
        lax.all_gather(output_weight, "shard", axis=0, tiled=True),
        lax.all_gather(expand_weight, "shard", axis=0, tiled=True),
        lax.all_gather(contract_weight, "shard", axis=0, tiled=True),
        lax.all_gather(first_gain, "shard", axis=0, tiled=True),
        lax.all_gather(first_shift, "shard", axis=0, tiled=True),
        lax.all_gather(query_bias, "shard", axis=0, tiled=True),
        lax.all_gather(value_bias, "shard", axis=0, tiled=True),
        lax.all_gather(output_bias, "shard", axis=0, tiled=True),
        lax.all_gather(second_gain, "shard", axis=0, tiled=True),
        lax.all_gather(second_shift, "shard", axis=0, tiled=True),
        lax.all_gather(expand_bias, "shard", axis=0, tiled=True),
        lax.all_gather(contract_bias, "shard", axis=0, tiled=True),
    )
    back_vectors = [entry.astype(jnp.float32) for entry in backward[4:]]
    error = cotangent.reshape(row_total, width) * row_live.reshape(row_total, 1).astype(jnp.float32)
    error_low = error.astype(jnp.bfloat16)
    contract_bias_grad = jnp.sum(error, axis=0)
    contract_grad = inner_rows(hidden_act, error_low)
    dpre = lax.dot_general(
        error_low, backward[3], (((1,), (1,)), ((), ())), preferred_element_type=jnp.float32
    ) * gelu_slope(pre)
    expand_bias_grad = jnp.sum(dpre, axis=0)
    dpre_low = dpre.astype(jnp.bfloat16)
    expand_grad = inner_rows(second_act, dpre_low)
    dsecond = lax.dot_general(
        dpre_low, backward[2], (((1,), (1,)), ((), ())), preferred_element_type=jnp.float32
    )
    second_gain_grad = jnp.sum(dsecond * second_normed, axis=0)
    second_shift_grad = jnp.sum(dsecond, axis=0)
    dresidual = error + norm_backward(dsecond, second_normed, second_inverse, back_vectors[5])
    output_bias_grad = jnp.sum(dresidual, axis=0)
    dresidual_low = dresidual.astype(jnp.bfloat16)
    output_grad = inner_rows(attended_flat, dresidual_low)
    dattended = lax.dot_general(
        dresidual_low, backward[1], (((1,), (1,)), ((), ())), preferred_element_type=jnp.float32
    ).astype(jnp.bfloat16)
    delta = jnp.sum(
        heads_view(dattended.astype(jnp.float32)) * heads_view(attended_flat.astype(jnp.float32)),
        axis=-1,
    )
    delta = delta.reshape(clip_count, slot_count, HEADS)
    dattended_clips = dattended.reshape(clip_count, slot_count, width)
    dqueries, pair_terms = lax.map(
        both_grads, (query_rows, dattended_clips, logsum, delta, pair_all, key_live)
    )
    pair_grads = lax.psum_scatter(pair_terms, "shard", scatter_dimension=1, tiled=True)
    dqueries_flat = dqueries.reshape(row_total, width)
    pair_flat = pair_grads.reshape(row_total, 2 * width)
    dmixed = jnp.concatenate([dqueries_flat, pair_flat], axis=1)
    query_bias_grad = jnp.sum(dqueries_flat, axis=0)
    value_bias_grad = jnp.sum(pair_flat[:, width:], axis=0)
    dmixed_low = dmixed.astype(jnp.bfloat16)
    attention_grad = inner_rows(first_act, dmixed_low)
    dfirst = lax.dot_general(
        dmixed_low, backward[0], (((1,), (1,)), ((), ())), preferred_element_type=jnp.float32
    )
    first_gain_grad = jnp.sum(dfirst * first_normed, axis=0)
    first_shift_grad = jnp.sum(dfirst, axis=0)
    input_grad = dresidual + norm_backward(dfirst, first_normed, first_inverse, back_vectors[0])
    shares = (
        lax.psum_scatter(attention_grad, "shard", scatter_dimension=0, tiled=True),
        lax.psum_scatter(output_grad, "shard", scatter_dimension=0, tiled=True),
        lax.psum_scatter(expand_grad, "shard", scatter_dimension=0, tiled=True),
        lax.psum_scatter(contract_grad, "shard", scatter_dimension=0, tiled=True),
        lax.psum_scatter(first_gain_grad, "shard", scatter_dimension=0, tiled=True),
        lax.psum_scatter(first_shift_grad, "shard", scatter_dimension=0, tiled=True),
        lax.psum_scatter(query_bias_grad, "shard", scatter_dimension=0, tiled=True),
        lax.psum_scatter(value_bias_grad, "shard", scatter_dimension=0, tiled=True),
        lax.psum_scatter(output_bias_grad, "shard", scatter_dimension=0, tiled=True),
        lax.psum_scatter(second_gain_grad, "shard", scatter_dimension=0, tiled=True),
        lax.psum_scatter(second_shift_grad, "shard", scatter_dimension=0, tiled=True),
        lax.psum_scatter(expand_bias_grad, "shard", scatter_dimension=0, tiled=True),
        lax.psum_scatter(contract_bias_grad, "shard", scatter_dimension=0, tiled=True),
    )
    totals = lax.psum(
        (
            shares[0],
            shares[1],
            shares[2],
            shares[3],
            shares[4],
            shares[5],
            shares[6],
            shares[7],
            shares[8],
            shares[9],
            shares[10],
            shares[11],
            shares[12],
        ),
        "rep",
    )
    return (
        block_output.reshape(clip_count, slot_count, width),
        input_grad.reshape(clip_count, slot_count, width),
        totals[0],
        totals[1],
        totals[2],
        totals[3],
        totals[4],
        totals[5],
        totals[6],
        totals[7],
        totals[8],
        totals[9],
        totals[10],
        totals[11],
        totals[12],
    )


def clip_layer(tokens, lengths, cotangent_of, weights, vectors, reduce, send_out):
    attention_weight, output_weight, later_weights = weights
    (first_gain, first_shift, query_bias, value_bias, output_bias, second_gain, second_shift,
     expand_bias, contract_bias) = vectors
    clip_count, frame_count, width = tokens.shape
    block_count = lengths.shape[1]
    slot_count = frame_count // block_count
    rows = clip_count * frame_count
    live = (jnp.arange(slot_count)[None, None, :] < lengths[:, :, None]).reshape(clip_count, frame_count)
    scale = HEAD ** (-0.5)
    inputs = tokens.reshape(rows, width).astype(jnp.float32)
    first_normed, first_inverse, first_act = norm_forward(inputs, first_gain, first_shift)
    mixed = jnp.dot(first_act, attention_weight, preferred_element_type=jnp.float32)
    mixed = mixed + jnp.concatenate([query_bias, jnp.zeros_like(query_bias), value_bias])
    mixed_low = mixed.astype(jnp.bfloat16).reshape(clip_count, frame_count, 3, HEADS, HEAD)
    queries = mixed_low[:, :, 0]
    keys = mixed_low[:, :, 1]
    values = mixed_low[:, :, 2]
    scores = jnp.einsum("cqhd,ckhd->chqk", queries, keys, preferred_element_type=jnp.float32) * scale
    scores = jnp.where(live[:, None, None, :], scores, NEGATIVE)
    highest = jnp.max(scores, axis=-1, keepdims=True)
    logsum = highest + jnp.log(jnp.sum(jnp.exp(scores - highest), axis=-1, keepdims=True))
    probs = jnp.exp(scores - logsum)
    expand_weight, contract_weight = later_weights(logsum[0, 0, 0, :1])
    probs_low = probs.astype(jnp.bfloat16)
    attended = jnp.einsum("chqk,ckhd->cqhd", probs_low, values, preferred_element_type=jnp.float32)
    attended_flat = attended.reshape(rows, width).astype(jnp.bfloat16)
    residual = inputs + jnp.dot(attended_flat, output_weight, preferred_element_type=jnp.float32) + output_bias
    second_normed, second_inverse, second_act = norm_forward(residual, second_gain, second_shift)
    pre = jnp.dot(second_act, expand_weight, preferred_element_type=jnp.float32) + expand_bias
    hidden_act = jax.nn.gelu(pre, approximate=False).astype(jnp.bfloat16)
    block_output = residual + jnp.dot(hidden_act, contract_weight, preferred_element_type=jnp.float32) + contract_bias
    cotangent = cotangent_of(pre[0, :1])
    error = cotangent.reshape(rows, width) * live.reshape(rows, 1).astype(jnp.float32)
    error_low = error.astype(jnp.bfloat16)
    contract_bias_grad = jnp.sum(error, axis=0)
    contract_grad = inner_rows(hidden_act, error_low)
    contract_chip = chip_sum(contract_grad)
    dpre = lax.dot_general(
        error_low, contract_weight, (((1,), (1,)), ((), ())), preferred_element_type=jnp.float32
    ) * gelu_slope(pre)
    expand_bias_grad = jnp.sum(dpre, axis=0)
    dpre_low = dpre.astype(jnp.bfloat16)
    contract_chip, dpre_low = lax.optimization_barrier((contract_chip, dpre_low))
    contract_part = shard_sum(contract_chip)
    expand_grad = inner_rows(second_act, dpre_low)
    expand_chip = chip_sum(expand_grad)
    dsecond = lax.optimization_barrier(lax.dot_general(
        dpre_low, expand_weight, (((1,), (1,)), ((), ())), preferred_element_type=jnp.float32
    ))
    second_gain_grad = jnp.sum(dsecond * second_normed, axis=0)
    second_shift_grad = jnp.sum(dsecond, axis=0)
    dresidual = error + norm_backward(dsecond, second_normed, second_inverse, second_gain)
    output_bias_grad = jnp.sum(dresidual, axis=0)
    dresidual_low = dresidual.astype(jnp.bfloat16)
    sent_output = send_out(block_output)
    expand_chip, dresidual_low = lax.optimization_barrier((expand_chip, dresidual_low))
    expand_part = shard_sum(expand_chip)
    output_grad = inner_rows(attended_flat, dresidual_low)
    output_chip = chip_sum(output_grad)
    dattended = lax.dot_general(
        dresidual_low, output_weight, (((1,), (1,)), ((), ())), preferred_element_type=jnp.float32
    ).astype(jnp.bfloat16)
    contract_part, output_chip, dattended = lax.optimization_barrier((contract_part, output_chip, dattended))
    output_part = shard_sum(output_chip)
    dattended_heads = dattended.reshape(clip_count, frame_count, HEADS, HEAD)
    attended_heads = attended_flat.reshape(clip_count, frame_count, HEADS, HEAD)
    delta = jnp.sum(
        dattended_heads.astype(jnp.float32) * attended_heads.astype(jnp.float32), axis=-1
    )
    dprob = jnp.einsum("cqhd,ckhd->chqk", dattended_heads, values, preferred_element_type=jnp.float32)
    dscore = (probs * (dprob - jnp.transpose(delta, (0, 2, 1))[:, :, :, None]) * scale).astype(jnp.bfloat16)
    dqueries = jnp.einsum("chqk,ckhd->cqhd", dscore, keys, preferred_element_type=jnp.float32)
    dkeys = jnp.einsum("chqk,cqhd->ckhd", dscore, queries, preferred_element_type=jnp.float32)
    dvalues = jnp.einsum("chqk,cqhd->ckhd", probs_low, dattended_heads, preferred_element_type=jnp.float32)
    dmixed = jnp.concatenate(
        [dqueries.reshape(rows, width), dkeys.reshape(rows, width), dvalues.reshape(rows, width)], axis=1
    )
    query_bias_grad = jnp.sum(dmixed[:, :width], axis=0)
    value_bias_grad = jnp.sum(dmixed[:, 2 * width:], axis=0)
    dmixed_low = dmixed.astype(jnp.bfloat16)
    contract_total = reduce(contract_part, contract_grad.shape[0])
    expand_part, contract_total, sent_output, dmixed_low = lax.optimization_barrier(
        (expand_part, contract_total, sent_output, dmixed_low)
    )
    expand_total = reduce(expand_part, expand_grad.shape[0])
    attention_grad = inner_rows(first_act, dmixed_low)
    dfirst = lax.optimization_barrier(lax.dot_general(
        dmixed_low, attention_weight, (((1,), (1,)), ((), ())), preferred_element_type=jnp.float32
    ))
    first_gain_grad = jnp.sum(dfirst * first_normed, axis=0)
    first_shift_grad = jnp.sum(dfirst, axis=0)
    input_grad = dresidual + norm_backward(dfirst, first_normed, first_inverse, first_gain)
    output_part, expand_total, input_grad = lax.optimization_barrier((output_part, expand_total, input_grad))
    weight_grads = (attention_grad, output_part, expand_total, contract_total)
    vector_grads = (first_gain_grad, first_shift_grad, query_bias_grad, value_bias_grad, output_bias_grad,
                    second_gain_grad, second_shift_grad, expand_bias_grad, contract_bias_grad)
    return (
        sent_output,
        input_grad,
        weight_grads,
        vector_grads,
    )


PAIR = [(0, 1), (1, 0)]
OUTER = ("outer", "inner")


def core_pick(core, first, second):
    return jnp.where(core == 0, first, second)


def gather_weight(shard_rows, extra=None):
    parts = lax.axis_size("shard")
    core = lax.axis_index("core")
    rows, width = shard_rows.shape
    half = rows // 2
    mine = lax.dynamic_slice_in_dim(shard_rows, core * half, half, axis=0)
    if extra is not None:
        mine = jnp.concatenate([mine, extra], axis=0)
    mine = lax.all_gather(mine, "shard", axis=0, tiled=False)
    other = lax.ppermute(mine, "core", PAIR)
    first = core_pick(core, mine, other)
    second = core_pick(core, other, mine)
    full = jnp.stack([first[:, :half], second[:, :half]], axis=1).reshape(parts * rows, width)
    if extra is None:
        return full, None
    return full, first[:, half:]


def chip_sum(grad, extra=None):
    parts = lax.axis_size("shard")
    core = lax.axis_index("core")
    width = grad.shape[1]
    rows = grad.shape[0] // parts
    half = rows // 2
    quarters = grad.reshape(parts, 2, half, width)
    keep = lax.dynamic_index_in_dim(quarters, core, axis=1, keepdims=False)
    send = lax.dynamic_index_in_dim(quarters, 1 - core, axis=1, keepdims=False)
    if extra is not None:
        on_first = (core == 0).astype(extra.dtype)
        keep = jnp.concatenate([keep, extra * on_first], axis=1)
        send = jnp.concatenate([send, extra * (1 - on_first)], axis=1)
    return keep + lax.ppermute(send, "core", PAIR)


def shard_sum(chip):
    part = lax.psum_scatter(chip, "shard", scatter_dimension=0, tiled=False)
    if lax.axis_size("inner") > 1:
        part = lax.psum(part, "inner")
    return part


def finish_sum(part, half):
    core = lax.axis_index("core")
    total = line_sum(part)
    other = lax.ppermute(total, "core", PAIR)
    first = core_pick(core, total, other)
    second = core_pick(core, other, total)
    return jnp.concatenate([first[:half], second[:half]], axis=0), first[half:]


def finish_many(parts, halves):
    core = lax.axis_index("core")
    flat = jnp.concatenate([part.reshape(-1) for part in parts])
    total = line_sum(flat)
    other = lax.ppermute(total, "core", PAIR)
    first = core_pick(core, total, other)
    second = core_pick(core, other, total)
    outs = []
    offset = 0
    for part, half in zip(parts, halves):
        size = part.size
        low = first[offset:offset + size].reshape(part.shape)
        high = second[offset:offset + size].reshape(part.shape)
        outs.append((jnp.concatenate([low[:half], high[:half]], axis=0), low[half:]))
        offset += size
    return outs


def reduce_weight(grad, extra=None):
    half = grad.shape[0] // lax.axis_size("shard") // 2
    return finish_sum(shard_sum(chip_sum(grad, extra)), half)


def line_sum(values):
    groups = lax.axis_size("outer")
    if groups == 1:
        return values
    if groups & (groups - 1):
        return lax.psum(values, "outer")
    here = lax.axis_index("outer")
    length = values.shape[0]
    padded = -(-length // groups) * groups
    held = jnp.pad(values, ((0, padded - length),) + ((0, 0),) * (values.ndim - 1))
    held = held.reshape((groups, padded // groups) + values.shape[1:])
    step = 1
    while step < groups:
        held = held.reshape((held.shape[0] // 2, 2) + held.shape[1:])
        bit = (here // step) % 2
        keep = lax.dynamic_index_in_dim(held, bit, axis=1, keepdims=False)
        send = lax.dynamic_index_in_dim(held, 1 - bit, axis=1, keepdims=False)
        held = keep + lax.ppermute(send, "outer", [(j, j ^ step) for j in range(groups)])
        step *= 2
    step = groups // 2
    while step >= 1:
        bit = (here // step) % 2
        other = lax.ppermute(held, "outer", [(j, j ^ step) for j in range(groups)])
        low = jnp.where(bit == 0, held, other)
        high = jnp.where(bit == 0, other, held)
        held = jnp.stack([low, high], axis=1)
        held = held.reshape((held.shape[0] * 2,) + held.shape[2:])
        step //= 2
    return held.reshape((padded,) + values.shape[1:])[:length]


def gather_packed(blocks, after=None):
    core = lax.axis_index("core")
    mine = lax.all_gather(jnp.concatenate(blocks, axis=0), "shard", axis=0, tiled=False)
    if after is not None:
        mine = mine + (after * 0).astype(mine.dtype)
    other = lax.ppermute(mine, "core", PAIR)
    return core_pick(core, mine, other), core_pick(core, other, mine)


def unpack_rows(first, second, begin, count, shape):
    parts = first.shape[0]
    rows, width = shape
    low = first[:, begin:begin + count].reshape(parts, -1, width)
    high = second[:, begin:begin + count].reshape(parts, -1, width)
    return jnp.stack([low, high], axis=1).reshape(rows, width)


def core_half(shard_rows):
    core = lax.axis_index("core")
    half = shard_rows.shape[0] // 2
    return lax.dynamic_slice_in_dim(shard_rows, core * half, half, axis=0)


def clip_local(tokens, lengths, cotangent, *params):
    clip_count, slot_count, width = tokens.shape
    parts = lax.axis_size("shard")
    place = lax.axis_index("shard")
    own = clip_count // parts
    weight_shards = params[:4]
    vector_shards = params[4:]
    wide = weight_shards[0].shape[1]
    vector_row = jnp.concatenate([entry.reshape(-1) for entry in vector_shards])
    pad = (-vector_row.shape[0]) % wide
    vector_rows = jnp.pad(vector_row, (0, pad)).reshape(-1, wide)
    attention_half = core_half(weight_shards[0])
    output_half = core_half(weight_shards[1]).reshape(-1, wide)
    first, second = gather_packed([attention_half, output_half, vector_rows])
    a_rows = attention_half.shape[0]
    o_rows = output_half.shape[0]
    attention_weight = unpack_rows(first, second, 0, a_rows, (parts * weight_shards[0].shape[0], wide))
    output_weight = unpack_rows(
        first, second, a_rows, o_rows, (parts * weight_shards[1].shape[0], weight_shards[1].shape[1])
    )
    vector_all = first[:, a_rows + o_rows:].reshape(parts, -1)[:, : vector_row.shape[0]]
    vectors = []
    offset = 0
    for entry in vector_shards:
        size = entry.shape[0]
        vectors.append(vector_all[:, offset:offset + size].reshape(parts * size).astype(jnp.float32))
        offset += size
    late = weight_shards[2].shape[1]
    expand_half = core_half(weight_shards[2])
    contract_half = core_half(weight_shards[3]).reshape(-1, late)

    def later_weights(after):
        first_b, second_b = gather_packed([expand_half, contract_half], after)
        e_rows = expand_half.shape[0]
        expand_weight = unpack_rows(first_b, second_b, 0, e_rows, (parts * weight_shards[2].shape[0], late))
        contract_weight = unpack_rows(
            first_b, second_b, e_rows, contract_half.shape[0],
            (parts * weight_shards[3].shape[0], weight_shards[3].shape[1]),
        )
        return expand_weight, contract_weight

    weights = (attention_weight, output_weight, later_weights)
    def exchange(rows):
        blocks = rows.reshape((parts, rows.shape[0] // parts) + rows.shape[1:])
        held = [lax.dynamic_index_in_dim(blocks, place, axis=0, keepdims=False)]
        for shift in range(1, parts):
            outgoing = lax.dynamic_index_in_dim(blocks, (place + shift) % parts, axis=0, keepdims=False)
            held.append(lax.ppermute(outgoing, "shard", [(i, (i + shift) % parts) for i in range(parts)]))
        stacked = jnp.stack(held[::-1], axis=0)
        doubled = jnp.concatenate([stacked, stacked], axis=0)
        start = (parts - (place + 1) % parts) % parts
        return lax.dynamic_slice_in_dim(doubled, start, parts, axis=0).reshape(rows.shape)

    def gather_rows(values, early=False):
        flat = values.reshape(clip_count * slot_count, width)
        moved = exchange(flat) if early else lax.all_to_all(flat, "shard", 0, 0, tiled=True)
        moved = moved.reshape(parts, own, slot_count, width)
        return jnp.transpose(moved, (1, 0, 2, 3)).reshape(own, parts * slot_count, width) if own > 1 else moved.reshape(own, parts * slot_count, width)

    def scatter_rows(values):
        rows = values.reshape(own, parts, slot_count, width)
        if own > 1:
            rows = jnp.transpose(rows, (1, 0, 2, 3))
        moved = lax.all_to_all(rows.reshape(own * parts * slot_count, width), "shard", 0, 0, tiled=True)
        return moved.reshape(clip_count, slot_count, width)

    tokens_clip = gather_rows(tokens, True)

    def cotangent_of(after):
        late = cotangent + (after * 0).astype(cotangent.dtype)
        return gather_rows(late)

    lengths_clip = lax.dynamic_slice_in_dim(lengths, place * own, own, axis=0)
    block_output, input_grad, weight_grads, vector_grads = clip_layer(
        tokens_clip, lengths_clip, cotangent_of, weights, vectors, lambda part, rows: finish_sum(part, rows // parts // 2)[0],
        scatter_rows,
    )
    input_grad = scatter_rows(input_grad)
    attention_grad = weight_grads[0]
    attention_width = attention_grad.shape[1]
    vector_parts = jnp.concatenate([entry.reshape(parts, -1) for entry in vector_grads], axis=1)
    vector_size = vector_parts.shape[1]
    vpad = (-vector_size) % attention_width
    vector_parts = jnp.pad(vector_parts, ((0, 0), (0, vpad))).reshape(parts, -1, attention_width)
    attention_part = shard_sum(chip_sum(attention_grad, vector_parts))
    output_part = weight_grads[1]
    (attention_total, vector_total), (output_total, _) = finish_many(
        [attention_part, output_part],
        [attention_grad.shape[0] // parts // 2, params[1].shape[0] // 2],
    )
    totals = (attention_total, output_total) + tuple(weight_grads[2:])
    vector_total = vector_total.reshape(-1)[:vector_size]
    vector_outs = []
    offset = 0
    for entry in vector_shards:
        size = entry.shape[0]
        vector_outs.append(vector_total[offset:offset + size])
        offset += size
    return (block_output, input_grad) + totals + tuple(vector_outs)


def split_rep(mesh):
    devices = mesh.devices
    rep, parts = devices.shape
    first = devices[0, 0]
    stride = None
    for index in range(1, rep):
        other = devices[index, 0]
        if tuple(other.coords) == tuple(first.coords) and other.core_on_chip != first.core_on_chip:
            stride = index
            break
    if stride is None or rep % (2 * stride):
        return None
    grid = devices.reshape(rep // (2 * stride), 2, stride, parts)
    for spot in np.ndindex(grid.shape[0], grid.shape[2], grid.shape[3]):
        low = grid[spot[0], 0, spot[1], spot[2]]
        high = grid[spot[0], 1, spot[1], spot[2]]
        if tuple(low.coords) != tuple(high.coords) or low.core_on_chip == high.core_on_chip:
            return None
    return Mesh(grid, ("outer", "core", "inner", "shard"))


def solution(mesh):
    def specs(rep):
        ins = (P(rep, "shard", None), P(rep, None), P(rep, "shard", None)) + (P("shard", None),) * 4 + (
            P("shard"),
        ) * 9
        outs = (P(rep, "shard", None), P(rep, "shard", None)) + (P("shard", None),) * 4 + (P("shard"),) * 9
        return ins, outs

    ins, outs = specs("rep")
    plain = jax.shard_map(local, mesh=mesh, in_specs=ins, out_specs=outs, check_vma=False)
    split = split_rep(mesh)
    if split is None:
        return plain
    ins, outs = specs(("outer", "core", "inner"))
    fast = jax.shard_map(clip_local, mesh=split, in_specs=ins, out_specs=outs, check_vma=False)
    rep, parts = mesh.devices.shape

    def run(*args):
        if (args[0].shape[0] // rep) % parts == 0:
            return fast(*args)
        return plain(*args)

    return run
```

```python
import jax
import jax.numpy as jnp
from jax import lax
from jax.sharding import Mesh, PartitionSpec as P
import numpy as np

HEADS = 12
HEAD = 64


EPSILON = 1e-05
NEGATIVE = -1e30


def norm_forward(values, gain, shift):
    centred = values - jnp.mean(values, axis=-1, keepdims=True)
    inverse = lax.rsqrt(jnp.mean(centred * centred, axis=-1, keepdims=True) + EPSILON)
    normed = centred * inverse
    return (normed, inverse, (normed * gain + shift).astype(jnp.bfloat16))


def norm_backward(upstream, normed, inverse, gain):
    scaled = upstream * gain
    return inverse * (
        scaled
        - jnp.mean(scaled, axis=-1, keepdims=True)
        - normed * jnp.mean(scaled * normed, axis=-1, keepdims=True)
    )


def gelu_slope(values):
    return (
        0.5 * (1.0 + jax.scipy.special.erf(values * 0.7071067811865476))
        + values * jnp.exp(-0.5 * values * values) * 0.3989422804014327
    )


def inner_rows(left, right):
    return lax.dot_general(
        left, right, (((0,), (0,)), ((), ())), preferred_element_type=jnp.float32
    )


def heads_view(matrix):
    return matrix.reshape(matrix.shape[0], HEADS, HEAD)


def score_block(query_rows, key_rows, key_live):
    scores = jnp.einsum(
        "qhd,khd->hqk",
        heads_view(query_rows),
        heads_view(key_rows),
        preferred_element_type=jnp.float32,
    ) * HEAD ** (-0.5)
    return jnp.where(key_live[None, None, :], scores, NEGATIVE)


def attend_clip(items):
    query_rows, pair_rows, key_live = items
    width = query_rows.shape[1]
    scores = score_block(query_rows, pair_rows[:, :width], key_live)
    highest = jnp.max(scores, axis=-1, keepdims=True)
    logsum = highest + jnp.log(jnp.sum(jnp.exp(scores - highest), axis=-1, keepdims=True))
    probs_low = jnp.exp(scores - logsum).astype(jnp.bfloat16)
    attended = jnp.einsum(
        "hqk,khd->qhd",
        probs_low,
        heads_view(pair_rows[:, width:]),
        preferred_element_type=jnp.float32,
    )
    return (attended.reshape(query_rows.shape[0], width).astype(jnp.bfloat16), logsum[:, :, 0].T)


def score_grads(query_rows, dattended, logsum, delta, pair_rows, key_live):
    width = query_rows.shape[1]
    scores = score_block(query_rows, pair_rows[:, :width], key_live)
    probs = jnp.exp(scores - logsum.T[:, :, None])
    dprob = jnp.einsum(
        "qhd,khd->hqk",
        heads_view(dattended),
        heads_view(pair_rows[:, width:]),
        preferred_element_type=jnp.float32,
    )
    dscore = (probs * (dprob - delta.T[:, :, None]) * HEAD ** (-0.5)).astype(jnp.bfloat16)
    return (probs.astype(jnp.bfloat16), dscore)


def both_grads(items):
    query_rows, dattended, logsum, delta, pair_rows, key_live = items
    width = query_rows.shape[1]
    probs_low, dscore = score_grads(query_rows, dattended, logsum, delta, pair_rows, key_live)
    dqueries = jnp.einsum(
        "hqk,khd->qhd", dscore, heads_view(pair_rows[:, :width]), preferred_element_type=jnp.float32
    ).reshape(query_rows.shape[0], width)
    dkeys = jnp.einsum(
        "hqk,qhd->khd", dscore, heads_view(query_rows), preferred_element_type=jnp.float32
    )
    dvalues = jnp.einsum(
        "hqk,qhd->khd", probs_low, heads_view(dattended), preferred_element_type=jnp.float32
    )
    key_count = pair_rows.shape[0]
    return (
        dqueries,
        jnp.concatenate(
            [dkeys.reshape(key_count, width), dvalues.reshape(key_count, width)], axis=1
        ),
    )


def local(
    tokens,
    lengths,
    cotangent,
    attention_weight,
    output_weight,
    expand_weight,
    contract_weight,
    first_gain,
    first_shift,
    query_bias,
    value_bias,
    output_bias,
    second_gain,
    second_shift,
    expand_bias,
    contract_bias,
):
    clip_count, slot_count, width = tokens.shape
    parts = lax.axis_size("shard")
    frame_count = slot_count * parts
    place = lax.axis_index("shard")
    row_total = clip_count * slot_count
    gathered = (
        lax.all_gather(attention_weight, "shard", axis=0, tiled=True),
        lax.all_gather(output_weight, "shard", axis=0, tiled=True),
        lax.all_gather(expand_weight, "shard", axis=0, tiled=True),
        lax.all_gather(contract_weight, "shard", axis=0, tiled=True),
        lax.all_gather(first_gain, "shard", axis=0, tiled=True),
        lax.all_gather(first_shift, "shard", axis=0, tiled=True),
        lax.all_gather(query_bias, "shard", axis=0, tiled=True),
        lax.all_gather(value_bias, "shard", axis=0, tiled=True),
        lax.all_gather(output_bias, "shard", axis=0, tiled=True),
        lax.all_gather(second_gain, "shard", axis=0, tiled=True),
        lax.all_gather(second_shift, "shard", axis=0, tiled=True),
        lax.all_gather(expand_bias, "shard", axis=0, tiled=True),
        lax.all_gather(contract_bias, "shard", axis=0, tiled=True),
    )
    vectors = [entry.astype(jnp.float32) for entry in gathered[4:]]
    own_length = jnp.sum(jnp.where(jnp.arange(parts)[None, :] == place, lengths, 0), axis=1)
    row_live = jnp.arange(slot_count)[None, :] < own_length[:, None]
    key_live = (jnp.arange(slot_count)[None, None, :] < lengths[:, :, None]).reshape(
        clip_count, frame_count
    )
    inputs = tokens.reshape(row_total, width).astype(jnp.float32)
    first_normed, first_inverse, first_act = norm_forward(inputs, vectors[0], vectors[1])
    mixed = jnp.dot(first_act, gathered[0], preferred_element_type=jnp.float32)
    mixed = mixed + jnp.concatenate([vectors[2], jnp.zeros_like(vectors[2]), vectors[3]])
    mixed_low = mixed.astype(jnp.bfloat16)
    query_rows = mixed_low[:, :width].reshape(clip_count, slot_count, width)
    pair_own = mixed_low[:, width:].reshape(clip_count, slot_count, 2 * width)
    pair_all = lax.all_gather(pair_own, "shard", axis=1, tiled=True)
    attended, logsum = lax.map(attend_clip, (query_rows, pair_all, key_live))
    attended_flat = attended.reshape(row_total, width)
    residual = (
        inputs
        + jnp.dot(attended_flat, gathered[1], preferred_element_type=jnp.float32)
        + vectors[4]
    )
    second_normed, second_inverse, second_act = norm_forward(residual, vectors[5], vectors[6])
    pre = jnp.dot(second_act, gathered[2], preferred_element_type=jnp.float32) + vectors[7]
    hidden_act = jax.nn.gelu(pre, approximate=False).astype(jnp.bfloat16)
    block_output = (
        residual + jnp.dot(hidden_act, gathered[3], preferred_element_type=jnp.float32) + vectors[8]
    )
    backward = (
        lax.all_gather(attention_weight, "shard", axis=0, tiled=True),
        lax.all_gather(output_weight, "shard", axis=0, tiled=True),
        lax.all_gather(expand_weight, "shard", axis=0, tiled=True),
        lax.all_gather(contract_weight, "shard", axis=0, tiled=True),
        lax.all_gather(first_gain, "shard", axis=0, tiled=True),
        lax.all_gather(first_shift, "shard", axis=0, tiled=True),
        lax.all_gather(query_bias, "shard", axis=0, tiled=True),
        lax.all_gather(value_bias, "shard", axis=0, tiled=True),
        lax.all_gather(output_bias, "shard", axis=0, tiled=True),
        lax.all_gather(second_gain, "shard", axis=0, tiled=True),
        lax.all_gather(second_shift, "shard", axis=0, tiled=True),
        lax.all_gather(expand_bias, "shard", axis=0, tiled=True),
        lax.all_gather(contract_bias, "shard", axis=0, tiled=True),
    )
    back_vectors = [entry.astype(jnp.float32) for entry in backward[4:]]
    error = cotangent.reshape(row_total, width) * row_live.reshape(row_total, 1).astype(jnp.float32)
    error_low = error.astype(jnp.bfloat16)
    contract_bias_grad = jnp.sum(error, axis=0)
    contract_grad = inner_rows(hidden_act, error_low)
    dpre = lax.dot_general(
        error_low, backward[3], (((1,), (1,)), ((), ())), preferred_element_type=jnp.float32
    ) * gelu_slope(pre)
    expand_bias_grad = jnp.sum(dpre, axis=0)
    dpre_low = dpre.astype(jnp.bfloat16)
    expand_grad = inner_rows(second_act, dpre_low)
    dsecond = lax.dot_general(
        dpre_low, backward[2], (((1,), (1,)), ((), ())), preferred_element_type=jnp.float32
    )
    second_gain_grad = jnp.sum(dsecond * second_normed, axis=0)
    second_shift_grad = jnp.sum(dsecond, axis=0)
    dresidual = error + norm_backward(dsecond, second_normed, second_inverse, back_vectors[5])
    output_bias_grad = jnp.sum(dresidual, axis=0)
    dresidual_low = dresidual.astype(jnp.bfloat16)
    output_grad = inner_rows(attended_flat, dresidual_low)
    dattended = lax.dot_general(
        dresidual_low, backward[1], (((1,), (1,)), ((), ())), preferred_element_type=jnp.float32
    ).astype(jnp.bfloat16)
    delta = jnp.sum(
        heads_view(dattended.astype(jnp.float32)) * heads_view(attended_flat.astype(jnp.float32)),
        axis=-1,
    )
    delta = delta.reshape(clip_count, slot_count, HEADS)
    dattended_clips = dattended.reshape(clip_count, slot_count, width)
    dqueries, pair_terms = lax.map(
        both_grads, (query_rows, dattended_clips, logsum, delta, pair_all, key_live)
    )
    pair_grads = lax.psum_scatter(pair_terms, "shard", scatter_dimension=1, tiled=True)
    dqueries_flat = dqueries.reshape(row_total, width)
    pair_flat = pair_grads.reshape(row_total, 2 * width)
    dmixed = jnp.concatenate([dqueries_flat, pair_flat], axis=1)
    query_bias_grad = jnp.sum(dqueries_flat, axis=0)
    value_bias_grad = jnp.sum(pair_flat[:, width:], axis=0)
    dmixed_low = dmixed.astype(jnp.bfloat16)
    attention_grad = inner_rows(first_act, dmixed_low)
    dfirst = lax.dot_general(
        dmixed_low, backward[0], (((1,), (1,)), ((), ())), preferred_element_type=jnp.float32
    )
    first_gain_grad = jnp.sum(dfirst * first_normed, axis=0)
    first_shift_grad = jnp.sum(dfirst, axis=0)
    input_grad = dresidual + norm_backward(dfirst, first_normed, first_inverse, back_vectors[0])
    shares = (
        lax.psum_scatter(attention_grad, "shard", scatter_dimension=0, tiled=True),
        lax.psum_scatter(output_grad, "shard", scatter_dimension=0, tiled=True),
        lax.psum_scatter(expand_grad, "shard", scatter_dimension=0, tiled=True),
        lax.psum_scatter(contract_grad, "shard", scatter_dimension=0, tiled=True),
        lax.psum_scatter(first_gain_grad, "shard", scatter_dimension=0, tiled=True),
        lax.psum_scatter(first_shift_grad, "shard", scatter_dimension=0, tiled=True),
        lax.psum_scatter(query_bias_grad, "shard", scatter_dimension=0, tiled=True),
        lax.psum_scatter(value_bias_grad, "shard", scatter_dimension=0, tiled=True),
        lax.psum_scatter(output_bias_grad, "shard", scatter_dimension=0, tiled=True),
        lax.psum_scatter(second_gain_grad, "shard", scatter_dimension=0, tiled=True),
        lax.psum_scatter(second_shift_grad, "shard", scatter_dimension=0, tiled=True),
        lax.psum_scatter(expand_bias_grad, "shard", scatter_dimension=0, tiled=True),
        lax.psum_scatter(contract_bias_grad, "shard", scatter_dimension=0, tiled=True),
    )
    totals = lax.psum(
        (
            shares[0],
            shares[1],
            shares[2],
            shares[3],
            shares[4],
            shares[5],
            shares[6],
            shares[7],
            shares[8],
            shares[9],
            shares[10],
            shares[11],
            shares[12],
        ),
        "rep",
    )
    return (
        block_output.reshape(clip_count, slot_count, width),
        input_grad.reshape(clip_count, slot_count, width),
        totals[0],
        totals[1],
        totals[2],
        totals[3],
        totals[4],
        totals[5],
        totals[6],
        totals[7],
        totals[8],
        totals[9],
        totals[10],
        totals[11],
        totals[12],
    )


def clip_layer(tokens, lengths, cotangent_of, weights, vectors, reduce, send_out):
    attention_weight, output_weight, later_weights = weights
    (first_gain, first_shift, query_bias, value_bias, output_bias, second_gain, second_shift,
     expand_bias, contract_bias) = vectors
    clip_count, frame_count, width = tokens.shape
    block_count = lengths.shape[1]
    slot_count = frame_count // block_count
    rows = clip_count * frame_count
    live = (jnp.arange(slot_count)[None, None, :] < lengths[:, :, None]).reshape(clip_count, frame_count)
    scale = HEAD ** (-0.5)
    inputs = tokens.reshape(rows, width).astype(jnp.float32)
    first_normed, first_inverse, first_act = norm_forward(inputs, first_gain, first_shift)
    mixed = jnp.dot(first_act, attention_weight, preferred_element_type=jnp.float32)
    mixed = mixed + jnp.concatenate([query_bias, jnp.zeros_like(query_bias), value_bias])
    mixed_low = mixed.astype(jnp.bfloat16).reshape(clip_count, frame_count, 3, HEADS, HEAD)
    queries = mixed_low[:, :, 0]
    keys = mixed_low[:, :, 1]
    values = mixed_low[:, :, 2]
    scores = jnp.einsum("cqhd,ckhd->chqk", queries, keys, preferred_element_type=jnp.float32) * scale
    scores = jnp.where(live[:, None, None, :], scores, NEGATIVE)
    highest = jnp.max(scores, axis=-1, keepdims=True)
    logsum = highest + jnp.log(jnp.sum(jnp.exp(scores - highest), axis=-1, keepdims=True))
    probs = jnp.exp(scores - logsum)
    expand_weight, contract_weight = later_weights(logsum[0, 0, 0, :1])
    probs_low = probs.astype(jnp.bfloat16)
    attended = jnp.einsum("chqk,ckhd->cqhd", probs_low, values, preferred_element_type=jnp.float32)
    attended_flat = attended.reshape(rows, width).astype(jnp.bfloat16)
    residual = inputs + jnp.dot(attended_flat, output_weight, preferred_element_type=jnp.float32) + output_bias
    second_normed, second_inverse, second_act = norm_forward(residual, second_gain, second_shift)
    pre = jnp.dot(second_act, expand_weight, preferred_element_type=jnp.float32) + expand_bias
    hidden_act = jax.nn.gelu(pre, approximate=False).astype(jnp.bfloat16)
    block_output = residual + jnp.dot(hidden_act, contract_weight, preferred_element_type=jnp.float32) + contract_bias
    cotangent = cotangent_of(pre[0, :1])
    error = cotangent.reshape(rows, width) * live.reshape(rows, 1).astype(jnp.float32)
    error_low = error.astype(jnp.bfloat16)
    contract_bias_grad = jnp.sum(error, axis=0)
    contract_grad = inner_rows(hidden_act, error_low)
    contract_chip = chip_sum(contract_grad)
    dpre = lax.dot_general(
        error_low, contract_weight, (((1,), (1,)), ((), ())), preferred_element_type=jnp.float32
    ) * gelu_slope(pre)
    expand_bias_grad = jnp.sum(dpre, axis=0)
    dpre_low = dpre.astype(jnp.bfloat16)
    contract_chip, dpre_low = lax.optimization_barrier((contract_chip, dpre_low))
    contract_part = shard_sum(contract_chip)
    expand_grad = inner_rows(second_act, dpre_low)
    expand_chip = chip_sum(expand_grad)
    dsecond = lax.optimization_barrier(lax.dot_general(
        dpre_low, expand_weight, (((1,), (1,)), ((), ())), preferred_element_type=jnp.float32
    ))
    second_gain_grad = jnp.sum(dsecond * second_normed, axis=0)
    second_shift_grad = jnp.sum(dsecond, axis=0)
    dresidual = error + norm_backward(dsecond, second_normed, second_inverse, second_gain)
    output_bias_grad = jnp.sum(dresidual, axis=0)
    dresidual_low = dresidual.astype(jnp.bfloat16)
    sent_output = send_out(block_output)
    expand_chip, dresidual_low = lax.optimization_barrier((expand_chip, dresidual_low))
    expand_part = shard_sum(expand_chip)
    output_grad = inner_rows(attended_flat, dresidual_low)
    output_chip = chip_sum(output_grad)
    dattended = lax.dot_general(
        dresidual_low, output_weight, (((1,), (1,)), ((), ())), preferred_element_type=jnp.float32
    ).astype(jnp.bfloat16)
    contract_part, output_chip, dattended = lax.optimization_barrier((contract_part, output_chip, dattended))
    output_part = shard_sum(output_chip)
    dattended_heads = dattended.reshape(clip_count, frame_count, HEADS, HEAD)
    attended_heads = attended_flat.reshape(clip_count, frame_count, HEADS, HEAD)
    delta = jnp.sum(
        dattended_heads.astype(jnp.float32) * attended_heads.astype(jnp.float32), axis=-1
    )
    dprob = jnp.einsum("cqhd,ckhd->chqk", dattended_heads, values, preferred_element_type=jnp.float32)
    dscore = (probs * (dprob - jnp.transpose(delta, (0, 2, 1))[:, :, :, None]) * scale).astype(jnp.bfloat16)
    dqueries = jnp.einsum("chqk,ckhd->cqhd", dscore, keys, preferred_element_type=jnp.float32)
    dkeys = jnp.einsum("chqk,cqhd->ckhd", dscore, queries, preferred_element_type=jnp.float32)
    dvalues = jnp.einsum("chqk,cqhd->ckhd", probs_low, dattended_heads, preferred_element_type=jnp.float32)
    dmixed = jnp.concatenate(
        [dqueries.reshape(rows, width), dkeys.reshape(rows, width), dvalues.reshape(rows, width)], axis=1
    )
    query_bias_grad = jnp.sum(dmixed[:, :width], axis=0)
    value_bias_grad = jnp.sum(dmixed[:, 2 * width:], axis=0)
    dmixed_low = dmixed.astype(jnp.bfloat16)
    contract_total = reduce(contract_part, contract_grad.shape[0])
    output_part, expand_part, contract_total, sent_output, dmixed_low = lax.optimization_barrier(
        (output_part, expand_part, contract_total, sent_output, dmixed_low)
    )
    expand_total = reduce(expand_part, expand_grad.shape[0])
    attention_grad = inner_rows(first_act, dmixed_low)
    dfirst = lax.optimization_barrier(lax.dot_general(
        dmixed_low, attention_weight, (((1,), (1,)), ((), ())), preferred_element_type=jnp.float32
    ))
    first_gain_grad = jnp.sum(dfirst * first_normed, axis=0)
    first_shift_grad = jnp.sum(dfirst, axis=0)
    input_grad = dresidual + norm_backward(dfirst, first_normed, first_inverse, first_gain)
    output_part, expand_total, input_grad = lax.optimization_barrier((output_part, expand_total, input_grad))
    weight_grads = (attention_grad, output_part, expand_total, contract_total)
    vector_grads = (first_gain_grad, first_shift_grad, query_bias_grad, value_bias_grad, output_bias_grad,
                    second_gain_grad, second_shift_grad, expand_bias_grad, contract_bias_grad)
    return (
        sent_output,
        input_grad,
        weight_grads,
        vector_grads,
    )


PAIR = [(0, 1), (1, 0)]
OUTER = ("outer", "inner")


def core_pick(core, first, second):
    return jnp.where(core == 0, first, second)


def gather_weight(shard_rows, extra=None):
    parts = lax.axis_size("shard")
    core = lax.axis_index("core")
    rows, width = shard_rows.shape
    half = rows // 2
    mine = lax.dynamic_slice_in_dim(shard_rows, core * half, half, axis=0)
    if extra is not None:
        mine = jnp.concatenate([mine, extra], axis=0)
    mine = lax.all_gather(mine, "shard", axis=0, tiled=False)
    other = lax.ppermute(mine, "core", PAIR)
    first = core_pick(core, mine, other)
    second = core_pick(core, other, mine)
    full = jnp.stack([first[:, :half], second[:, :half]], axis=1).reshape(parts * rows, width)
    if extra is None:
        return full, None
    return full, first[:, half:]


def chip_sum(grad, extra=None):
    parts = lax.axis_size("shard")
    core = lax.axis_index("core")
    width = grad.shape[1]
    rows = grad.shape[0] // parts
    half = rows // 2
    quarters = grad.reshape(parts, 2, half, width)
    keep = lax.dynamic_index_in_dim(quarters, core, axis=1, keepdims=False)
    send = lax.dynamic_index_in_dim(quarters, 1 - core, axis=1, keepdims=False)
    if extra is not None:
        on_first = (core == 0).astype(extra.dtype)
        keep = jnp.concatenate([keep, extra * on_first], axis=1)
        send = jnp.concatenate([send, extra * (1 - on_first)], axis=1)
    return keep + lax.ppermute(send, "core", PAIR)


def shard_sum(chip):
    part = lax.psum_scatter(chip, "shard", scatter_dimension=0, tiled=False)
    if lax.axis_size("inner") > 1:
        part = lax.psum(part, "inner")
    return part


def finish_sum(part, half):
    core = lax.axis_index("core")
    total = line_sum(part)
    other = lax.ppermute(total, "core", PAIR)
    first = core_pick(core, total, other)
    second = core_pick(core, other, total)
    return jnp.concatenate([first[:half], second[:half]], axis=0), first[half:]


def finish_many(parts, halves):
    core = lax.axis_index("core")
    flat = jnp.concatenate([part.reshape(-1) for part in parts])
    total = line_sum(flat)
    other = lax.ppermute(total, "core", PAIR)
    first = core_pick(core, total, other)
    second = core_pick(core, other, total)
    outs = []
    offset = 0
    for part, half in zip(parts, halves):
        size = part.size
        low = first[offset:offset + size].reshape(part.shape)
        high = second[offset:offset + size].reshape(part.shape)
        outs.append((jnp.concatenate([low[:half], high[:half]], axis=0), low[half:]))
        offset += size
    return outs


def reduce_weight(grad, extra=None):
    half = grad.shape[0] // lax.axis_size("shard") // 2
    return finish_sum(shard_sum(chip_sum(grad, extra)), half)


def line_sum(values):
    groups = lax.axis_size("outer")
    if groups == 1:
        return values
    if groups & (groups - 1):
        return lax.psum(values, "outer")
    here = lax.axis_index("outer")
    length = values.shape[0]
    padded = -(-length // groups) * groups
    held = jnp.pad(values, ((0, padded - length),) + ((0, 0),) * (values.ndim - 1))
    held = held.reshape((groups, padded // groups) + values.shape[1:])
    step = 1
    while step < groups:
        held = held.reshape((held.shape[0] // 2, 2) + held.shape[1:])
        bit = (here // step) % 2
        keep = lax.dynamic_index_in_dim(held, bit, axis=1, keepdims=False)
        send = lax.dynamic_index_in_dim(held, 1 - bit, axis=1, keepdims=False)
        held = keep + lax.ppermute(send, "outer", [(j, j ^ step) for j in range(groups)])
        step *= 2
    step = groups // 2
    while step >= 1:
        bit = (here // step) % 2
        other = lax.ppermute(held, "outer", [(j, j ^ step) for j in range(groups)])
        low = jnp.where(bit == 0, held, other)
        high = jnp.where(bit == 0, other, held)
        held = jnp.stack([low, high], axis=1)
        held = held.reshape((held.shape[0] * 2,) + held.shape[2:])
        step //= 2
    return held.reshape((padded,) + values.shape[1:])[:length]


def gather_packed(blocks, after=None):
    core = lax.axis_index("core")
    mine = lax.all_gather(jnp.concatenate(blocks, axis=0), "shard", axis=0, tiled=False)
    if after is not None:
        mine = mine + (after * 0).astype(mine.dtype)
    other = lax.ppermute(mine, "core", PAIR)
    return core_pick(core, mine, other), core_pick(core, other, mine)


def unpack_rows(first, second, begin, count, shape):
    parts = first.shape[0]
    rows, width = shape
    low = first[:, begin:begin + count].reshape(parts, -1, width)
    high = second[:, begin:begin + count].reshape(parts, -1, width)
    return jnp.stack([low, high], axis=1).reshape(rows, width)


def core_half(shard_rows):
    core = lax.axis_index("core")
    half = shard_rows.shape[0] // 2
    return lax.dynamic_slice_in_dim(shard_rows, core * half, half, axis=0)


def clip_local(tokens, lengths, cotangent, *params):
    clip_count, slot_count, width = tokens.shape
    parts = lax.axis_size("shard")
    place = lax.axis_index("shard")
    own = clip_count // parts
    weight_shards = params[:4]
    vector_shards = params[4:]
    wide = weight_shards[0].shape[1]
    vector_row = jnp.concatenate([entry.reshape(-1) for entry in vector_shards])
    pad = (-vector_row.shape[0]) % wide
    vector_rows = jnp.pad(vector_row, (0, pad)).reshape(-1, wide)
    attention_half = core_half(weight_shards[0])
    output_half = core_half(weight_shards[1]).reshape(-1, wide)
    first, second = gather_packed([attention_half, output_half, vector_rows])
    a_rows = attention_half.shape[0]
    o_rows = output_half.shape[0]
    attention_weight = unpack_rows(first, second, 0, a_rows, (parts * weight_shards[0].shape[0], wide))
    output_weight = unpack_rows(
        first, second, a_rows, o_rows, (parts * weight_shards[1].shape[0], weight_shards[1].shape[1])
    )
    vector_all = first[:, a_rows + o_rows:].reshape(parts, -1)[:, : vector_row.shape[0]]
    vectors = []
    offset = 0
    for entry in vector_shards:
        size = entry.shape[0]
        vectors.append(vector_all[:, offset:offset + size].reshape(parts * size).astype(jnp.float32))
        offset += size
    late = weight_shards[2].shape[1]
    expand_half = core_half(weight_shards[2])
    contract_half = core_half(weight_shards[3]).reshape(-1, late)

    def later_weights(after):
        first_b, second_b = gather_packed([expand_half, contract_half], after)
        e_rows = expand_half.shape[0]
        expand_weight = unpack_rows(first_b, second_b, 0, e_rows, (parts * weight_shards[2].shape[0], late))
        contract_weight = unpack_rows(
            first_b, second_b, e_rows, contract_half.shape[0],
            (parts * weight_shards[3].shape[0], weight_shards[3].shape[1]),
        )
        return expand_weight, contract_weight

    weights = (attention_weight, output_weight, later_weights)
    def exchange(rows):
        blocks = rows.reshape((parts, rows.shape[0] // parts) + rows.shape[1:])
        held = [lax.dynamic_index_in_dim(blocks, place, axis=0, keepdims=False)]
        for shift in range(1, parts):
            outgoing = lax.dynamic_index_in_dim(blocks, (place + shift) % parts, axis=0, keepdims=False)
            held.append(lax.ppermute(outgoing, "shard", [(i, (i + shift) % parts) for i in range(parts)]))
        stacked = jnp.stack(held[::-1], axis=0)
        doubled = jnp.concatenate([stacked, stacked], axis=0)
        start = (parts - (place + 1) % parts) % parts
        return lax.dynamic_slice_in_dim(doubled, start, parts, axis=0).reshape(rows.shape)

    def gather_rows(values, early=False):
        flat = values.reshape(clip_count * slot_count, width)
        moved = exchange(flat) if early else lax.all_to_all(flat, "shard", 0, 0, tiled=True)
        moved = moved.reshape(parts, own, slot_count, width)
        return jnp.transpose(moved, (1, 0, 2, 3)).reshape(own, parts * slot_count, width) if own > 1 else moved.reshape(own, parts * slot_count, width)

    def scatter_rows(values):
        rows = values.reshape(own, parts, slot_count, width)
        if own > 1:
            rows = jnp.transpose(rows, (1, 0, 2, 3))
        moved = lax.all_to_all(rows.reshape(own * parts * slot_count, width), "shard", 0, 0, tiled=True)
        return moved.reshape(clip_count, slot_count, width)

    tokens_clip = gather_rows(tokens, True)

    def cotangent_of(after):
        late = cotangent + (after * 0).astype(cotangent.dtype)
        return gather_rows(late)

    lengths_clip = lax.dynamic_slice_in_dim(lengths, place * own, own, axis=0)
    block_output, input_grad, weight_grads, vector_grads = clip_layer(
        tokens_clip, lengths_clip, cotangent_of, weights, vectors, lambda part, rows: finish_sum(part, rows // parts // 2)[0],
        scatter_rows,
    )
    input_grad = scatter_rows(input_grad)
    attention_grad = weight_grads[0]
    attention_width = attention_grad.shape[1]
    vector_parts = jnp.concatenate([entry.reshape(parts, -1) for entry in vector_grads], axis=1)
    vector_size = vector_parts.shape[1]
    vpad = (-vector_size) % attention_width
    vector_parts = jnp.pad(vector_parts, ((0, 0), (0, vpad))).reshape(parts, -1, attention_width)
    attention_part = shard_sum(chip_sum(attention_grad, vector_parts))
    output_part = weight_grads[1]
    (attention_total, vector_total), (output_total, _) = finish_many(
        [attention_part, output_part],
        [attention_grad.shape[0] // parts // 2, params[1].shape[0] // 2],
    )
    totals = (attention_total, output_total) + tuple(weight_grads[2:])
    vector_total = vector_total.reshape(-1)[:vector_size]
    vector_outs = []
    offset = 0
    for entry in vector_shards:
        size = entry.shape[0]
        vector_outs.append(vector_total[offset:offset + size])
        offset += size
    return (block_output, input_grad) + totals + tuple(vector_outs)


def split_rep(mesh):
    devices = mesh.devices
    rep, parts = devices.shape
    first = devices[0, 0]
    stride = None
    for index in range(1, rep):
        other = devices[index, 0]
        if tuple(other.coords) == tuple(first.coords) and other.core_on_chip != first.core_on_chip:
            stride = index
            break
    if stride is None or rep % (2 * stride):
        return None
    grid = devices.reshape(rep // (2 * stride), 2, stride, parts)
    for spot in np.ndindex(grid.shape[0], grid.shape[2], grid.shape[3]):
        low = grid[spot[0], 0, spot[1], spot[2]]
        high = grid[spot[0], 1, spot[1], spot[2]]
        if tuple(low.coords) != tuple(high.coords) or low.core_on_chip == high.core_on_chip:
            return None
    return Mesh(grid, ("outer", "core", "inner", "shard"))


def solution(mesh):
    def specs(rep):
        ins = (P(rep, "shard", None), P(rep, None), P(rep, "shard", None)) + (P("shard", None),) * 4 + (
            P("shard"),
        ) * 9
        outs = (P(rep, "shard", None), P(rep, "shard", None)) + (P("shard", None),) * 4 + (P("shard"),) * 9
        return ins, outs

    ins, outs = specs("rep")
    plain = jax.shard_map(local, mesh=mesh, in_specs=ins, out_specs=outs, check_vma=False)
    split = split_rep(mesh)
    if split is None:
        return plain
    ins, outs = specs(("outer", "core", "inner"))
    fast = jax.shard_map(clip_local, mesh=split, in_specs=ins, out_specs=outs, check_vma=False)
    rep, parts = mesh.devices.shape

    def run(*args):
        if (args[0].shape[0] // rep) % parts == 0:
            return fast(*args)
        return plain(*args)

    return run
```

```python
import jax
import jax.numpy as jnp
from jax import lax
from jax.sharding import Mesh, PartitionSpec as P
import numpy as np

HEADS = 12
HEAD = 64


EPSILON = 1e-05
NEGATIVE = -1e30


def norm_forward(values, gain, shift):
    centred = values - jnp.mean(values, axis=-1, keepdims=True)
    inverse = lax.rsqrt(jnp.mean(centred * centred, axis=-1, keepdims=True) + EPSILON)
    normed = centred * inverse
    return (normed, inverse, (normed * gain + shift).astype(jnp.bfloat16))


def norm_backward(upstream, normed, inverse, gain):
    scaled = upstream * gain
    return inverse * (
        scaled
        - jnp.mean(scaled, axis=-1, keepdims=True)
        - normed * jnp.mean(scaled * normed, axis=-1, keepdims=True)
    )


def gelu_slope(values):
    return (
        0.5 * (1.0 + jax.scipy.special.erf(values * 0.7071067811865476))
        + values * jnp.exp(-0.5 * values * values) * 0.3989422804014327
    )


def inner_rows(left, right):
    return lax.dot_general(
        left, right, (((0,), (0,)), ((), ())), preferred_element_type=jnp.float32
    )


def heads_view(matrix):
    return matrix.reshape(matrix.shape[0], HEADS, HEAD)


def score_block(query_rows, key_rows, key_live):
    scores = jnp.einsum(
        "qhd,khd->hqk",
        heads_view(query_rows),
        heads_view(key_rows),
        preferred_element_type=jnp.float32,
    ) * HEAD ** (-0.5)
    return jnp.where(key_live[None, None, :], scores, NEGATIVE)


def attend_clip(items):
    query_rows, pair_rows, key_live = items
    width = query_rows.shape[1]
    scores = score_block(query_rows, pair_rows[:, :width], key_live)
    highest = jnp.max(scores, axis=-1, keepdims=True)
    logsum = highest + jnp.log(jnp.sum(jnp.exp(scores - highest), axis=-1, keepdims=True))
    probs_low = jnp.exp(scores - logsum).astype(jnp.bfloat16)
    attended = jnp.einsum(
        "hqk,khd->qhd",
        probs_low,
        heads_view(pair_rows[:, width:]),
        preferred_element_type=jnp.float32,
    )
    return (attended.reshape(query_rows.shape[0], width).astype(jnp.bfloat16), logsum[:, :, 0].T)


def score_grads(query_rows, dattended, logsum, delta, pair_rows, key_live):
    width = query_rows.shape[1]
    scores = score_block(query_rows, pair_rows[:, :width], key_live)
    probs = jnp.exp(scores - logsum.T[:, :, None])
    dprob = jnp.einsum(
        "qhd,khd->hqk",
        heads_view(dattended),
        heads_view(pair_rows[:, width:]),
        preferred_element_type=jnp.float32,
    )
    dscore = (probs * (dprob - delta.T[:, :, None]) * HEAD ** (-0.5)).astype(jnp.bfloat16)
    return (probs.astype(jnp.bfloat16), dscore)


def both_grads(items):
    query_rows, dattended, logsum, delta, pair_rows, key_live = items
    width = query_rows.shape[1]
    probs_low, dscore = score_grads(query_rows, dattended, logsum, delta, pair_rows, key_live)
    dqueries = jnp.einsum(
        "hqk,khd->qhd", dscore, heads_view(pair_rows[:, :width]), preferred_element_type=jnp.float32
    ).reshape(query_rows.shape[0], width)
    dkeys = jnp.einsum(
        "hqk,qhd->khd", dscore, heads_view(query_rows), preferred_element_type=jnp.float32
    )
    dvalues = jnp.einsum(
        "hqk,qhd->khd", probs_low, heads_view(dattended), preferred_element_type=jnp.float32
    )
    key_count = pair_rows.shape[0]
    return (
        dqueries,
        jnp.concatenate(
            [dkeys.reshape(key_count, width), dvalues.reshape(key_count, width)], axis=1
        ),
    )


def local(
    tokens,
    lengths,
    cotangent,
    attention_weight,
    output_weight,
    expand_weight,
    contract_weight,
    first_gain,
    first_shift,
    query_bias,
    value_bias,
    output_bias,
    second_gain,
    second_shift,
    expand_bias,
    contract_bias,
):
    clip_count, slot_count, width = tokens.shape
    parts = lax.axis_size("shard")
    frame_count = slot_count * parts
    place = lax.axis_index("shard")
    row_total = clip_count * slot_count
    gathered = (
        lax.all_gather(attention_weight, "shard", axis=0, tiled=True),
        lax.all_gather(output_weight, "shard", axis=0, tiled=True),
        lax.all_gather(expand_weight, "shard", axis=0, tiled=True),
        lax.all_gather(contract_weight, "shard", axis=0, tiled=True),
        lax.all_gather(first_gain, "shard", axis=0, tiled=True),
        lax.all_gather(first_shift, "shard", axis=0, tiled=True),
        lax.all_gather(query_bias, "shard", axis=0, tiled=True),
        lax.all_gather(value_bias, "shard", axis=0, tiled=True),
        lax.all_gather(output_bias, "shard", axis=0, tiled=True),
        lax.all_gather(second_gain, "shard", axis=0, tiled=True),
        lax.all_gather(second_shift, "shard", axis=0, tiled=True),
        lax.all_gather(expand_bias, "shard", axis=0, tiled=True),
        lax.all_gather(contract_bias, "shard", axis=0, tiled=True),
    )
    vectors = [entry.astype(jnp.float32) for entry in gathered[4:]]
    own_length = jnp.sum(jnp.where(jnp.arange(parts)[None, :] == place, lengths, 0), axis=1)
    row_live = jnp.arange(slot_count)[None, :] < own_length[:, None]
    key_live = (jnp.arange(slot_count)[None, None, :] < lengths[:, :, None]).reshape(
        clip_count, frame_count
    )
    inputs = tokens.reshape(row_total, width).astype(jnp.float32)
    first_normed, first_inverse, first_act = norm_forward(inputs, vectors[0], vectors[1])
    mixed = jnp.dot(first_act, gathered[0], preferred_element_type=jnp.float32)
    mixed = mixed + jnp.concatenate([vectors[2], jnp.zeros_like(vectors[2]), vectors[3]])
    mixed_low = mixed.astype(jnp.bfloat16)
    query_rows = mixed_low[:, :width].reshape(clip_count, slot_count, width)
    pair_own = mixed_low[:, width:].reshape(clip_count, slot_count, 2 * width)
    pair_all = lax.all_gather(pair_own, "shard", axis=1, tiled=True)
    attended, logsum = lax.map(attend_clip, (query_rows, pair_all, key_live))
    attended_flat = attended.reshape(row_total, width)
    residual = (
        inputs
        + jnp.dot(attended_flat, gathered[1], preferred_element_type=jnp.float32)
        + vectors[4]
    )
    second_normed, second_inverse, second_act = norm_forward(residual, vectors[5], vectors[6])
    pre = jnp.dot(second_act, gathered[2], preferred_element_type=jnp.float32) + vectors[7]
    hidden_act = jax.nn.gelu(pre, approximate=False).astype(jnp.bfloat16)
    block_output = (
        residual + jnp.dot(hidden_act, gathered[3], preferred_element_type=jnp.float32) + vectors[8]
    )
    backward = (
        lax.all_gather(attention_weight, "shard", axis=0, tiled=True),
        lax.all_gather(output_weight, "shard", axis=0, tiled=True),
        lax.all_gather(expand_weight, "shard", axis=0, tiled=True),
        lax.all_gather(contract_weight, "shard", axis=0, tiled=True),
        lax.all_gather(first_gain, "shard", axis=0, tiled=True),
        lax.all_gather(first_shift, "shard", axis=0, tiled=True),
        lax.all_gather(query_bias, "shard", axis=0, tiled=True),
        lax.all_gather(value_bias, "shard", axis=0, tiled=True),
        lax.all_gather(output_bias, "shard", axis=0, tiled=True),
        lax.all_gather(second_gain, "shard", axis=0, tiled=True),
        lax.all_gather(second_shift, "shard", axis=0, tiled=True),
        lax.all_gather(expand_bias, "shard", axis=0, tiled=True),
        lax.all_gather(contract_bias, "shard", axis=0, tiled=True),
    )
    back_vectors = [entry.astype(jnp.float32) for entry in backward[4:]]
    error = cotangent.reshape(row_total, width) * row_live.reshape(row_total, 1).astype(jnp.float32)
    error_low = error.astype(jnp.bfloat16)
    contract_bias_grad = jnp.sum(error, axis=0)
    contract_grad = inner_rows(hidden_act, error_low)
    dpre = lax.dot_general(
        error_low, backward[3], (((1,), (1,)), ((), ())), preferred_element_type=jnp.float32
    ) * gelu_slope(pre)
    expand_bias_grad = jnp.sum(dpre, axis=0)
    dpre_low = dpre.astype(jnp.bfloat16)
    expand_grad = inner_rows(second_act, dpre_low)
    dsecond = lax.dot_general(
        dpre_low, backward[2], (((1,), (1,)), ((), ())), preferred_element_type=jnp.float32
    )
    second_gain_grad = jnp.sum(dsecond * second_normed, axis=0)
    second_shift_grad = jnp.sum(dsecond, axis=0)
    dresidual = error + norm_backward(dsecond, second_normed, second_inverse, back_vectors[5])
    output_bias_grad = jnp.sum(dresidual, axis=0)
    dresidual_low = dresidual.astype(jnp.bfloat16)
    output_grad = inner_rows(attended_flat, dresidual_low)
    dattended = lax.dot_general(
        dresidual_low, backward[1], (((1,), (1,)), ((), ())), preferred_element_type=jnp.float32
    ).astype(jnp.bfloat16)
    delta = jnp.sum(
        heads_view(dattended.astype(jnp.float32)) * heads_view(attended_flat.astype(jnp.float32)),
        axis=-1,
    )
    delta = delta.reshape(clip_count, slot_count, HEADS)
    dattended_clips = dattended.reshape(clip_count, slot_count, width)
    dqueries, pair_terms = lax.map(
        both_grads, (query_rows, dattended_clips, logsum, delta, pair_all, key_live)
    )
    pair_grads = lax.psum_scatter(pair_terms, "shard", scatter_dimension=1, tiled=True)
    dqueries_flat = dqueries.reshape(row_total, width)
    pair_flat = pair_grads.reshape(row_total, 2 * width)
    dmixed = jnp.concatenate([dqueries_flat, pair_flat], axis=1)
    query_bias_grad = jnp.sum(dqueries_flat, axis=0)
    value_bias_grad = jnp.sum(pair_flat[:, width:], axis=0)
    dmixed_low = dmixed.astype(jnp.bfloat16)
    attention_grad = inner_rows(first_act, dmixed_low)
    dfirst = lax.dot_general(
        dmixed_low, backward[0], (((1,), (1,)), ((), ())), preferred_element_type=jnp.float32
    )
    first_gain_grad = jnp.sum(dfirst * first_normed, axis=0)
    first_shift_grad = jnp.sum(dfirst, axis=0)
    input_grad = dresidual + norm_backward(dfirst, first_normed, first_inverse, back_vectors[0])
    shares = (
        lax.psum_scatter(attention_grad, "shard", scatter_dimension=0, tiled=True),
        lax.psum_scatter(output_grad, "shard", scatter_dimension=0, tiled=True),
        lax.psum_scatter(expand_grad, "shard", scatter_dimension=0, tiled=True),
        lax.psum_scatter(contract_grad, "shard", scatter_dimension=0, tiled=True),
        lax.psum_scatter(first_gain_grad, "shard", scatter_dimension=0, tiled=True),
        lax.psum_scatter(first_shift_grad, "shard", scatter_dimension=0, tiled=True),
        lax.psum_scatter(query_bias_grad, "shard", scatter_dimension=0, tiled=True),
        lax.psum_scatter(value_bias_grad, "shard", scatter_dimension=0, tiled=True),
        lax.psum_scatter(output_bias_grad, "shard", scatter_dimension=0, tiled=True),
        lax.psum_scatter(second_gain_grad, "shard", scatter_dimension=0, tiled=True),
        lax.psum_scatter(second_shift_grad, "shard", scatter_dimension=0, tiled=True),
        lax.psum_scatter(expand_bias_grad, "shard", scatter_dimension=0, tiled=True),
        lax.psum_scatter(contract_bias_grad, "shard", scatter_dimension=0, tiled=True),
    )
    totals = lax.psum(
        (
            shares[0],
            shares[1],
            shares[2],
            shares[3],
            shares[4],
            shares[5],
            shares[6],
            shares[7],
            shares[8],
            shares[9],
            shares[10],
            shares[11],
            shares[12],
        ),
        "rep",
    )
    return (
        block_output.reshape(clip_count, slot_count, width),
        input_grad.reshape(clip_count, slot_count, width),
        totals[0],
        totals[1],
        totals[2],
        totals[3],
        totals[4],
        totals[5],
        totals[6],
        totals[7],
        totals[8],
        totals[9],
        totals[10],
        totals[11],
        totals[12],
    )


def clip_layer(tokens, lengths, cotangent_of, weights, vectors, reduce, send_out):
    attention_weight, output_weight, later_weights = weights
    (first_gain, first_shift, query_bias, value_bias, output_bias, second_gain, second_shift,
     expand_bias, contract_bias) = vectors
    clip_count, frame_count, width = tokens.shape
    block_count = lengths.shape[1]
    slot_count = frame_count // block_count
    rows = clip_count * frame_count
    live = (jnp.arange(slot_count)[None, None, :] < lengths[:, :, None]).reshape(clip_count, frame_count)
    scale = HEAD ** (-0.5)
    inputs = tokens.reshape(rows, width).astype(jnp.float32)
    first_normed, first_inverse, first_act = norm_forward(inputs, first_gain, first_shift)
    mixed = jnp.dot(first_act, attention_weight, preferred_element_type=jnp.float32)
    mixed = mixed + jnp.concatenate([query_bias, jnp.zeros_like(query_bias), value_bias])
    mixed_low = mixed.astype(jnp.bfloat16).reshape(clip_count, frame_count, 3, HEADS, HEAD)
    queries = mixed_low[:, :, 0]
    keys = mixed_low[:, :, 1]
    values = mixed_low[:, :, 2]
    scores = jnp.einsum("cqhd,ckhd->chqk", queries, keys, preferred_element_type=jnp.float32) * scale
    scores = jnp.where(live[:, None, None, :], scores, NEGATIVE)
    highest = jnp.max(scores, axis=-1, keepdims=True)
    logsum = highest + jnp.log(jnp.sum(jnp.exp(scores - highest), axis=-1, keepdims=True))
    probs = jnp.exp(scores - logsum)
    expand_weight, contract_weight = later_weights(logsum[0, 0, 0, :1])
    probs_low = probs.astype(jnp.bfloat16)
    attended = jnp.einsum("chqk,ckhd->cqhd", probs_low, values, preferred_element_type=jnp.float32)
    attended_flat = attended.reshape(rows, width).astype(jnp.bfloat16)
    residual = inputs + jnp.dot(attended_flat, output_weight, preferred_element_type=jnp.float32) + output_bias
    second_normed, second_inverse, second_act = norm_forward(residual, second_gain, second_shift)
    pre = jnp.dot(second_act, expand_weight, preferred_element_type=jnp.float32) + expand_bias
    hidden_act = jax.nn.gelu(pre, approximate=False).astype(jnp.bfloat16)
    block_output = residual + jnp.dot(hidden_act, contract_weight, preferred_element_type=jnp.float32) + contract_bias
    cotangent = cotangent_of(pre[0, :1])
    error = cotangent.reshape(rows, width) * live.reshape(rows, 1).astype(jnp.float32)
    error_low = error.astype(jnp.bfloat16)
    contract_bias_grad = jnp.sum(error, axis=0)
    contract_grad = inner_rows(hidden_act, error_low)
    contract_chip = chip_sum(contract_grad)
    dpre = lax.dot_general(
        error_low, contract_weight, (((1,), (1,)), ((), ())), preferred_element_type=jnp.float32
    ) * gelu_slope(pre)
    expand_bias_grad = jnp.sum(dpre, axis=0)
    dpre_low = dpre.astype(jnp.bfloat16)
    contract_chip, dpre_low = lax.optimization_barrier((contract_chip, dpre_low))
    contract_part = shard_sum(contract_chip)
    expand_grad = inner_rows(second_act, dpre_low)
    expand_chip = chip_sum(expand_grad)
    dsecond = lax.optimization_barrier(lax.dot_general(
        dpre_low, expand_weight, (((1,), (1,)), ((), ())), preferred_element_type=jnp.float32
    ))
    second_gain_grad = jnp.sum(dsecond * second_normed, axis=0)
    second_shift_grad = jnp.sum(dsecond, axis=0)
    dresidual = error + norm_backward(dsecond, second_normed, second_inverse, second_gain)
    output_bias_grad = jnp.sum(dresidual, axis=0)
    dresidual_low = dresidual.astype(jnp.bfloat16)
    sent_output = send_out(block_output)
    expand_chip, dresidual_low = lax.optimization_barrier((expand_chip, dresidual_low))
    expand_part = shard_sum(expand_chip)
    output_grad = inner_rows(attended_flat, dresidual_low)
    output_chip = chip_sum(output_grad)
    dattended = lax.dot_general(
        dresidual_low, output_weight, (((1,), (1,)), ((), ())), preferred_element_type=jnp.float32
    ).astype(jnp.bfloat16)
    contract_part, output_chip, dattended = lax.optimization_barrier((contract_part, output_chip, dattended))
    output_part = shard_sum(output_chip)
    dattended_heads = dattended.reshape(clip_count, frame_count, HEADS, HEAD)
    attended_heads = attended_flat.reshape(clip_count, frame_count, HEADS, HEAD)
    delta = jnp.sum(
        dattended_heads.astype(jnp.float32) * attended_heads.astype(jnp.float32), axis=-1
    )
    dprob = jnp.einsum("cqhd,ckhd->chqk", dattended_heads, values, preferred_element_type=jnp.float32)
    dscore = (probs * (dprob - jnp.transpose(delta, (0, 2, 1))[:, :, :, None]) * scale).astype(jnp.bfloat16)
    dqueries = jnp.einsum("chqk,ckhd->cqhd", dscore, keys, preferred_element_type=jnp.float32)
    dkeys = jnp.einsum("chqk,cqhd->ckhd", dscore, queries, preferred_element_type=jnp.float32)
    dvalues = jnp.einsum("chqk,cqhd->ckhd", probs_low, dattended_heads, preferred_element_type=jnp.float32)
    dmixed = jnp.concatenate(
        [dqueries.reshape(rows, width), dkeys.reshape(rows, width), dvalues.reshape(rows, width)], axis=1
    )
    query_bias_grad = jnp.sum(dmixed[:, :width], axis=0)
    value_bias_grad = jnp.sum(dmixed[:, 2 * width:], axis=0)
    dmixed_low = dmixed.astype(jnp.bfloat16)
    contract_total = reduce([contract_part], [contract_grad.shape[0]])[0]
    output_part, expand_part, contract_total, sent_output, dmixed_low = lax.optimization_barrier(
        (output_part, expand_part, contract_total, sent_output, dmixed_low)
    )
    expand_total, output_total = reduce([expand_part, output_part], [expand_grad.shape[0], output_grad.shape[0]])
    attention_grad = inner_rows(first_act, dmixed_low)
    dfirst = lax.optimization_barrier(lax.dot_general(
        dmixed_low, attention_weight, (((1,), (1,)), ((), ())), preferred_element_type=jnp.float32
    ))
    first_gain_grad = jnp.sum(dfirst * first_normed, axis=0)
    first_shift_grad = jnp.sum(dfirst, axis=0)
    input_grad = dresidual + norm_backward(dfirst, first_normed, first_inverse, first_gain)
    output_total, expand_total, input_grad = lax.optimization_barrier((output_total, expand_total, input_grad))
    weight_grads = (attention_grad, output_total, expand_total, contract_total)
    vector_grads = (first_gain_grad, first_shift_grad, query_bias_grad, value_bias_grad, output_bias_grad,
                    second_gain_grad, second_shift_grad, expand_bias_grad, contract_bias_grad)
    return (
        sent_output,
        input_grad,
        weight_grads,
        vector_grads,
    )


PAIR = [(0, 1), (1, 0)]
OUTER = ("outer", "inner")


def core_pick(core, first, second):
    return jnp.where(core == 0, first, second)


def gather_weight(shard_rows, extra=None):
    parts = lax.axis_size("shard")
    core = lax.axis_index("core")
    rows, width = shard_rows.shape
    half = rows // 2
    mine = lax.dynamic_slice_in_dim(shard_rows, core * half, half, axis=0)
    if extra is not None:
        mine = jnp.concatenate([mine, extra], axis=0)
    mine = lax.all_gather(mine, "shard", axis=0, tiled=False)
    other = lax.ppermute(mine, "core", PAIR)
    first = core_pick(core, mine, other)
    second = core_pick(core, other, mine)
    full = jnp.stack([first[:, :half], second[:, :half]], axis=1).reshape(parts * rows, width)
    if extra is None:
        return full, None
    return full, first[:, half:]


def chip_sum(grad, extra=None):
    parts = lax.axis_size("shard")
    core = lax.axis_index("core")
    width = grad.shape[1]
    rows = grad.shape[0] // parts
    half = rows // 2
    quarters = grad.reshape(parts, 2, half, width)
    keep = lax.dynamic_index_in_dim(quarters, core, axis=1, keepdims=False)
    send = lax.dynamic_index_in_dim(quarters, 1 - core, axis=1, keepdims=False)
    if extra is not None:
        on_first = (core == 0).astype(extra.dtype)
        keep = jnp.concatenate([keep, extra * on_first], axis=1)
        send = jnp.concatenate([send, extra * (1 - on_first)], axis=1)
    return keep + lax.ppermute(send, "core", PAIR)


def shard_sum(chip):
    part = lax.psum_scatter(chip, "shard", scatter_dimension=0, tiled=False)
    if lax.axis_size("inner") > 1:
        part = lax.psum(part, "inner")
    return part


def finish_sum(part, half):
    core = lax.axis_index("core")
    total = line_sum(part)
    other = lax.ppermute(total, "core", PAIR)
    first = core_pick(core, total, other)
    second = core_pick(core, other, total)
    return jnp.concatenate([first[:half], second[:half]], axis=0), first[half:]


def finish_many(parts, halves):
    core = lax.axis_index("core")
    flat = jnp.concatenate([part.reshape(-1) for part in parts])
    total = line_sum(flat)
    other = lax.ppermute(total, "core", PAIR)
    first = core_pick(core, total, other)
    second = core_pick(core, other, total)
    outs = []
    offset = 0
    for part, half in zip(parts, halves):
        size = part.size
        low = first[offset:offset + size].reshape(part.shape)
        high = second[offset:offset + size].reshape(part.shape)
        outs.append((jnp.concatenate([low[:half], high[:half]], axis=0), low[half:]))
        offset += size
    return outs


def reduce_weight(grad, extra=None):
    half = grad.shape[0] // lax.axis_size("shard") // 2
    return finish_sum(shard_sum(chip_sum(grad, extra)), half)


def line_sum(values):
    groups = lax.axis_size("outer")
    if groups == 1:
        return values
    if groups & (groups - 1):
        return lax.psum(values, "outer")
    here = lax.axis_index("outer")
    length = values.shape[0]
    padded = -(-length // groups) * groups
    held = jnp.pad(values, ((0, padded - length),) + ((0, 0),) * (values.ndim - 1))
    held = held.reshape((groups, padded // groups) + values.shape[1:])
    step = 1
    while step < groups:
        held = held.reshape((held.shape[0] // 2, 2) + held.shape[1:])
        bit = (here // step) % 2
        keep = lax.dynamic_index_in_dim(held, bit, axis=1, keepdims=False)
        send = lax.dynamic_index_in_dim(held, 1 - bit, axis=1, keepdims=False)
        held = keep + lax.ppermute(send, "outer", [(j, j ^ step) for j in range(groups)])
        step *= 2
    step = groups // 2
    while step >= 1:
        bit = (here // step) % 2
        other = lax.ppermute(held, "outer", [(j, j ^ step) for j in range(groups)])
        low = jnp.where(bit == 0, held, other)
        high = jnp.where(bit == 0, other, held)
        held = jnp.stack([low, high], axis=1)
        held = held.reshape((held.shape[0] * 2,) + held.shape[2:])
        step //= 2
    return held.reshape((padded,) + values.shape[1:])[:length]


def gather_packed(blocks, after=None):
    core = lax.axis_index("core")
    mine = lax.all_gather(jnp.concatenate(blocks, axis=0), "shard", axis=0, tiled=False)
    if after is not None:
        mine = mine + (after * 0).astype(mine.dtype)
    other = lax.ppermute(mine, "core", PAIR)
    return core_pick(core, mine, other), core_pick(core, other, mine)


def unpack_rows(first, second, begin, count, shape):
    parts = first.shape[0]
    rows, width = shape
    low = first[:, begin:begin + count].reshape(parts, -1, width)
    high = second[:, begin:begin + count].reshape(parts, -1, width)
    return jnp.stack([low, high], axis=1).reshape(rows, width)


def core_half(shard_rows):
    core = lax.axis_index("core")
    half = shard_rows.shape[0] // 2
    return lax.dynamic_slice_in_dim(shard_rows, core * half, half, axis=0)


def clip_local(tokens, lengths, cotangent, *params):
    clip_count, slot_count, width = tokens.shape
    parts = lax.axis_size("shard")
    place = lax.axis_index("shard")
    own = clip_count // parts
    weight_shards = params[:4]
    vector_shards = params[4:]
    wide = weight_shards[0].shape[1]
    vector_row = jnp.concatenate([entry.reshape(-1) for entry in vector_shards])
    pad = (-vector_row.shape[0]) % wide
    vector_rows = jnp.pad(vector_row, (0, pad)).reshape(-1, wide)
    attention_half = core_half(weight_shards[0])
    output_half = core_half(weight_shards[1]).reshape(-1, wide)
    first, second = gather_packed([attention_half, output_half, vector_rows])
    a_rows = attention_half.shape[0]
    o_rows = output_half.shape[0]
    attention_weight = unpack_rows(first, second, 0, a_rows, (parts * weight_shards[0].shape[0], wide))
    output_weight = unpack_rows(
        first, second, a_rows, o_rows, (parts * weight_shards[1].shape[0], weight_shards[1].shape[1])
    )
    vector_all = first[:, a_rows + o_rows:].reshape(parts, -1)[:, : vector_row.shape[0]]
    vectors = []
    offset = 0
    for entry in vector_shards:
        size = entry.shape[0]
        vectors.append(vector_all[:, offset:offset + size].reshape(parts * size).astype(jnp.float32))
        offset += size
    late = weight_shards[2].shape[1]
    expand_half = core_half(weight_shards[2])
    contract_half = core_half(weight_shards[3]).reshape(-1, late)

    def later_weights(after):
        first_b, second_b = gather_packed([expand_half, contract_half], after)
        e_rows = expand_half.shape[0]
        expand_weight = unpack_rows(first_b, second_b, 0, e_rows, (parts * weight_shards[2].shape[0], late))
        contract_weight = unpack_rows(
            first_b, second_b, e_rows, contract_half.shape[0],
            (parts * weight_shards[3].shape[0], weight_shards[3].shape[1]),
        )
        return expand_weight, contract_weight

    weights = (attention_weight, output_weight, later_weights)
    def exchange(rows):
        blocks = rows.reshape((parts, rows.shape[0] // parts) + rows.shape[1:])
        held = [lax.dynamic_index_in_dim(blocks, place, axis=0, keepdims=False)]
        for shift in range(1, parts):
            outgoing = lax.dynamic_index_in_dim(blocks, (place + shift) % parts, axis=0, keepdims=False)
            held.append(lax.ppermute(outgoing, "shard", [(i, (i + shift) % parts) for i in range(parts)]))
        stacked = jnp.stack(held[::-1], axis=0)
        doubled = jnp.concatenate([stacked, stacked], axis=0)
        start = (parts - (place + 1) % parts) % parts
        return lax.dynamic_slice_in_dim(doubled, start, parts, axis=0).reshape(rows.shape)

    def gather_rows(values, early=False):
        flat = values.reshape(clip_count * slot_count, width)
        moved = exchange(flat) if early else lax.all_to_all(flat, "shard", 0, 0, tiled=True)
        moved = moved.reshape(parts, own, slot_count, width)
        return jnp.transpose(moved, (1, 0, 2, 3)).reshape(own, parts * slot_count, width) if own > 1 else moved.reshape(own, parts * slot_count, width)

    def scatter_rows(values):
        rows = values.reshape(own, parts, slot_count, width)
        if own > 1:
            rows = jnp.transpose(rows, (1, 0, 2, 3))
        moved = lax.all_to_all(rows.reshape(own * parts * slot_count, width), "shard", 0, 0, tiled=True)
        return moved.reshape(clip_count, slot_count, width)

    tokens_clip = gather_rows(tokens, True)

    def cotangent_of(after):
        late = cotangent + (after * 0).astype(cotangent.dtype)
        return gather_rows(late)

    lengths_clip = lax.dynamic_slice_in_dim(lengths, place * own, own, axis=0)
    block_output, input_grad, weight_grads, vector_grads = clip_layer(
        tokens_clip, lengths_clip, cotangent_of, weights, vectors, lambda many, rows: [entry[0] for entry in finish_many(many, [count // parts // 2 for count in rows])],
        scatter_rows,
    )
    input_grad = scatter_rows(input_grad)
    attention_grad = weight_grads[0]
    attention_width = attention_grad.shape[1]
    vector_parts = jnp.concatenate([entry.reshape(parts, -1) for entry in vector_grads], axis=1)
    vector_size = vector_parts.shape[1]
    vpad = (-vector_size) % attention_width
    vector_parts = jnp.pad(vector_parts, ((0, 0), (0, vpad))).reshape(parts, -1, attention_width)
    attention_part = shard_sum(chip_sum(attention_grad, vector_parts))
    ((attention_total, vector_total),) = finish_many([attention_part], [attention_grad.shape[0] // parts // 2])
    totals = (attention_total,) + tuple(weight_grads[1:])
    vector_total = vector_total.reshape(-1)[:vector_size]
    vector_outs = []
    offset = 0
    for entry in vector_shards:
        size = entry.shape[0]
        vector_outs.append(vector_total[offset:offset + size])
        offset += size
    return (block_output, input_grad) + totals + tuple(vector_outs)


def split_rep(mesh):
    devices = mesh.devices
    rep, parts = devices.shape
    first = devices[0, 0]
    stride = None
    for index in range(1, rep):
        other = devices[index, 0]
        if tuple(other.coords) == tuple(first.coords) and other.core_on_chip != first.core_on_chip:
            stride = index
            break
    if stride is None or rep % (2 * stride):
        return None
    grid = devices.reshape(rep // (2 * stride), 2, stride, parts)
    for spot in np.ndindex(grid.shape[0], grid.shape[2], grid.shape[3]):
        low = grid[spot[0], 0, spot[1], spot[2]]
        high = grid[spot[0], 1, spot[1], spot[2]]
        if tuple(low.coords) != tuple(high.coords) or low.core_on_chip == high.core_on_chip:
            return None
    return Mesh(grid, ("outer", "core", "inner", "shard"))


def solution(mesh):
    def specs(rep):
        ins = (P(rep, "shard", None), P(rep, None), P(rep, "shard", None)) + (P("shard", None),) * 4 + (
            P("shard"),
        ) * 9
        outs = (P(rep, "shard", None), P(rep, "shard", None)) + (P("shard", None),) * 4 + (P("shard"),) * 9
        return ins, outs

    ins, outs = specs("rep")
    plain = jax.shard_map(local, mesh=mesh, in_specs=ins, out_specs=outs, check_vma=False)
    split = split_rep(mesh)
    if split is None:
        return plain
    ins, outs = specs(("outer", "core", "inner"))
    fast = jax.shard_map(clip_local, mesh=split, in_specs=ins, out_specs=outs, check_vma=False)
    rep, parts = mesh.devices.shape

    def run(*args):
        if (args[0].shape[0] // rep) % parts == 0:
            return fast(*args)
        return plain(*args)

    return run
```

```python
import jax
import jax.numpy as jnp
from jax import lax
from jax.sharding import Mesh, PartitionSpec as P
import numpy as np

HEADS = 12
HEAD = 64


EPSILON = 1e-05
NEGATIVE = -1e30


def norm_forward(values, gain, shift):
    centred = values - jnp.mean(values, axis=-1, keepdims=True)
    inverse = lax.rsqrt(jnp.mean(centred * centred, axis=-1, keepdims=True) + EPSILON)
    normed = centred * inverse
    return (normed, inverse, (normed * gain + shift).astype(jnp.bfloat16))


def norm_backward(upstream, normed, inverse, gain):
    scaled = upstream * gain
    return inverse * (
        scaled
        - jnp.mean(scaled, axis=-1, keepdims=True)
        - normed * jnp.mean(scaled * normed, axis=-1, keepdims=True)
    )


def gelu_slope(values):
    return (
        0.5 * (1.0 + jax.scipy.special.erf(values * 0.7071067811865476))
        + values * jnp.exp(-0.5 * values * values) * 0.3989422804014327
    )


def inner_rows(left, right):
    return lax.dot_general(
        left, right, (((0,), (0,)), ((), ())), preferred_element_type=jnp.float32
    )


def heads_view(matrix):
    return matrix.reshape(matrix.shape[0], HEADS, HEAD)


def score_block(query_rows, key_rows, key_live):
    scores = jnp.einsum(
        "qhd,khd->hqk",
        heads_view(query_rows),
        heads_view(key_rows),
        preferred_element_type=jnp.float32,
    ) * HEAD ** (-0.5)
    return jnp.where(key_live[None, None, :], scores, NEGATIVE)


def attend_clip(items):
    query_rows, pair_rows, key_live = items
    width = query_rows.shape[1]
    scores = score_block(query_rows, pair_rows[:, :width], key_live)
    highest = jnp.max(scores, axis=-1, keepdims=True)
    logsum = highest + jnp.log(jnp.sum(jnp.exp(scores - highest), axis=-1, keepdims=True))
    probs_low = jnp.exp(scores - logsum).astype(jnp.bfloat16)
    attended = jnp.einsum(
        "hqk,khd->qhd",
        probs_low,
        heads_view(pair_rows[:, width:]),
        preferred_element_type=jnp.float32,
    )
    return (attended.reshape(query_rows.shape[0], width).astype(jnp.bfloat16), logsum[:, :, 0].T)


def score_grads(query_rows, dattended, logsum, delta, pair_rows, key_live):
    width = query_rows.shape[1]
    scores = score_block(query_rows, pair_rows[:, :width], key_live)
    probs = jnp.exp(scores - logsum.T[:, :, None])
    dprob = jnp.einsum(
        "qhd,khd->hqk",
        heads_view(dattended),
        heads_view(pair_rows[:, width:]),
        preferred_element_type=jnp.float32,
    )
    dscore = (probs * (dprob - delta.T[:, :, None]) * HEAD ** (-0.5)).astype(jnp.bfloat16)
    return (probs.astype(jnp.bfloat16), dscore)


def both_grads(items):
    query_rows, dattended, logsum, delta, pair_rows, key_live = items
    width = query_rows.shape[1]
    probs_low, dscore = score_grads(query_rows, dattended, logsum, delta, pair_rows, key_live)
    dqueries = jnp.einsum(
        "hqk,khd->qhd", dscore, heads_view(pair_rows[:, :width]), preferred_element_type=jnp.float32
    ).reshape(query_rows.shape[0], width)
    dkeys = jnp.einsum(
        "hqk,qhd->khd", dscore, heads_view(query_rows), preferred_element_type=jnp.float32
    )
    dvalues = jnp.einsum(
        "hqk,qhd->khd", probs_low, heads_view(dattended), preferred_element_type=jnp.float32
    )
    key_count = pair_rows.shape[0]
    return (
        dqueries,
        jnp.concatenate(
            [dkeys.reshape(key_count, width), dvalues.reshape(key_count, width)], axis=1
        ),
    )


def local(
    tokens,
    lengths,
    cotangent,
    attention_weight,
    output_weight,
    expand_weight,
    contract_weight,
    first_gain,
    first_shift,
    query_bias,
    value_bias,
    output_bias,
    second_gain,
    second_shift,
    expand_bias,
    contract_bias,
):
    clip_count, slot_count, width = tokens.shape
    parts = lax.axis_size("shard")
    frame_count = slot_count * parts
    place = lax.axis_index("shard")
    row_total = clip_count * slot_count
    gathered = (
        lax.all_gather(attention_weight, "shard", axis=0, tiled=True),
        lax.all_gather(output_weight, "shard", axis=0, tiled=True),
        lax.all_gather(expand_weight, "shard", axis=0, tiled=True),
        lax.all_gather(contract_weight, "shard", axis=0, tiled=True),
        lax.all_gather(first_gain, "shard", axis=0, tiled=True),
        lax.all_gather(first_shift, "shard", axis=0, tiled=True),
        lax.all_gather(query_bias, "shard", axis=0, tiled=True),
        lax.all_gather(value_bias, "shard", axis=0, tiled=True),
        lax.all_gather(output_bias, "shard", axis=0, tiled=True),
        lax.all_gather(second_gain, "shard", axis=0, tiled=True),
        lax.all_gather(second_shift, "shard", axis=0, tiled=True),
        lax.all_gather(expand_bias, "shard", axis=0, tiled=True),
        lax.all_gather(contract_bias, "shard", axis=0, tiled=True),
    )
    vectors = [entry.astype(jnp.float32) for entry in gathered[4:]]
    own_length = jnp.sum(jnp.where(jnp.arange(parts)[None, :] == place, lengths, 0), axis=1)
    row_live = jnp.arange(slot_count)[None, :] < own_length[:, None]
    key_live = (jnp.arange(slot_count)[None, None, :] < lengths[:, :, None]).reshape(
        clip_count, frame_count
    )
    inputs = tokens.reshape(row_total, width).astype(jnp.float32)
    first_normed, first_inverse, first_act = norm_forward(inputs, vectors[0], vectors[1])
    mixed = jnp.dot(first_act, gathered[0], preferred_element_type=jnp.float32)
    mixed = mixed + jnp.concatenate([vectors[2], jnp.zeros_like(vectors[2]), vectors[3]])
    mixed_low = mixed.astype(jnp.bfloat16)
    query_rows = mixed_low[:, :width].reshape(clip_count, slot_count, width)
    pair_own = mixed_low[:, width:].reshape(clip_count, slot_count, 2 * width)
    pair_all = lax.all_gather(pair_own, "shard", axis=1, tiled=True)
    attended, logsum = lax.map(attend_clip, (query_rows, pair_all, key_live))
    attended_flat = attended.reshape(row_total, width)
    residual = (
        inputs
        + jnp.dot(attended_flat, gathered[1], preferred_element_type=jnp.float32)
        + vectors[4]
    )
    second_normed, second_inverse, second_act = norm_forward(residual, vectors[5], vectors[6])
    pre = jnp.dot(second_act, gathered[2], preferred_element_type=jnp.float32) + vectors[7]
    hidden_act = jax.nn.gelu(pre, approximate=False).astype(jnp.bfloat16)
    block_output = (
        residual + jnp.dot(hidden_act, gathered[3], preferred_element_type=jnp.float32) + vectors[8]
    )
    backward = (
        lax.all_gather(attention_weight, "shard", axis=0, tiled=True),
        lax.all_gather(output_weight, "shard", axis=0, tiled=True),
        lax.all_gather(expand_weight, "shard", axis=0, tiled=True),
        lax.all_gather(contract_weight, "shard", axis=0, tiled=True),
        lax.all_gather(first_gain, "shard", axis=0, tiled=True),
        lax.all_gather(first_shift, "shard", axis=0, tiled=True),
        lax.all_gather(query_bias, "shard", axis=0, tiled=True),
        lax.all_gather(value_bias, "shard", axis=0, tiled=True),
        lax.all_gather(output_bias, "shard", axis=0, tiled=True),
        lax.all_gather(second_gain, "shard", axis=0, tiled=True),
        lax.all_gather(second_shift, "shard", axis=0, tiled=True),
        lax.all_gather(expand_bias, "shard", axis=0, tiled=True),
        lax.all_gather(contract_bias, "shard", axis=0, tiled=True),
    )
    back_vectors = [entry.astype(jnp.float32) for entry in backward[4:]]
    error = cotangent.reshape(row_total, width) * row_live.reshape(row_total, 1).astype(jnp.float32)
    error_low = error.astype(jnp.bfloat16)
    contract_bias_grad = jnp.sum(error, axis=0)
    contract_grad = inner_rows(hidden_act, error_low)
    dpre = lax.dot_general(
        error_low, backward[3], (((1,), (1,)), ((), ())), preferred_element_type=jnp.float32
    ) * gelu_slope(pre)
    expand_bias_grad = jnp.sum(dpre, axis=0)
    dpre_low = dpre.astype(jnp.bfloat16)
    expand_grad = inner_rows(second_act, dpre_low)
    dsecond = lax.dot_general(
        dpre_low, backward[2], (((1,), (1,)), ((), ())), preferred_element_type=jnp.float32
    )
    second_gain_grad = jnp.sum(dsecond * second_normed, axis=0)
    second_shift_grad = jnp.sum(dsecond, axis=0)
    dresidual = error + norm_backward(dsecond, second_normed, second_inverse, back_vectors[5])
    output_bias_grad = jnp.sum(dresidual, axis=0)
    dresidual_low = dresidual.astype(jnp.bfloat16)
    output_grad = inner_rows(attended_flat, dresidual_low)
    dattended = lax.dot_general(
        dresidual_low, backward[1], (((1,), (1,)), ((), ())), preferred_element_type=jnp.float32
    ).astype(jnp.bfloat16)
    delta = jnp.sum(
        heads_view(dattended.astype(jnp.float32)) * heads_view(attended_flat.astype(jnp.float32)),
        axis=-1,
    )
    delta = delta.reshape(clip_count, slot_count, HEADS)
    dattended_clips = dattended.reshape(clip_count, slot_count, width)
    dqueries, pair_terms = lax.map(
        both_grads, (query_rows, dattended_clips, logsum, delta, pair_all, key_live)
    )
    pair_grads = lax.psum_scatter(pair_terms, "shard", scatter_dimension=1, tiled=True)
    dqueries_flat = dqueries.reshape(row_total, width)
    pair_flat = pair_grads.reshape(row_total, 2 * width)
    dmixed = jnp.concatenate([dqueries_flat, pair_flat], axis=1)
    query_bias_grad = jnp.sum(dqueries_flat, axis=0)
    value_bias_grad = jnp.sum(pair_flat[:, width:], axis=0)
    dmixed_low = dmixed.astype(jnp.bfloat16)
    attention_grad = inner_rows(first_act, dmixed_low)
    dfirst = lax.dot_general(
        dmixed_low, backward[0], (((1,), (1,)), ((), ())), preferred_element_type=jnp.float32
    )
    first_gain_grad = jnp.sum(dfirst * first_normed, axis=0)
    first_shift_grad = jnp.sum(dfirst, axis=0)
    input_grad = dresidual + norm_backward(dfirst, first_normed, first_inverse, back_vectors[0])
    shares = (
        lax.psum_scatter(attention_grad, "shard", scatter_dimension=0, tiled=True),
        lax.psum_scatter(output_grad, "shard", scatter_dimension=0, tiled=True),
        lax.psum_scatter(expand_grad, "shard", scatter_dimension=0, tiled=True),
        lax.psum_scatter(contract_grad, "shard", scatter_dimension=0, tiled=True),
        lax.psum_scatter(first_gain_grad, "shard", scatter_dimension=0, tiled=True),
        lax.psum_scatter(first_shift_grad, "shard", scatter_dimension=0, tiled=True),
        lax.psum_scatter(query_bias_grad, "shard", scatter_dimension=0, tiled=True),
        lax.psum_scatter(value_bias_grad, "shard", scatter_dimension=0, tiled=True),
        lax.psum_scatter(output_bias_grad, "shard", scatter_dimension=0, tiled=True),
        lax.psum_scatter(second_gain_grad, "shard", scatter_dimension=0, tiled=True),
        lax.psum_scatter(second_shift_grad, "shard", scatter_dimension=0, tiled=True),
        lax.psum_scatter(expand_bias_grad, "shard", scatter_dimension=0, tiled=True),
        lax.psum_scatter(contract_bias_grad, "shard", scatter_dimension=0, tiled=True),
    )
    totals = lax.psum(
        (
            shares[0],
            shares[1],
            shares[2],
            shares[3],
            shares[4],
            shares[5],
            shares[6],
            shares[7],
            shares[8],
            shares[9],
            shares[10],
            shares[11],
            shares[12],
        ),
        "rep",
    )
    return (
        block_output.reshape(clip_count, slot_count, width),
        input_grad.reshape(clip_count, slot_count, width),
        totals[0],
        totals[1],
        totals[2],
        totals[3],
        totals[4],
        totals[5],
        totals[6],
        totals[7],
        totals[8],
        totals[9],
        totals[10],
        totals[11],
        totals[12],
    )


def clip_layer(tokens, lengths, cotangent_of, weights, vectors, reduce, send_out):
    attention_weight, output_weight, later_weights = weights
    (first_gain, first_shift, query_bias, value_bias, output_bias, second_gain, second_shift,
     expand_bias, contract_bias) = vectors
    clip_count, frame_count, width = tokens.shape
    block_count = lengths.shape[1]
    slot_count = frame_count // block_count
    rows = clip_count * frame_count
    live = (jnp.arange(slot_count)[None, None, :] < lengths[:, :, None]).reshape(clip_count, frame_count)
    scale = HEAD ** (-0.5)
    inputs = tokens.reshape(rows, width).astype(jnp.float32)
    first_normed, first_inverse, first_act = norm_forward(inputs, first_gain, first_shift)
    mixed = jnp.dot(first_act, attention_weight, preferred_element_type=jnp.float32)
    mixed = mixed + jnp.concatenate([query_bias, jnp.zeros_like(query_bias), value_bias])
    mixed_low = mixed.astype(jnp.bfloat16).reshape(clip_count, frame_count, 3, HEADS, HEAD)
    queries = mixed_low[:, :, 0]
    keys = mixed_low[:, :, 1]
    values = mixed_low[:, :, 2]
    scores = jnp.einsum("cqhd,ckhd->chqk", queries, keys, preferred_element_type=jnp.float32) * scale
    scores = jnp.where(live[:, None, None, :], scores, NEGATIVE)
    highest = jnp.max(scores, axis=-1, keepdims=True)
    logsum = highest + jnp.log(jnp.sum(jnp.exp(scores - highest), axis=-1, keepdims=True))
    probs = jnp.exp(scores - logsum)
    expand_weight, contract_weight = later_weights(logsum[0, 0, 0, :1])
    probs_low = probs.astype(jnp.bfloat16)
    attended = jnp.einsum("chqk,ckhd->cqhd", probs_low, values, preferred_element_type=jnp.float32)
    attended_flat = attended.reshape(rows, width).astype(jnp.bfloat16)
    residual = inputs + jnp.dot(attended_flat, output_weight, preferred_element_type=jnp.float32) + output_bias
    second_normed, second_inverse, second_act = norm_forward(residual, second_gain, second_shift)
    pre = jnp.dot(second_act, expand_weight, preferred_element_type=jnp.float32) + expand_bias
    hidden_act = jax.nn.gelu(pre, approximate=False).astype(jnp.bfloat16)
    block_output = residual + jnp.dot(hidden_act, contract_weight, preferred_element_type=jnp.float32) + contract_bias
    cotangent = cotangent_of(pre[0, :1])
    error = cotangent.reshape(rows, width) * live.reshape(rows, 1).astype(jnp.float32)
    error_low = error.astype(jnp.bfloat16)
    contract_bias_grad = jnp.sum(error, axis=0)
    contract_grad = inner_rows(hidden_act, error_low)
    contract_chip = chip_sum(contract_grad)
    dpre = lax.dot_general(
        error_low, contract_weight, (((1,), (1,)), ((), ())), preferred_element_type=jnp.float32
    ) * gelu_slope(pre)
    expand_bias_grad = jnp.sum(dpre, axis=0)
    dpre_low = dpre.astype(jnp.bfloat16)
    contract_chip, dpre_low = lax.optimization_barrier((contract_chip, dpre_low))
    contract_part = shard_sum(contract_chip)
    expand_grad = inner_rows(second_act, dpre_low)
    expand_chip = chip_sum(expand_grad)
    dsecond = lax.optimization_barrier(lax.dot_general(
        dpre_low, expand_weight, (((1,), (1,)), ((), ())), preferred_element_type=jnp.float32
    ))
    second_gain_grad = jnp.sum(dsecond * second_normed, axis=0)
    second_shift_grad = jnp.sum(dsecond, axis=0)
    dresidual = error + norm_backward(dsecond, second_normed, second_inverse, second_gain)
    output_bias_grad = jnp.sum(dresidual, axis=0)
    dresidual_low = dresidual.astype(jnp.bfloat16)
    sent_output = send_out(block_output)
    expand_chip, dresidual_low = lax.optimization_barrier((expand_chip, dresidual_low))
    expand_part = shard_sum(expand_chip)
    output_grad = inner_rows(attended_flat, dresidual_low)
    output_chip = chip_sum(output_grad)
    dattended = lax.dot_general(
        dresidual_low, output_weight, (((1,), (1,)), ((), ())), preferred_element_type=jnp.float32
    ).astype(jnp.bfloat16)
    output_chip, dattended = lax.optimization_barrier((output_chip, dattended))
    output_part = shard_sum(output_chip)
    dattended_heads = dattended.reshape(clip_count, frame_count, HEADS, HEAD)
    attended_heads = attended_flat.reshape(clip_count, frame_count, HEADS, HEAD)
    delta = jnp.sum(
        dattended_heads.astype(jnp.float32) * attended_heads.astype(jnp.float32), axis=-1
    )
    dprob = jnp.einsum("cqhd,ckhd->chqk", dattended_heads, values, preferred_element_type=jnp.float32)
    dscore = (probs * (dprob - jnp.transpose(delta, (0, 2, 1))[:, :, :, None]) * scale).astype(jnp.bfloat16)
    contract_part, dscore = lax.optimization_barrier((contract_part, dscore))
    dqueries = jnp.einsum("chqk,ckhd->cqhd", dscore, keys, preferred_element_type=jnp.float32)
    dkeys = jnp.einsum("chqk,cqhd->ckhd", dscore, queries, preferred_element_type=jnp.float32)
    dvalues = jnp.einsum("chqk,cqhd->ckhd", probs_low, dattended_heads, preferred_element_type=jnp.float32)
    dmixed = jnp.concatenate(
        [dqueries.reshape(rows, width), dkeys.reshape(rows, width), dvalues.reshape(rows, width)], axis=1
    )
    query_bias_grad = jnp.sum(dmixed[:, :width], axis=0)
    value_bias_grad = jnp.sum(dmixed[:, 2 * width:], axis=0)
    dmixed_low = dmixed.astype(jnp.bfloat16)
    contract_total = reduce(contract_part, contract_grad.shape[0])
    output_part, expand_part, contract_total, sent_output, dmixed_low = lax.optimization_barrier(
        (output_part, expand_part, contract_total, sent_output, dmixed_low)
    )
    expand_total = reduce(expand_part, expand_grad.shape[0])
    attention_grad = inner_rows(first_act, dmixed_low)
    dfirst = lax.optimization_barrier(lax.dot_general(
        dmixed_low, attention_weight, (((1,), (1,)), ((), ())), preferred_element_type=jnp.float32
    ))
    first_gain_grad = jnp.sum(dfirst * first_normed, axis=0)
    first_shift_grad = jnp.sum(dfirst, axis=0)
    input_grad = dresidual + norm_backward(dfirst, first_normed, first_inverse, first_gain)
    output_part, expand_total, input_grad = lax.optimization_barrier((output_part, expand_total, input_grad))
    weight_grads = (attention_grad, output_part, expand_total, contract_total)
    vector_grads = (first_gain_grad, first_shift_grad, query_bias_grad, value_bias_grad, output_bias_grad,
                    second_gain_grad, second_shift_grad, expand_bias_grad, contract_bias_grad)
    return (
        sent_output,
        input_grad,
        weight_grads,
        vector_grads,
    )


PAIR = [(0, 1), (1, 0)]
OUTER = ("outer", "inner")


def core_pick(core, first, second):
    return jnp.where(core == 0, first, second)


def gather_weight(shard_rows, extra=None):
    parts = lax.axis_size("shard")
    core = lax.axis_index("core")
    rows, width = shard_rows.shape
    half = rows // 2
    mine = lax.dynamic_slice_in_dim(shard_rows, core * half, half, axis=0)
    if extra is not None:
        mine = jnp.concatenate([mine, extra], axis=0)
    mine = lax.all_gather(mine, "shard", axis=0, tiled=False)
    other = lax.ppermute(mine, "core", PAIR)
    first = core_pick(core, mine, other)
    second = core_pick(core, other, mine)
    full = jnp.stack([first[:, :half], second[:, :half]], axis=1).reshape(parts * rows, width)
    if extra is None:
        return full, None
    return full, first[:, half:]


def chip_sum(grad, extra=None):
    parts = lax.axis_size("shard")
    core = lax.axis_index("core")
    width = grad.shape[1]
    rows = grad.shape[0] // parts
    half = rows // 2
    quarters = grad.reshape(parts, 2, half, width)
    keep = lax.dynamic_index_in_dim(quarters, core, axis=1, keepdims=False)
    send = lax.dynamic_index_in_dim(quarters, 1 - core, axis=1, keepdims=False)
    if extra is not None:
        on_first = (core == 0).astype(extra.dtype)
        keep = jnp.concatenate([keep, extra * on_first], axis=1)
        send = jnp.concatenate([send, extra * (1 - on_first)], axis=1)
    return keep + lax.ppermute(send, "core", PAIR)


def shard_sum(chip):
    part = lax.psum_scatter(chip, "shard", scatter_dimension=0, tiled=False)
    if lax.axis_size("inner") > 1:
        part = lax.psum(part, "inner")
    return part


def finish_sum(part, half):
    core = lax.axis_index("core")
    total = line_sum(part)
    other = lax.ppermute(total, "core", PAIR)
    first = core_pick(core, total, other)
    second = core_pick(core, other, total)
    return jnp.concatenate([first[:half], second[:half]], axis=0), first[half:]


def finish_many(parts, halves):
    core = lax.axis_index("core")
    flat = jnp.concatenate([part.reshape(-1) for part in parts])
    total = line_sum(flat)
    other = lax.ppermute(total, "core", PAIR)
    first = core_pick(core, total, other)
    second = core_pick(core, other, total)
    outs = []
    offset = 0
    for part, half in zip(parts, halves):
        size = part.size
        low = first[offset:offset + size].reshape(part.shape)
        high = second[offset:offset + size].reshape(part.shape)
        outs.append((jnp.concatenate([low[:half], high[:half]], axis=0), low[half:]))
        offset += size
    return outs


def reduce_weight(grad, extra=None):
    half = grad.shape[0] // lax.axis_size("shard") // 2
    return finish_sum(shard_sum(chip_sum(grad, extra)), half)


def line_sum(values):
    groups = lax.axis_size("outer")
    if groups == 1:
        return values
    if groups & (groups - 1):
        return lax.psum(values, "outer")
    here = lax.axis_index("outer")
    length = values.shape[0]
    padded = -(-length // groups) * groups
    held = jnp.pad(values, ((0, padded - length),) + ((0, 0),) * (values.ndim - 1))
    held = held.reshape((groups, padded // groups) + values.shape[1:])
    step = 1
    while step < groups:
        held = held.reshape((held.shape[0] // 2, 2) + held.shape[1:])
        bit = (here // step) % 2
        keep = lax.dynamic_index_in_dim(held, bit, axis=1, keepdims=False)
        send = lax.dynamic_index_in_dim(held, 1 - bit, axis=1, keepdims=False)
        held = keep + lax.ppermute(send, "outer", [(j, j ^ step) for j in range(groups)])
        step *= 2
    step = groups // 2
    while step >= 1:
        bit = (here // step) % 2
        other = lax.ppermute(held, "outer", [(j, j ^ step) for j in range(groups)])
        low = jnp.where(bit == 0, held, other)
        high = jnp.where(bit == 0, other, held)
        held = jnp.stack([low, high], axis=1)
        held = held.reshape((held.shape[0] * 2,) + held.shape[2:])
        step //= 2
    return held.reshape((padded,) + values.shape[1:])[:length]


def gather_packed(blocks, after=None):
    core = lax.axis_index("core")
    mine = lax.all_gather(jnp.concatenate(blocks, axis=0), "shard", axis=0, tiled=False)
    if after is not None:
        mine = mine + (after * 0).astype(mine.dtype)
    other = lax.ppermute(mine, "core", PAIR)
    return core_pick(core, mine, other), core_pick(core, other, mine)


def unpack_rows(first, second, begin, count, shape):
    parts = first.shape[0]
    rows, width = shape
    low = first[:, begin:begin + count].reshape(parts, -1, width)
    high = second[:, begin:begin + count].reshape(parts, -1, width)
    return jnp.stack([low, high], axis=1).reshape(rows, width)


def core_half(shard_rows):
    core = lax.axis_index("core")
    half = shard_rows.shape[0] // 2
    return lax.dynamic_slice_in_dim(shard_rows, core * half, half, axis=0)


def clip_local(tokens, lengths, cotangent, *params):
    clip_count, slot_count, width = tokens.shape
    parts = lax.axis_size("shard")
    place = lax.axis_index("shard")
    own = clip_count // parts
    weight_shards = params[:4]
    vector_shards = params[4:]
    wide = weight_shards[0].shape[1]
    vector_row = jnp.concatenate([entry.reshape(-1) for entry in vector_shards])
    pad = (-vector_row.shape[0]) % wide
    vector_rows = jnp.pad(vector_row, (0, pad)).reshape(-1, wide)
    attention_half = core_half(weight_shards[0])
    output_half = core_half(weight_shards[1]).reshape(-1, wide)
    first, second = gather_packed([attention_half, output_half, vector_rows])
    a_rows = attention_half.shape[0]
    o_rows = output_half.shape[0]
    attention_weight = unpack_rows(first, second, 0, a_rows, (parts * weight_shards[0].shape[0], wide))
    output_weight = unpack_rows(
        first, second, a_rows, o_rows, (parts * weight_shards[1].shape[0], weight_shards[1].shape[1])
    )
    vector_all = first[:, a_rows + o_rows:].reshape(parts, -1)[:, : vector_row.shape[0]]
    vectors = []
    offset = 0
    for entry in vector_shards:
        size = entry.shape[0]
        vectors.append(vector_all[:, offset:offset + size].reshape(parts * size).astype(jnp.float32))
        offset += size
    late = weight_shards[2].shape[1]
    expand_half = core_half(weight_shards[2])
    contract_half = core_half(weight_shards[3]).reshape(-1, late)

    def later_weights(after):
        first_b, second_b = gather_packed([expand_half, contract_half], after)
        e_rows = expand_half.shape[0]
        expand_weight = unpack_rows(first_b, second_b, 0, e_rows, (parts * weight_shards[2].shape[0], late))
        contract_weight = unpack_rows(
            first_b, second_b, e_rows, contract_half.shape[0],
            (parts * weight_shards[3].shape[0], weight_shards[3].shape[1]),
        )
        return expand_weight, contract_weight

    weights = (attention_weight, output_weight, later_weights)
    def exchange(rows):
        blocks = rows.reshape((parts, rows.shape[0] // parts) + rows.shape[1:])
        held = [lax.dynamic_index_in_dim(blocks, place, axis=0, keepdims=False)]
        for shift in range(1, parts):
            outgoing = lax.dynamic_index_in_dim(blocks, (place + shift) % parts, axis=0, keepdims=False)
            held.append(lax.ppermute(outgoing, "shard", [(i, (i + shift) % parts) for i in range(parts)]))
        stacked = jnp.stack(held[::-1], axis=0)
        doubled = jnp.concatenate([stacked, stacked], axis=0)
        start = (parts - (place + 1) % parts) % parts
        return lax.dynamic_slice_in_dim(doubled, start, parts, axis=0).reshape(rows.shape)

    def gather_rows(values, early=False):
        flat = values.reshape(clip_count * slot_count, width)
        moved = exchange(flat) if early else lax.all_to_all(flat, "shard", 0, 0, tiled=True)
        moved = moved.reshape(parts, own, slot_count, width)
        return jnp.transpose(moved, (1, 0, 2, 3)).reshape(own, parts * slot_count, width) if own > 1 else moved.reshape(own, parts * slot_count, width)

    def scatter_rows(values):
        rows = values.reshape(own, parts, slot_count, width)
        if own > 1:
            rows = jnp.transpose(rows, (1, 0, 2, 3))
        moved = lax.all_to_all(rows.reshape(own * parts * slot_count, width), "shard", 0, 0, tiled=True)
        return moved.reshape(clip_count, slot_count, width)

    tokens_clip = gather_rows(tokens, True)

    def cotangent_of(after):
        late = cotangent + (after * 0).astype(cotangent.dtype)
        return gather_rows(late)

    lengths_clip = lax.dynamic_slice_in_dim(lengths, place * own, own, axis=0)
    block_output, input_grad, weight_grads, vector_grads = clip_layer(
        tokens_clip, lengths_clip, cotangent_of, weights, vectors, lambda part, rows: finish_sum(part, rows // parts // 2)[0],
        scatter_rows,
    )
    input_grad = scatter_rows(input_grad)
    attention_grad = weight_grads[0]
    attention_width = attention_grad.shape[1]
    vector_parts = jnp.concatenate([entry.reshape(parts, -1) for entry in vector_grads], axis=1)
    vector_size = vector_parts.shape[1]
    vpad = (-vector_size) % attention_width
    vector_parts = jnp.pad(vector_parts, ((0, 0), (0, vpad))).reshape(parts, -1, attention_width)
    attention_part = shard_sum(chip_sum(attention_grad, vector_parts))
    output_part = weight_grads[1]
    (attention_total, vector_total), (output_total, _) = finish_many(
        [attention_part, output_part],
        [attention_grad.shape[0] // parts // 2, params[1].shape[0] // 2],
    )
    totals = (attention_total, output_total) + tuple(weight_grads[2:])
    vector_total = vector_total.reshape(-1)[:vector_size]
    vector_outs = []
    offset = 0
    for entry in vector_shards:
        size = entry.shape[0]
        vector_outs.append(vector_total[offset:offset + size])
        offset += size
    return (block_output, input_grad) + totals + tuple(vector_outs)


def split_rep(mesh):
    devices = mesh.devices
    rep, parts = devices.shape
    first = devices[0, 0]
    stride = None
    for index in range(1, rep):
        other = devices[index, 0]
        if tuple(other.coords) == tuple(first.coords) and other.core_on_chip != first.core_on_chip:
            stride = index
            break
    if stride is None or rep % (2 * stride):
        return None
    grid = devices.reshape(rep // (2 * stride), 2, stride, parts)
    for spot in np.ndindex(grid.shape[0], grid.shape[2], grid.shape[3]):
        low = grid[spot[0], 0, spot[1], spot[2]]
        high = grid[spot[0], 1, spot[1], spot[2]]
        if tuple(low.coords) != tuple(high.coords) or low.core_on_chip == high.core_on_chip:
            return None
    return Mesh(grid, ("outer", "core", "inner", "shard"))


def solution(mesh):
    def specs(rep):
        ins = (P(rep, "shard", None), P(rep, None), P(rep, "shard", None)) + (P("shard", None),) * 4 + (
            P("shard"),
        ) * 9
        outs = (P(rep, "shard", None), P(rep, "shard", None)) + (P("shard", None),) * 4 + (P("shard"),) * 9
        return ins, outs

    ins, outs = specs("rep")
    plain = jax.shard_map(local, mesh=mesh, in_specs=ins, out_specs=outs, check_vma=False)
    split = split_rep(mesh)
    if split is None:
        return plain
    ins, outs = specs(("outer", "core", "inner"))
    fast = jax.shard_map(clip_local, mesh=split, in_specs=ins, out_specs=outs, check_vma=False)
    rep, parts = mesh.devices.shape

    def run(*args):
        if (args[0].shape[0] // rep) % parts == 0:
            return fast(*args)
        return plain(*args)

    return run
```

```python
import jax
import jax.numpy as jnp
from jax import lax
from jax.sharding import Mesh, PartitionSpec as P
import numpy as np

HEADS = 12
HEAD = 64


EPSILON = 1e-05
NEGATIVE = -1e30


def norm_forward(values, gain, shift):
    centred = values - jnp.mean(values, axis=-1, keepdims=True)
    inverse = lax.rsqrt(jnp.mean(centred * centred, axis=-1, keepdims=True) + EPSILON)
    normed = centred * inverse
    return (normed, inverse, (normed * gain + shift).astype(jnp.bfloat16))


def norm_backward(upstream, normed, inverse, gain):
    scaled = upstream * gain
    return inverse * (
        scaled
        - jnp.mean(scaled, axis=-1, keepdims=True)
        - normed * jnp.mean(scaled * normed, axis=-1, keepdims=True)
    )


def gelu_slope(values):
    return (
        0.5 * (1.0 + jax.scipy.special.erf(values * 0.7071067811865476))
        + values * jnp.exp(-0.5 * values * values) * 0.3989422804014327
    )


def inner_rows(left, right):
    return lax.dot_general(
        left, right, (((0,), (0,)), ((), ())), preferred_element_type=jnp.float32
    )


def heads_view(matrix):
    return matrix.reshape(matrix.shape[0], HEADS, HEAD)


def score_block(query_rows, key_rows, key_live):
    scores = jnp.einsum(
        "qhd,khd->hqk",
        heads_view(query_rows),
        heads_view(key_rows),
        preferred_element_type=jnp.float32,
    ) * HEAD ** (-0.5)
    return jnp.where(key_live[None, None, :], scores, NEGATIVE)


def attend_clip(items):
    query_rows, pair_rows, key_live = items
    width = query_rows.shape[1]
    scores = score_block(query_rows, pair_rows[:, :width], key_live)
    highest = jnp.max(scores, axis=-1, keepdims=True)
    logsum = highest + jnp.log(jnp.sum(jnp.exp(scores - highest), axis=-1, keepdims=True))
    probs_low = jnp.exp(scores - logsum).astype(jnp.bfloat16)
    attended = jnp.einsum(
        "hqk,khd->qhd",
        probs_low,
        heads_view(pair_rows[:, width:]),
        preferred_element_type=jnp.float32,
    )
    return (attended.reshape(query_rows.shape[0], width).astype(jnp.bfloat16), logsum[:, :, 0].T)


def score_grads(query_rows, dattended, logsum, delta, pair_rows, key_live):
    width = query_rows.shape[1]
    scores = score_block(query_rows, pair_rows[:, :width], key_live)
    probs = jnp.exp(scores - logsum.T[:, :, None])
    dprob = jnp.einsum(
        "qhd,khd->hqk",
        heads_view(dattended),
        heads_view(pair_rows[:, width:]),
        preferred_element_type=jnp.float32,
    )
    dscore = (probs * (dprob - delta.T[:, :, None]) * HEAD ** (-0.5)).astype(jnp.bfloat16)
    return (probs.astype(jnp.bfloat16), dscore)


def both_grads(items):
    query_rows, dattended, logsum, delta, pair_rows, key_live = items
    width = query_rows.shape[1]
    probs_low, dscore = score_grads(query_rows, dattended, logsum, delta, pair_rows, key_live)
    dqueries = jnp.einsum(
        "hqk,khd->qhd", dscore, heads_view(pair_rows[:, :width]), preferred_element_type=jnp.float32
    ).reshape(query_rows.shape[0], width)
    dkeys = jnp.einsum(
        "hqk,qhd->khd", dscore, heads_view(query_rows), preferred_element_type=jnp.float32
    )
    dvalues = jnp.einsum(
        "hqk,qhd->khd", probs_low, heads_view(dattended), preferred_element_type=jnp.float32
    )
    key_count = pair_rows.shape[0]
    return (
        dqueries,
        jnp.concatenate(
            [dkeys.reshape(key_count, width), dvalues.reshape(key_count, width)], axis=1
        ),
    )


def local(
    tokens,
    lengths,
    cotangent,
    attention_weight,
    output_weight,
    expand_weight,
    contract_weight,
    first_gain,
    first_shift,
    query_bias,
    value_bias,
    output_bias,
    second_gain,
    second_shift,
    expand_bias,
    contract_bias,
):
    clip_count, slot_count, width = tokens.shape
    parts = lax.axis_size("shard")
    frame_count = slot_count * parts
    place = lax.axis_index("shard")
    row_total = clip_count * slot_count
    gathered = (
        lax.all_gather(attention_weight, "shard", axis=0, tiled=True),
        lax.all_gather(output_weight, "shard", axis=0, tiled=True),
        lax.all_gather(expand_weight, "shard", axis=0, tiled=True),
        lax.all_gather(contract_weight, "shard", axis=0, tiled=True),
        lax.all_gather(first_gain, "shard", axis=0, tiled=True),
        lax.all_gather(first_shift, "shard", axis=0, tiled=True),
        lax.all_gather(query_bias, "shard", axis=0, tiled=True),
        lax.all_gather(value_bias, "shard", axis=0, tiled=True),
        lax.all_gather(output_bias, "shard", axis=0, tiled=True),
        lax.all_gather(second_gain, "shard", axis=0, tiled=True),
        lax.all_gather(second_shift, "shard", axis=0, tiled=True),
        lax.all_gather(expand_bias, "shard", axis=0, tiled=True),
        lax.all_gather(contract_bias, "shard", axis=0, tiled=True),
    )
    vectors = [entry.astype(jnp.float32) for entry in gathered[4:]]
    own_length = jnp.sum(jnp.where(jnp.arange(parts)[None, :] == place, lengths, 0), axis=1)
    row_live = jnp.arange(slot_count)[None, :] < own_length[:, None]
    key_live = (jnp.arange(slot_count)[None, None, :] < lengths[:, :, None]).reshape(
        clip_count, frame_count
    )
    inputs = tokens.reshape(row_total, width).astype(jnp.float32)
    first_normed, first_inverse, first_act = norm_forward(inputs, vectors[0], vectors[1])
    mixed = jnp.dot(first_act, gathered[0], preferred_element_type=jnp.float32)
    mixed = mixed + jnp.concatenate([vectors[2], jnp.zeros_like(vectors[2]), vectors[3]])
    mixed_low = mixed.astype(jnp.bfloat16)
    query_rows = mixed_low[:, :width].reshape(clip_count, slot_count, width)
    pair_own = mixed_low[:, width:].reshape(clip_count, slot_count, 2 * width)
    pair_all = lax.all_gather(pair_own, "shard", axis=1, tiled=True)
    attended, logsum = lax.map(attend_clip, (query_rows, pair_all, key_live))
    attended_flat = attended.reshape(row_total, width)
    residual = (
        inputs
        + jnp.dot(attended_flat, gathered[1], preferred_element_type=jnp.float32)
        + vectors[4]
    )
    second_normed, second_inverse, second_act = norm_forward(residual, vectors[5], vectors[6])
    pre = jnp.dot(second_act, gathered[2], preferred_element_type=jnp.float32) + vectors[7]
    hidden_act = jax.nn.gelu(pre, approximate=False).astype(jnp.bfloat16)
    block_output = (
        residual + jnp.dot(hidden_act, gathered[3], preferred_element_type=jnp.float32) + vectors[8]
    )
    backward = (
        lax.all_gather(attention_weight, "shard", axis=0, tiled=True),
        lax.all_gather(output_weight, "shard", axis=0, tiled=True),
        lax.all_gather(expand_weight, "shard", axis=0, tiled=True),
        lax.all_gather(contract_weight, "shard", axis=0, tiled=True),
        lax.all_gather(first_gain, "shard", axis=0, tiled=True),
        lax.all_gather(first_shift, "shard", axis=0, tiled=True),
        lax.all_gather(query_bias, "shard", axis=0, tiled=True),
        lax.all_gather(value_bias, "shard", axis=0, tiled=True),
        lax.all_gather(output_bias, "shard", axis=0, tiled=True),
        lax.all_gather(second_gain, "shard", axis=0, tiled=True),
        lax.all_gather(second_shift, "shard", axis=0, tiled=True),
        lax.all_gather(expand_bias, "shard", axis=0, tiled=True),
        lax.all_gather(contract_bias, "shard", axis=0, tiled=True),
    )
    back_vectors = [entry.astype(jnp.float32) for entry in backward[4:]]
    error = cotangent.reshape(row_total, width) * row_live.reshape(row_total, 1).astype(jnp.float32)
    error_low = error.astype(jnp.bfloat16)
    contract_bias_grad = jnp.sum(error, axis=0)
    contract_grad = inner_rows(hidden_act, error_low)
    dpre = lax.dot_general(
        error_low, backward[3], (((1,), (1,)), ((), ())), preferred_element_type=jnp.float32
    ) * gelu_slope(pre)
    expand_bias_grad = jnp.sum(dpre, axis=0)
    dpre_low = dpre.astype(jnp.bfloat16)
    expand_grad = inner_rows(second_act, dpre_low)
    dsecond = lax.dot_general(
        dpre_low, backward[2], (((1,), (1,)), ((), ())), preferred_element_type=jnp.float32
    )
    second_gain_grad = jnp.sum(dsecond * second_normed, axis=0)
    second_shift_grad = jnp.sum(dsecond, axis=0)
    dresidual = error + norm_backward(dsecond, second_normed, second_inverse, back_vectors[5])
    output_bias_grad = jnp.sum(dresidual, axis=0)
    dresidual_low = dresidual.astype(jnp.bfloat16)
    output_grad = inner_rows(attended_flat, dresidual_low)
    dattended = lax.dot_general(
        dresidual_low, backward[1], (((1,), (1,)), ((), ())), preferred_element_type=jnp.float32
    ).astype(jnp.bfloat16)
    delta = jnp.sum(
        heads_view(dattended.astype(jnp.float32)) * heads_view(attended_flat.astype(jnp.float32)),
        axis=-1,
    )
    delta = delta.reshape(clip_count, slot_count, HEADS)
    dattended_clips = dattended.reshape(clip_count, slot_count, width)
    dqueries, pair_terms = lax.map(
        both_grads, (query_rows, dattended_clips, logsum, delta, pair_all, key_live)
    )
    pair_grads = lax.psum_scatter(pair_terms, "shard", scatter_dimension=1, tiled=True)
    dqueries_flat = dqueries.reshape(row_total, width)
    pair_flat = pair_grads.reshape(row_total, 2 * width)
    dmixed = jnp.concatenate([dqueries_flat, pair_flat], axis=1)
    query_bias_grad = jnp.sum(dqueries_flat, axis=0)
    value_bias_grad = jnp.sum(pair_flat[:, width:], axis=0)
    dmixed_low = dmixed.astype(jnp.bfloat16)
    attention_grad = inner_rows(first_act, dmixed_low)
    dfirst = lax.dot_general(
        dmixed_low, backward[0], (((1,), (1,)), ((), ())), preferred_element_type=jnp.float32
    )
    first_gain_grad = jnp.sum(dfirst * first_normed, axis=0)
    first_shift_grad = jnp.sum(dfirst, axis=0)
    input_grad = dresidual + norm_backward(dfirst, first_normed, first_inverse, back_vectors[0])
    shares = (
        lax.psum_scatter(attention_grad, "shard", scatter_dimension=0, tiled=True),
        lax.psum_scatter(output_grad, "shard", scatter_dimension=0, tiled=True),
        lax.psum_scatter(expand_grad, "shard", scatter_dimension=0, tiled=True),
        lax.psum_scatter(contract_grad, "shard", scatter_dimension=0, tiled=True),
        lax.psum_scatter(first_gain_grad, "shard", scatter_dimension=0, tiled=True),
        lax.psum_scatter(first_shift_grad, "shard", scatter_dimension=0, tiled=True),
        lax.psum_scatter(query_bias_grad, "shard", scatter_dimension=0, tiled=True),
        lax.psum_scatter(value_bias_grad, "shard", scatter_dimension=0, tiled=True),
        lax.psum_scatter(output_bias_grad, "shard", scatter_dimension=0, tiled=True),
        lax.psum_scatter(second_gain_grad, "shard", scatter_dimension=0, tiled=True),
        lax.psum_scatter(second_shift_grad, "shard", scatter_dimension=0, tiled=True),
        lax.psum_scatter(expand_bias_grad, "shard", scatter_dimension=0, tiled=True),
        lax.psum_scatter(contract_bias_grad, "shard", scatter_dimension=0, tiled=True),
    )
    totals = lax.psum(
        (
            shares[0],
            shares[1],
            shares[2],
            shares[3],
            shares[4],
            shares[5],
            shares[6],
            shares[7],
            shares[8],
            shares[9],
            shares[10],
            shares[11],
            shares[12],
        ),
        "rep",
    )
    return (
        block_output.reshape(clip_count, slot_count, width),
        input_grad.reshape(clip_count, slot_count, width),
        totals[0],
        totals[1],
        totals[2],
        totals[3],
        totals[4],
        totals[5],
        totals[6],
        totals[7],
        totals[8],
        totals[9],
        totals[10],
        totals[11],
        totals[12],
    )


def clip_layer(tokens, lengths, cotangent_of, weights, vectors, reduce, send_out):
    attention_weight, output_weight, later_weights = weights
    (first_gain, first_shift, query_bias, value_bias, output_bias, second_gain, second_shift,
     expand_bias, contract_bias) = vectors
    clip_count, frame_count, width = tokens.shape
    block_count = lengths.shape[1]
    slot_count = frame_count // block_count
    rows = clip_count * frame_count
    live = (jnp.arange(slot_count)[None, None, :] < lengths[:, :, None]).reshape(clip_count, frame_count)
    scale = HEAD ** (-0.5)
    inputs = tokens.reshape(rows, width).astype(jnp.float32)
    first_normed, first_inverse, first_act = norm_forward(inputs, first_gain, first_shift)
    mixed = jnp.dot(first_act, attention_weight, preferred_element_type=jnp.float32)
    mixed = mixed + jnp.concatenate([query_bias, jnp.zeros_like(query_bias), value_bias])
    mixed_low = mixed.astype(jnp.bfloat16).reshape(clip_count, frame_count, 3, HEADS, HEAD)
    queries = mixed_low[:, :, 0]
    keys = mixed_low[:, :, 1]
    values = mixed_low[:, :, 2]
    scores = jnp.einsum("cqhd,ckhd->chqk", queries, keys, preferred_element_type=jnp.float32) * scale
    scores = jnp.where(live[:, None, None, :], scores, NEGATIVE)
    highest = jnp.max(scores, axis=-1, keepdims=True)
    logsum = highest + jnp.log(jnp.sum(jnp.exp(scores - highest), axis=-1, keepdims=True))
    probs = jnp.exp(scores - logsum)
    expand_weight, contract_weight = later_weights(logsum[0, 0, 0, :1])
    probs_low = probs.astype(jnp.bfloat16)
    attended = jnp.einsum("chqk,ckhd->cqhd", probs_low, values, preferred_element_type=jnp.float32)
    attended_flat = attended.reshape(rows, width).astype(jnp.bfloat16)
    residual = inputs + jnp.dot(attended_flat, output_weight, preferred_element_type=jnp.float32) + output_bias
    second_normed, second_inverse, second_act = norm_forward(residual, second_gain, second_shift)
    pre = jnp.dot(second_act, expand_weight, preferred_element_type=jnp.float32) + expand_bias
    hidden_act = jax.nn.gelu(pre, approximate=False).astype(jnp.bfloat16)
    block_output = residual + jnp.dot(hidden_act, contract_weight, preferred_element_type=jnp.float32) + contract_bias
    cotangent = cotangent_of(pre[0, :1])
    error = cotangent.reshape(rows, width) * live.reshape(rows, 1).astype(jnp.float32)
    error_low = error.astype(jnp.bfloat16)
    contract_bias_grad = jnp.sum(error, axis=0)
    contract_grad = inner_rows(hidden_act, error_low)
    contract_chip = chip_sum(contract_grad)
    dpre = lax.dot_general(
        error_low, contract_weight, (((1,), (1,)), ((), ())), preferred_element_type=jnp.float32
    ) * gelu_slope(pre)
    expand_bias_grad = jnp.sum(dpre, axis=0)
    dpre_low = dpre.astype(jnp.bfloat16)
    contract_chip, dpre_low = lax.optimization_barrier((contract_chip, dpre_low))
    contract_part = shard_sum(contract_chip)
    expand_grad = inner_rows(second_act, dpre_low)
    expand_chip = chip_sum(expand_grad)
    dsecond = lax.dot_general(
        dpre_low, expand_weight, (((1,), (1,)), ((), ())), preferred_element_type=jnp.float32
    )
    second_gain_grad = jnp.sum(dsecond * second_normed, axis=0)
    second_shift_grad = jnp.sum(dsecond, axis=0)
    dresidual = error + norm_backward(dsecond, second_normed, second_inverse, second_gain)
    output_bias_grad = jnp.sum(dresidual, axis=0)
    dresidual_low = dresidual.astype(jnp.bfloat16)
    sent_output = send_out(block_output)
    expand_chip, dresidual_low = lax.optimization_barrier((expand_chip, dresidual_low))
    expand_part = shard_sum(expand_chip)
    output_grad = inner_rows(attended_flat, dresidual_low)
    output_chip = chip_sum(output_grad)
    dattended = lax.dot_general(
        dresidual_low, output_weight, (((1,), (1,)), ((), ())), preferred_element_type=jnp.float32
    ).astype(jnp.bfloat16)
    contract_part, output_chip, dattended = lax.optimization_barrier((contract_part, output_chip, dattended))
    output_part = shard_sum(output_chip)
    dattended_heads = dattended.reshape(clip_count, frame_count, HEADS, HEAD)
    attended_heads = attended_flat.reshape(clip_count, frame_count, HEADS, HEAD)
    delta = jnp.sum(
        dattended_heads.astype(jnp.float32) * attended_heads.astype(jnp.float32), axis=-1
    )
    dprob = jnp.einsum("cqhd,ckhd->chqk", dattended_heads, values, preferred_element_type=jnp.float32)
    dscore = (probs * (dprob - jnp.transpose(delta, (0, 2, 1))[:, :, :, None]) * scale).astype(jnp.bfloat16)
    dqueries = jnp.einsum("chqk,ckhd->cqhd", dscore, keys, preferred_element_type=jnp.float32)
    dkeys = jnp.einsum("chqk,cqhd->ckhd", dscore, queries, preferred_element_type=jnp.float32)
    dvalues = jnp.einsum("chqk,cqhd->ckhd", probs_low, dattended_heads, preferred_element_type=jnp.float32)
    dmixed = jnp.concatenate(
        [dqueries.reshape(rows, width), dkeys.reshape(rows, width), dvalues.reshape(rows, width)], axis=1
    )
    query_bias_grad = jnp.sum(dmixed[:, :width], axis=0)
    value_bias_grad = jnp.sum(dmixed[:, 2 * width:], axis=0)
    dmixed_low = dmixed.astype(jnp.bfloat16)
    contract_total = reduce(contract_part, contract_grad.shape[0])
    output_part, expand_part, contract_total, sent_output, dmixed_low = lax.optimization_barrier(
        (output_part, expand_part, contract_total, sent_output, dmixed_low)
    )
    expand_total = reduce(expand_part, expand_grad.shape[0])
    attention_grad = inner_rows(first_act, dmixed_low)
    dfirst = lax.optimization_barrier(lax.dot_general(
        dmixed_low, attention_weight, (((1,), (1,)), ((), ())), preferred_element_type=jnp.float32
    ))
    first_gain_grad = jnp.sum(dfirst * first_normed, axis=0)
    first_shift_grad = jnp.sum(dfirst, axis=0)
    input_grad = dresidual + norm_backward(dfirst, first_normed, first_inverse, first_gain)
    output_part, expand_total, input_grad = lax.optimization_barrier((output_part, expand_total, input_grad))
    weight_grads = (attention_grad, output_part, expand_total, contract_total)
    vector_grads = (first_gain_grad, first_shift_grad, query_bias_grad, value_bias_grad, output_bias_grad,
                    second_gain_grad, second_shift_grad, expand_bias_grad, contract_bias_grad)
    return (
        sent_output,
        input_grad,
        weight_grads,
        vector_grads,
    )


PAIR = [(0, 1), (1, 0)]
OUTER = ("outer", "inner")


def core_pick(core, first, second):
    return jnp.where(core == 0, first, second)


def gather_weight(shard_rows, extra=None):
    parts = lax.axis_size("shard")
    core = lax.axis_index("core")
    rows, width = shard_rows.shape
    half = rows // 2
    mine = lax.dynamic_slice_in_dim(shard_rows, core * half, half, axis=0)
    if extra is not None:
        mine = jnp.concatenate([mine, extra], axis=0)
    mine = lax.all_gather(mine, "shard", axis=0, tiled=False)
    other = lax.ppermute(mine, "core", PAIR)
    first = core_pick(core, mine, other)
    second = core_pick(core, other, mine)
    full = jnp.stack([first[:, :half], second[:, :half]], axis=1).reshape(parts * rows, width)
    if extra is None:
        return full, None
    return full, first[:, half:]


def chip_sum(grad, extra=None):
    parts = lax.axis_size("shard")
    core = lax.axis_index("core")
    width = grad.shape[1]
    rows = grad.shape[0] // parts
    half = rows // 2
    quarters = grad.reshape(parts, 2, half, width)
    keep = lax.dynamic_index_in_dim(quarters, core, axis=1, keepdims=False)
    send = lax.dynamic_index_in_dim(quarters, 1 - core, axis=1, keepdims=False)
    if extra is not None:
        on_first = (core == 0).astype(extra.dtype)
        keep = jnp.concatenate([keep, extra * on_first], axis=1)
        send = jnp.concatenate([send, extra * (1 - on_first)], axis=1)
    return keep + lax.ppermute(send, "core", PAIR)


def shard_sum(chip):
    part = lax.psum_scatter(chip, "shard", scatter_dimension=0, tiled=False)
    if lax.axis_size("inner") > 1:
        part = lax.psum(part, "inner")
    return part


def finish_sum(part, half):
    core = lax.axis_index("core")
    total = line_sum(part)
    other = lax.ppermute(total, "core", PAIR)
    first = core_pick(core, total, other)
    second = core_pick(core, other, total)
    return jnp.concatenate([first[:half], second[:half]], axis=0), first[half:]


def finish_many(parts, halves):
    core = lax.axis_index("core")
    flat = jnp.concatenate([part.reshape(-1) for part in parts])
    total = line_sum(flat)
    other = lax.ppermute(total, "core", PAIR)
    first = core_pick(core, total, other)
    second = core_pick(core, other, total)
    outs = []
    offset = 0
    for part, half in zip(parts, halves):
        size = part.size
        low = first[offset:offset + size].reshape(part.shape)
        high = second[offset:offset + size].reshape(part.shape)
        outs.append((jnp.concatenate([low[:half], high[:half]], axis=0), low[half:]))
        offset += size
    return outs


def reduce_weight(grad, extra=None):
    half = grad.shape[0] // lax.axis_size("shard") // 2
    return finish_sum(shard_sum(chip_sum(grad, extra)), half)


def line_sum(values):
    groups = lax.axis_size("outer")
    if groups == 1:
        return values
    if groups & (groups - 1):
        return lax.psum(values, "outer")
    here = lax.axis_index("outer")
    length = values.shape[0]
    padded = -(-length // groups) * groups
    held = jnp.pad(values, ((0, padded - length),) + ((0, 0),) * (values.ndim - 1))
    held = held.reshape((groups, padded // groups) + values.shape[1:])
    step = 1
    while step < groups:
        held = held.reshape((held.shape[0] // 2, 2) + held.shape[1:])
        bit = (here // step) % 2
        keep = lax.dynamic_index_in_dim(held, bit, axis=1, keepdims=False)
        send = lax.dynamic_index_in_dim(held, 1 - bit, axis=1, keepdims=False)
        held = keep + lax.ppermute(send, "outer", [(j, j ^ step) for j in range(groups)])
        step *= 2
    step = groups // 2
    while step >= 1:
        bit = (here // step) % 2
        other = lax.ppermute(held, "outer", [(j, j ^ step) for j in range(groups)])
        low = jnp.where(bit == 0, held, other)
        high = jnp.where(bit == 0, other, held)
        held = jnp.stack([low, high], axis=1)
        held = held.reshape((held.shape[0] * 2,) + held.shape[2:])
        step //= 2
    return held.reshape((padded,) + values.shape[1:])[:length]


def gather_packed(blocks, after=None):
    core = lax.axis_index("core")
    mine = lax.all_gather(jnp.concatenate(blocks, axis=0), "shard", axis=0, tiled=False)
    if after is not None:
        mine = mine + (after * 0).astype(mine.dtype)
    other = lax.ppermute(mine, "core", PAIR)
    return core_pick(core, mine, other), core_pick(core, other, mine)


def unpack_rows(first, second, begin, count, shape):
    parts = first.shape[0]
    rows, width = shape
    low = first[:, begin:begin + count].reshape(parts, -1, width)
    high = second[:, begin:begin + count].reshape(parts, -1, width)
    return jnp.stack([low, high], axis=1).reshape(rows, width)


def core_half(shard_rows):
    core = lax.axis_index("core")
    half = shard_rows.shape[0] // 2
    return lax.dynamic_slice_in_dim(shard_rows, core * half, half, axis=0)


def clip_local(tokens, lengths, cotangent, *params):
    clip_count, slot_count, width = tokens.shape
    parts = lax.axis_size("shard")
    place = lax.axis_index("shard")
    own = clip_count // parts
    weight_shards = params[:4]
    vector_shards = params[4:]
    wide = weight_shards[0].shape[1]
    vector_row = jnp.concatenate([entry.reshape(-1) for entry in vector_shards])
    pad = (-vector_row.shape[0]) % wide
    vector_rows = jnp.pad(vector_row, (0, pad)).reshape(-1, wide)
    attention_half = core_half(weight_shards[0])
    output_half = core_half(weight_shards[1]).reshape(-1, wide)
    first, second = gather_packed([attention_half, output_half, vector_rows])
    a_rows = attention_half.shape[0]
    o_rows = output_half.shape[0]
    attention_weight = unpack_rows(first, second, 0, a_rows, (parts * weight_shards[0].shape[0], wide))
    output_weight = unpack_rows(
        first, second, a_rows, o_rows, (parts * weight_shards[1].shape[0], weight_shards[1].shape[1])
    )
    vector_all = first[:, a_rows + o_rows:].reshape(parts, -1)[:, : vector_row.shape[0]]
    vectors = []
    offset = 0
    for entry in vector_shards:
        size = entry.shape[0]
        vectors.append(vector_all[:, offset:offset + size].reshape(parts * size).astype(jnp.float32))
        offset += size
    late = weight_shards[2].shape[1]
    expand_half = core_half(weight_shards[2])
    contract_half = core_half(weight_shards[3]).reshape(-1, late)

    def later_weights(after):
        first_b, second_b = gather_packed([expand_half, contract_half], after)
        e_rows = expand_half.shape[0]
        expand_weight = unpack_rows(first_b, second_b, 0, e_rows, (parts * weight_shards[2].shape[0], late))
        contract_weight = unpack_rows(
            first_b, second_b, e_rows, contract_half.shape[0],
            (parts * weight_shards[3].shape[0], weight_shards[3].shape[1]),
        )
        return expand_weight, contract_weight

    weights = (attention_weight, output_weight, later_weights)
    def exchange(rows):
        blocks = rows.reshape((parts, rows.shape[0] // parts) + rows.shape[1:])
        held = [lax.dynamic_index_in_dim(blocks, place, axis=0, keepdims=False)]
        for shift in range(1, parts):
            outgoing = lax.dynamic_index_in_dim(blocks, (place + shift) % parts, axis=0, keepdims=False)
            held.append(lax.ppermute(outgoing, "shard", [(i, (i + shift) % parts) for i in range(parts)]))
        stacked = jnp.stack(held[::-1], axis=0)
        doubled = jnp.concatenate([stacked, stacked], axis=0)
        start = (parts - (place + 1) % parts) % parts
        return lax.dynamic_slice_in_dim(doubled, start, parts, axis=0).reshape(rows.shape)

    def gather_rows(values, early=False):
        flat = values.reshape(clip_count * slot_count, width)
        moved = exchange(flat) if early else lax.all_to_all(flat, "shard", 0, 0, tiled=True)
        moved = moved.reshape(parts, own, slot_count, width)
        return jnp.transpose(moved, (1, 0, 2, 3)).reshape(own, parts * slot_count, width) if own > 1 else moved.reshape(own, parts * slot_count, width)

    def scatter_rows(values):
        rows = values.reshape(own, parts, slot_count, width)
        if own > 1:
            rows = jnp.transpose(rows, (1, 0, 2, 3))
        moved = lax.all_to_all(rows.reshape(own * parts * slot_count, width), "shard", 0, 0, tiled=True)
        return moved.reshape(clip_count, slot_count, width)

    tokens_clip = gather_rows(tokens, True)

    def cotangent_of(after):
        late = cotangent + (after * 0).astype(cotangent.dtype)
        return gather_rows(late)

    lengths_clip = lax.dynamic_slice_in_dim(lengths, place * own, own, axis=0)
    block_output, input_grad, weight_grads, vector_grads = clip_layer(
        tokens_clip, lengths_clip, cotangent_of, weights, vectors, lambda part, rows: finish_sum(part, rows // parts // 2)[0],
        scatter_rows,
    )
    input_grad = scatter_rows(input_grad)
    attention_grad = weight_grads[0]
    attention_width = attention_grad.shape[1]
    vector_parts = jnp.concatenate([entry.reshape(parts, -1) for entry in vector_grads], axis=1)
    vector_size = vector_parts.shape[1]
    vpad = (-vector_size) % attention_width
    vector_parts = jnp.pad(vector_parts, ((0, 0), (0, vpad))).reshape(parts, -1, attention_width)
    attention_part = shard_sum(chip_sum(attention_grad, vector_parts))
    output_part = weight_grads[1]
    (attention_total, vector_total), (output_total, _) = finish_many(
        [attention_part, output_part],
        [attention_grad.shape[0] // parts // 2, params[1].shape[0] // 2],
    )
    totals = (attention_total, output_total) + tuple(weight_grads[2:])
    vector_total = vector_total.reshape(-1)[:vector_size]
    vector_outs = []
    offset = 0
    for entry in vector_shards:
        size = entry.shape[0]
        vector_outs.append(vector_total[offset:offset + size])
        offset += size
    return (block_output, input_grad) + totals + tuple(vector_outs)


def split_rep(mesh):
    devices = mesh.devices
    rep, parts = devices.shape
    first = devices[0, 0]
    stride = None
    for index in range(1, rep):
        other = devices[index, 0]
        if tuple(other.coords) == tuple(first.coords) and other.core_on_chip != first.core_on_chip:
            stride = index
            break
    if stride is None or rep % (2 * stride):
        return None
    grid = devices.reshape(rep // (2 * stride), 2, stride, parts)
    for spot in np.ndindex(grid.shape[0], grid.shape[2], grid.shape[3]):
        low = grid[spot[0], 0, spot[1], spot[2]]
        high = grid[spot[0], 1, spot[1], spot[2]]
        if tuple(low.coords) != tuple(high.coords) or low.core_on_chip == high.core_on_chip:
            return None
    return Mesh(grid, ("outer", "core", "inner", "shard"))


def solution(mesh):
    def specs(rep):
        ins = (P(rep, "shard", None), P(rep, None), P(rep, "shard", None)) + (P("shard", None),) * 4 + (
            P("shard"),
        ) * 9
        outs = (P(rep, "shard", None), P(rep, "shard", None)) + (P("shard", None),) * 4 + (P("shard"),) * 9
        return ins, outs

    ins, outs = specs("rep")
    plain = jax.shard_map(local, mesh=mesh, in_specs=ins, out_specs=outs, check_vma=False)
    split = split_rep(mesh)
    if split is None:
        return plain
    ins, outs = specs(("outer", "core", "inner"))
    fast = jax.shard_map(clip_local, mesh=split, in_specs=ins, out_specs=outs, check_vma=False)
    rep, parts = mesh.devices.shape

    def run(*args):
        if (args[0].shape[0] // rep) % parts == 0:
            return fast(*args)
        return plain(*args)

    return run
```

```python
import jax
import jax.numpy as jnp
from jax import lax
from jax.sharding import Mesh, PartitionSpec as P
import numpy as np

HEADS = 12
HEAD = 64


EPSILON = 1e-05
NEGATIVE = -1e30


def norm_forward(values, gain, shift):
    centred = values - jnp.mean(values, axis=-1, keepdims=True)
    inverse = lax.rsqrt(jnp.mean(centred * centred, axis=-1, keepdims=True) + EPSILON)
    normed = centred * inverse
    return (normed, inverse, (normed * gain + shift).astype(jnp.bfloat16))


def norm_backward(upstream, normed, inverse, gain):
    scaled = upstream * gain
    return inverse * (
        scaled
        - jnp.mean(scaled, axis=-1, keepdims=True)
        - normed * jnp.mean(scaled * normed, axis=-1, keepdims=True)
    )


def gelu_slope(values):
    return (
        0.5 * (1.0 + jax.scipy.special.erf(values * 0.7071067811865476))
        + values * jnp.exp(-0.5 * values * values) * 0.3989422804014327
    )


def inner_rows(left, right):
    return lax.dot_general(
        left, right, (((0,), (0,)), ((), ())), preferred_element_type=jnp.float32
    )


def heads_view(matrix):
    return matrix.reshape(matrix.shape[0], HEADS, HEAD)


def score_block(query_rows, key_rows, key_live):
    scores = jnp.einsum(
        "qhd,khd->hqk",
        heads_view(query_rows),
        heads_view(key_rows),
        preferred_element_type=jnp.float32,
    ) * HEAD ** (-0.5)
    return jnp.where(key_live[None, None, :], scores, NEGATIVE)


def attend_clip(items):
    query_rows, pair_rows, key_live = items
    width = query_rows.shape[1]
    scores = score_block(query_rows, pair_rows[:, :width], key_live)
    highest = jnp.max(scores, axis=-1, keepdims=True)
    logsum = highest + jnp.log(jnp.sum(jnp.exp(scores - highest), axis=-1, keepdims=True))
    probs_low = jnp.exp(scores - logsum).astype(jnp.bfloat16)
    attended = jnp.einsum(
        "hqk,khd->qhd",
        probs_low,
        heads_view(pair_rows[:, width:]),
        preferred_element_type=jnp.float32,
    )
    return (attended.reshape(query_rows.shape[0], width).astype(jnp.bfloat16), logsum[:, :, 0].T)


def score_grads(query_rows, dattended, logsum, delta, pair_rows, key_live):
    width = query_rows.shape[1]
    scores = score_block(query_rows, pair_rows[:, :width], key_live)
    probs = jnp.exp(scores - logsum.T[:, :, None])
    dprob = jnp.einsum(
        "qhd,khd->hqk",
        heads_view(dattended),
        heads_view(pair_rows[:, width:]),
        preferred_element_type=jnp.float32,
    )
    dscore = (probs * (dprob - delta.T[:, :, None]) * HEAD ** (-0.5)).astype(jnp.bfloat16)
    return (probs.astype(jnp.bfloat16), dscore)


def both_grads(items):
    query_rows, dattended, logsum, delta, pair_rows, key_live = items
    width = query_rows.shape[1]
    probs_low, dscore = score_grads(query_rows, dattended, logsum, delta, pair_rows, key_live)
    dqueries = jnp.einsum(
        "hqk,khd->qhd", dscore, heads_view(pair_rows[:, :width]), preferred_element_type=jnp.float32
    ).reshape(query_rows.shape[0], width)
    dkeys = jnp.einsum(
        "hqk,qhd->khd", dscore, heads_view(query_rows), preferred_element_type=jnp.float32
    )
    dvalues = jnp.einsum(
        "hqk,qhd->khd", probs_low, heads_view(dattended), preferred_element_type=jnp.float32
    )
    key_count = pair_rows.shape[0]
    return (
        dqueries,
        jnp.concatenate(
            [dkeys.reshape(key_count, width), dvalues.reshape(key_count, width)], axis=1
        ),
    )


def local(
    tokens,
    lengths,
    cotangent,
    attention_weight,
    output_weight,
    expand_weight,
    contract_weight,
    first_gain,
    first_shift,
    query_bias,
    value_bias,
    output_bias,
    second_gain,
    second_shift,
    expand_bias,
    contract_bias,
):
    clip_count, slot_count, width = tokens.shape
    parts = lax.axis_size("shard")
    frame_count = slot_count * parts
    place = lax.axis_index("shard")
    row_total = clip_count * slot_count
    gathered = (
        lax.all_gather(attention_weight, "shard", axis=0, tiled=True),
        lax.all_gather(output_weight, "shard", axis=0, tiled=True),
        lax.all_gather(expand_weight, "shard", axis=0, tiled=True),
        lax.all_gather(contract_weight, "shard", axis=0, tiled=True),
        lax.all_gather(first_gain, "shard", axis=0, tiled=True),
        lax.all_gather(first_shift, "shard", axis=0, tiled=True),
        lax.all_gather(query_bias, "shard", axis=0, tiled=True),
        lax.all_gather(value_bias, "shard", axis=0, tiled=True),
        lax.all_gather(output_bias, "shard", axis=0, tiled=True),
        lax.all_gather(second_gain, "shard", axis=0, tiled=True),
        lax.all_gather(second_shift, "shard", axis=0, tiled=True),
        lax.all_gather(expand_bias, "shard", axis=0, tiled=True),
        lax.all_gather(contract_bias, "shard", axis=0, tiled=True),
    )
    vectors = [entry.astype(jnp.float32) for entry in gathered[4:]]
    own_length = jnp.sum(jnp.where(jnp.arange(parts)[None, :] == place, lengths, 0), axis=1)
    row_live = jnp.arange(slot_count)[None, :] < own_length[:, None]
    key_live = (jnp.arange(slot_count)[None, None, :] < lengths[:, :, None]).reshape(
        clip_count, frame_count
    )
    inputs = tokens.reshape(row_total, width).astype(jnp.float32)
    first_normed, first_inverse, first_act = norm_forward(inputs, vectors[0], vectors[1])
    mixed = jnp.dot(first_act, gathered[0], preferred_element_type=jnp.float32)
    mixed = mixed + jnp.concatenate([vectors[2], jnp.zeros_like(vectors[2]), vectors[3]])
    mixed_low = mixed.astype(jnp.bfloat16)
    query_rows = mixed_low[:, :width].reshape(clip_count, slot_count, width)
    pair_own = mixed_low[:, width:].reshape(clip_count, slot_count, 2 * width)
    pair_all = lax.all_gather(pair_own, "shard", axis=1, tiled=True)
    attended, logsum = lax.map(attend_clip, (query_rows, pair_all, key_live))
    attended_flat = attended.reshape(row_total, width)
    residual = (
        inputs
        + jnp.dot(attended_flat, gathered[1], preferred_element_type=jnp.float32)
        + vectors[4]
    )
    second_normed, second_inverse, second_act = norm_forward(residual, vectors[5], vectors[6])
    pre = jnp.dot(second_act, gathered[2], preferred_element_type=jnp.float32) + vectors[7]
    hidden_act = jax.nn.gelu(pre, approximate=False).astype(jnp.bfloat16)
    block_output = (
        residual + jnp.dot(hidden_act, gathered[3], preferred_element_type=jnp.float32) + vectors[8]
    )
    backward = (
        lax.all_gather(attention_weight, "shard", axis=0, tiled=True),
        lax.all_gather(output_weight, "shard", axis=0, tiled=True),
        lax.all_gather(expand_weight, "shard", axis=0, tiled=True),
        lax.all_gather(contract_weight, "shard", axis=0, tiled=True),
        lax.all_gather(first_gain, "shard", axis=0, tiled=True),
        lax.all_gather(first_shift, "shard", axis=0, tiled=True),
        lax.all_gather(query_bias, "shard", axis=0, tiled=True),
        lax.all_gather(value_bias, "shard", axis=0, tiled=True),
        lax.all_gather(output_bias, "shard", axis=0, tiled=True),
        lax.all_gather(second_gain, "shard", axis=0, tiled=True),
        lax.all_gather(second_shift, "shard", axis=0, tiled=True),
        lax.all_gather(expand_bias, "shard", axis=0, tiled=True),
        lax.all_gather(contract_bias, "shard", axis=0, tiled=True),
    )
    back_vectors = [entry.astype(jnp.float32) for entry in backward[4:]]
    error = cotangent.reshape(row_total, width) * row_live.reshape(row_total, 1).astype(jnp.float32)
    error_low = error.astype(jnp.bfloat16)
    contract_bias_grad = jnp.sum(error, axis=0)
    contract_grad = inner_rows(hidden_act, error_low)
    dpre = lax.dot_general(
        error_low, backward[3], (((1,), (1,)), ((), ())), preferred_element_type=jnp.float32
    ) * gelu_slope(pre)
    expand_bias_grad = jnp.sum(dpre, axis=0)
    dpre_low = dpre.astype(jnp.bfloat16)
    expand_grad = inner_rows(second_act, dpre_low)
    dsecond = lax.dot_general(
        dpre_low, backward[2], (((1,), (1,)), ((), ())), preferred_element_type=jnp.float32
    )
    second_gain_grad = jnp.sum(dsecond * second_normed, axis=0)
    second_shift_grad = jnp.sum(dsecond, axis=0)
    dresidual = error + norm_backward(dsecond, second_normed, second_inverse, back_vectors[5])
    output_bias_grad = jnp.sum(dresidual, axis=0)
    dresidual_low = dresidual.astype(jnp.bfloat16)
    output_grad = inner_rows(attended_flat, dresidual_low)
    dattended = lax.dot_general(
        dresidual_low, backward[1], (((1,), (1,)), ((), ())), preferred_element_type=jnp.float32
    ).astype(jnp.bfloat16)
    delta = jnp.sum(
        heads_view(dattended.astype(jnp.float32)) * heads_view(attended_flat.astype(jnp.float32)),
        axis=-1,
    )
    delta = delta.reshape(clip_count, slot_count, HEADS)
    dattended_clips = dattended.reshape(clip_count, slot_count, width)
    dqueries, pair_terms = lax.map(
        both_grads, (query_rows, dattended_clips, logsum, delta, pair_all, key_live)
    )
    pair_grads = lax.psum_scatter(pair_terms, "shard", scatter_dimension=1, tiled=True)
    dqueries_flat = dqueries.reshape(row_total, width)
    pair_flat = pair_grads.reshape(row_total, 2 * width)
    dmixed = jnp.concatenate([dqueries_flat, pair_flat], axis=1)
    query_bias_grad = jnp.sum(dqueries_flat, axis=0)
    value_bias_grad = jnp.sum(pair_flat[:, width:], axis=0)
    dmixed_low = dmixed.astype(jnp.bfloat16)
    attention_grad = inner_rows(first_act, dmixed_low)
    dfirst = lax.dot_general(
        dmixed_low, backward[0], (((1,), (1,)), ((), ())), preferred_element_type=jnp.float32
    )
    first_gain_grad = jnp.sum(dfirst * first_normed, axis=0)
    first_shift_grad = jnp.sum(dfirst, axis=0)
    input_grad = dresidual + norm_backward(dfirst, first_normed, first_inverse, back_vectors[0])
    shares = (
        lax.psum_scatter(attention_grad, "shard", scatter_dimension=0, tiled=True),
        lax.psum_scatter(output_grad, "shard", scatter_dimension=0, tiled=True),
        lax.psum_scatter(expand_grad, "shard", scatter_dimension=0, tiled=True),
        lax.psum_scatter(contract_grad, "shard", scatter_dimension=0, tiled=True),
        lax.psum_scatter(first_gain_grad, "shard", scatter_dimension=0, tiled=True),
        lax.psum_scatter(first_shift_grad, "shard", scatter_dimension=0, tiled=True),
        lax.psum_scatter(query_bias_grad, "shard", scatter_dimension=0, tiled=True),
        lax.psum_scatter(value_bias_grad, "shard", scatter_dimension=0, tiled=True),
        lax.psum_scatter(output_bias_grad, "shard", scatter_dimension=0, tiled=True),
        lax.psum_scatter(second_gain_grad, "shard", scatter_dimension=0, tiled=True),
        lax.psum_scatter(second_shift_grad, "shard", scatter_dimension=0, tiled=True),
        lax.psum_scatter(expand_bias_grad, "shard", scatter_dimension=0, tiled=True),
        lax.psum_scatter(contract_bias_grad, "shard", scatter_dimension=0, tiled=True),
    )
    totals = lax.psum(
        (
            shares[0],
            shares[1],
            shares[2],
            shares[3],
            shares[4],
            shares[5],
            shares[6],
            shares[7],
            shares[8],
            shares[9],
            shares[10],
            shares[11],
            shares[12],
        ),
        "rep",
    )
    return (
        block_output.reshape(clip_count, slot_count, width),
        input_grad.reshape(clip_count, slot_count, width),
        totals[0],
        totals[1],
        totals[2],
        totals[3],
        totals[4],
        totals[5],
        totals[6],
        totals[7],
        totals[8],
        totals[9],
        totals[10],
        totals[11],
        totals[12],
    )


def clip_layer(tokens, lengths, cotangent_of, weights, vectors, reduce, send_out):
    attention_weight, output_weight, later_weights = weights
    (first_gain, first_shift, query_bias, value_bias, output_bias, second_gain, second_shift,
     expand_bias, contract_bias) = vectors
    clip_count, frame_count, width = tokens.shape
    block_count = lengths.shape[1]
    slot_count = frame_count // block_count
    rows = clip_count * frame_count
    live = (jnp.arange(slot_count)[None, None, :] < lengths[:, :, None]).reshape(clip_count, frame_count)
    scale = HEAD ** (-0.5)
    inputs = tokens.reshape(rows, width).astype(jnp.float32)
    first_normed, first_inverse, first_act = norm_forward(inputs, first_gain, first_shift)
    mixed = jnp.dot(first_act, attention_weight, preferred_element_type=jnp.float32)
    mixed = mixed + jnp.concatenate([query_bias, jnp.zeros_like(query_bias), value_bias])
    mixed_low = mixed.astype(jnp.bfloat16).reshape(clip_count, frame_count, 3, HEADS, HEAD)
    queries = mixed_low[:, :, 0]
    keys = mixed_low[:, :, 1]
    values = mixed_low[:, :, 2]
    scores = jnp.einsum("cqhd,ckhd->chqk", queries, keys, preferred_element_type=jnp.float32) * scale
    scores = jnp.where(live[:, None, None, :], scores, NEGATIVE)
    highest = jnp.max(scores, axis=-1, keepdims=True)
    logsum = highest + jnp.log(jnp.sum(jnp.exp(scores - highest), axis=-1, keepdims=True))
    probs = jnp.exp(scores - logsum)
    expand_weight, contract_weight = later_weights(logsum[0, 0, 0, :1])
    probs_low = probs.astype(jnp.bfloat16)
    attended = jnp.einsum("chqk,ckhd->cqhd", probs_low, values, preferred_element_type=jnp.float32)
    attended_flat = attended.reshape(rows, width).astype(jnp.bfloat16)
    residual = inputs + jnp.dot(attended_flat, output_weight, preferred_element_type=jnp.float32) + output_bias
    second_normed, second_inverse, second_act = norm_forward(residual, second_gain, second_shift)
    pre = jnp.dot(second_act, expand_weight, preferred_element_type=jnp.float32) + expand_bias
    hidden_act = jax.nn.gelu(pre, approximate=False).astype(jnp.bfloat16)
    block_output = residual + jnp.dot(hidden_act, contract_weight, preferred_element_type=jnp.float32) + contract_bias
    cotangent = cotangent_of(pre[0, :1])
    error = cotangent.reshape(rows, width) * live.reshape(rows, 1).astype(jnp.float32)
    error_low = error.astype(jnp.bfloat16)
    contract_bias_grad = jnp.sum(error, axis=0)
    contract_grad = inner_rows(hidden_act, error_low)
    contract_chip = chip_sum(contract_grad)
    dpre = lax.dot_general(
        error_low, contract_weight, (((1,), (1,)), ((), ())), preferred_element_type=jnp.float32
    ) * gelu_slope(pre)
    expand_bias_grad = jnp.sum(dpre, axis=0)
    dpre_low = dpre.astype(jnp.bfloat16)
    contract_chip, dpre_low = lax.optimization_barrier((contract_chip, dpre_low))
    contract_part = shard_sum(contract_chip)
    expand_grad = inner_rows(second_act, dpre_low)
    expand_chip = chip_sum(expand_grad)
    dsecond = lax.dot_general(
        dpre_low, expand_weight, (((1,), (1,)), ((), ())), preferred_element_type=jnp.float32
    )
    second_gain_grad = jnp.sum(dsecond * second_normed, axis=0)
    second_shift_grad = jnp.sum(dsecond, axis=0)
    dresidual = error + norm_backward(dsecond, second_normed, second_inverse, second_gain)
    output_bias_grad = jnp.sum(dresidual, axis=0)
    dresidual_low = dresidual.astype(jnp.bfloat16)
    sent_output = send_out(block_output)
    expand_chip, dresidual_low = lax.optimization_barrier((expand_chip, dresidual_low))
    expand_part = shard_sum(expand_chip)
    output_grad = inner_rows(attended_flat, dresidual_low)
    output_chip = chip_sum(output_grad)
    dattended = lax.dot_general(
        dresidual_low, output_weight, (((1,), (1,)), ((), ())), preferred_element_type=jnp.float32
    ).astype(jnp.bfloat16)
    contract_part, output_chip, dattended = lax.optimization_barrier((contract_part, output_chip, dattended))
    output_part = shard_sum(output_chip)
    dattended_heads = dattended.reshape(clip_count, frame_count, HEADS, HEAD)
    attended_heads = attended_flat.reshape(clip_count, frame_count, HEADS, HEAD)
    delta = jnp.sum(
        dattended_heads.astype(jnp.float32) * attended_heads.astype(jnp.float32), axis=-1
    )
    dprob = jnp.einsum("cqhd,ckhd->chqk", dattended_heads, values, preferred_element_type=jnp.float32)
    dscore = (probs * (dprob - jnp.transpose(delta, (0, 2, 1))[:, :, :, None]) * scale).astype(jnp.bfloat16)
    dqueries = jnp.einsum("chqk,ckhd->cqhd", dscore, keys, preferred_element_type=jnp.float32)
    dkeys = jnp.einsum("chqk,cqhd->ckhd", dscore, queries, preferred_element_type=jnp.float32)
    dvalues = jnp.einsum("chqk,cqhd->ckhd", probs_low, dattended_heads, preferred_element_type=jnp.float32)
    dmixed = jnp.concatenate(
        [dqueries.reshape(rows, width), dkeys.reshape(rows, width), dvalues.reshape(rows, width)], axis=1
    )
    query_bias_grad = jnp.sum(dmixed[:, :width], axis=0)
    value_bias_grad = jnp.sum(dmixed[:, 2 * width:], axis=0)
    dmixed_low = dmixed.astype(jnp.bfloat16)
    contract_total = reduce(contract_part, contract_grad.shape[0])
    output_part, expand_part, contract_total, sent_output, dmixed_low = lax.optimization_barrier(
        (output_part, expand_part, contract_total, sent_output, dmixed_low)
    )
    expand_total = reduce(expand_part, expand_grad.shape[0])
    attention_grad = inner_rows(first_act, dmixed_low)
    dfirst = lax.dot_general(
        dmixed_low, attention_weight, (((1,), (1,)), ((), ())), preferred_element_type=jnp.float32
    )
    first_gain_grad = jnp.sum(dfirst * first_normed, axis=0)
    first_shift_grad = jnp.sum(dfirst, axis=0)
    input_grad = dresidual + norm_backward(dfirst, first_normed, first_inverse, first_gain)
    output_part, expand_total, input_grad = lax.optimization_barrier((output_part, expand_total, input_grad))
    weight_grads = (attention_grad, output_part, expand_total, contract_total)
    vector_grads = (first_gain_grad, first_shift_grad, query_bias_grad, value_bias_grad, output_bias_grad,
                    second_gain_grad, second_shift_grad, expand_bias_grad, contract_bias_grad)
    return (
        sent_output,
        input_grad,
        weight_grads,
        vector_grads,
    )


PAIR = [(0, 1), (1, 0)]
OUTER = ("outer", "inner")


def core_pick(core, first, second):
    return jnp.where(core == 0, first, second)


def gather_weight(shard_rows, extra=None):
    parts = lax.axis_size("shard")
    core = lax.axis_index("core")
    rows, width = shard_rows.shape
    half = rows // 2
    mine = lax.dynamic_slice_in_dim(shard_rows, core * half, half, axis=0)
    if extra is not None:
        mine = jnp.concatenate([mine, extra], axis=0)
    mine = lax.all_gather(mine, "shard", axis=0, tiled=False)
    other = lax.ppermute(mine, "core", PAIR)
    first = core_pick(core, mine, other)
    second = core_pick(core, other, mine)
    full = jnp.stack([first[:, :half], second[:, :half]], axis=1).reshape(parts * rows, width)
    if extra is None:
        return full, None
    return full, first[:, half:]


def chip_sum(grad, extra=None):
    parts = lax.axis_size("shard")
    core = lax.axis_index("core")
    width = grad.shape[1]
    rows = grad.shape[0] // parts
    half = rows // 2
    quarters = grad.reshape(parts, 2, half, width)
    keep = lax.dynamic_index_in_dim(quarters, core, axis=1, keepdims=False)
    send = lax.dynamic_index_in_dim(quarters, 1 - core, axis=1, keepdims=False)
    if extra is not None:
        on_first = (core == 0).astype(extra.dtype)
        keep = jnp.concatenate([keep, extra * on_first], axis=1)
        send = jnp.concatenate([send, extra * (1 - on_first)], axis=1)
    return keep + lax.ppermute(send, "core", PAIR)


def shard_sum(chip):
    part = lax.psum_scatter(chip, "shard", scatter_dimension=0, tiled=False)
    if lax.axis_size("inner") > 1:
        part = lax.psum(part, "inner")
    return part


def finish_sum(part, half):
    core = lax.axis_index("core")
    total = line_sum(part)
    other = lax.ppermute(total, "core", PAIR)
    first = core_pick(core, total, other)
    second = core_pick(core, other, total)
    return jnp.concatenate([first[:half], second[:half]], axis=0), first[half:]


def finish_many(parts, halves):
    core = lax.axis_index("core")
    flat = jnp.concatenate([part.reshape(-1) for part in parts])
    total = line_sum(flat)
    other = lax.ppermute(total, "core", PAIR)
    first = core_pick(core, total, other)
    second = core_pick(core, other, total)
    outs = []
    offset = 0
    for part, half in zip(parts, halves):
        size = part.size
        low = first[offset:offset + size].reshape(part.shape)
        high = second[offset:offset + size].reshape(part.shape)
        outs.append((jnp.concatenate([low[:half], high[:half]], axis=0), low[half:]))
        offset += size
    return outs


def reduce_weight(grad, extra=None):
    half = grad.shape[0] // lax.axis_size("shard") // 2
    return finish_sum(shard_sum(chip_sum(grad, extra)), half)


def line_sum(values):
    groups = lax.axis_size("outer")
    if groups == 1:
        return values
    if groups & (groups - 1):
        return lax.psum(values, "outer")
    here = lax.axis_index("outer")
    length = values.shape[0]
    padded = -(-length // groups) * groups
    held = jnp.pad(values, ((0, padded - length),) + ((0, 0),) * (values.ndim - 1))
    held = held.reshape((groups, padded // groups) + values.shape[1:])
    step = 1
    while step < groups:
        held = held.reshape((held.shape[0] // 2, 2) + held.shape[1:])
        bit = (here // step) % 2
        keep = lax.dynamic_index_in_dim(held, bit, axis=1, keepdims=False)
        send = lax.dynamic_index_in_dim(held, 1 - bit, axis=1, keepdims=False)
        held = keep + lax.ppermute(send, "outer", [(j, j ^ step) for j in range(groups)])
        step *= 2
    step = groups // 2
    while step >= 1:
        bit = (here // step) % 2
        other = lax.ppermute(held, "outer", [(j, j ^ step) for j in range(groups)])
        low = jnp.where(bit == 0, held, other)
        high = jnp.where(bit == 0, other, held)
        held = jnp.stack([low, high], axis=1)
        held = held.reshape((held.shape[0] * 2,) + held.shape[2:])
        step //= 2
    return held.reshape((padded,) + values.shape[1:])[:length]


def gather_packed(blocks, after=None):
    core = lax.axis_index("core")
    mine = lax.all_gather(jnp.concatenate(blocks, axis=0), "shard", axis=0, tiled=False)
    if after is not None:
        mine = mine + (after * 0).astype(mine.dtype)
    other = lax.ppermute(mine, "core", PAIR)
    return core_pick(core, mine, other), core_pick(core, other, mine)


def unpack_rows(first, second, begin, count, shape):
    parts = first.shape[0]
    rows, width = shape
    low = first[:, begin:begin + count].reshape(parts, -1, width)
    high = second[:, begin:begin + count].reshape(parts, -1, width)
    return jnp.stack([low, high], axis=1).reshape(rows, width)


def core_half(shard_rows):
    core = lax.axis_index("core")
    half = shard_rows.shape[0] // 2
    return lax.dynamic_slice_in_dim(shard_rows, core * half, half, axis=0)


def clip_local(tokens, lengths, cotangent, *params):
    clip_count, slot_count, width = tokens.shape
    parts = lax.axis_size("shard")
    place = lax.axis_index("shard")
    own = clip_count // parts
    weight_shards = params[:4]
    vector_shards = params[4:]
    wide = weight_shards[0].shape[1]
    vector_row = jnp.concatenate([entry.reshape(-1) for entry in vector_shards])
    pad = (-vector_row.shape[0]) % wide
    vector_rows = jnp.pad(vector_row, (0, pad)).reshape(-1, wide)
    attention_half = core_half(weight_shards[0])
    output_half = core_half(weight_shards[1]).reshape(-1, wide)
    first, second = gather_packed([attention_half, output_half, vector_rows])
    a_rows = attention_half.shape[0]
    o_rows = output_half.shape[0]
    attention_weight = unpack_rows(first, second, 0, a_rows, (parts * weight_shards[0].shape[0], wide))
    output_weight = unpack_rows(
        first, second, a_rows, o_rows, (parts * weight_shards[1].shape[0], weight_shards[1].shape[1])
    )
    vector_all = first[:, a_rows + o_rows:].reshape(parts, -1)[:, : vector_row.shape[0]]
    vectors = []
    offset = 0
    for entry in vector_shards:
        size = entry.shape[0]
        vectors.append(vector_all[:, offset:offset + size].reshape(parts * size).astype(jnp.float32))
        offset += size
    late = weight_shards[2].shape[1]
    expand_half = core_half(weight_shards[2])
    contract_half = core_half(weight_shards[3]).reshape(-1, late)

    def later_weights(after):
        first_b, second_b = gather_packed([expand_half, contract_half], after)
        e_rows = expand_half.shape[0]
        expand_weight = unpack_rows(first_b, second_b, 0, e_rows, (parts * weight_shards[2].shape[0], late))
        contract_weight = unpack_rows(
            first_b, second_b, e_rows, contract_half.shape[0],
            (parts * weight_shards[3].shape[0], weight_shards[3].shape[1]),
        )
        return expand_weight, contract_weight

    weights = (attention_weight, output_weight, later_weights)
    def exchange(rows):
        blocks = rows.reshape((parts, rows.shape[0] // parts) + rows.shape[1:])
        held = [lax.dynamic_index_in_dim(blocks, place, axis=0, keepdims=False)]
        for shift in range(1, parts):
            outgoing = lax.dynamic_index_in_dim(blocks, (place + shift) % parts, axis=0, keepdims=False)
            held.append(lax.ppermute(outgoing, "shard", [(i, (i + shift) % parts) for i in range(parts)]))
        stacked = jnp.stack(held[::-1], axis=0)
        doubled = jnp.concatenate([stacked, stacked], axis=0)
        start = (parts - (place + 1) % parts) % parts
        return lax.dynamic_slice_in_dim(doubled, start, parts, axis=0).reshape(rows.shape)

    def gather_rows(values, early=False):
        flat = values.reshape(clip_count * slot_count, width)
        moved = exchange(flat) if early else lax.all_to_all(flat, "shard", 0, 0, tiled=True)
        moved = moved.reshape(parts, own, slot_count, width)
        return jnp.transpose(moved, (1, 0, 2, 3)).reshape(own, parts * slot_count, width) if own > 1 else moved.reshape(own, parts * slot_count, width)

    def scatter_rows(values):
        rows = values.reshape(own, parts, slot_count, width)
        if own > 1:
            rows = jnp.transpose(rows, (1, 0, 2, 3))
        moved = lax.all_to_all(rows.reshape(own * parts * slot_count, width), "shard", 0, 0, tiled=True)
        return moved.reshape(clip_count, slot_count, width)

    tokens_clip = gather_rows(tokens, True)

    def cotangent_of(after):
        late = cotangent + (after * 0).astype(cotangent.dtype)
        return gather_rows(late)

    lengths_clip = lax.dynamic_slice_in_dim(lengths, place * own, own, axis=0)
    block_output, input_grad, weight_grads, vector_grads = clip_layer(
        tokens_clip, lengths_clip, cotangent_of, weights, vectors, lambda part, rows: finish_sum(part, rows // parts // 2)[0],
        scatter_rows,
    )
    input_grad = scatter_rows(input_grad)
    attention_grad = weight_grads[0]
    attention_width = attention_grad.shape[1]
    vector_parts = jnp.concatenate([entry.reshape(parts, -1) for entry in vector_grads], axis=1)
    vector_size = vector_parts.shape[1]
    vpad = (-vector_size) % attention_width
    vector_parts = jnp.pad(vector_parts, ((0, 0), (0, vpad))).reshape(parts, -1, attention_width)
    attention_part = shard_sum(chip_sum(attention_grad, vector_parts))
    output_part = weight_grads[1]
    (attention_total, vector_total), (output_total, _) = finish_many(
        [attention_part, output_part],
        [attention_grad.shape[0] // parts // 2, params[1].shape[0] // 2],
    )
    totals = (attention_total, output_total) + tuple(weight_grads[2:])
    vector_total = vector_total.reshape(-1)[:vector_size]
    vector_outs = []
    offset = 0
    for entry in vector_shards:
        size = entry.shape[0]
        vector_outs.append(vector_total[offset:offset + size])
        offset += size
    return (block_output, input_grad) + totals + tuple(vector_outs)


def split_rep(mesh):
    devices = mesh.devices
    rep, parts = devices.shape
    first = devices[0, 0]
    stride = None
    for index in range(1, rep):
        other = devices[index, 0]
        if tuple(other.coords) == tuple(first.coords) and other.core_on_chip != first.core_on_chip:
            stride = index
            break
    if stride is None or rep % (2 * stride):
        return None
    grid = devices.reshape(rep // (2 * stride), 2, stride, parts)
    for spot in np.ndindex(grid.shape[0], grid.shape[2], grid.shape[3]):
        low = grid[spot[0], 0, spot[1], spot[2]]
        high = grid[spot[0], 1, spot[1], spot[2]]
        if tuple(low.coords) != tuple(high.coords) or low.core_on_chip == high.core_on_chip:
            return None
    return Mesh(grid, ("outer", "core", "inner", "shard"))


def solution(mesh):
    def specs(rep):
        ins = (P(rep, "shard", None), P(rep, None), P(rep, "shard", None)) + (P("shard", None),) * 4 + (
            P("shard"),
        ) * 9
        outs = (P(rep, "shard", None), P(rep, "shard", None)) + (P("shard", None),) * 4 + (P("shard"),) * 9
        return ins, outs

    ins, outs = specs("rep")
    plain = jax.shard_map(local, mesh=mesh, in_specs=ins, out_specs=outs, check_vma=False)
    split = split_rep(mesh)
    if split is None:
        return plain
    ins, outs = specs(("outer", "core", "inner"))
    fast = jax.shard_map(clip_local, mesh=split, in_specs=ins, out_specs=outs, check_vma=False)
    rep, parts = mesh.devices.shape

    def run(*args):
        if (args[0].shape[0] // rep) % parts == 0:
            return fast(*args)
        return plain(*args)

    return run
```

```python
import jax
import jax.numpy as jnp
from jax import lax
from jax.sharding import Mesh, PartitionSpec as P
import numpy as np

HEADS = 12
HEAD = 64


EPSILON = 1e-05
NEGATIVE = -1e30


def norm_forward(values, gain, shift):
    centred = values - jnp.mean(values, axis=-1, keepdims=True)
    inverse = lax.rsqrt(jnp.mean(centred * centred, axis=-1, keepdims=True) + EPSILON)
    normed = centred * inverse
    return (normed, inverse, (normed * gain + shift).astype(jnp.bfloat16))


def norm_backward(upstream, normed, inverse, gain):
    scaled = upstream * gain
    return inverse * (
        scaled
        - jnp.mean(scaled, axis=-1, keepdims=True)
        - normed * jnp.mean(scaled * normed, axis=-1, keepdims=True)
    )


def gelu_slope(values):
    return (
        0.5 * (1.0 + jax.scipy.special.erf(values * 0.7071067811865476))
        + values * jnp.exp(-0.5 * values * values) * 0.3989422804014327
    )


def inner_rows(left, right):
    return lax.dot_general(
        left, right, (((0,), (0,)), ((), ())), preferred_element_type=jnp.float32
    )


def heads_view(matrix):
    return matrix.reshape(matrix.shape[0], HEADS, HEAD)


def score_block(query_rows, key_rows, key_live):
    scores = jnp.einsum(
        "qhd,khd->hqk",
        heads_view(query_rows),
        heads_view(key_rows),
        preferred_element_type=jnp.float32,
    ) * HEAD ** (-0.5)
    return jnp.where(key_live[None, None, :], scores, NEGATIVE)


def attend_clip(items):
    query_rows, pair_rows, key_live = items
    width = query_rows.shape[1]
    scores = score_block(query_rows, pair_rows[:, :width], key_live)
    highest = jnp.max(scores, axis=-1, keepdims=True)
    logsum = highest + jnp.log(jnp.sum(jnp.exp(scores - highest), axis=-1, keepdims=True))
    probs_low = jnp.exp(scores - logsum).astype(jnp.bfloat16)
    attended = jnp.einsum(
        "hqk,khd->qhd",
        probs_low,
        heads_view(pair_rows[:, width:]),
        preferred_element_type=jnp.float32,
    )
    return (attended.reshape(query_rows.shape[0], width).astype(jnp.bfloat16), logsum[:, :, 0].T)


def score_grads(query_rows, dattended, logsum, delta, pair_rows, key_live):
    width = query_rows.shape[1]
    scores = score_block(query_rows, pair_rows[:, :width], key_live)
    probs = jnp.exp(scores - logsum.T[:, :, None])
    dprob = jnp.einsum(
        "qhd,khd->hqk",
        heads_view(dattended),
        heads_view(pair_rows[:, width:]),
        preferred_element_type=jnp.float32,
    )
    dscore = (probs * (dprob - delta.T[:, :, None]) * HEAD ** (-0.5)).astype(jnp.bfloat16)
    return (probs.astype(jnp.bfloat16), dscore)


def both_grads(items):
    query_rows, dattended, logsum, delta, pair_rows, key_live = items
    width = query_rows.shape[1]
    probs_low, dscore = score_grads(query_rows, dattended, logsum, delta, pair_rows, key_live)
    dqueries = jnp.einsum(
        "hqk,khd->qhd", dscore, heads_view(pair_rows[:, :width]), preferred_element_type=jnp.float32
    ).reshape(query_rows.shape[0], width)
    dkeys = jnp.einsum(
        "hqk,qhd->khd", dscore, heads_view(query_rows), preferred_element_type=jnp.float32
    )
    dvalues = jnp.einsum(
        "hqk,qhd->khd", probs_low, heads_view(dattended), preferred_element_type=jnp.float32
    )
    key_count = pair_rows.shape[0]
    return (
        dqueries,
        jnp.concatenate(
            [dkeys.reshape(key_count, width), dvalues.reshape(key_count, width)], axis=1
        ),
    )


def local(
    tokens,
    lengths,
    cotangent,
    attention_weight,
    output_weight,
    expand_weight,
    contract_weight,
    first_gain,
    first_shift,
    query_bias,
    value_bias,
    output_bias,
    second_gain,
    second_shift,
    expand_bias,
    contract_bias,
):
    clip_count, slot_count, width = tokens.shape
    parts = lax.axis_size("shard")
    frame_count = slot_count * parts
    place = lax.axis_index("shard")
    row_total = clip_count * slot_count
    gathered = (
        lax.all_gather(attention_weight, "shard", axis=0, tiled=True),
        lax.all_gather(output_weight, "shard", axis=0, tiled=True),
        lax.all_gather(expand_weight, "shard", axis=0, tiled=True),
        lax.all_gather(contract_weight, "shard", axis=0, tiled=True),
        lax.all_gather(first_gain, "shard", axis=0, tiled=True),
        lax.all_gather(first_shift, "shard", axis=0, tiled=True),
        lax.all_gather(query_bias, "shard", axis=0, tiled=True),
        lax.all_gather(value_bias, "shard", axis=0, tiled=True),
        lax.all_gather(output_bias, "shard", axis=0, tiled=True),
        lax.all_gather(second_gain, "shard", axis=0, tiled=True),
        lax.all_gather(second_shift, "shard", axis=0, tiled=True),
        lax.all_gather(expand_bias, "shard", axis=0, tiled=True),
        lax.all_gather(contract_bias, "shard", axis=0, tiled=True),
    )
    vectors = [entry.astype(jnp.float32) for entry in gathered[4:]]
    own_length = jnp.sum(jnp.where(jnp.arange(parts)[None, :] == place, lengths, 0), axis=1)
    row_live = jnp.arange(slot_count)[None, :] < own_length[:, None]
    key_live = (jnp.arange(slot_count)[None, None, :] < lengths[:, :, None]).reshape(
        clip_count, frame_count
    )
    inputs = tokens.reshape(row_total, width).astype(jnp.float32)
    first_normed, first_inverse, first_act = norm_forward(inputs, vectors[0], vectors[1])
    mixed = jnp.dot(first_act, gathered[0], preferred_element_type=jnp.float32)
    mixed = mixed + jnp.concatenate([vectors[2], jnp.zeros_like(vectors[2]), vectors[3]])
    mixed_low = mixed.astype(jnp.bfloat16)
    query_rows = mixed_low[:, :width].reshape(clip_count, slot_count, width)
    pair_own = mixed_low[:, width:].reshape(clip_count, slot_count, 2 * width)
    pair_all = lax.all_gather(pair_own, "shard", axis=1, tiled=True)
    attended, logsum = lax.map(attend_clip, (query_rows, pair_all, key_live))
    attended_flat = attended.reshape(row_total, width)
    residual = (
        inputs
        + jnp.dot(attended_flat, gathered[1], preferred_element_type=jnp.float32)
        + vectors[4]
    )
    second_normed, second_inverse, second_act = norm_forward(residual, vectors[5], vectors[6])
    pre = jnp.dot(second_act, gathered[2], preferred_element_type=jnp.float32) + vectors[7]
    hidden_act = jax.nn.gelu(pre, approximate=False).astype(jnp.bfloat16)
    block_output = (
        residual + jnp.dot(hidden_act, gathered[3], preferred_element_type=jnp.float32) + vectors[8]
    )
    backward = (
        lax.all_gather(attention_weight, "shard", axis=0, tiled=True),
        lax.all_gather(output_weight, "shard", axis=0, tiled=True),
        lax.all_gather(expand_weight, "shard", axis=0, tiled=True),
        lax.all_gather(contract_weight, "shard", axis=0, tiled=True),
        lax.all_gather(first_gain, "shard", axis=0, tiled=True),
        lax.all_gather(first_shift, "shard", axis=0, tiled=True),
        lax.all_gather(query_bias, "shard", axis=0, tiled=True),
        lax.all_gather(value_bias, "shard", axis=0, tiled=True),
        lax.all_gather(output_bias, "shard", axis=0, tiled=True),
        lax.all_gather(second_gain, "shard", axis=0, tiled=True),
        lax.all_gather(second_shift, "shard", axis=0, tiled=True),
        lax.all_gather(expand_bias, "shard", axis=0, tiled=True),
        lax.all_gather(contract_bias, "shard", axis=0, tiled=True),
    )
    back_vectors = [entry.astype(jnp.float32) for entry in backward[4:]]
    error = cotangent.reshape(row_total, width) * row_live.reshape(row_total, 1).astype(jnp.float32)
    error_low = error.astype(jnp.bfloat16)
    contract_bias_grad = jnp.sum(error, axis=0)
    contract_grad = inner_rows(hidden_act, error_low)
    dpre = lax.dot_general(
        error_low, backward[3], (((1,), (1,)), ((), ())), preferred_element_type=jnp.float32
    ) * gelu_slope(pre)
    expand_bias_grad = jnp.sum(dpre, axis=0)
    dpre_low = dpre.astype(jnp.bfloat16)
    expand_grad = inner_rows(second_act, dpre_low)
    dsecond = lax.dot_general(
        dpre_low, backward[2], (((1,), (1,)), ((), ())), preferred_element_type=jnp.float32
    )
    second_gain_grad = jnp.sum(dsecond * second_normed, axis=0)
    second_shift_grad = jnp.sum(dsecond, axis=0)
    dresidual = error + norm_backward(dsecond, second_normed, second_inverse, back_vectors[5])
    output_bias_grad = jnp.sum(dresidual, axis=0)
    dresidual_low = dresidual.astype(jnp.bfloat16)
    output_grad = inner_rows(attended_flat, dresidual_low)
    dattended = lax.dot_general(
        dresidual_low, backward[1], (((1,), (1,)), ((), ())), preferred_element_type=jnp.float32
    ).astype(jnp.bfloat16)
    delta = jnp.sum(
        heads_view(dattended.astype(jnp.float32)) * heads_view(attended_flat.astype(jnp.float32)),
        axis=-1,
    )
    delta = delta.reshape(clip_count, slot_count, HEADS)
    dattended_clips = dattended.reshape(clip_count, slot_count, width)
    dqueries, pair_terms = lax.map(
        both_grads, (query_rows, dattended_clips, logsum, delta, pair_all, key_live)
    )
    pair_grads = lax.psum_scatter(pair_terms, "shard", scatter_dimension=1, tiled=True)
    dqueries_flat = dqueries.reshape(row_total, width)
    pair_flat = pair_grads.reshape(row_total, 2 * width)
    dmixed = jnp.concatenate([dqueries_flat, pair_flat], axis=1)
    query_bias_grad = jnp.sum(dqueries_flat, axis=0)
    value_bias_grad = jnp.sum(pair_flat[:, width:], axis=0)
    dmixed_low = dmixed.astype(jnp.bfloat16)
    attention_grad = inner_rows(first_act, dmixed_low)
    dfirst = lax.dot_general(
        dmixed_low, backward[0], (((1,), (1,)), ((), ())), preferred_element_type=jnp.float32
    )
    first_gain_grad = jnp.sum(dfirst * first_normed, axis=0)
    first_shift_grad = jnp.sum(dfirst, axis=0)
    input_grad = dresidual + norm_backward(dfirst, first_normed, first_inverse, back_vectors[0])
    shares = (
        lax.psum_scatter(attention_grad, "shard", scatter_dimension=0, tiled=True),
        lax.psum_scatter(output_grad, "shard", scatter_dimension=0, tiled=True),
        lax.psum_scatter(expand_grad, "shard", scatter_dimension=0, tiled=True),
        lax.psum_scatter(contract_grad, "shard", scatter_dimension=0, tiled=True),
        lax.psum_scatter(first_gain_grad, "shard", scatter_dimension=0, tiled=True),
        lax.psum_scatter(first_shift_grad, "shard", scatter_dimension=0, tiled=True),
        lax.psum_scatter(query_bias_grad, "shard", scatter_dimension=0, tiled=True),
        lax.psum_scatter(value_bias_grad, "shard", scatter_dimension=0, tiled=True),
        lax.psum_scatter(output_bias_grad, "shard", scatter_dimension=0, tiled=True),
        lax.psum_scatter(second_gain_grad, "shard", scatter_dimension=0, tiled=True),
        lax.psum_scatter(second_shift_grad, "shard", scatter_dimension=0, tiled=True),
        lax.psum_scatter(expand_bias_grad, "shard", scatter_dimension=0, tiled=True),
        lax.psum_scatter(contract_bias_grad, "shard", scatter_dimension=0, tiled=True),
    )
    totals = lax.psum(
        (
            shares[0],
            shares[1],
            shares[2],
            shares[3],
            shares[4],
            shares[5],
            shares[6],
            shares[7],
            shares[8],
            shares[9],
            shares[10],
            shares[11],
            shares[12],
        ),
        "rep",
    )
    return (
        block_output.reshape(clip_count, slot_count, width),
        input_grad.reshape(clip_count, slot_count, width),
        totals[0],
        totals[1],
        totals[2],
        totals[3],
        totals[4],
        totals[5],
        totals[6],
        totals[7],
        totals[8],
        totals[9],
        totals[10],
        totals[11],
        totals[12],
    )


def clip_layer(tokens, lengths, cotangent_of, weights, vectors, reduce, send_out):
    attention_weight, output_weight, later_weights = weights
    (first_gain, first_shift, query_bias, value_bias, output_bias, second_gain, second_shift,
     expand_bias, contract_bias) = vectors
    clip_count, frame_count, width = tokens.shape
    block_count = lengths.shape[1]
    slot_count = frame_count // block_count
    rows = clip_count * frame_count
    live = (jnp.arange(slot_count)[None, None, :] < lengths[:, :, None]).reshape(clip_count, frame_count)
    scale = HEAD ** (-0.5)
    inputs = tokens.reshape(rows, width).astype(jnp.float32)
    first_normed, first_inverse, first_act = norm_forward(inputs, first_gain, first_shift)
    mixed = jnp.dot(first_act, attention_weight, preferred_element_type=jnp.float32)
    mixed = mixed + jnp.concatenate([query_bias, jnp.zeros_like(query_bias), value_bias])
    mixed_low = mixed.astype(jnp.bfloat16).reshape(clip_count, frame_count, 3, HEADS, HEAD)
    queries = mixed_low[:, :, 0]
    keys = mixed_low[:, :, 1]
    values = mixed_low[:, :, 2]
    scores = jnp.einsum("cqhd,ckhd->chqk", queries, keys, preferred_element_type=jnp.float32) * scale
    scores = jnp.where(live[:, None, None, :], scores, NEGATIVE)
    highest = jnp.max(scores, axis=-1, keepdims=True)
    logsum = highest + jnp.log(jnp.sum(jnp.exp(scores - highest), axis=-1, keepdims=True))
    probs = jnp.exp(scores - logsum)
    expand_weight, contract_weight = later_weights(logsum[0, 0, 0, :1])
    probs_low = probs.astype(jnp.bfloat16)
    attended = jnp.einsum("chqk,ckhd->cqhd", probs_low, values, preferred_element_type=jnp.float32)
    attended_flat = attended.reshape(rows, width).astype(jnp.bfloat16)
    residual = inputs + jnp.dot(attended_flat, output_weight, preferred_element_type=jnp.float32) + output_bias
    second_normed, second_inverse, second_act = norm_forward(residual, second_gain, second_shift)
    pre = jnp.dot(second_act, expand_weight, preferred_element_type=jnp.float32) + expand_bias
    hidden_act = jax.nn.gelu(pre, approximate=False).astype(jnp.bfloat16)
    block_output = residual + jnp.dot(hidden_act, contract_weight, preferred_element_type=jnp.float32) + contract_bias
    cotangent = cotangent_of(pre[0, :1])
    error = cotangent.reshape(rows, width) * live.reshape(rows, 1).astype(jnp.float32)
    error_low = error.astype(jnp.bfloat16)
    contract_bias_grad = jnp.sum(error, axis=0)
    contract_grad = inner_rows(hidden_act, error_low)
    contract_chip = chip_sum(contract_grad)
    dpre = lax.dot_general(
        error_low, contract_weight, (((1,), (1,)), ((), ())), preferred_element_type=jnp.float32
    ) * gelu_slope(pre)
    expand_bias_grad = jnp.sum(dpre, axis=0)
    dpre_low = dpre.astype(jnp.bfloat16)
    contract_chip, dpre_low = lax.optimization_barrier((contract_chip, dpre_low))
    contract_part = shard_sum(contract_chip)
    expand_grad = inner_rows(second_act, dpre_low)
    expand_chip = chip_sum(expand_grad)
    dsecond = lax.dot_general(
        dpre_low, expand_weight, (((1,), (1,)), ((), ())), preferred_element_type=jnp.float32
    )
    second_gain_grad = jnp.sum(dsecond * second_normed, axis=0)
    second_shift_grad = jnp.sum(dsecond, axis=0)
    dresidual = error + norm_backward(dsecond, second_normed, second_inverse, second_gain)
    output_bias_grad = jnp.sum(dresidual, axis=0)
    dresidual_low = dresidual.astype(jnp.bfloat16)
    sent_output = send_out(block_output)
    expand_chip, dresidual_low = lax.optimization_barrier((expand_chip, dresidual_low))
    expand_part = shard_sum(expand_chip)
    output_grad = inner_rows(attended_flat, dresidual_low)
    output_chip = chip_sum(output_grad)
    dattended = lax.dot_general(
        dresidual_low, output_weight, (((1,), (1,)), ((), ())), preferred_element_type=jnp.float32
    ).astype(jnp.bfloat16)
    contract_part, output_chip, dattended = lax.optimization_barrier((contract_part, output_chip, dattended))
    output_part = shard_sum(output_chip)
    dattended_heads = dattended.reshape(clip_count, frame_count, HEADS, HEAD)
    attended_heads = attended_flat.reshape(clip_count, frame_count, HEADS, HEAD)
    delta = jnp.sum(
        dattended_heads.astype(jnp.float32) * attended_heads.astype(jnp.float32), axis=-1
    )
    dprob = jnp.einsum("cqhd,ckhd->chqk", dattended_heads, values, preferred_element_type=jnp.float32)
    dscore = (probs * (dprob - jnp.transpose(delta, (0, 2, 1))[:, :, :, None]) * scale).astype(jnp.bfloat16)
    dqueries = jnp.einsum("chqk,ckhd->cqhd", dscore, keys, preferred_element_type=jnp.float32)
    dkeys = jnp.einsum("chqk,cqhd->ckhd", dscore, queries, preferred_element_type=jnp.float32)
    dvalues = jnp.einsum("chqk,cqhd->ckhd", probs_low, dattended_heads, preferred_element_type=jnp.float32)
    dmixed = jnp.concatenate(
        [dqueries.reshape(rows, width), dkeys.reshape(rows, width), dvalues.reshape(rows, width)], axis=1
    )
    query_bias_grad = jnp.sum(dmixed[:, :width], axis=0)
    value_bias_grad = jnp.sum(dmixed[:, 2 * width:], axis=0)
    dmixed_low = dmixed.astype(jnp.bfloat16)
    value_grad = inner_rows(first_act, dvalues.reshape(rows, width).astype(jnp.bfloat16))
    value_part = shard_sum(chip_sum(value_grad))
    contract_total = reduce(contract_part, contract_grad.shape[0])
    output_part, value_part, expand_part, contract_total, sent_output, dmixed_low = lax.optimization_barrier(
        (output_part, value_part, expand_part, contract_total, sent_output, dmixed_low)
    )
    expand_total = reduce(expand_part, expand_grad.shape[0])
    attention_grad = inner_rows(first_act, dmixed_low[:, : 2 * width])
    dfirst = lax.optimization_barrier(lax.dot_general(
        dmixed_low, attention_weight, (((1,), (1,)), ((), ())), preferred_element_type=jnp.float32
    ))
    first_gain_grad = jnp.sum(dfirst * first_normed, axis=0)
    first_shift_grad = jnp.sum(dfirst, axis=0)
    input_grad = dresidual + norm_backward(dfirst, first_normed, first_inverse, first_gain)
    output_part, expand_total, input_grad = lax.optimization_barrier((output_part, expand_total, input_grad))
    weight_grads = (attention_grad, output_part, expand_total, contract_total, value_part)
    vector_grads = (first_gain_grad, first_shift_grad, query_bias_grad, value_bias_grad, output_bias_grad,
                    second_gain_grad, second_shift_grad, expand_bias_grad, contract_bias_grad)
    return (
        sent_output,
        input_grad,
        weight_grads,
        vector_grads,
    )


PAIR = [(0, 1), (1, 0)]
OUTER = ("outer", "inner")


def core_pick(core, first, second):
    return jnp.where(core == 0, first, second)


def gather_weight(shard_rows, extra=None):
    parts = lax.axis_size("shard")
    core = lax.axis_index("core")
    rows, width = shard_rows.shape
    half = rows // 2
    mine = lax.dynamic_slice_in_dim(shard_rows, core * half, half, axis=0)
    if extra is not None:
        mine = jnp.concatenate([mine, extra], axis=0)
    mine = lax.all_gather(mine, "shard", axis=0, tiled=False)
    other = lax.ppermute(mine, "core", PAIR)
    first = core_pick(core, mine, other)
    second = core_pick(core, other, mine)
    full = jnp.stack([first[:, :half], second[:, :half]], axis=1).reshape(parts * rows, width)
    if extra is None:
        return full, None
    return full, first[:, half:]


def chip_sum(grad, extra=None):
    parts = lax.axis_size("shard")
    core = lax.axis_index("core")
    width = grad.shape[1]
    rows = grad.shape[0] // parts
    half = rows // 2
    quarters = grad.reshape(parts, 2, half, width)
    keep = lax.dynamic_index_in_dim(quarters, core, axis=1, keepdims=False)
    send = lax.dynamic_index_in_dim(quarters, 1 - core, axis=1, keepdims=False)
    if extra is not None:
        on_first = (core == 0).astype(extra.dtype)
        keep = jnp.concatenate([keep, extra * on_first], axis=1)
        send = jnp.concatenate([send, extra * (1 - on_first)], axis=1)
    return keep + lax.ppermute(send, "core", PAIR)


def shard_sum(chip):
    part = lax.psum_scatter(chip, "shard", scatter_dimension=0, tiled=False)
    if lax.axis_size("inner") > 1:
        part = lax.psum(part, "inner")
    return part


def finish_sum(part, half):
    core = lax.axis_index("core")
    total = line_sum(part)
    other = lax.ppermute(total, "core", PAIR)
    first = core_pick(core, total, other)
    second = core_pick(core, other, total)
    return jnp.concatenate([first[:half], second[:half]], axis=0), first[half:]


def finish_many(parts, halves):
    core = lax.axis_index("core")
    flat = jnp.concatenate([part.reshape(-1) for part in parts])
    total = line_sum(flat)
    other = lax.ppermute(total, "core", PAIR)
    first = core_pick(core, total, other)
    second = core_pick(core, other, total)
    outs = []
    offset = 0
    for part, half in zip(parts, halves):
        size = part.size
        low = first[offset:offset + size].reshape(part.shape)
        high = second[offset:offset + size].reshape(part.shape)
        outs.append((jnp.concatenate([low[:half], high[:half]], axis=0), low[half:]))
        offset += size
    return outs


def reduce_weight(grad, extra=None):
    half = grad.shape[0] // lax.axis_size("shard") // 2
    return finish_sum(shard_sum(chip_sum(grad, extra)), half)


def line_sum(values):
    groups = lax.axis_size("outer")
    if groups == 1:
        return values
    if groups & (groups - 1):
        return lax.psum(values, "outer")
    here = lax.axis_index("outer")
    length = values.shape[0]
    padded = -(-length // groups) * groups
    held = jnp.pad(values, ((0, padded - length),) + ((0, 0),) * (values.ndim - 1))
    held = held.reshape((groups, padded // groups) + values.shape[1:])
    step = 1
    while step < groups:
        held = held.reshape((held.shape[0] // 2, 2) + held.shape[1:])
        bit = (here // step) % 2
        keep = lax.dynamic_index_in_dim(held, bit, axis=1, keepdims=False)
        send = lax.dynamic_index_in_dim(held, 1 - bit, axis=1, keepdims=False)
        held = keep + lax.ppermute(send, "outer", [(j, j ^ step) for j in range(groups)])
        step *= 2
    step = groups // 2
    while step >= 1:
        bit = (here // step) % 2
        other = lax.ppermute(held, "outer", [(j, j ^ step) for j in range(groups)])
        low = jnp.where(bit == 0, held, other)
        high = jnp.where(bit == 0, other, held)
        held = jnp.stack([low, high], axis=1)
        held = held.reshape((held.shape[0] * 2,) + held.shape[2:])
        step //= 2
    return held.reshape((padded,) + values.shape[1:])[:length]


def gather_packed(blocks, after=None):
    core = lax.axis_index("core")
    mine = lax.all_gather(jnp.concatenate(blocks, axis=0), "shard", axis=0, tiled=False)
    if after is not None:
        mine = mine + (after * 0).astype(mine.dtype)
    other = lax.ppermute(mine, "core", PAIR)
    return core_pick(core, mine, other), core_pick(core, other, mine)


def unpack_rows(first, second, begin, count, shape):
    parts = first.shape[0]
    rows, width = shape
    low = first[:, begin:begin + count].reshape(parts, -1, width)
    high = second[:, begin:begin + count].reshape(parts, -1, width)
    return jnp.stack([low, high], axis=1).reshape(rows, width)


def core_half(shard_rows):
    core = lax.axis_index("core")
    half = shard_rows.shape[0] // 2
    return lax.dynamic_slice_in_dim(shard_rows, core * half, half, axis=0)


def clip_local(tokens, lengths, cotangent, *params):
    clip_count, slot_count, width = tokens.shape
    parts = lax.axis_size("shard")
    place = lax.axis_index("shard")
    own = clip_count // parts
    weight_shards = params[:4]
    vector_shards = params[4:]
    wide = weight_shards[0].shape[1]
    vector_row = jnp.concatenate([entry.reshape(-1) for entry in vector_shards])
    pad = (-vector_row.shape[0]) % wide
    vector_rows = jnp.pad(vector_row, (0, pad)).reshape(-1, wide)
    attention_half = core_half(weight_shards[0])
    output_half = core_half(weight_shards[1]).reshape(-1, wide)
    first, second = gather_packed([attention_half, output_half, vector_rows])
    a_rows = attention_half.shape[0]
    o_rows = output_half.shape[0]
    attention_weight = unpack_rows(first, second, 0, a_rows, (parts * weight_shards[0].shape[0], wide))
    output_weight = unpack_rows(
        first, second, a_rows, o_rows, (parts * weight_shards[1].shape[0], weight_shards[1].shape[1])
    )
    vector_all = first[:, a_rows + o_rows:].reshape(parts, -1)[:, : vector_row.shape[0]]
    vectors = []
    offset = 0
    for entry in vector_shards:
        size = entry.shape[0]
        vectors.append(vector_all[:, offset:offset + size].reshape(parts * size).astype(jnp.float32))
        offset += size
    late = weight_shards[2].shape[1]
    expand_half = core_half(weight_shards[2])
    contract_half = core_half(weight_shards[3]).reshape(-1, late)

    def later_weights(after):
        first_b, second_b = gather_packed([expand_half, contract_half], after)
        e_rows = expand_half.shape[0]
        expand_weight = unpack_rows(first_b, second_b, 0, e_rows, (parts * weight_shards[2].shape[0], late))
        contract_weight = unpack_rows(
            first_b, second_b, e_rows, contract_half.shape[0],
            (parts * weight_shards[3].shape[0], weight_shards[3].shape[1]),
        )
        return expand_weight, contract_weight

    weights = (attention_weight, output_weight, later_weights)
    def exchange(rows):
        blocks = rows.reshape((parts, rows.shape[0] // parts) + rows.shape[1:])
        held = [lax.dynamic_index_in_dim(blocks, place, axis=0, keepdims=False)]
        for shift in range(1, parts):
            outgoing = lax.dynamic_index_in_dim(blocks, (place + shift) % parts, axis=0, keepdims=False)
            held.append(lax.ppermute(outgoing, "shard", [(i, (i + shift) % parts) for i in range(parts)]))
        stacked = jnp.stack(held[::-1], axis=0)
        doubled = jnp.concatenate([stacked, stacked], axis=0)
        start = (parts - (place + 1) % parts) % parts
        return lax.dynamic_slice_in_dim(doubled, start, parts, axis=0).reshape(rows.shape)

    def gather_rows(values, early=False):
        flat = values.reshape(clip_count * slot_count, width)
        moved = exchange(flat) if early else lax.all_to_all(flat, "shard", 0, 0, tiled=True)
        moved = moved.reshape(parts, own, slot_count, width)
        return jnp.transpose(moved, (1, 0, 2, 3)).reshape(own, parts * slot_count, width) if own > 1 else moved.reshape(own, parts * slot_count, width)

    def scatter_rows(values):
        rows = values.reshape(own, parts, slot_count, width)
        if own > 1:
            rows = jnp.transpose(rows, (1, 0, 2, 3))
        moved = lax.all_to_all(rows.reshape(own * parts * slot_count, width), "shard", 0, 0, tiled=True)
        return moved.reshape(clip_count, slot_count, width)

    tokens_clip = gather_rows(tokens, True)

    def cotangent_of(after):
        late = cotangent + (after * 0).astype(cotangent.dtype)
        return gather_rows(late)

    lengths_clip = lax.dynamic_slice_in_dim(lengths, place * own, own, axis=0)
    block_output, input_grad, weight_grads, vector_grads = clip_layer(
        tokens_clip, lengths_clip, cotangent_of, weights, vectors, lambda part, rows: finish_sum(part, rows // parts // 2)[0],
        scatter_rows,
    )
    input_grad = scatter_rows(input_grad)
    attention_grad = weight_grads[0]
    attention_width = attention_grad.shape[1]
    vector_parts = jnp.concatenate([entry.reshape(parts, -1) for entry in vector_grads], axis=1)
    vector_size = vector_parts.shape[1]
    vpad = (-vector_size) % attention_width
    vector_parts = jnp.pad(vector_parts, ((0, 0), (0, vpad))).reshape(parts, -1, attention_width)
    attention_part = shard_sum(chip_sum(attention_grad, vector_parts))
    output_part = weight_grads[1]
    value_part = weight_grads[4]
    half = attention_grad.shape[0] // parts // 2
    (qk_total, vector_total), (output_total, _), (value_total, _) = finish_many(
        [attention_part, output_part, value_part],
        [half, params[1].shape[0] // 2, half],
    )
    attention_total = jnp.concatenate([qk_total, value_total], axis=1)
    totals = (attention_total, output_total) + tuple(weight_grads[2:4])
    vector_total = vector_total.reshape(-1)[:vector_size]
    vector_outs = []
    offset = 0
    for entry in vector_shards:
        size = entry.shape[0]
        vector_outs.append(vector_total[offset:offset + size])
        offset += size
    return (block_output, input_grad) + totals + tuple(vector_outs)


def split_rep(mesh):
    devices = mesh.devices
    rep, parts = devices.shape
    first = devices[0, 0]
    stride = None
    for index in range(1, rep):
        other = devices[index, 0]
        if tuple(other.coords) == tuple(first.coords) and other.core_on_chip != first.core_on_chip:
            stride = index
            break
    if stride is None or rep % (2 * stride):
        return None
    grid = devices.reshape(rep // (2 * stride), 2, stride, parts)
    for spot in np.ndindex(grid.shape[0], grid.shape[2], grid.shape[3]):
        low = grid[spot[0], 0, spot[1], spot[2]]
        high = grid[spot[0], 1, spot[1], spot[2]]
        if tuple(low.coords) != tuple(high.coords) or low.core_on_chip == high.core_on_chip:
            return None
    return Mesh(grid, ("outer", "core", "inner", "shard"))


def solution(mesh):
    def specs(rep):
        ins = (P(rep, "shard", None), P(rep, None), P(rep, "shard", None)) + (P("shard", None),) * 4 + (
            P("shard"),
        ) * 9
        outs = (P(rep, "shard", None), P(rep, "shard", None)) + (P("shard", None),) * 4 + (P("shard"),) * 9
        return ins, outs

    ins, outs = specs("rep")
    plain = jax.shard_map(local, mesh=mesh, in_specs=ins, out_specs=outs, check_vma=False)
    split = split_rep(mesh)
    if split is None:
        return plain
    ins, outs = specs(("outer", "core", "inner"))
    fast = jax.shard_map(clip_local, mesh=split, in_specs=ins, out_specs=outs, check_vma=False)
    rep, parts = mesh.devices.shape

    def run(*args):
        if (args[0].shape[0] // rep) % parts == 0:
            return fast(*args)
        return plain(*args)

    return run
```

```python
import jax
import jax.numpy as jnp
from jax import lax
from jax.sharding import Mesh, PartitionSpec as P
import numpy as np

HEADS = 12
HEAD = 64


EPSILON = 1e-05
NEGATIVE = -1e30


def norm_forward(values, gain, shift):
    centred = values - jnp.mean(values, axis=-1, keepdims=True)
    inverse = lax.rsqrt(jnp.mean(centred * centred, axis=-1, keepdims=True) + EPSILON)
    normed = centred * inverse
    return (normed, inverse, (normed * gain + shift).astype(jnp.bfloat16))


def norm_backward(upstream, normed, inverse, gain):
    scaled = upstream * gain
    return inverse * (
        scaled
        - jnp.mean(scaled, axis=-1, keepdims=True)
        - normed * jnp.mean(scaled * normed, axis=-1, keepdims=True)
    )


def gelu_slope(values):
    return (
        0.5 * (1.0 + jax.scipy.special.erf(values * 0.7071067811865476))
        + values * jnp.exp(-0.5 * values * values) * 0.3989422804014327
    )


def inner_rows(left, right):
    return lax.dot_general(
        left, right, (((0,), (0,)), ((), ())), preferred_element_type=jnp.float32
    )


def heads_view(matrix):
    return matrix.reshape(matrix.shape[0], HEADS, HEAD)


def score_block(query_rows, key_rows, key_live):
    scores = jnp.einsum(
        "qhd,khd->hqk",
        heads_view(query_rows),
        heads_view(key_rows),
        preferred_element_type=jnp.float32,
    ) * HEAD ** (-0.5)
    return jnp.where(key_live[None, None, :], scores, NEGATIVE)


def attend_clip(items):
    query_rows, pair_rows, key_live = items
    width = query_rows.shape[1]
    scores = score_block(query_rows, pair_rows[:, :width], key_live)
    highest = jnp.max(scores, axis=-1, keepdims=True)
    logsum = highest + jnp.log(jnp.sum(jnp.exp(scores - highest), axis=-1, keepdims=True))
    probs_low = jnp.exp(scores - logsum).astype(jnp.bfloat16)
    attended = jnp.einsum(
        "hqk,khd->qhd",
        probs_low,
        heads_view(pair_rows[:, width:]),
        preferred_element_type=jnp.float32,
    )
    return (attended.reshape(query_rows.shape[0], width).astype(jnp.bfloat16), logsum[:, :, 0].T)


def score_grads(query_rows, dattended, logsum, delta, pair_rows, key_live):
    width = query_rows.shape[1]
    scores = score_block(query_rows, pair_rows[:, :width], key_live)
    probs = jnp.exp(scores - logsum.T[:, :, None])
    dprob = jnp.einsum(
        "qhd,khd->hqk",
        heads_view(dattended),
        heads_view(pair_rows[:, width:]),
        preferred_element_type=jnp.float32,
    )
    dscore = (probs * (dprob - delta.T[:, :, None]) * HEAD ** (-0.5)).astype(jnp.bfloat16)
    return (probs.astype(jnp.bfloat16), dscore)


def both_grads(items):
    query_rows, dattended, logsum, delta, pair_rows, key_live = items
    width = query_rows.shape[1]
    probs_low, dscore = score_grads(query_rows, dattended, logsum, delta, pair_rows, key_live)
    dqueries = jnp.einsum(
        "hqk,khd->qhd", dscore, heads_view(pair_rows[:, :width]), preferred_element_type=jnp.float32
    ).reshape(query_rows.shape[0], width)
    dkeys = jnp.einsum(
        "hqk,qhd->khd", dscore, heads_view(query_rows), preferred_element_type=jnp.float32
    )
    dvalues = jnp.einsum(
        "hqk,qhd->khd", probs_low, heads_view(dattended), preferred_element_type=jnp.float32
    )
    key_count = pair_rows.shape[0]
    return (
        dqueries,
        jnp.concatenate(
            [dkeys.reshape(key_count, width), dvalues.reshape(key_count, width)], axis=1
        ),
    )


def local(
    tokens,
    lengths,
    cotangent,
    attention_weight,
    output_weight,
    expand_weight,
    contract_weight,
    first_gain,
    first_shift,
    query_bias,
    value_bias,
    output_bias,
    second_gain,
    second_shift,
    expand_bias,
    contract_bias,
):
    clip_count, slot_count, width = tokens.shape
    parts = lax.axis_size("shard")
    frame_count = slot_count * parts
    place = lax.axis_index("shard")
    row_total = clip_count * slot_count
    gathered = (
        lax.all_gather(attention_weight, "shard", axis=0, tiled=True),
        lax.all_gather(output_weight, "shard", axis=0, tiled=True),
        lax.all_gather(expand_weight, "shard", axis=0, tiled=True),
        lax.all_gather(contract_weight, "shard", axis=0, tiled=True),
        lax.all_gather(first_gain, "shard", axis=0, tiled=True),
        lax.all_gather(first_shift, "shard", axis=0, tiled=True),
        lax.all_gather(query_bias, "shard", axis=0, tiled=True),
        lax.all_gather(value_bias, "shard", axis=0, tiled=True),
        lax.all_gather(output_bias, "shard", axis=0, tiled=True),
        lax.all_gather(second_gain, "shard", axis=0, tiled=True),
        lax.all_gather(second_shift, "shard", axis=0, tiled=True),
        lax.all_gather(expand_bias, "shard", axis=0, tiled=True),
        lax.all_gather(contract_bias, "shard", axis=0, tiled=True),
    )
    vectors = [entry.astype(jnp.float32) for entry in gathered[4:]]
    own_length = jnp.sum(jnp.where(jnp.arange(parts)[None, :] == place, lengths, 0), axis=1)
    row_live = jnp.arange(slot_count)[None, :] < own_length[:, None]
    key_live = (jnp.arange(slot_count)[None, None, :] < lengths[:, :, None]).reshape(
        clip_count, frame_count
    )
    inputs = tokens.reshape(row_total, width).astype(jnp.float32)
    first_normed, first_inverse, first_act = norm_forward(inputs, vectors[0], vectors[1])
    mixed = jnp.dot(first_act, gathered[0], preferred_element_type=jnp.float32)
    mixed = mixed + jnp.concatenate([vectors[2], jnp.zeros_like(vectors[2]), vectors[3]])
    mixed_low = mixed.astype(jnp.bfloat16)
    query_rows = mixed_low[:, :width].reshape(clip_count, slot_count, width)
    pair_own = mixed_low[:, width:].reshape(clip_count, slot_count, 2 * width)
    pair_all = lax.all_gather(pair_own, "shard", axis=1, tiled=True)
    attended, logsum = lax.map(attend_clip, (query_rows, pair_all, key_live))
    attended_flat = attended.reshape(row_total, width)
    residual = (
        inputs
        + jnp.dot(attended_flat, gathered[1], preferred_element_type=jnp.float32)
        + vectors[4]
    )
    second_normed, second_inverse, second_act = norm_forward(residual, vectors[5], vectors[6])
    pre = jnp.dot(second_act, gathered[2], preferred_element_type=jnp.float32) + vectors[7]
    hidden_act = jax.nn.gelu(pre, approximate=False).astype(jnp.bfloat16)
    block_output = (
        residual + jnp.dot(hidden_act, gathered[3], preferred_element_type=jnp.float32) + vectors[8]
    )
    backward = (
        lax.all_gather(attention_weight, "shard", axis=0, tiled=True),
        lax.all_gather(output_weight, "shard", axis=0, tiled=True),
        lax.all_gather(expand_weight, "shard", axis=0, tiled=True),
        lax.all_gather(contract_weight, "shard", axis=0, tiled=True),
        lax.all_gather(first_gain, "shard", axis=0, tiled=True),
        lax.all_gather(first_shift, "shard", axis=0, tiled=True),
        lax.all_gather(query_bias, "shard", axis=0, tiled=True),
        lax.all_gather(value_bias, "shard", axis=0, tiled=True),
        lax.all_gather(output_bias, "shard", axis=0, tiled=True),
        lax.all_gather(second_gain, "shard", axis=0, tiled=True),
        lax.all_gather(second_shift, "shard", axis=0, tiled=True),
        lax.all_gather(expand_bias, "shard", axis=0, tiled=True),
        lax.all_gather(contract_bias, "shard", axis=0, tiled=True),
    )
    back_vectors = [entry.astype(jnp.float32) for entry in backward[4:]]
    error = cotangent.reshape(row_total, width) * row_live.reshape(row_total, 1).astype(jnp.float32)
    error_low = error.astype(jnp.bfloat16)
    contract_bias_grad = jnp.sum(error, axis=0)
    contract_grad = inner_rows(hidden_act, error_low)
    dpre = lax.dot_general(
        error_low, backward[3], (((1,), (1,)), ((), ())), preferred_element_type=jnp.float32
    ) * gelu_slope(pre)
    expand_bias_grad = jnp.sum(dpre, axis=0)
    dpre_low = dpre.astype(jnp.bfloat16)
    expand_grad = inner_rows(second_act, dpre_low)
    dsecond = lax.dot_general(
        dpre_low, backward[2], (((1,), (1,)), ((), ())), preferred_element_type=jnp.float32
    )
    second_gain_grad = jnp.sum(dsecond * second_normed, axis=0)
    second_shift_grad = jnp.sum(dsecond, axis=0)
    dresidual = error + norm_backward(dsecond, second_normed, second_inverse, back_vectors[5])
    output_bias_grad = jnp.sum(dresidual, axis=0)
    dresidual_low = dresidual.astype(jnp.bfloat16)
    output_grad = inner_rows(attended_flat, dresidual_low)
    dattended = lax.dot_general(
        dresidual_low, backward[1], (((1,), (1,)), ((), ())), preferred_element_type=jnp.float32
    ).astype(jnp.bfloat16)
    delta = jnp.sum(
        heads_view(dattended.astype(jnp.float32)) * heads_view(attended_flat.astype(jnp.float32)),
        axis=-1,
    )
    delta = delta.reshape(clip_count, slot_count, HEADS)
    dattended_clips = dattended.reshape(clip_count, slot_count, width)
    dqueries, pair_terms = lax.map(
        both_grads, (query_rows, dattended_clips, logsum, delta, pair_all, key_live)
    )
    pair_grads = lax.psum_scatter(pair_terms, "shard", scatter_dimension=1, tiled=True)
    dqueries_flat = dqueries.reshape(row_total, width)
    pair_flat = pair_grads.reshape(row_total, 2 * width)
    dmixed = jnp.concatenate([dqueries_flat, pair_flat], axis=1)
    query_bias_grad = jnp.sum(dqueries_flat, axis=0)
    value_bias_grad = jnp.sum(pair_flat[:, width:], axis=0)
    dmixed_low = dmixed.astype(jnp.bfloat16)
    attention_grad = inner_rows(first_act, dmixed_low)
    dfirst = lax.dot_general(
        dmixed_low, backward[0], (((1,), (1,)), ((), ())), preferred_element_type=jnp.float32
    )
    first_gain_grad = jnp.sum(dfirst * first_normed, axis=0)
    first_shift_grad = jnp.sum(dfirst, axis=0)
    input_grad = dresidual + norm_backward(dfirst, first_normed, first_inverse, back_vectors[0])
    shares = (
        lax.psum_scatter(attention_grad, "shard", scatter_dimension=0, tiled=True),
        lax.psum_scatter(output_grad, "shard", scatter_dimension=0, tiled=True),
        lax.psum_scatter(expand_grad, "shard", scatter_dimension=0, tiled=True),
        lax.psum_scatter(contract_grad, "shard", scatter_dimension=0, tiled=True),
        lax.psum_scatter(first_gain_grad, "shard", scatter_dimension=0, tiled=True),
        lax.psum_scatter(first_shift_grad, "shard", scatter_dimension=0, tiled=True),
        lax.psum_scatter(query_bias_grad, "shard", scatter_dimension=0, tiled=True),
        lax.psum_scatter(value_bias_grad, "shard", scatter_dimension=0, tiled=True),
        lax.psum_scatter(output_bias_grad, "shard", scatter_dimension=0, tiled=True),
        lax.psum_scatter(second_gain_grad, "shard", scatter_dimension=0, tiled=True),
        lax.psum_scatter(second_shift_grad, "shard", scatter_dimension=0, tiled=True),
        lax.psum_scatter(expand_bias_grad, "shard", scatter_dimension=0, tiled=True),
        lax.psum_scatter(contract_bias_grad, "shard", scatter_dimension=0, tiled=True),
    )
    totals = lax.psum(
        (
            shares[0],
            shares[1],
            shares[2],
            shares[3],
            shares[4],
            shares[5],
            shares[6],
            shares[7],
            shares[8],
            shares[9],
            shares[10],
            shares[11],
            shares[12],
        ),
        "rep",
    )
    return (
        block_output.reshape(clip_count, slot_count, width),
        input_grad.reshape(clip_count, slot_count, width),
        totals[0],
        totals[1],
        totals[2],
        totals[3],
        totals[4],
        totals[5],
        totals[6],
        totals[7],
        totals[8],
        totals[9],
        totals[10],
        totals[11],
        totals[12],
    )


def clip_layer(tokens, lengths, cotangent_of, weights, vectors, reduce, send_out):
    attention_weight, output_weight, later_weights = weights
    (first_gain, first_shift, query_bias, value_bias, output_bias, second_gain, second_shift,
     expand_bias, contract_bias) = vectors
    clip_count, frame_count, width = tokens.shape
    block_count = lengths.shape[1]
    slot_count = frame_count // block_count
    rows = clip_count * frame_count
    live = (jnp.arange(slot_count)[None, None, :] < lengths[:, :, None]).reshape(clip_count, frame_count)
    scale = HEAD ** (-0.5)
    inputs = tokens.reshape(rows, width).astype(jnp.float32)
    first_normed, first_inverse, first_act = norm_forward(inputs, first_gain, first_shift)
    mixed = jnp.dot(first_act, attention_weight, preferred_element_type=jnp.float32)
    mixed = mixed + jnp.concatenate([query_bias, jnp.zeros_like(query_bias), value_bias])
    mixed_low = mixed.astype(jnp.bfloat16).reshape(clip_count, frame_count, 3, HEADS, HEAD)
    queries = mixed_low[:, :, 0]
    keys = mixed_low[:, :, 1]
    values = mixed_low[:, :, 2]
    scores = jnp.einsum("cqhd,ckhd->chqk", queries, keys, preferred_element_type=jnp.float32) * scale
    scores = jnp.where(live[:, None, None, :], scores, NEGATIVE)
    highest = jnp.max(scores, axis=-1, keepdims=True)
    logsum = highest + jnp.log(jnp.sum(jnp.exp(scores - highest), axis=-1, keepdims=True))
    probs = jnp.exp(scores - logsum)
    expand_weight, contract_weight = later_weights(logsum[0, 0, 0, :1])
    probs_low = probs.astype(jnp.bfloat16)
    attended = jnp.einsum("chqk,ckhd->cqhd", probs_low, values, preferred_element_type=jnp.float32)
    attended_flat = attended.reshape(rows, width).astype(jnp.bfloat16)
    residual = inputs + jnp.dot(attended_flat, output_weight, preferred_element_type=jnp.float32) + output_bias
    second_normed, second_inverse, second_act = norm_forward(residual, second_gain, second_shift)
    pre = jnp.dot(second_act, expand_weight, preferred_element_type=jnp.float32) + expand_bias
    hidden_act = jax.nn.gelu(pre, approximate=False).astype(jnp.bfloat16)
    block_output = residual + jnp.dot(hidden_act, contract_weight, preferred_element_type=jnp.float32) + contract_bias
    cotangent = cotangent_of(pre[0, :1])
    error = cotangent.reshape(rows, width) * live.reshape(rows, 1).astype(jnp.float32)
    error_low = error.astype(jnp.bfloat16)
    contract_bias_grad = jnp.sum(error, axis=0)
    contract_grad = inner_rows(hidden_act, error_low)
    contract_chip = chip_sum(contract_grad)
    dpre = lax.dot_general(
        error_low, contract_weight, (((1,), (1,)), ((), ())), preferred_element_type=jnp.float32
    ) * gelu_slope(pre)
    expand_bias_grad = jnp.sum(dpre, axis=0)
    dpre_low = dpre.astype(jnp.bfloat16)
    contract_chip, dpre_low = lax.optimization_barrier((contract_chip, dpre_low))
    contract_part = shard_sum(contract_chip)
    expand_grad = inner_rows(second_act, dpre_low)
    expand_chip = chip_sum(expand_grad)
    dsecond = lax.dot_general(
        dpre_low, expand_weight, (((1,), (1,)), ((), ())), preferred_element_type=jnp.float32
    )
    second_gain_grad = jnp.sum(dsecond * second_normed, axis=0)
    second_shift_grad = jnp.sum(dsecond, axis=0)
    dresidual = error + norm_backward(dsecond, second_normed, second_inverse, second_gain)
    output_bias_grad = jnp.sum(dresidual, axis=0)
    dresidual_low = dresidual.astype(jnp.bfloat16)
    sent_output = send_out(block_output)
    expand_chip, dresidual_low = lax.optimization_barrier((expand_chip, dresidual_low))
    expand_part = shard_sum(expand_chip)
    output_grad = inner_rows(attended_flat, dresidual_low)
    output_chip = chip_sum(output_grad)
    dattended = lax.dot_general(
        dresidual_low, output_weight, (((1,), (1,)), ((), ())), preferred_element_type=jnp.float32
    ).astype(jnp.bfloat16)
    contract_part, output_chip, dattended = lax.optimization_barrier((contract_part, output_chip, dattended))
    output_part = shard_sum(output_chip)
    dattended_heads = dattended.reshape(clip_count, frame_count, HEADS, HEAD)
    attended_heads = attended_flat.reshape(clip_count, frame_count, HEADS, HEAD)
    delta = jnp.sum(
        dattended_heads.astype(jnp.float32) * attended_heads.astype(jnp.float32), axis=-1
    )
    dprob = jnp.einsum("cqhd,ckhd->chqk", dattended_heads, values, preferred_element_type=jnp.float32)
    dscore = (probs * (dprob - jnp.transpose(delta, (0, 2, 1))[:, :, :, None]) * scale).astype(jnp.bfloat16)
    dqueries = jnp.einsum("chqk,ckhd->cqhd", dscore, keys, preferred_element_type=jnp.float32)
    dkeys = jnp.einsum("chqk,cqhd->ckhd", dscore, queries, preferred_element_type=jnp.float32)
    dvalues = jnp.einsum("chqk,cqhd->ckhd", probs_low, dattended_heads, preferred_element_type=jnp.float32)
    dmixed = jnp.concatenate(
        [dqueries.reshape(rows, width), dkeys.reshape(rows, width), dvalues.reshape(rows, width)], axis=1
    )
    query_bias_grad = jnp.sum(dmixed[:, :width], axis=0)
    value_bias_grad = jnp.sum(dmixed[:, 2 * width:], axis=0)
    dmixed_low = dmixed.astype(jnp.bfloat16)
    contract_total = reduce(contract_part, contract_grad.shape[0])
    output_part, expand_part, contract_total, sent_output, dmixed_low = lax.optimization_barrier(
        (output_part, expand_part, contract_total, sent_output, dmixed_low)
    )
    expand_total = reduce(expand_part, expand_grad.shape[0])
    attention_grad = inner_rows(first_act, dmixed_low)
    dfirst = lax.optimization_barrier(lax.dot_general(
        dmixed_low, attention_weight, (((1,), (1,)), ((), ())), preferred_element_type=jnp.float32
    ))
    first_gain_grad = jnp.sum(dfirst * first_normed, axis=0)
    first_shift_grad = jnp.sum(dfirst, axis=0)
    input_grad = dresidual + norm_backward(dfirst, first_normed, first_inverse, first_gain)
    output_part, expand_total, input_grad = lax.optimization_barrier((output_part, expand_total, input_grad))
    weight_grads = (attention_grad, output_part, expand_total, contract_total)
    vector_grads = (first_gain_grad, first_shift_grad, query_bias_grad, value_bias_grad, output_bias_grad,
                    second_gain_grad, second_shift_grad, expand_bias_grad, contract_bias_grad)
    return (
        sent_output,
        input_grad,
        weight_grads,
        vector_grads,
    )


PAIR = [(0, 1), (1, 0)]
OUTER = ("outer", "inner")


def core_pick(core, first, second):
    return jnp.where(core == 0, first, second)


def gather_weight(shard_rows, extra=None):
    parts = lax.axis_size("shard")
    core = lax.axis_index("core")
    rows, width = shard_rows.shape
    half = rows // 2
    mine = lax.dynamic_slice_in_dim(shard_rows, core * half, half, axis=0)
    if extra is not None:
        mine = jnp.concatenate([mine, extra], axis=0)
    mine = lax.all_gather(mine, "shard", axis=0, tiled=False)
    other = lax.ppermute(mine, "core", PAIR)
    first = core_pick(core, mine, other)
    second = core_pick(core, other, mine)
    full = jnp.stack([first[:, :half], second[:, :half]], axis=1).reshape(parts * rows, width)
    if extra is None:
        return full, None
    return full, first[:, half:]


def chip_sum(grad, extra=None):
    parts = lax.axis_size("shard")
    core = lax.axis_index("core")
    width = grad.shape[1]
    rows = grad.shape[0] // parts
    half = rows // 2
    quarters = grad.reshape(parts, 2, half, width)
    keep = lax.dynamic_index_in_dim(quarters, core, axis=1, keepdims=False)
    send = lax.dynamic_index_in_dim(quarters, 1 - core, axis=1, keepdims=False)
    if extra is not None:
        on_first = (core == 0).astype(extra.dtype)
        keep = jnp.concatenate([keep, extra * on_first], axis=1)
        send = jnp.concatenate([send, extra * (1 - on_first)], axis=1)
    return keep + lax.ppermute(send, "core", PAIR)


def shard_sum(chip):
    part = lax.psum_scatter(chip.astype(jnp.bfloat16), "shard", scatter_dimension=0, tiled=False)
    part = part.astype(jnp.float32)
    if lax.axis_size("inner") > 1:
        part = lax.psum(part, "inner")
    return part


def finish_sum(part, half):
    core = lax.axis_index("core")
    total = line_sum(part)
    other = lax.ppermute(total, "core", PAIR)
    first = core_pick(core, total, other)
    second = core_pick(core, other, total)
    return jnp.concatenate([first[:half], second[:half]], axis=0), first[half:]


def finish_many(parts, halves):
    core = lax.axis_index("core")
    flat = jnp.concatenate([part.reshape(-1) for part in parts])
    total = line_sum(flat)
    other = lax.ppermute(total, "core", PAIR)
    first = core_pick(core, total, other)
    second = core_pick(core, other, total)
    outs = []
    offset = 0
    for part, half in zip(parts, halves):
        size = part.size
        low = first[offset:offset + size].reshape(part.shape)
        high = second[offset:offset + size].reshape(part.shape)
        outs.append((jnp.concatenate([low[:half], high[:half]], axis=0), low[half:]))
        offset += size
    return outs


def reduce_weight(grad, extra=None):
    half = grad.shape[0] // lax.axis_size("shard") // 2
    return finish_sum(shard_sum(chip_sum(grad, extra)), half)


def line_sum(values):
    groups = lax.axis_size("outer")
    if groups == 1:
        return values
    if groups & (groups - 1):
        return lax.psum(values, "outer")
    here = lax.axis_index("outer")
    length = values.shape[0]
    padded = -(-length // groups) * groups
    held = jnp.pad(values, ((0, padded - length),) + ((0, 0),) * (values.ndim - 1))
    held = held.reshape((groups, padded // groups) + values.shape[1:])
    step = 1
    while step < groups:
        held = held.reshape((held.shape[0] // 2, 2) + held.shape[1:])
        bit = (here // step) % 2
        keep = lax.dynamic_index_in_dim(held, bit, axis=1, keepdims=False)
        send = lax.dynamic_index_in_dim(held, 1 - bit, axis=1, keepdims=False)
        held = keep + lax.ppermute(send, "outer", [(j, j ^ step) for j in range(groups)])
        step *= 2
    step = groups // 2
    while step >= 1:
        bit = (here // step) % 2
        other = lax.ppermute(held, "outer", [(j, j ^ step) for j in range(groups)])
        low = jnp.where(bit == 0, held, other)
        high = jnp.where(bit == 0, other, held)
        held = jnp.stack([low, high], axis=1)
        held = held.reshape((held.shape[0] * 2,) + held.shape[2:])
        step //= 2
    return held.reshape((padded,) + values.shape[1:])[:length]


def gather_packed(blocks, after=None):
    core = lax.axis_index("core")
    mine = lax.all_gather(jnp.concatenate(blocks, axis=0), "shard", axis=0, tiled=False)
    if after is not None:
        mine = mine + (after * 0).astype(mine.dtype)
    other = lax.ppermute(mine, "core", PAIR)
    return core_pick(core, mine, other), core_pick(core, other, mine)


def unpack_rows(first, second, begin, count, shape):
    parts = first.shape[0]
    rows, width = shape
    low = first[:, begin:begin + count].reshape(parts, -1, width)
    high = second[:, begin:begin + count].reshape(parts, -1, width)
    return jnp.stack([low, high], axis=1).reshape(rows, width)


def core_half(shard_rows):
    core = lax.axis_index("core")
    half = shard_rows.shape[0] // 2
    return lax.dynamic_slice_in_dim(shard_rows, core * half, half, axis=0)


def clip_local(tokens, lengths, cotangent, *params):
    clip_count, slot_count, width = tokens.shape
    parts = lax.axis_size("shard")
    place = lax.axis_index("shard")
    own = clip_count // parts
    weight_shards = params[:4]
    vector_shards = params[4:]
    wide = weight_shards[0].shape[1]
    vector_row = jnp.concatenate([entry.reshape(-1) for entry in vector_shards])
    pad = (-vector_row.shape[0]) % wide
    vector_rows = jnp.pad(vector_row, (0, pad)).reshape(-1, wide)
    attention_half = core_half(weight_shards[0])
    output_half = core_half(weight_shards[1]).reshape(-1, wide)
    first, second = gather_packed([attention_half, output_half, vector_rows])
    a_rows = attention_half.shape[0]
    o_rows = output_half.shape[0]
    attention_weight = unpack_rows(first, second, 0, a_rows, (parts * weight_shards[0].shape[0], wide))
    output_weight = unpack_rows(
        first, second, a_rows, o_rows, (parts * weight_shards[1].shape[0], weight_shards[1].shape[1])
    )
    vector_all = first[:, a_rows + o_rows:].reshape(parts, -1)[:, : vector_row.shape[0]]
    vectors = []
    offset = 0
    for entry in vector_shards:
        size = entry.shape[0]
        vectors.append(vector_all[:, offset:offset + size].reshape(parts * size).astype(jnp.float32))
        offset += size
    late = weight_shards[2].shape[1]
    expand_half = core_half(weight_shards[2])
    contract_half = core_half(weight_shards[3]).reshape(-1, late)

    def later_weights(after):
        first_b, second_b = gather_packed([expand_half, contract_half], after)
        e_rows = expand_half.shape[0]
        expand_weight = unpack_rows(first_b, second_b, 0, e_rows, (parts * weight_shards[2].shape[0], late))
        contract_weight = unpack_rows(
            first_b, second_b, e_rows, contract_half.shape[0],
            (parts * weight_shards[3].shape[0], weight_shards[3].shape[1]),
        )
        return expand_weight, contract_weight

    weights = (attention_weight, output_weight, later_weights)
    def exchange(rows):
        blocks = rows.reshape((parts, rows.shape[0] // parts) + rows.shape[1:])
        held = [lax.dynamic_index_in_dim(blocks, place, axis=0, keepdims=False)]
        for shift in range(1, parts):
            outgoing = lax.dynamic_index_in_dim(blocks, (place + shift) % parts, axis=0, keepdims=False)
            held.append(lax.ppermute(outgoing, "shard", [(i, (i + shift) % parts) for i in range(parts)]))
        stacked = jnp.stack(held[::-1], axis=0)
        doubled = jnp.concatenate([stacked, stacked], axis=0)
        start = (parts - (place + 1) % parts) % parts
        return lax.dynamic_slice_in_dim(doubled, start, parts, axis=0).reshape(rows.shape)

    def gather_rows(values, early=False):
        flat = values.reshape(clip_count * slot_count, width)
        moved = exchange(flat) if early else lax.all_to_all(flat, "shard", 0, 0, tiled=True)
        moved = moved.reshape(parts, own, slot_count, width)
        return jnp.transpose(moved, (1, 0, 2, 3)).reshape(own, parts * slot_count, width) if own > 1 else moved.reshape(own, parts * slot_count, width)

    def scatter_rows(values):
        rows = values.reshape(own, parts, slot_count, width)
        if own > 1:
            rows = jnp.transpose(rows, (1, 0, 2, 3))
        moved = lax.all_to_all(rows.reshape(own * parts * slot_count, width), "shard", 0, 0, tiled=True)
        return moved.reshape(clip_count, slot_count, width)

    tokens_clip = gather_rows(tokens, True)

    def cotangent_of(after):
        late = cotangent + (after * 0).astype(cotangent.dtype)
        return gather_rows(late)

    lengths_clip = lax.dynamic_slice_in_dim(lengths, place * own, own, axis=0)
    block_output, input_grad, weight_grads, vector_grads = clip_layer(
        tokens_clip, lengths_clip, cotangent_of, weights, vectors, lambda part, rows: finish_sum(part, rows // parts // 2)[0],
        scatter_rows,
    )
    input_grad = scatter_rows(input_grad)
    attention_grad = weight_grads[0]
    attention_width = attention_grad.shape[1]
    vector_parts = jnp.concatenate([entry.reshape(parts, -1) for entry in vector_grads], axis=1)
    vector_size = vector_parts.shape[1]
    vpad = (-vector_size) % attention_width
    vector_parts = jnp.pad(vector_parts, ((0, 0), (0, vpad))).reshape(parts, -1, attention_width)
    attention_part = shard_sum(chip_sum(attention_grad, vector_parts))
    output_part = weight_grads[1]
    (attention_total, vector_total), (output_total, _) = finish_many(
        [attention_part, output_part],
        [attention_grad.shape[0] // parts // 2, params[1].shape[0] // 2],
    )
    totals = (attention_total, output_total) + tuple(weight_grads[2:])
    vector_total = vector_total.reshape(-1)[:vector_size]
    vector_outs = []
    offset = 0
    for entry in vector_shards:
        size = entry.shape[0]
        vector_outs.append(vector_total[offset:offset + size])
        offset += size
    return (block_output, input_grad) + totals + tuple(vector_outs)


def split_rep(mesh):
    devices = mesh.devices
    rep, parts = devices.shape
    first = devices[0, 0]
    stride = None
    for index in range(1, rep):
        other = devices[index, 0]
        if tuple(other.coords) == tuple(first.coords) and other.core_on_chip != first.core_on_chip:
            stride = index
            break
    if stride is None or rep % (2 * stride):
        return None
    grid = devices.reshape(rep // (2 * stride), 2, stride, parts)
    for spot in np.ndindex(grid.shape[0], grid.shape[2], grid.shape[3]):
        low = grid[spot[0], 0, spot[1], spot[2]]
        high = grid[spot[0], 1, spot[1], spot[2]]
        if tuple(low.coords) != tuple(high.coords) or low.core_on_chip == high.core_on_chip:
            return None
    return Mesh(grid, ("outer", "core", "inner", "shard"))


def solution(mesh):
    def specs(rep):
        ins = (P(rep, "shard", None), P(rep, None), P(rep, "shard", None)) + (P("shard", None),) * 4 + (
            P("shard"),
        ) * 9
        outs = (P(rep, "shard", None), P(rep, "shard", None)) + (P("shard", None),) * 4 + (P("shard"),) * 9
        return ins, outs

    ins, outs = specs("rep")
    plain = jax.shard_map(local, mesh=mesh, in_specs=ins, out_specs=outs, check_vma=False)
    split = split_rep(mesh)
    if split is None:
        return plain
    ins, outs = specs(("outer", "core", "inner"))
    fast = jax.shard_map(clip_local, mesh=split, in_specs=ins, out_specs=outs, check_vma=False)
    rep, parts = mesh.devices.shape

    def run(*args):
        if (args[0].shape[0] // rep) % parts == 0:
            return fast(*args)
        return plain(*args)

    return run
```
